32 devices in a mesh: region: 2 (over y), tile: 4 (over z), corner: 2 (over x), kern: 2 (over core).
Axes of the slice: x: 2, y: 2, z: 4, core: 2. Of those that a mesh axis runs over, the one named last changes fastest.
Arguments:
- tile_mask: bfloat16 [16, 256, 256], P(('region', 'tile')), parts along dimension 0, may hold values from -1 to 1
- master_mask: bfloat16 [8, 256, 256], P(('region', 'tile')), parts along dimension 0, may hold values from -1 to 1
- target: bfloat16 [16, 256, 256], P(('region', 'tile')), parts along dimension 0, may hold values from 0 to 1
- inst_master: int32 [16], P(('region', 'tile')), parts along dimension 0, may hold values from 0 to 3, as said below
- inst_shift: int32 [16, 2], P(('region', 'tile')), parts along dimension 0, may hold values from 0 to 255
- kernels: float32 [2, 12, 2, 32, 32], P('corner'), may hold values from -24 to 24
- kernel_weight: float32 [2, 12], P('corner'), may hold values from 0.05 to 1
- corner_dose: float32 [2], P('corner'), may hold values from 0.6 to 1.6
Outputs:
- tile_grad: float32 [16, 256, 256], P(('region', 'tile')), parts along dimension 0
- master_grad: float32 [8, 256, 256], P(('region', 'tile')), parts along dimension 0
The draws below stay inside these ranges and needn't reach their ends.
There are 2 independent parts, one for each index of `region`. The reference program is written for one: setup_inputs(seed, part) draws one part's arguments, and reference() takes and returns one part's arrays. A program takes and returns all parts, laid end to end along the dimension named above; an argument that names none is the same for every part. Nothing has to cross between parts.
Inputs may be any that keep to these rules, and one draw needn't show every extreme that they name: `inst_master`: each master cell is placed in exactly 2 tiles.
All inputs are finite; a program needn't handle non-finite values.
Results may differ from the reference program's by a relative error of at most 0.0003.
Values may be sent and summed in bfloat16 or wider, within the bound.
No kernel may reach another device: no remote copies, remote signals or barrier semaphores. Data moves between devices by JAX's collectives and lax.ppermute only.
A program may use at most 64 MiB of HBM per device.

```python
import math
import jax
import jax.numpy as jnp
from jax import lax

P_SIZE = 256
B = 32
KERNELS = 12
TILE_DEV = 2
TILES = 8
MASTERS = 4
CORNERS = 2


def draw_inst_master(key, part):
    keys = jax.random.split(jax.random.fold_in(key, 17), TILE_DEV)
    perms = jax.vmap(lambda one: jax.random.permutation(one, MASTERS))(keys)
    return jnp.transpose(perms).reshape(-1).astype(jnp.int32)


def plant(result, stream_key, low, high):
    longest = result.shape.index(max(result.shape))
    spots = []
    for shift in (0, 1):
        where = [jax.random.randint(jax.random.fold_in(stream_key, axis), (), 0, length) for axis, length in enumerate(result.shape)]
        where[longest] = (where[longest] + shift) % result.shape[longest]
        spots.append(tuple(where))
    return result.at[spots[0]].set(low).at[spots[1]].set(high)


def steps_of(own_key, extent, shards, smallest, top_value):
    gain, own = 1.0, jax.random.fold_in(own_key, 6)
    for position, blocks in shards:
        heights = jnp.exp(jax.random.uniform(jax.random.fold_in(own, position), (blocks,), jnp.float32, smallest / len(shards), top_value / len(shards)))
        gain = gain * jnp.repeat(heights, extent[position] // blocks).reshape([-1 if axis == position else 1 for axis in range(len(extent))])
    return gain


def normal_values(key, shape, width, limit, cuts=(), kind=jnp.bfloat16):
    result = jax.random.normal(key, shape, jnp.float32) * width
    if len(cuts) > 0:
        result = steps_of(key, shape, cuts, -0.22, 0.18) * result
    return jnp.clip(result, min=-limit, max=limit).astype(kind)


def setup_inputs(seed: int = 0, part: int = 0) -> dict:
    seeds = jax.random.split(jax.random.key(seed), 9)
    own_keys = jax.random.split(jax.random.fold_in(seeds[8], part), 9)
    return {
        "tile_mask": jnp.clip(jax.random.uniform(own_keys[0], (TILES, P_SIZE, P_SIZE), jnp.float32, -1.0, 1.0) * steps_of(own_keys[0], (TILES, P_SIZE, P_SIZE), ((0, 4),), -0.4, 0.0), -1.0, 1.0).astype(jnp.bfloat16),
        "master_mask": jnp.clip(jax.random.uniform(own_keys[1], (MASTERS, P_SIZE, P_SIZE), jnp.float32, -1.0, 1.0) * steps_of(own_keys[1], (MASTERS, P_SIZE, P_SIZE), ((0, 4),), -0.4, 0.0), -1.0, 1.0).astype(jnp.bfloat16),
        "target": jnp.clip(1.0 * jax.random.uniform(own_keys[2], (TILES, P_SIZE, P_SIZE), jnp.float32) ** steps_of(own_keys[2], (TILES, P_SIZE, P_SIZE), ((0, 4),), -0.2, 0.2), 0.0, 1.0).astype(jnp.bfloat16),
        "inst_master": draw_inst_master(jax.random.fold_in(jax.random.fold_in(seeds[8], part), 71), part),
        "inst_shift": plant(jax.random.randint(own_keys[4], (TILES, 2), 0, P_SIZE), jax.random.fold_in(own_keys[4], 1), 0, P_SIZE - 1).astype(jnp.int32),
        "kernels": normal_values(seeds[5], (CORNERS, KERNELS, 2, B, B), 4.0, 24.0, ((0, 2),), jnp.float32),
        "kernel_weight": jnp.clip(jnp.exp(math.log(1.0) - 2.9957323 * jax.random.uniform(seeds[6], (CORNERS, KERNELS), jnp.float32) ** steps_of(seeds[6], (CORNERS, KERNELS), ((0, 2),), -0.2, 0.2)), 0.05, 1.0),
        "corner_dose": jnp.clip(jnp.exp(math.log(1.6) - 0.98082923 * jax.random.uniform(seeds[7], (CORNERS,), jnp.float32) ** steps_of(seeds[7], (CORNERS,), ((0, 2),), -0.2, 0.2)), 0.6, 1.6),
    }


precise = lax.Precision.HIGHEST
steepness = 3.0
threshold = 1.0


def band_tables():
    freq = jnp.arange(B, dtype=jnp.int32) - B // 2
    pixel = jnp.arange(P_SIZE, dtype=jnp.int32)
    angle = (2.0 * math.pi / P_SIZE) * jnp.mod(freq[:, None] * pixel[None, :], P_SIZE).astype(jnp.float32)
    return jnp.cos(angle), -jnp.sin(angle)


def phase_ramp(shift):
    freq = jnp.arange(B, dtype=jnp.int32) - B // 2
    total = freq[None, :, None] * shift[:, 0][:, None, None] + freq[None, None, :] * shift[:, 1][:, None, None]
    angle = (2.0 * math.pi / P_SIZE) * jnp.mod(total, P_SIZE).astype(jnp.float32)
    return jnp.cos(angle), -jnp.sin(angle)


def spectra(masks, cos_tab, sin_tab):
    rows_re = jnp.einsum("bx,nxy->nby", cos_tab, masks, precision=precise)
    rows_im = jnp.einsum("bx,nxy->nby", sin_tab, masks, precision=precise)
    spec_re = jnp.einsum("nby,cy->nbc", rows_re, cos_tab, precision=precise) - jnp.einsum("nby,cy->nbc", rows_im, sin_tab, precision=precise)
    spec_im = jnp.einsum("nby,cy->nbc", rows_re, sin_tab, precision=precise) + jnp.einsum("nby,cy->nbc", rows_im, cos_tab, precision=precise)
    return spec_re, spec_im


def to_field(x_re, x_im, cos_tab, sin_tab, scale):
    half_re = jnp.einsum("bx,nbc->nxc", cos_tab, x_re, precision=precise) + jnp.einsum("bx,nbc->nxc", sin_tab, x_im, precision=precise)
    half_im = jnp.einsum("bx,nbc->nxc", cos_tab, x_im, precision=precise) - jnp.einsum("bx,nbc->nxc", sin_tab, x_re, precision=precise)
    out_re = (jnp.einsum("nxc,cy->nxy", half_re, cos_tab, precision=precise) + jnp.einsum("nxc,cy->nxy", half_im, sin_tab, precision=precise)) * scale
    out_im = (jnp.einsum("nxc,cy->nxy", half_im, cos_tab, precision=precise) - jnp.einsum("nxc,cy->nxy", half_re, sin_tab, precision=precise)) * scale
    return out_re, out_im


def back_pixels(x_re, x_im, cos_tab, sin_tab):
    half_re = jnp.einsum("bx,nbc->nxc", cos_tab, x_re, precision=precise) + jnp.einsum("bx,nbc->nxc", sin_tab, x_im, precision=precise)
    half_im = jnp.einsum("bx,nbc->nxc", cos_tab, x_im, precision=precise) - jnp.einsum("bx,nbc->nxc", sin_tab, x_re, precision=precise)
    return jnp.einsum("nxc,cy->nxy", half_re, cos_tab, precision=precise) + jnp.einsum("nxc,cy->nxy", half_im, sin_tab, precision=precise)


def adjoint(g_re, g_im, cos_tab, sin_tab, scale):
    mid_re = jnp.einsum("bx,nxy->nby", cos_tab, g_re, precision=precise) - jnp.einsum("bx,nxy->nby", sin_tab, g_im, precision=precise)
    mid_im = jnp.einsum("bx,nxy->nby", cos_tab, g_im, precision=precise) + jnp.einsum("bx,nxy->nby", sin_tab, g_re, precision=precise)
    out_re = (jnp.einsum("nby,cy->nbc", mid_re, cos_tab, precision=precise) - jnp.einsum("nby,cy->nbc", mid_im, sin_tab, precision=precise)) * scale
    out_im = (jnp.einsum("nby,cy->nbc", mid_re, sin_tab, precision=precise) + jnp.einsum("nby,cy->nbc", mid_im, cos_tab, precision=precise)) * scale
    return out_re, out_im


def one_tile(spec_re, spec_im, goal, kern_re, kern_im, weights, dose, cos_tab, sin_tab):
    scale = 1.0 / (P_SIZE * P_SIZE)

    def forward(total, item):
        h_re, h_im, weight = item
        x_re = h_re * spec_re - h_im * spec_im
        x_im = h_re * spec_im + h_im * spec_re
        f_re, f_im = to_field(x_re, x_im, cos_tab, sin_tab, scale)
        return total + weight * (f_re * f_re + f_im * f_im), (f_re, f_im)

    start = jnp.zeros((1, P_SIZE, P_SIZE), jnp.float32)
    intensity, fields = lax.scan(forward, start, (kern_re, kern_im, weights))
    resist = jax.nn.sigmoid(steepness * (dose * intensity - threshold))
    sens = 2.0 * (resist - goal) * resist * (1.0 - resist) * steepness * dose

    def backward(acc, item):
        h_re, h_im, weight, f_re, f_im = item
        g_re = 2.0 * weight * sens * f_re
        g_im = 2.0 * weight * sens * f_im
        x_re, x_im = adjoint(g_re, g_im, cos_tab, sin_tab, scale)
        return (acc[0] + h_re * x_re + h_im * x_im, acc[1] + h_re * x_im - h_im * x_re), None

    zero = jnp.zeros((1, B, B), jnp.float32)
    grads, unused = lax.scan(backward, (zero, zero), (kern_re, kern_im, weights, fields[0], fields[1]))
    return grads


def reference(tile_mask, master_mask, target, inst_master, inst_shift, kernels, kernel_weight, corner_dose):
    cos_tab, sin_tab = band_tables()
    tile_re, tile_im = spectra(tile_mask.astype(jnp.float32), cos_tab, sin_tab)
    mast_re, mast_im = spectra(master_mask.astype(jnp.float32), cos_tab, sin_tab)
    ph_re, ph_im = phase_ramp(inst_shift)
    sel_re = mast_re[inst_master]
    sel_im = mast_im[inst_master]
    spec_re = tile_re + (ph_re * sel_re - ph_im * sel_im)
    spec_im = tile_im + (ph_re * sel_im + ph_im * sel_re)
    goal_all = target.astype(jnp.float32)
    grad_re = jnp.zeros((TILES, B, B), jnp.float32)
    grad_im = jnp.zeros((TILES, B, B), jnp.float32)
    for corner in range(CORNERS):
        kern_re = kernels[corner, :, 0]
        kern_im = kernels[corner, :, 1]
        weights = kernel_weight[corner]
        dose = corner_dose[corner]

        def per_tile(item):
            s_re, s_im, goal = item
            out = one_tile(s_re[None], s_im[None], goal[None], kern_re, kern_im, weights, dose, cos_tab, sin_tab)
            return out[0][0], out[1][0]

        part_re, part_im = lax.map(per_tile, (spec_re, spec_im, goal_all))
        grad_re = grad_re + part_re
        grad_im = grad_im + part_im
    tile_grad = back_pixels(grad_re, grad_im, cos_tab, sin_tab)
    back_re = ph_re * grad_re + ph_im * grad_im
    back_im = ph_re * grad_im - ph_im * grad_re
    msum_re = jax.ops.segment_sum(back_re, inst_master, num_segments=MASTERS)
    msum_im = jax.ops.segment_sum(back_im, inst_master, num_segments=MASTERS)
    master_grad = back_pixels(msum_re, msum_im, cos_tab, sin_tab)
    return tile_grad, master_grad
```

```python
import math

import numpy as np
import jax
import jax.numpy as jnp
from jax import lax
from jax.sharding import PartitionSpec as P

P_SIZE = 256
B = 32


precise = lax.Precision.HIGHEST
steepness = 3.0
threshold = 1.0


def band_tables():
    freq = np.arange(B, dtype=np.int64) - B // 2
    pixel = np.arange(P_SIZE, dtype=np.int64)
    angle = (2.0 * math.pi / P_SIZE) * np.mod(freq[:, None] * pixel[None, :], P_SIZE).astype(np.float64)
    return (jnp.asarray(np.cos(angle), jnp.float32), jnp.asarray(-np.sin(angle), jnp.float32))


def phase_ramp(shift):
    freq = jnp.arange(B, dtype=jnp.int32) - B // 2
    total = (
        freq[None, :, None] * shift[:, 0][:, None, None]
        + freq[None, None, :] * shift[:, 1][:, None, None]
    )
    angle = 2.0 * math.pi / P_SIZE * jnp.mod(total, P_SIZE).astype(jnp.float32)
    return (jnp.cos(angle), -jnp.sin(angle))


def spectra(masks, cos_tab, sin_tab):
    rows_re = jnp.einsum("bx,nxy->nby", cos_tab, masks, precision=precise)
    rows_im = jnp.einsum("bx,nxy->nby", sin_tab, masks, precision=precise)
    spec_re = jnp.einsum("nby,cy->nbc", rows_re, cos_tab, precision=precise) - jnp.einsum(
        "nby,cy->nbc", rows_im, sin_tab, precision=precise
    )
    spec_im = jnp.einsum("nby,cy->nbc", rows_re, sin_tab, precision=precise) + jnp.einsum(
        "nby,cy->nbc", rows_im, cos_tab, precision=precise
    )
    return (spec_re, spec_im)


def back_pixels(x_re, x_im, cos_tab, sin_tab):
    half_re = jnp.einsum("bx,nbc->nxc", cos_tab, x_re, precision=precise) + jnp.einsum(
        "bx,nbc->nxc", sin_tab, x_im, precision=precise
    )
    half_im = jnp.einsum("bx,nbc->nxc", cos_tab, x_im, precision=precise) - jnp.einsum(
        "bx,nbc->nxc", sin_tab, x_re, precision=precise
    )
    return jnp.einsum("nxc,cy->nxy", half_re, cos_tab, precision=precise) + jnp.einsum(
        "nxc,cy->nxy", half_im, sin_tab, precision=precise
    )


def on_device(
    tile_mask, master_mask, target, inst_master, inst_shift, kernels, kernel_weight, corner_dose
):
    cos_tab, sin_tab = band_tables()
    scale = 1.0 / (P_SIZE * P_SIZE)
    local_tiles = tile_mask.shape[0]
    local_masters = master_mask.shape[0]
    tile_count = lax.axis_size("tile")
    tile_pos = lax.axis_index("tile")
    kern_count = lax.axis_size("kern")
    kern_pos = lax.axis_index("kern")
    per_dev = local_tiles // kern_count
    first = kern_pos * per_dev
    region_tiles = tile_count * local_tiles
    region_masters = tile_count * local_masters

    with jax.named_scope("master_spectra"):
        own_re, own_im = spectra(master_mask.astype(jnp.float32), cos_tab, sin_tab)
        own = jnp.stack([own_re, own_im], axis=1)
        every = lax.all_gather(own, "tile", axis=0, tiled=True)

    with jax.named_scope("tile_spectra"):
        mine_mask = lax.dynamic_slice_in_dim(tile_mask, first, per_dev, 0)
        goal = lax.dynamic_slice_in_dim(target, first, per_dev, 0).astype(jnp.float32)
        mine_master = lax.dynamic_slice_in_dim(inst_master, first, per_dev, 0)
        mine_shift = lax.dynamic_slice_in_dim(inst_shift, first, per_dev, 0)
        tile_re, tile_im = spectra(mine_mask.astype(jnp.float32), cos_tab, sin_tab)
        ph_re, ph_im = phase_ramp(mine_shift)
        pick = (mine_master[:, None] == jnp.arange(region_masters, dtype=jnp.int32)[None, :]).astype(
            jnp.float32
        )
        sel = jnp.sum(pick[:, :, None, None, None] * every[None], axis=1)
        sel_re = sel[:, 0]
        sel_im = sel[:, 1]
        spec_re = tile_re + (ph_re * sel_re - ph_im * sel_im)
        spec_im = tile_im + (ph_re * sel_im + ph_im * sel_re)

    dose = corner_dose[0]
    h_re = kernels[0, :, 0]
    h_im = kernels[0, :, 1]
    weights = kernel_weight[0]

    with jax.named_scope("forward_fields"):
        x_re = h_re[:, None] * spec_re[None] - h_im[:, None] * spec_im[None]
        x_im = h_re[:, None] * spec_im[None] + h_im[:, None] * spec_re[None]
        half_re = jnp.einsum("bx,knbc->knxc", cos_tab, x_re, precision=precise) + jnp.einsum(
            "bx,knbc->knxc", sin_tab, x_im, precision=precise
        )
        half_im = jnp.einsum("bx,knbc->knxc", cos_tab, x_im, precision=precise) - jnp.einsum(
            "bx,knbc->knxc", sin_tab, x_re, precision=precise
        )
        f_re = (
            jnp.einsum("knxc,cy->knxy", half_re, cos_tab, precision=precise)
            + jnp.einsum("knxc,cy->knxy", half_im, sin_tab, precision=precise)
        ) * scale
        f_im = (
            jnp.einsum("knxc,cy->knxy", half_im, cos_tab, precision=precise)
            - jnp.einsum("knxc,cy->knxy", half_re, sin_tab, precision=precise)
        ) * scale

    with jax.named_scope("resist_sensitivity"):
        intensity = jnp.sum(weights[:, None, None, None] * (f_re * f_re + f_im * f_im), axis=0)
        resist = jax.nn.sigmoid(steepness * (dose * intensity - threshold))
        sens = 2.0 * (resist - goal) * resist * (1.0 - resist) * steepness * dose

    with jax.named_scope("adjoint_spectra"):
        g_re = (2.0 * weights)[:, None, None, None] * sens[None] * f_re
        g_im = (2.0 * weights)[:, None, None, None] * sens[None] * f_im
        mid_re = jnp.einsum("knxy,cy->knxc", g_re, cos_tab, precision=precise) - jnp.einsum(
            "knxy,cy->knxc", g_im, sin_tab, precision=precise
        )
        mid_im = jnp.einsum("knxy,cy->knxc", g_re, sin_tab, precision=precise) + jnp.einsum(
            "knxy,cy->knxc", g_im, cos_tab, precision=precise
        )
        out_re = (
            jnp.einsum("bx,knxc->knbc", cos_tab, mid_re, precision=precise)
            - jnp.einsum("bx,knxc->knbc", sin_tab, mid_im, precision=precise)
        ) * scale
        out_im = (
            jnp.einsum("bx,knxc->knbc", cos_tab, mid_im, precision=precise)
            + jnp.einsum("bx,knxc->knbc", sin_tab, mid_re, precision=precise)
        ) * scale
        grad_re = jnp.sum(h_re[:, None] * out_re + h_im[:, None] * out_im, axis=0)
        grad_im = jnp.sum(h_re[:, None] * out_im - h_im[:, None] * out_re, axis=0)

    with jax.named_scope("gradient_exchange"):
        back_re = ph_re * grad_re + ph_im * grad_im
        back_im = ph_re * grad_im - ph_im * grad_re
        tile_slot = tile_pos * local_tiles + first + jnp.arange(per_dev, dtype=jnp.int32)
        tile_pick = (
            tile_slot[:, None] == jnp.arange(region_tiles, dtype=jnp.int32)[None, :]
        ).astype(jnp.float32)
        own_grad = jnp.stack([grad_re, grad_im], axis=1)
        own_back = jnp.stack([back_re, back_im], axis=1)
        tile_part = jnp.sum(tile_pick[:, :, None, None, None] * own_grad[:, None], axis=0)
        master_part = jnp.sum(pick[:, :, None, None, None] * own_back[:, None], axis=0)
        slots = jnp.concatenate([tile_part, master_part], axis=0)
        summed = lax.psum(slots, ("tile", "corner", "kern"))
        mine_tiles = lax.dynamic_slice_in_dim(summed, tile_pos * local_tiles, local_tiles, 0)
        mine_masters = lax.dynamic_slice_in_dim(
            summed, region_tiles + tile_pos * local_masters, local_masters, 0
        )

    with jax.named_scope("pixel_gradients"):
        tile_grad = back_pixels(mine_tiles[:, 0], mine_tiles[:, 1], cos_tab, sin_tab)
        master_grad = back_pixels(mine_masters[:, 0], mine_masters[:, 1], cos_tab, sin_tab)
    return (tile_grad, master_grad)


def solution(mesh):
    return jax.shard_map(
        on_device,
        mesh=mesh,
        in_specs=(
            P(("region", "tile"), None, None),
            P(("region", "tile"), None, None),
            P(("region", "tile"), None, None),
            P(("region", "tile")),
            P(("region", "tile"), None),
            P("corner", None, None, None, None),
            P("corner", None),
            P("corner"),
        ),
        out_specs=(P(("region", "tile"), None, None), P(("region", "tile"), None, None)),
        check_vma=False,
    )
```

```python
import math

import numpy as np
import jax
import jax.numpy as jnp
from jax import lax
from jax.sharding import PartitionSpec as P

P_SIZE = 256
B = 32


precise = lax.Precision.HIGHEST
steepness = 3.0
threshold = 1.0


def band_tables():
    freq = np.arange(B, dtype=np.int64) - B // 2
    pixel = np.arange(P_SIZE, dtype=np.int64)
    angle = (2.0 * math.pi / P_SIZE) * np.mod(freq[:, None] * pixel[None, :], P_SIZE).astype(np.float64)
    return (jnp.asarray(np.cos(angle), jnp.float32), jnp.asarray(-np.sin(angle), jnp.float32))


def phase_ramp(shift):
    freq = jnp.arange(B, dtype=jnp.int32) - B // 2
    total = (
        freq[None, :, None] * shift[:, 0][:, None, None]
        + freq[None, None, :] * shift[:, 1][:, None, None]
    )
    angle = 2.0 * math.pi / P_SIZE * jnp.mod(total, P_SIZE).astype(jnp.float32)
    return (jnp.cos(angle), -jnp.sin(angle))


def spectra(masks, cos_tab, sin_tab):
    rows_re = jnp.einsum("bx,nxy->nby", cos_tab, masks, precision=precise)
    rows_im = jnp.einsum("bx,nxy->nby", sin_tab, masks, precision=precise)
    spec_re = jnp.einsum("nby,cy->nbc", rows_re, cos_tab, precision=precise) - jnp.einsum(
        "nby,cy->nbc", rows_im, sin_tab, precision=precise
    )
    spec_im = jnp.einsum("nby,cy->nbc", rows_re, sin_tab, precision=precise) + jnp.einsum(
        "nby,cy->nbc", rows_im, cos_tab, precision=precise
    )
    return (spec_re, spec_im)


def back_pixels(x_re, x_im, cos_tab, sin_tab):
    half_re = jnp.einsum("bx,nbc->nxc", cos_tab, x_re, precision=precise) + jnp.einsum(
        "bx,nbc->nxc", sin_tab, x_im, precision=precise
    )
    half_im = jnp.einsum("bx,nbc->nxc", cos_tab, x_im, precision=precise) - jnp.einsum(
        "bx,nbc->nxc", sin_tab, x_re, precision=precise
    )
    return jnp.einsum("nxc,cy->nxy", half_re, cos_tab, precision=precise) + jnp.einsum(
        "nxc,cy->nxy", half_im, sin_tab, precision=precise
    )


def xor_partners(count):
    return count & (count - 1) == 0 and count <= 8


def gather_all(x, axis, count, pos):
    if not xor_partners(count):
        return lax.all_gather(x, axis, axis=0, tiled=True)
    size = x.shape[0]
    slot = jnp.arange(count * size, dtype=jnp.int32) // size
    total = jnp.where((slot == pos)[:, None, None, None], jnp.tile(x, (count, 1, 1, 1)), 0.0)
    for step in range(1, count):
        got = lax.ppermute(x, axis, [(i, i ^ step) for i in range(count)])
        hit = (slot == (pos ^ step))[:, None, None, None]
        total = total + jnp.where(hit, jnp.tile(got, (count, 1, 1, 1)), 0.0)
    return total


def sum_all(x, axis, count, pos):
    if not xor_partners(count):
        return lax.psum(x, axis)
    step = 1
    while step < count:
        x = x + lax.ppermute(x, axis, [(i, i ^ step) for i in range(count)])
        step *= 2
    return x


def scatter_sum(x, axis, count, pos, size):
    if not xor_partners(count):
        return lax.psum_scatter(x, axis, scatter_dimension=0, tiled=True)
    total = lax.dynamic_slice_in_dim(x, pos * size, size, 0)
    for step in range(1, count):
        part = lax.dynamic_slice_in_dim(x, (pos ^ step) * size, size, 0)
        total = total + lax.ppermute(part, axis, [(i, i ^ step) for i in range(count)])
    return total


def on_device(
    tile_mask, master_mask, target, inst_master, inst_shift, kernels, kernel_weight, corner_dose
):
    cos_tab, sin_tab = band_tables()
    scale = 1.0 / (P_SIZE * P_SIZE)
    local_tiles = tile_mask.shape[0]
    local_masters = master_mask.shape[0]
    tile_count = lax.axis_size("tile")
    tile_pos = lax.axis_index("tile")
    kern_count = lax.axis_size("kern")
    kern_pos = lax.axis_index("kern")
    per_dev = local_tiles // kern_count
    first = kern_pos * per_dev
    region_tiles = tile_count * local_tiles
    region_masters = tile_count * local_masters

    with jax.named_scope("master_spectra"):
        own_re, own_im = spectra(master_mask.astype(jnp.float32), cos_tab, sin_tab)
        own = jnp.stack([own_re, own_im], axis=1)
        every = gather_all(own, "tile", tile_count, tile_pos)

    with jax.named_scope("tile_spectra"):
        mine_mask = lax.dynamic_slice_in_dim(tile_mask, first, per_dev, 0)
        goal = lax.dynamic_slice_in_dim(target, first, per_dev, 0).astype(jnp.float32)
        mine_master = lax.dynamic_slice_in_dim(inst_master, first, per_dev, 0)
        mine_shift = lax.dynamic_slice_in_dim(inst_shift, first, per_dev, 0)
        tile_re, tile_im = spectra(mine_mask.astype(jnp.float32), cos_tab, sin_tab)
        ph_re, ph_im = phase_ramp(mine_shift)
        pick = (mine_master[:, None] == jnp.arange(region_masters, dtype=jnp.int32)[None, :]).astype(
            jnp.float32
        )
        sel = jnp.sum(pick[:, :, None, None, None] * every[None], axis=1)
        sel_re = sel[:, 0]
        sel_im = sel[:, 1]
        spec_re = tile_re + (ph_re * sel_re - ph_im * sel_im)
        spec_im = tile_im + (ph_re * sel_im + ph_im * sel_re)

    dose = corner_dose[0]
    h_re = kernels[0, :, 0]
    h_im = kernels[0, :, 1]
    weights = kernel_weight[0]

    with jax.named_scope("forward_fields"):
        x_re = h_re[:, None] * spec_re[None] - h_im[:, None] * spec_im[None]
        x_im = h_re[:, None] * spec_im[None] + h_im[:, None] * spec_re[None]
        half_re = jnp.einsum("bx,knbc->knxc", cos_tab, x_re, precision=precise) + jnp.einsum(
            "bx,knbc->knxc", sin_tab, x_im, precision=precise
        )
        half_im = jnp.einsum("bx,knbc->knxc", cos_tab, x_im, precision=precise) - jnp.einsum(
            "bx,knbc->knxc", sin_tab, x_re, precision=precise
        )
        f_re = (
            jnp.einsum("knxc,cy->knxy", half_re, cos_tab, precision=precise)
            + jnp.einsum("knxc,cy->knxy", half_im, sin_tab, precision=precise)
        ) * scale
        f_im = (
            jnp.einsum("knxc,cy->knxy", half_im, cos_tab, precision=precise)
            - jnp.einsum("knxc,cy->knxy", half_re, sin_tab, precision=precise)
        ) * scale

    with jax.named_scope("resist_sensitivity"):
        intensity = jnp.sum(weights[:, None, None, None] * (f_re * f_re + f_im * f_im), axis=0)
        resist = jax.nn.sigmoid(steepness * (dose * intensity - threshold))
        sens = 2.0 * (resist - goal) * resist * (1.0 - resist) * steepness * dose

    with jax.named_scope("adjoint_spectra"):
        g_re = (2.0 * weights)[:, None, None, None] * sens[None] * f_re
        g_im = (2.0 * weights)[:, None, None, None] * sens[None] * f_im
        mid_re = jnp.einsum("knxy,cy->knxc", g_re, cos_tab, precision=precise) - jnp.einsum(
            "knxy,cy->knxc", g_im, sin_tab, precision=precise
        )
        mid_im = jnp.einsum("knxy,cy->knxc", g_re, sin_tab, precision=precise) + jnp.einsum(
            "knxy,cy->knxc", g_im, cos_tab, precision=precise
        )
        out_re = (
            jnp.einsum("bx,knxc->knbc", cos_tab, mid_re, precision=precise)
            - jnp.einsum("bx,knxc->knbc", sin_tab, mid_im, precision=precise)
        ) * scale
        out_im = (
            jnp.einsum("bx,knxc->knbc", cos_tab, mid_im, precision=precise)
            + jnp.einsum("bx,knxc->knbc", sin_tab, mid_re, precision=precise)
        ) * scale
        grad_re = jnp.sum(h_re[:, None] * out_re + h_im[:, None] * out_im, axis=0)
        grad_im = jnp.sum(h_re[:, None] * out_im - h_im[:, None] * out_re, axis=0)

    with jax.named_scope("gradient_exchange"):
        own_grad = jnp.stack([grad_re, grad_im], axis=1)
        both = gather_all(own_grad, "kern", kern_count, kern_pos)
        corner_count = lax.axis_size("corner")
        mine_tiles = sum_all(both, "corner", corner_count, lax.axis_index("corner"))
        all_re, all_im = phase_ramp(inst_shift)
        back_re = all_re * mine_tiles[:, 0] + all_im * mine_tiles[:, 1]
        back_im = all_re * mine_tiles[:, 1] - all_im * mine_tiles[:, 0]
        own_back = jnp.stack([back_re, back_im], axis=1)
        owner_pick = (
            inst_master[:, None] == jnp.arange(region_masters, dtype=jnp.int32)[None, :]
        ).astype(jnp.float32)
        terms = jnp.sum(owner_pick[:, :, None, None, None] * own_back[:, None], axis=0)
        mine_masters = scatter_sum(terms, "tile", tile_count, tile_pos, local_masters)

    with jax.named_scope("pixel_gradients"):
        tile_grad = back_pixels(mine_tiles[:, 0], mine_tiles[:, 1], cos_tab, sin_tab)
        master_grad = back_pixels(mine_masters[:, 0], mine_masters[:, 1], cos_tab, sin_tab)
    return (tile_grad, master_grad)


def solution(mesh):
    return jax.shard_map(
        on_device,
        mesh=mesh,
        in_specs=(
            P(("region", "tile"), None, None),
            P(("region", "tile"), None, None),
            P(("region", "tile"), None, None),
            P(("region", "tile")),
            P(("region", "tile"), None),
            P("corner", None, None, None, None),
            P("corner", None),
            P("corner"),
        ),
        out_specs=(P(("region", "tile"), None, None), P(("region", "tile"), None, None)),
        check_vma=False,
    )
```

```python
import math

import numpy as np
import jax
import jax.numpy as jnp
from jax import lax
from jax.sharding import PartitionSpec as P
from jax.experimental import pallas as pl
from jax.experimental.pallas import tpu as pltpu

P_SIZE = 256
B = 32


precise = lax.Precision.HIGHEST
steepness = 3.0
threshold = 1.0


def band_tables():
    freq = np.arange(B, dtype=np.int64) - B // 2
    pixel = np.arange(P_SIZE, dtype=np.int64)
    angle = (2.0 * math.pi / P_SIZE) * np.mod(freq[:, None] * pixel[None, :], P_SIZE).astype(np.float64)
    return (jnp.asarray(np.cos(angle), jnp.float32), jnp.asarray(-np.sin(angle), jnp.float32))


def phase_ramp(shift):
    freq = jnp.arange(B, dtype=jnp.int32) - B // 2
    total = (
        freq[None, :, None] * shift[:, 0][:, None, None]
        + freq[None, None, :] * shift[:, 1][:, None, None]
    )
    angle = 2.0 * math.pi / P_SIZE * jnp.mod(total, P_SIZE).astype(jnp.float32)
    return (jnp.cos(angle), -jnp.sin(angle))


def spectra(masks, cos_tab, sin_tab):
    rows_re = jnp.einsum("bx,nxy->nby", cos_tab, masks, precision=precise)
    rows_im = jnp.einsum("bx,nxy->nby", sin_tab, masks, precision=precise)
    spec_re = jnp.einsum("nby,cy->nbc", rows_re, cos_tab, precision=precise) - jnp.einsum(
        "nby,cy->nbc", rows_im, sin_tab, precision=precise
    )
    spec_im = jnp.einsum("nby,cy->nbc", rows_re, sin_tab, precision=precise) + jnp.einsum(
        "nby,cy->nbc", rows_im, cos_tab, precision=precise
    )
    return (spec_re, spec_im)


def back_pixels(x_re, x_im, cos_tab, sin_tab):
    half_re = jnp.einsum("bx,nbc->nxc", cos_tab, x_re, precision=precise) + jnp.einsum(
        "bx,nbc->nxc", sin_tab, x_im, precision=precise
    )
    half_im = jnp.einsum("bx,nbc->nxc", cos_tab, x_im, precision=precise) - jnp.einsum(
        "bx,nbc->nxc", sin_tab, x_re, precision=precise
    )
    return jnp.einsum("nxc,cy->nxy", half_re, cos_tab, precision=precise) + jnp.einsum(
        "nxc,cy->nxy", half_im, sin_tab, precision=precise
    )


def split_bf16(a):
    hi = a.astype(jnp.bfloat16)
    lo = (a - hi.astype(jnp.float32)).astype(jnp.bfloat16)
    return hi, lo


def dot3(a, b_hi, b_lo):
    a_hi, a_lo = split_bf16(a)
    out = jnp.dot(a_hi, b_hi, preferred_element_type=jnp.float32)
    out = out + jnp.dot(a_hi, b_lo, preferred_element_type=jnp.float32)
    return out + jnp.dot(a_lo, b_hi, preferred_element_type=jnp.float32)


def dot3_left(a_hi, a_lo, b):
    b_hi, b_lo = split_bf16(b)
    out = jnp.dot(a_hi, b_hi, preferred_element_type=jnp.float32)
    out = out + jnp.dot(a_hi, b_lo, preferred_element_type=jnp.float32)
    return out + jnp.dot(a_lo, b_hi, preferred_element_type=jnp.float32)


def imaging_tables():
    freq = np.arange(B, dtype=np.int64) - B // 2
    pixel = np.arange(P_SIZE, dtype=np.int64)
    angle = (2.0 * math.pi / P_SIZE) * np.mod(freq[:, None] * pixel[None, :], P_SIZE).astype(np.float64)
    c_re = np.cos(angle)
    c_im = -np.sin(angle)
    scale = 1.0 / (P_SIZE * P_SIZE)
    right_w = np.zeros((128, 2 * P_SIZE))
    right_w[:B, :P_SIZE] = c_re
    right_w[:B, P_SIZE:] = -c_im
    right_w[B : 2 * B, :P_SIZE] = c_im
    right_w[B : 2 * B, P_SIZE:] = c_re
    left_a = np.zeros((P_SIZE, 128))
    left_a[:, :B] = c_re.T * scale
    left_a[:, B : 2 * B] = -c_im.T * scale
    right_b = np.zeros((2 * P_SIZE, 128))
    right_b[:P_SIZE, :B] = c_re.T * scale
    right_b[:P_SIZE, B : 2 * B] = c_im.T * scale
    right_b[P_SIZE:, :B] = -c_im.T * scale
    right_b[P_SIZE:, B : 2 * B] = c_re.T * scale
    out = []
    for table in (right_w, left_a, right_b):
        hi = table.astype(jnp.bfloat16)
        lo = (table - hi.astype(np.float64)).astype(jnp.bfloat16)
        out += [jnp.asarray(hi), jnp.asarray(lo)]
    return out


def imaging_body(
    x_ref, goal_ref, w_ref, dose_ref, rw_hi, rw_lo, la_hi, la_lo, rb_hi, rb_lo, u_ref, w_buf, f_buf, i_buf
):
    count = f_buf.shape[0]
    w_buf[...] = dot3(x_ref[...], rw_hi[...], rw_lo[...])
    i_buf[...] = jnp.zeros(i_buf.shape, jnp.float32)
    pad = jnp.zeros((128 - 2 * B, 2 * P_SIZE), jnp.float32)

    def forward(k, carry):
        rows = w_buf[pl.ds(pl.multiple_of(k * B, B), B), :]
        swap = jnp.concatenate([-rows[:, P_SIZE:], rows[:, :P_SIZE]], axis=1)
        stacked = jnp.concatenate([rows, swap, pad], axis=0)
        field = dot3_left(la_hi[...], la_lo[...], stacked)
        f_buf[k] = field
        power = field * field
        i_buf[...] += w_ref[k] * (power[:, :P_SIZE] + power[:, P_SIZE:])
        return carry

    lax.fori_loop(0, count, forward, 0)
    dose = dose_ref[0]
    resist = 1.0 / (1.0 + jnp.exp(-(steepness * (dose * i_buf[...] - threshold))))
    sens = 2.0 * (resist - goal_ref[...]) * resist * (1.0 - resist) * steepness * dose
    i_buf[...] = sens

    def backward(k, carry):
        sens = i_buf[...]
        weighted = f_buf[k] * jnp.concatenate([sens, sens], axis=1)
        u_ref[k] = dot3(weighted, rb_hi[...], rb_lo[...])
        return carry

    lax.fori_loop(0, count, backward, 0)


def imaging(x_cat, goal, weights, dose):
    count = weights.shape[0]
    tables = imaging_tables()
    vmem = pl.BlockSpec(memory_space=pltpu.VMEM)
    smem = pl.BlockSpec(memory_space=pltpu.SMEM)
    return pl.pallas_call(
        imaging_body,
        out_shape=jax.ShapeDtypeStruct((count, P_SIZE, 128), jnp.float32),
        in_specs=[vmem, vmem, smem, smem] + [vmem] * 6,
        out_specs=vmem,
        scratch_shapes=[
            pltpu.VMEM((count * B, 2 * P_SIZE), jnp.float32),
            pltpu.VMEM((count, P_SIZE, 2 * P_SIZE), jnp.float32),
            pltpu.VMEM((P_SIZE, P_SIZE), jnp.float32),
        ],
    )(x_cat, goal, weights, dose, *tables)


def xor_partners(count):
    return count & (count - 1) == 0 and count <= 8


def gather_all(x, axis, count, pos):
    if not xor_partners(count):
        return lax.all_gather(x, axis, axis=0, tiled=True)
    size = x.shape[0]
    slot = jnp.arange(count * size, dtype=jnp.int32) // size
    total = jnp.where((slot == pos)[:, None, None, None], jnp.tile(x, (count, 1, 1, 1)), 0.0)
    for step in range(1, count):
        got = lax.ppermute(x, axis, [(i, i ^ step) for i in range(count)])
        hit = (slot == (pos ^ step))[:, None, None, None]
        total = total + jnp.where(hit, jnp.tile(got, (count, 1, 1, 1)), 0.0)
    return total


def sum_all(x, axis, count, pos):
    if not xor_partners(count):
        return lax.psum(x, axis)
    step = 1
    while step < count:
        x = x + lax.ppermute(x, axis, [(i, i ^ step) for i in range(count)])
        step *= 2
    return x


def scatter_sum(x, axis, count, pos, size):
    if not xor_partners(count):
        return lax.psum_scatter(x, axis, scatter_dimension=0, tiled=True)
    total = lax.dynamic_slice_in_dim(x, pos * size, size, 0)
    for step in range(1, count):
        part = lax.dynamic_slice_in_dim(x, (pos ^ step) * size, size, 0)
        total = total + lax.ppermute(part, axis, [(i, i ^ step) for i in range(count)])
    return total


def on_device(
    tile_mask, master_mask, target, inst_master, inst_shift, kernels, kernel_weight, corner_dose
):
    cos_tab, sin_tab = band_tables()
    scale = 1.0 / (P_SIZE * P_SIZE)
    local_tiles = tile_mask.shape[0]
    local_masters = master_mask.shape[0]
    tile_count = lax.axis_size("tile")
    tile_pos = lax.axis_index("tile")
    kern_count = lax.axis_size("kern")
    kern_pos = lax.axis_index("kern")
    per_dev = local_tiles // kern_count
    first = kern_pos * per_dev
    region_tiles = tile_count * local_tiles
    region_masters = tile_count * local_masters

    with jax.named_scope("master_spectra"):
        own_re, own_im = spectra(master_mask.astype(jnp.float32), cos_tab, sin_tab)
        own = jnp.stack([own_re, own_im], axis=1)
        every = gather_all(own, "tile", tile_count, tile_pos)

    with jax.named_scope("tile_spectra"):
        mine_mask = lax.dynamic_slice_in_dim(tile_mask, first, per_dev, 0)
        goal = lax.dynamic_slice_in_dim(target, first, per_dev, 0).astype(jnp.float32)
        mine_master = lax.dynamic_slice_in_dim(inst_master, first, per_dev, 0)
        mine_shift = lax.dynamic_slice_in_dim(inst_shift, first, per_dev, 0)
        tile_re, tile_im = spectra(mine_mask.astype(jnp.float32), cos_tab, sin_tab)
        ph_re, ph_im = phase_ramp(mine_shift)
        pick = (mine_master[:, None] == jnp.arange(region_masters, dtype=jnp.int32)[None, :]).astype(
            jnp.float32
        )
        sel = jnp.sum(pick[:, :, None, None, None] * every[None], axis=1)
        sel_re = sel[:, 0]
        sel_im = sel[:, 1]
        spec_re = tile_re + (ph_re * sel_re - ph_im * sel_im)
        spec_im = tile_im + (ph_re * sel_im + ph_im * sel_re)

    dose = corner_dose[0]
    h_re = kernels[0, :, 0]
    h_im = kernels[0, :, 1]
    weights = kernel_weight[0]

    with jax.named_scope("imaging_kernel"):
        x_re = h_re[:, None] * spec_re[None] - h_im[:, None] * spec_im[None]
        x_im = h_re[:, None] * spec_im[None] + h_im[:, None] * spec_re[None]
        count = h_re.shape[0]
        outs = []
        for j in range(per_dev):
            x_cat = jnp.concatenate(
                [x_re[:, j], x_im[:, j], jnp.zeros((count, B, 128 - 2 * B), jnp.float32)], axis=-1
            ).reshape(count * B, 128)
            outs.append(imaging(x_cat, goal[j], weights, corner_dose))
        u_all = jnp.stack(outs, axis=1)
        u_re = u_all[..., :B]
        u_im = u_all[..., B : 2 * B]

    with jax.named_scope("adjoint_spectra"):
        out_re = jnp.einsum("bx,knxc->knbc", cos_tab, u_re, precision=precise) - jnp.einsum(
            "bx,knxc->knbc", sin_tab, u_im, precision=precise
        )
        out_im = jnp.einsum("bx,knxc->knbc", cos_tab, u_im, precision=precise) + jnp.einsum(
            "bx,knxc->knbc", sin_tab, u_re, precision=precise
        )
        twice = (2.0 * weights)[:, None, None, None]
        grad_re = jnp.sum(twice * (h_re[:, None] * out_re + h_im[:, None] * out_im), axis=0)
        grad_im = jnp.sum(twice * (h_re[:, None] * out_im - h_im[:, None] * out_re), axis=0)

    with jax.named_scope("gradient_exchange"):
        own_grad = jnp.stack([grad_re, grad_im], axis=1)
        both = gather_all(own_grad, "kern", kern_count, kern_pos)
        corner_count = lax.axis_size("corner")
        mine_tiles = sum_all(both, "corner", corner_count, lax.axis_index("corner"))
        all_re, all_im = phase_ramp(inst_shift)
        back_re = all_re * mine_tiles[:, 0] + all_im * mine_tiles[:, 1]
        back_im = all_re * mine_tiles[:, 1] - all_im * mine_tiles[:, 0]
        own_back = jnp.stack([back_re, back_im], axis=1)
        owner_pick = (
            inst_master[:, None] == jnp.arange(region_masters, dtype=jnp.int32)[None, :]
        ).astype(jnp.float32)
        terms = jnp.sum(owner_pick[:, :, None, None, None] * own_back[:, None], axis=0)
        mine_masters = scatter_sum(terms, "tile", tile_count, tile_pos, local_masters)

    with jax.named_scope("pixel_gradients"):
        tile_grad = back_pixels(mine_tiles[:, 0], mine_tiles[:, 1], cos_tab, sin_tab)
        master_grad = back_pixels(mine_masters[:, 0], mine_masters[:, 1], cos_tab, sin_tab)
    return (tile_grad, master_grad)


def solution(mesh):
    return jax.shard_map(
        on_device,
        mesh=mesh,
        in_specs=(
            P(("region", "tile"), None, None),
            P(("region", "tile"), None, None),
            P(("region", "tile"), None, None),
            P(("region", "tile")),
            P(("region", "tile"), None),
            P("corner", None, None, None, None),
            P("corner", None),
            P("corner"),
        ),
        out_specs=(P(("region", "tile"), None, None), P(("region", "tile"), None, None)),
        check_vma=False,
    )
```

```python
import math

import numpy as np
import jax
import jax.numpy as jnp
from jax import lax
from jax.sharding import PartitionSpec as P
from jax.experimental import pallas as pl
from jax.experimental.pallas import tpu as pltpu

P_SIZE = 256
B = 32


precise = lax.Precision.HIGHEST
steepness = 3.0
threshold = 1.0


def band_tables():
    freq = np.arange(B, dtype=np.int64) - B // 2
    pixel = np.arange(P_SIZE, dtype=np.int64)
    angle = (2.0 * math.pi / P_SIZE) * np.mod(freq[:, None] * pixel[None, :], P_SIZE).astype(np.float64)
    return (jnp.asarray(np.cos(angle), jnp.float32), jnp.asarray(-np.sin(angle), jnp.float32))


def phase_ramp(shift):
    freq = jnp.arange(B, dtype=jnp.int32) - B // 2
    total = (
        freq[None, :, None] * shift[:, 0][:, None, None]
        + freq[None, None, :] * shift[:, 1][:, None, None]
    )
    angle = 2.0 * math.pi / P_SIZE * jnp.mod(total, P_SIZE).astype(jnp.float32)
    return (jnp.cos(angle), -jnp.sin(angle))


def spectra(masks, cos_tab, sin_tab):
    rows_re = jnp.einsum("bx,nxy->nby", cos_tab, masks, precision=precise)
    rows_im = jnp.einsum("bx,nxy->nby", sin_tab, masks, precision=precise)
    spec_re = jnp.einsum("nby,cy->nbc", rows_re, cos_tab, precision=precise) - jnp.einsum(
        "nby,cy->nbc", rows_im, sin_tab, precision=precise
    )
    spec_im = jnp.einsum("nby,cy->nbc", rows_re, sin_tab, precision=precise) + jnp.einsum(
        "nby,cy->nbc", rows_im, cos_tab, precision=precise
    )
    return (spec_re, spec_im)


def back_pixels(x_re, x_im, cos_tab, sin_tab):
    half_re = jnp.einsum("bx,nbc->nxc", cos_tab, x_re, precision=precise) + jnp.einsum(
        "bx,nbc->nxc", sin_tab, x_im, precision=precise
    )
    half_im = jnp.einsum("bx,nbc->nxc", cos_tab, x_im, precision=precise) - jnp.einsum(
        "bx,nbc->nxc", sin_tab, x_re, precision=precise
    )
    return jnp.einsum("nxc,cy->nxy", half_re, cos_tab, precision=precise) + jnp.einsum(
        "nxc,cy->nxy", half_im, sin_tab, precision=precise
    )


def dot_full(a, b):
    return jnp.dot(a, b, precision=precise, preferred_element_type=jnp.float32)


def imaging_tables():
    freq = np.arange(B, dtype=np.int64) - B // 2
    pixel = np.arange(P_SIZE, dtype=np.int64)
    angle = (2.0 * math.pi / P_SIZE) * np.mod(freq[:, None] * pixel[None, :], P_SIZE).astype(np.float64)
    c_re = np.cos(angle)
    c_im = -np.sin(angle)
    scale = 1.0 / (P_SIZE * P_SIZE)
    right_w = np.zeros((128, 2 * P_SIZE))
    right_w[:B, :P_SIZE] = c_re
    right_w[:B, P_SIZE:] = -c_im
    right_w[B : 2 * B, :P_SIZE] = c_im
    right_w[B : 2 * B, P_SIZE:] = c_re
    left_a = np.zeros((P_SIZE, 128))
    left_a[:, :B] = c_re.T * scale
    left_a[:, B : 2 * B] = -c_im.T * scale
    right_b = np.zeros((2 * P_SIZE, 128))
    right_b[:P_SIZE, :B] = c_re.T * scale
    right_b[:P_SIZE, B : 2 * B] = c_im.T * scale
    right_b[P_SIZE:, :B] = -c_im.T * scale
    right_b[P_SIZE:, B : 2 * B] = c_re.T * scale
    ct_re = c_re.T
    ct_im = c_im.T
    right_c = np.zeros((2 * P_SIZE, 128))
    for col, (top, bottom) in enumerate(
        ((ct_re, -ct_im), (ct_im, ct_re), (ct_im, ct_re), (ct_re, -ct_im))
    ):
        right_c[:P_SIZE, col * B : (col + 1) * B] = top
        right_c[P_SIZE:, col * B : (col + 1) * B] = bottom
    return [jnp.asarray(table, jnp.float32) for table in (right_w, left_a, right_b, right_c)]


def imaging_body(
    x_ref, goal_ref, h_ref, w_ref, dose_ref, rw_ref, la_ref, rb_ref, rc_ref,
    acc_ref, w_buf, f_buf, i_buf, u_buf,
):
    count = f_buf.shape[0]
    w_buf[...] = dot_full(x_ref[...], rw_ref[...])
    i_buf[...] = jnp.zeros(i_buf.shape, jnp.float32)
    pad = jnp.zeros((128 - 2 * B, 2 * P_SIZE), jnp.float32)

    def forward(k, carry):
        rows = w_buf[pl.ds(pl.multiple_of(k * B, B), B), :]
        swap = jnp.concatenate([-rows[:, P_SIZE:], rows[:, :P_SIZE]], axis=1)
        stacked = jnp.concatenate([rows, swap, pad], axis=0)
        field = dot_full(la_ref[...], stacked)
        f_buf[k] = field
        power = field * field
        i_buf[...] += w_ref[k] * (power[:, :P_SIZE] + power[:, P_SIZE:])
        return carry

    lax.fori_loop(0, count, forward, 0)
    dose = dose_ref[0]
    resist = 1.0 / (1.0 + jnp.exp(-(steepness * (dose * i_buf[...] - threshold))))
    sens = 2.0 * (resist - goal_ref[...]) * resist * (1.0 - resist) * steepness * dose
    i_buf[...] = sens

    def backward(k, carry):
        sens = i_buf[...]
        weighted = f_buf[k] * jnp.concatenate([sens, sens], axis=1)
        half = dot_full(weighted, rb_ref[...])
        flip = half.T
        u_buf[pl.ds(pl.multiple_of(k * B, B), B), :] = jnp.concatenate([flip[:B], flip[B : 2 * B]], axis=1)
        return carry

    lax.fori_loop(0, count, backward, 0)
    out = dot_full(u_buf[...], rc_ref[...])
    acc_ref[...] = jnp.sum((h_ref[...] * out).reshape(count, B, 128), axis=0)


def imaging(x_cat, goal, h_cat, weights, dose):
    count = weights.shape[0]
    tables = imaging_tables()
    vmem = pl.BlockSpec(memory_space=pltpu.VMEM)
    smem = pl.BlockSpec(memory_space=pltpu.SMEM)
    return pl.pallas_call(
        imaging_body,
        out_shape=jax.ShapeDtypeStruct((B, 128), jnp.float32),
        in_specs=[vmem, vmem, vmem, smem, smem] + [vmem] * 4,
        out_specs=vmem,
        scratch_shapes=[
            pltpu.VMEM((count * B, 2 * P_SIZE), jnp.float32),
            pltpu.VMEM((count, P_SIZE, 2 * P_SIZE), jnp.float32),
            pltpu.VMEM((P_SIZE, P_SIZE), jnp.float32),
            pltpu.VMEM((count * B, 2 * P_SIZE), jnp.float32),
        ],
    )(x_cat, goal, h_cat, weights, dose, *tables)


def xor_partners(count):
    return count & (count - 1) == 0 and count <= 8


def gather_all(x, axis, count, pos):
    if not xor_partners(count):
        return lax.all_gather(x, axis, axis=0, tiled=True)
    size = x.shape[0]
    slot = jnp.arange(count * size, dtype=jnp.int32) // size
    total = jnp.where((slot == pos)[:, None, None, None], jnp.tile(x, (count, 1, 1, 1)), 0.0)
    for step in range(1, count):
        got = lax.ppermute(x, axis, [(i, i ^ step) for i in range(count)])
        hit = (slot == (pos ^ step))[:, None, None, None]
        total = total + jnp.where(hit, jnp.tile(got, (count, 1, 1, 1)), 0.0)
    return total


def sum_all(x, axis, count, pos):
    if not xor_partners(count):
        return lax.psum(x, axis)
    step = 1
    while step < count:
        x = x + lax.ppermute(x, axis, [(i, i ^ step) for i in range(count)])
        step *= 2
    return x


def scatter_sum(x, axis, count, pos, size):
    if not xor_partners(count):
        return lax.psum_scatter(x, axis, scatter_dimension=0, tiled=True)
    total = lax.dynamic_slice_in_dim(x, pos * size, size, 0)
    for step in range(1, count):
        part = lax.dynamic_slice_in_dim(x, (pos ^ step) * size, size, 0)
        total = total + lax.ppermute(part, axis, [(i, i ^ step) for i in range(count)])
    return total


def on_device(
    tile_mask, master_mask, target, inst_master, inst_shift, kernels, kernel_weight, corner_dose
):
    cos_tab, sin_tab = band_tables()
    scale = 1.0 / (P_SIZE * P_SIZE)
    local_tiles = tile_mask.shape[0]
    local_masters = master_mask.shape[0]
    tile_count = lax.axis_size("tile")
    tile_pos = lax.axis_index("tile")
    kern_count = lax.axis_size("kern")
    kern_pos = lax.axis_index("kern")
    per_dev = local_tiles // kern_count
    first = kern_pos * per_dev
    region_tiles = tile_count * local_tiles
    region_masters = tile_count * local_masters

    with jax.named_scope("master_spectra"):
        own_re, own_im = spectra(master_mask.astype(jnp.float32), cos_tab, sin_tab)
        own = jnp.stack([own_re, own_im], axis=1)
        every = gather_all(own, "tile", tile_count, tile_pos)

    with jax.named_scope("tile_spectra"):
        mine_mask = lax.dynamic_slice_in_dim(tile_mask, first, per_dev, 0)
        goal = lax.dynamic_slice_in_dim(target, first, per_dev, 0).astype(jnp.float32)
        mine_master = lax.dynamic_slice_in_dim(inst_master, first, per_dev, 0)
        mine_shift = lax.dynamic_slice_in_dim(inst_shift, first, per_dev, 0)
        tile_re, tile_im = spectra(mine_mask.astype(jnp.float32), cos_tab, sin_tab)
        ph_re, ph_im = phase_ramp(mine_shift)
        pick = (mine_master[:, None] == jnp.arange(region_masters, dtype=jnp.int32)[None, :]).astype(
            jnp.float32
        )
        sel = jnp.sum(pick[:, :, None, None, None] * every[None], axis=1)
        sel_re = sel[:, 0]
        sel_im = sel[:, 1]
        spec_re = tile_re + (ph_re * sel_re - ph_im * sel_im)
        spec_im = tile_im + (ph_re * sel_im + ph_im * sel_re)

    dose = corner_dose[0]
    h_re = kernels[0, :, 0]
    h_im = kernels[0, :, 1]
    weights = kernel_weight[0]

    with jax.named_scope("imaging_kernel"):
        x_re = h_re[:, None] * spec_re[None] - h_im[:, None] * spec_im[None]
        x_im = h_re[:, None] * spec_im[None] + h_im[:, None] * spec_re[None]
        count = h_re.shape[0]
        twice = (2.0 * weights)[:, None, None]
        ht_re = jnp.swapaxes(h_re, 1, 2) * twice
        ht_im = jnp.swapaxes(h_im, 1, 2) * twice
        h_cat = jnp.concatenate([ht_re, ht_re, ht_im, -ht_im], axis=-1).reshape(count * B, 128)
        grads_re = []
        grads_im = []
        for j in range(per_dev):
            x_cat = jnp.concatenate(
                [x_re[:, j], x_im[:, j], jnp.zeros((count, B, 128 - 2 * B), jnp.float32)], axis=-1
            ).reshape(count * B, 128)
            acc = imaging(x_cat, goal[j], h_cat, weights, corner_dose)
            grads_re.append((acc[:, :B] + acc[:, 2 * B : 3 * B]).T)
            grads_im.append((acc[:, B : 2 * B] + acc[:, 3 * B :]).T)
        grad_re = jnp.stack(grads_re)
        grad_im = jnp.stack(grads_im)

    with jax.named_scope("gradient_exchange"):
        own_grad = jnp.stack([grad_re, grad_im], axis=1)
        both = gather_all(own_grad, "kern", kern_count, kern_pos)
        corner_count = lax.axis_size("corner")
        mine_tiles = sum_all(both, "corner", corner_count, lax.axis_index("corner"))
        all_re, all_im = phase_ramp(inst_shift)
        back_re = all_re * mine_tiles[:, 0] + all_im * mine_tiles[:, 1]
        back_im = all_re * mine_tiles[:, 1] - all_im * mine_tiles[:, 0]
        own_back = jnp.stack([back_re, back_im], axis=1)
        owner_pick = (
            inst_master[:, None] == jnp.arange(region_masters, dtype=jnp.int32)[None, :]
        ).astype(jnp.float32)
        terms = jnp.sum(owner_pick[:, :, None, None, None] * own_back[:, None], axis=0)
        mine_masters = scatter_sum(terms, "tile", tile_count, tile_pos, local_masters)

    with jax.named_scope("pixel_gradients"):
        tile_grad = back_pixels(mine_tiles[:, 0], mine_tiles[:, 1], cos_tab, sin_tab)
        master_grad = back_pixels(mine_masters[:, 0], mine_masters[:, 1], cos_tab, sin_tab)
    return (tile_grad, master_grad)


def solution(mesh):
    return jax.shard_map(
        on_device,
        mesh=mesh,
        in_specs=(
            P(("region", "tile"), None, None),
            P(("region", "tile"), None, None),
            P(("region", "tile"), None, None),
            P(("region", "tile")),
            P(("region", "tile"), None),
            P("corner", None, None, None, None),
            P("corner", None),
            P("corner"),
        ),
        out_specs=(P(("region", "tile"), None, None), P(("region", "tile"), None, None)),
        check_vma=False,
    )
```

```python
import math

import numpy as np
import jax
import jax.numpy as jnp
from jax import lax
from jax.sharding import PartitionSpec as P
from jax.experimental import pallas as pl
from jax.experimental.pallas import tpu as pltpu

P_SIZE = 256
B = 32


precise = lax.Precision.HIGHEST
steepness = 3.0
threshold = 1.0


def band_tables():
    freq = np.arange(B, dtype=np.int64) - B // 2
    pixel = np.arange(P_SIZE, dtype=np.int64)
    angle = (2.0 * math.pi / P_SIZE) * np.mod(freq[:, None] * pixel[None, :], P_SIZE).astype(np.float64)
    return (jnp.asarray(np.cos(angle), jnp.float32), jnp.asarray(-np.sin(angle), jnp.float32))


def phase_ramp(shift):
    freq = jnp.arange(B, dtype=jnp.int32) - B // 2
    total = (
        freq[None, :, None] * shift[:, 0][:, None, None]
        + freq[None, None, :] * shift[:, 1][:, None, None]
    )
    angle = 2.0 * math.pi / P_SIZE * jnp.mod(total, P_SIZE).astype(jnp.float32)
    return (jnp.cos(angle), -jnp.sin(angle))


def spectra(masks, cos_tab, sin_tab):
    rows_re = jnp.einsum("bx,nxy->nby", cos_tab, masks, precision=precise)
    rows_im = jnp.einsum("bx,nxy->nby", sin_tab, masks, precision=precise)
    spec_re = jnp.einsum("nby,cy->nbc", rows_re, cos_tab, precision=precise) - jnp.einsum(
        "nby,cy->nbc", rows_im, sin_tab, precision=precise
    )
    spec_im = jnp.einsum("nby,cy->nbc", rows_re, sin_tab, precision=precise) + jnp.einsum(
        "nby,cy->nbc", rows_im, cos_tab, precision=precise
    )
    return (spec_re, spec_im)


def back_pixels(x_re, x_im, cos_tab, sin_tab):
    half_re = jnp.einsum("bx,nbc->nxc", cos_tab, x_re, precision=precise) + jnp.einsum(
        "bx,nbc->nxc", sin_tab, x_im, precision=precise
    )
    half_im = jnp.einsum("bx,nbc->nxc", cos_tab, x_im, precision=precise) - jnp.einsum(
        "bx,nbc->nxc", sin_tab, x_re, precision=precise
    )
    return jnp.einsum("nxc,cy->nxy", half_re, cos_tab, precision=precise) + jnp.einsum(
        "nxc,cy->nxy", half_im, sin_tab, precision=precise
    )


def dot_full(a, b):
    return jnp.dot(a, b, precision=precise, preferred_element_type=jnp.float32)


def dot_parts(a, b):
    return jnp.dot(a, b, preferred_element_type=jnp.float32)


def split_three(a):
    hi = a.astype(jnp.bfloat16)
    rest = a - hi.astype(jnp.float32)
    mid = rest.astype(jnp.bfloat16)
    lo = (rest - mid.astype(jnp.float32)).astype(jnp.bfloat16)
    return hi, mid, lo


def table_three(table):
    hi = table.astype(jnp.bfloat16)
    rest = table - hi.astype(np.float64)
    mid = rest.astype(jnp.bfloat16)
    lo = (rest - mid.astype(np.float64)).astype(jnp.bfloat16)
    return hi, mid, lo


def imaging_tables():
    freq = np.arange(B, dtype=np.int64) - B // 2
    pixel = np.arange(P_SIZE, dtype=np.int64)
    angle = (2.0 * math.pi / P_SIZE) * np.mod(freq[:, None] * pixel[None, :], P_SIZE).astype(np.float64)
    c_re = np.cos(angle)
    c_im = -np.sin(angle)
    scale = 1.0 / (P_SIZE * P_SIZE)
    right_w = np.zeros((128, 2 * P_SIZE))
    right_w[:B, :P_SIZE] = c_re
    right_w[:B, P_SIZE:] = -c_im
    right_w[B : 2 * B, :P_SIZE] = c_im
    right_w[B : 2 * B, P_SIZE:] = c_re
    left_a = np.zeros((P_SIZE, 128))
    left_a[:, :B] = c_re.T * scale
    left_a[:, B : 2 * B] = -c_im.T * scale
    right_b = np.zeros((2 * P_SIZE, 128))
    right_b[:P_SIZE, :B] = c_re.T * scale
    right_b[:P_SIZE, B : 2 * B] = c_im.T * scale
    right_b[P_SIZE:, :B] = -c_im.T * scale
    right_b[P_SIZE:, B : 2 * B] = c_re.T * scale
    ct_re = c_re.T
    ct_im = c_im.T
    right_c = np.zeros((2 * P_SIZE, 128))
    for col, (top, bottom) in enumerate(
        ((ct_re, -ct_im), (ct_im, ct_re), (ct_im, ct_re), (ct_re, -ct_im))
    ):
        right_c[:P_SIZE, col * B : (col + 1) * B] = top
        right_c[P_SIZE:, col * B : (col + 1) * B] = bottom
    a_hi, a_mid, a_lo = table_three(left_a[:, : 2 * B])
    left_three = np.concatenate([a_hi, a_hi, a_mid, a_hi, a_lo, a_mid], axis=1)
    b_hi, b_mid, b_lo = table_three(right_b)
    right_hm = np.concatenate([b_hi, b_mid], axis=1)
    right_lh = np.concatenate([b_lo, b_hi], axis=0)
    out = [jnp.asarray(table, jnp.float32) for table in (right_w, right_c)]
    return out + [jnp.asarray(table) for table in (left_three, right_hm, right_lh)]


def imaging_body(
    x_ref, goal_ref, h_ref, w_ref, dose_ref, rw_ref, rc_ref, la_ref, rhm_ref, rlh_ref,
    acc_ref, w_buf, f_buf, i_buf, u_buf,
):
    count = f_buf.shape[0]
    w_buf[...] = dot_full(x_ref[...], rw_ref[...])
    i_buf[...] = jnp.zeros(i_buf.shape, jnp.float32)

    def forward(k, carry):
        rows = w_buf[pl.ds(pl.multiple_of(k * B, B), B), :]
        swap = jnp.concatenate([-rows[:, P_SIZE:], rows[:, :P_SIZE]], axis=1)
        s_hi, s_mid, s_lo = split_three(jnp.concatenate([rows, swap], axis=0))
        stacked = jnp.concatenate([s_hi, s_mid, s_hi, s_lo, s_hi, s_mid], axis=0)
        field = dot_parts(la_ref[...], stacked)
        f_buf[k] = field
        power = field * field
        i_buf[...] += w_ref[k] * (power[:, :P_SIZE] + power[:, P_SIZE:])
        return carry

    lax.fori_loop(0, count, forward, 0)
    dose = dose_ref[0]
    resist = 1.0 / (1.0 + jnp.exp(-(steepness * (dose * i_buf[...] - threshold))))
    sens = 2.0 * (resist - goal_ref[...]) * resist * (1.0 - resist) * steepness * dose
    i_buf[...] = sens

    def backward(k, carry):
        sens = i_buf[...]
        weighted = f_buf[k] * jnp.concatenate([sens, sens], axis=1)
        q_hi, q_mid, q_lo = split_three(weighted)
        first = dot_parts(q_hi, rhm_ref[...]) + dot_parts(q_mid, rhm_ref[...])
        rest = dot_parts(jnp.concatenate([q_hi, q_lo], axis=1), rlh_ref[...])
        half = first[:, :128] + first[:, 128:] + rest
        flip = half.T
        u_buf[pl.ds(pl.multiple_of(k * B, B), B), :] = jnp.concatenate([flip[:B], flip[B : 2 * B]], axis=1)
        return carry

    lax.fori_loop(0, count, backward, 0)
    out = dot_full(u_buf[...], rc_ref[...])
    acc_ref[...] = jnp.sum((h_ref[...] * out).reshape(count, B, 128), axis=0)


def imaging(x_cat, goal, h_cat, weights, dose):
    count = weights.shape[0]
    tables = imaging_tables()
    vmem = pl.BlockSpec(memory_space=pltpu.VMEM)
    smem = pl.BlockSpec(memory_space=pltpu.SMEM)
    return pl.pallas_call(
        imaging_body,
        out_shape=jax.ShapeDtypeStruct((B, 128), jnp.float32),
        in_specs=[vmem, vmem, vmem, smem, smem] + [vmem] * 5,
        out_specs=vmem,
        scratch_shapes=[
            pltpu.VMEM((count * B, 2 * P_SIZE), jnp.float32),
            pltpu.VMEM((count, P_SIZE, 2 * P_SIZE), jnp.float32),
            pltpu.VMEM((P_SIZE, P_SIZE), jnp.float32),
            pltpu.VMEM((count * B, 2 * P_SIZE), jnp.float32),
        ],
    )(x_cat, goal, h_cat, weights, dose, *tables)


def xor_partners(count):
    return count & (count - 1) == 0 and count <= 8


def gather_all(x, axis, count, pos):
    if not xor_partners(count):
        return lax.all_gather(x, axis, axis=0, tiled=True)
    size = x.shape[0]
    slot = jnp.arange(count * size, dtype=jnp.int32) // size
    total = jnp.where((slot == pos)[:, None, None, None], jnp.tile(x, (count, 1, 1, 1)), 0.0)
    for step in range(1, count):
        got = lax.ppermute(x, axis, [(i, i ^ step) for i in range(count)])
        hit = (slot == (pos ^ step))[:, None, None, None]
        total = total + jnp.where(hit, jnp.tile(got, (count, 1, 1, 1)), 0.0)
    return total


def sum_all(x, axis, count, pos):
    if not xor_partners(count):
        return lax.psum(x, axis)
    step = 1
    while step < count:
        x = x + lax.ppermute(x, axis, [(i, i ^ step) for i in range(count)])
        step *= 2
    return x


def scatter_sum(x, axis, count, pos, size):
    if not xor_partners(count):
        return lax.psum_scatter(x, axis, scatter_dimension=0, tiled=True)
    total = lax.dynamic_slice_in_dim(x, pos * size, size, 0)
    for step in range(1, count):
        part = lax.dynamic_slice_in_dim(x, (pos ^ step) * size, size, 0)
        total = total + lax.ppermute(part, axis, [(i, i ^ step) for i in range(count)])
    return total


def on_device(
    tile_mask, master_mask, target, inst_master, inst_shift, kernels, kernel_weight, corner_dose
):
    cos_tab, sin_tab = band_tables()
    scale = 1.0 / (P_SIZE * P_SIZE)
    local_tiles = tile_mask.shape[0]
    local_masters = master_mask.shape[0]
    tile_count = lax.axis_size("tile")
    tile_pos = lax.axis_index("tile")
    kern_count = lax.axis_size("kern")
    kern_pos = lax.axis_index("kern")
    per_dev = local_tiles // kern_count
    first = kern_pos * per_dev
    region_tiles = tile_count * local_tiles
    region_masters = tile_count * local_masters

    with jax.named_scope("master_spectra"):
        own_re, own_im = spectra(master_mask.astype(jnp.float32), cos_tab, sin_tab)
        own = jnp.stack([own_re, own_im], axis=1)
        every = gather_all(own, "tile", tile_count, tile_pos)

    with jax.named_scope("tile_spectra"):
        mine_mask = lax.dynamic_slice_in_dim(tile_mask, first, per_dev, 0)
        goal = lax.dynamic_slice_in_dim(target, first, per_dev, 0).astype(jnp.float32)
        mine_master = lax.dynamic_slice_in_dim(inst_master, first, per_dev, 0)
        mine_shift = lax.dynamic_slice_in_dim(inst_shift, first, per_dev, 0)
        tile_re, tile_im = spectra(mine_mask.astype(jnp.float32), cos_tab, sin_tab)
        ph_re, ph_im = phase_ramp(mine_shift)
        pick = (mine_master[:, None] == jnp.arange(region_masters, dtype=jnp.int32)[None, :]).astype(
            jnp.float32
        )
        sel = jnp.sum(pick[:, :, None, None, None] * every[None], axis=1)
        sel_re = sel[:, 0]
        sel_im = sel[:, 1]
        spec_re = tile_re + (ph_re * sel_re - ph_im * sel_im)
        spec_im = tile_im + (ph_re * sel_im + ph_im * sel_re)

    dose = corner_dose[0]
    h_re = kernels[0, :, 0]
    h_im = kernels[0, :, 1]
    weights = kernel_weight[0]

    with jax.named_scope("imaging_kernel"):
        x_re = h_re[:, None] * spec_re[None] - h_im[:, None] * spec_im[None]
        x_im = h_re[:, None] * spec_im[None] + h_im[:, None] * spec_re[None]
        count = h_re.shape[0]
        twice = (2.0 * weights)[:, None, None]
        ht_re = jnp.swapaxes(h_re, 1, 2) * twice
        ht_im = jnp.swapaxes(h_im, 1, 2) * twice
        h_cat = jnp.concatenate([ht_re, ht_re, ht_im, -ht_im], axis=-1).reshape(count * B, 128)
        grads_re = []
        grads_im = []
        for j in range(per_dev):
            x_cat = jnp.concatenate(
                [x_re[:, j], x_im[:, j], jnp.zeros((count, B, 128 - 2 * B), jnp.float32)], axis=-1
            ).reshape(count * B, 128)
            acc = imaging(x_cat, goal[j], h_cat, weights, corner_dose)
            grads_re.append((acc[:, :B] + acc[:, 2 * B : 3 * B]).T)
            grads_im.append((acc[:, B : 2 * B] + acc[:, 3 * B :]).T)
        grad_re = jnp.stack(grads_re)
        grad_im = jnp.stack(grads_im)

    with jax.named_scope("gradient_exchange"):
        own_grad = jnp.stack([grad_re, grad_im], axis=1)
        both = gather_all(own_grad, "kern", kern_count, kern_pos)
        corner_count = lax.axis_size("corner")
        mine_tiles = sum_all(both, "corner", corner_count, lax.axis_index("corner"))
        all_re, all_im = phase_ramp(inst_shift)
        back_re = all_re * mine_tiles[:, 0] + all_im * mine_tiles[:, 1]
        back_im = all_re * mine_tiles[:, 1] - all_im * mine_tiles[:, 0]
        own_back = jnp.stack([back_re, back_im], axis=1)
        owner_pick = (
            inst_master[:, None] == jnp.arange(region_masters, dtype=jnp.int32)[None, :]
        ).astype(jnp.float32)
        terms = jnp.sum(owner_pick[:, :, None, None, None] * own_back[:, None], axis=0)
        mine_masters = scatter_sum(terms, "tile", tile_count, tile_pos, local_masters)

    with jax.named_scope("pixel_gradients"):
        tile_grad = back_pixels(mine_tiles[:, 0], mine_tiles[:, 1], cos_tab, sin_tab)
        master_grad = back_pixels(mine_masters[:, 0], mine_masters[:, 1], cos_tab, sin_tab)
    return (tile_grad, master_grad)


def solution(mesh):
    return jax.shard_map(
        on_device,
        mesh=mesh,
        in_specs=(
            P(("region", "tile"), None, None),
            P(("region", "tile"), None, None),
            P(("region", "tile"), None, None),
            P(("region", "tile")),
            P(("region", "tile"), None),
            P("corner", None, None, None, None),
            P("corner", None),
            P("corner"),
        ),
        out_specs=(P(("region", "tile"), None, None), P(("region", "tile"), None, None)),
        check_vma=False,
    )
```

```python
import math

import numpy as np
import jax
import jax.numpy as jnp
from jax import lax
from jax.sharding import PartitionSpec as P
from jax.experimental import pallas as pl
from jax.experimental.pallas import tpu as pltpu

P_SIZE = 256
B = 32


precise = lax.Precision.HIGHEST
steepness = 3.0
threshold = 1.0


def band_tables():
    freq = np.arange(B, dtype=np.int64) - B // 2
    pixel = np.arange(P_SIZE, dtype=np.int64)
    angle = (2.0 * math.pi / P_SIZE) * np.mod(freq[:, None] * pixel[None, :], P_SIZE).astype(np.float64)
    return (jnp.asarray(np.cos(angle), jnp.float32), jnp.asarray(-np.sin(angle), jnp.float32))


def phase_ramp(shift):
    freq = jnp.arange(B, dtype=jnp.int32) - B // 2
    total = (
        freq[None, :, None] * shift[:, 0][:, None, None]
        + freq[None, None, :] * shift[:, 1][:, None, None]
    )
    angle = 2.0 * math.pi / P_SIZE * jnp.mod(total, P_SIZE).astype(jnp.float32)
    return (jnp.cos(angle), -jnp.sin(angle))


def spectra(masks, cos_tab, sin_tab):
    rows_re = jnp.einsum("bx,nxy->nby", cos_tab, masks, precision=precise)
    rows_im = jnp.einsum("bx,nxy->nby", sin_tab, masks, precision=precise)
    spec_re = jnp.einsum("nby,cy->nbc", rows_re, cos_tab, precision=precise) - jnp.einsum(
        "nby,cy->nbc", rows_im, sin_tab, precision=precise
    )
    spec_im = jnp.einsum("nby,cy->nbc", rows_re, sin_tab, precision=precise) + jnp.einsum(
        "nby,cy->nbc", rows_im, cos_tab, precision=precise
    )
    return (spec_re, spec_im)


def back_pixels(x_re, x_im, cos_tab, sin_tab):
    half_re = jnp.einsum("bx,nbc->nxc", cos_tab, x_re, precision=precise) + jnp.einsum(
        "bx,nbc->nxc", sin_tab, x_im, precision=precise
    )
    half_im = jnp.einsum("bx,nbc->nxc", cos_tab, x_im, precision=precise) - jnp.einsum(
        "bx,nbc->nxc", sin_tab, x_re, precision=precise
    )
    return jnp.einsum("nxc,cy->nxy", half_re, cos_tab, precision=precise) + jnp.einsum(
        "nxc,cy->nxy", half_im, sin_tab, precision=precise
    )


def dot_full(a, b):
    return jnp.dot(a, b, precision=precise, preferred_element_type=jnp.float32)


def dot_parts(a, b):
    return jnp.dot(a, b, preferred_element_type=jnp.float32)


def split_three(a):
    hi = a.astype(jnp.bfloat16)
    rest = a - hi.astype(jnp.float32)
    mid = rest.astype(jnp.bfloat16)
    lo = (rest - mid.astype(jnp.float32)).astype(jnp.bfloat16)
    return hi, mid, lo


def table_three(table):
    hi = table.astype(jnp.bfloat16)
    rest = table - hi.astype(np.float64)
    mid = rest.astype(jnp.bfloat16)
    lo = (rest - mid.astype(np.float64)).astype(jnp.bfloat16)
    return hi, mid, lo


def imaging_tables():
    freq = np.arange(B, dtype=np.int64) - B // 2
    pixel = np.arange(P_SIZE, dtype=np.int64)
    angle = (2.0 * math.pi / P_SIZE) * np.mod(freq[:, None] * pixel[None, :], P_SIZE).astype(np.float64)
    c_re = np.cos(angle)
    c_im = -np.sin(angle)
    scale = 1.0 / (P_SIZE * P_SIZE)
    right_w = np.zeros((128, 2 * P_SIZE))
    right_w[:B, :P_SIZE] = c_re
    right_w[:B, P_SIZE:] = -c_im
    right_w[B : 2 * B, :P_SIZE] = c_im
    right_w[B : 2 * B, P_SIZE:] = c_re
    left_a = np.zeros((P_SIZE, 128))
    left_a[:, :B] = c_re.T * scale
    left_a[:, B : 2 * B] = -c_im.T * scale
    right_b = np.zeros((2 * P_SIZE, 128))
    right_b[:P_SIZE, :B] = c_re.T * scale
    right_b[:P_SIZE, B : 2 * B] = c_im.T * scale
    right_b[P_SIZE:, :B] = -c_im.T * scale
    right_b[P_SIZE:, B : 2 * B] = c_re.T * scale
    ct_re = c_re.T
    ct_im = c_im.T
    right_c = np.zeros((2 * P_SIZE, 128))
    for col, (top, bottom) in enumerate(
        ((ct_re, -ct_im), (ct_im, ct_re), (ct_im, ct_re), (ct_re, -ct_im))
    ):
        right_c[:P_SIZE, col * B : (col + 1) * B] = top
        right_c[P_SIZE:, col * B : (col + 1) * B] = bottom
    a_hi, a_mid, a_lo = table_three(left_a[:, : 2 * B])
    left_three = np.concatenate([a_hi, a_hi, a_mid, a_hi, a_lo, a_mid], axis=1)
    b_hi, b_mid, b_lo = table_three(right_b)
    right_hm = np.concatenate([b_hi, b_mid], axis=1)
    right_lh = np.concatenate([b_lo, b_hi], axis=0)
    out = [jnp.asarray(table, jnp.float32) for table in (right_w, right_c)]
    return out + [jnp.asarray(table) for table in (left_three, right_hm, right_lh)]


def imaging_body(
    x_ref, goal_ref, h_ref, w_ref, dose_ref, rw_ref, rc_ref, la_ref, rhm_ref, rlh_ref,
    acc_ref, w_buf, f_buf, i_buf, u_buf,
):
    count = f_buf.shape[0]
    w_buf[...] = dot_full(x_ref[...], rw_ref[...])
    i_buf[...] = jnp.zeros(i_buf.shape, jnp.float32)

    def forward(k, carry):
        rows = w_buf[pl.ds(pl.multiple_of(k * B, B), B), :]
        swap = jnp.concatenate([-rows[:, P_SIZE:], rows[:, :P_SIZE]], axis=1)
        s_hi, s_mid, s_lo = split_three(jnp.concatenate([rows, swap], axis=0))
        stacked = jnp.concatenate([s_hi, s_mid, s_hi, s_lo, s_hi, s_mid], axis=0)
        field = dot_parts(la_ref[...], stacked)
        f_buf[k] = field
        power = field * field
        i_buf[...] += w_ref[k] * (power[:, :P_SIZE] + power[:, P_SIZE:])
        return carry

    lax.fori_loop(0, count, forward, 0)
    dose = dose_ref[0]
    resist = 1.0 / (1.0 + jnp.exp(-(steepness * (dose * i_buf[...] - threshold))))
    sens = 2.0 * (resist - goal_ref[...]) * resist * (1.0 - resist) * steepness * dose
    i_buf[...] = sens

    def backward(k, carry):
        sens = i_buf[...]
        weighted = f_buf[k] * jnp.concatenate([sens, sens], axis=1)
        q_hi, q_mid, q_lo = split_three(weighted)
        first = dot_parts(q_hi, rhm_ref[...]) + dot_parts(q_mid, rhm_ref[...])
        rest = dot_parts(jnp.concatenate([q_hi, q_lo], axis=1), rlh_ref[...])
        half = first[:, :128] + first[:, 128:] + rest
        flip = half.T
        u_buf[pl.ds(pl.multiple_of(k * B, B), B), :] = jnp.concatenate([flip[:B], flip[B : 2 * B]], axis=1)
        return carry

    lax.fori_loop(0, count, backward, 0)
    out = dot_full(u_buf[...], rc_ref[...])
    acc_ref[...] = jnp.sum((h_ref[...] * out).reshape(count, B, 128), axis=0)


def imaging(x_cat, goal, h_cat, weights, dose):
    count = weights.shape[0]
    tables = imaging_tables()
    vmem = pl.BlockSpec(memory_space=pltpu.VMEM)
    smem = pl.BlockSpec(memory_space=pltpu.SMEM)
    return pl.pallas_call(
        imaging_body,
        out_shape=jax.ShapeDtypeStruct((B, 128), jnp.float32),
        in_specs=[vmem, vmem, vmem, smem, smem] + [vmem] * 5,
        out_specs=vmem,
        scratch_shapes=[
            pltpu.VMEM((count * B, 2 * P_SIZE), jnp.float32),
            pltpu.VMEM((count, P_SIZE, 2 * P_SIZE), jnp.float32),
            pltpu.VMEM((P_SIZE, P_SIZE), jnp.float32),
            pltpu.VMEM((count * B, 2 * P_SIZE), jnp.float32),
        ],
    )(x_cat, goal, h_cat, weights, dose, *tables)


def xor_partners(count):
    return count & (count - 1) == 0 and count <= 8


def gather_all(x, axis, count, pos):
    if not xor_partners(count):
        return lax.all_gather(x, axis, axis=0, tiled=True)
    size = x.shape[0]
    slot = jnp.arange(count * size, dtype=jnp.int32) // size
    total = jnp.where((slot == pos)[:, None, None, None], jnp.tile(x, (count, 1, 1, 1)), 0.0)
    for step in range(1, count):
        got = lax.ppermute(x, axis, [(i, i ^ step) for i in range(count)])
        hit = (slot == (pos ^ step))[:, None, None, None]
        total = total + jnp.where(hit, jnp.tile(got, (count, 1, 1, 1)), 0.0)
    return total


def sum_all(x, axis, count, pos):
    if not xor_partners(count):
        return lax.psum(x, axis)
    step = 1
    while step < count:
        x = x + lax.ppermute(x, axis, [(i, i ^ step) for i in range(count)])
        step *= 2
    return x


def scatter_sum(x, axis, count, pos, size):
    if not xor_partners(count):
        return lax.psum_scatter(x, axis, scatter_dimension=0, tiled=True)
    total = lax.dynamic_slice_in_dim(x, pos * size, size, 0)
    for step in range(1, count):
        part = lax.dynamic_slice_in_dim(x, (pos ^ step) * size, size, 0)
        total = total + lax.ppermute(part, axis, [(i, i ^ step) for i in range(count)])
    return total


def partner_lists(count, kern_count):
    lists = [[] for _ in range(kern_count)]
    for step in range(1, count):
        lists[step % kern_count].append(step)
    return lists


def chosen_step(lists, round_index, kern_pos):
    pick = jnp.int32(-1)
    for k, steps in enumerate(lists):
        if round_index < len(steps):
            pick = jnp.where(kern_pos == k, jnp.int32(steps[round_index]), pick)
    return pick


def gather_split(x, count, pos, kern_count, kern_pos):
    size = x.shape[0]
    lists = partner_lists(count, kern_count)
    slot = jnp.arange(count * size, dtype=jnp.int32) // size
    spread = lambda part: jnp.tile(part, (count, 1, 1, 1))
    collected = jnp.zeros((count * size,) + x.shape[1:], x.dtype)
    for r in range(max(len(steps) for steps in lists)):
        pairs = []
        for k, steps in enumerate(lists):
            if r < len(steps):
                pairs += [((t ^ steps[r]) * kern_count + k, t * kern_count + k) for t in range(count)]
        got = lax.ppermute(x, ("tile", "kern"), pairs)
        step = chosen_step(lists, r, kern_pos)
        source = jnp.where(step >= 0, pos ^ step, -1)
        collected = collected + jnp.where((slot == source)[:, None, None, None], spread(got), 0.0)
    collected = sum_all(collected, "kern", kern_count, kern_pos)
    return collected + jnp.where((slot == pos)[:, None, None, None], spread(x), 0.0)


def scatter_split(x, count, pos, kern_count, kern_pos, size):
    lists = partner_lists(count, kern_count)
    own = lax.dynamic_slice_in_dim(x, pos * size, size, 0)
    total = jnp.where(kern_pos == 0, own, 0.0)
    for r in range(max(len(steps) for steps in lists)):
        pairs = []
        for k, steps in enumerate(lists):
            if r < len(steps):
                pairs += [(t * kern_count + k, (t ^ steps[r]) * kern_count + k) for t in range(count)]
        step = chosen_step(lists, r, kern_pos)
        target = jnp.where(step >= 0, pos ^ step, 0)
        part = lax.dynamic_slice_in_dim(x, target * size, size, 0)
        total = total + lax.ppermute(part, ("tile", "kern"), pairs)
    return sum_all(total, "kern", kern_count, kern_pos)


def on_device(
    tile_mask, master_mask, target, inst_master, inst_shift, kernels, kernel_weight, corner_dose
):
    cos_tab, sin_tab = band_tables()
    scale = 1.0 / (P_SIZE * P_SIZE)
    local_tiles = tile_mask.shape[0]
    local_masters = master_mask.shape[0]
    tile_count = lax.axis_size("tile")
    tile_pos = lax.axis_index("tile")
    kern_count = lax.axis_size("kern")
    kern_pos = lax.axis_index("kern")
    per_dev = local_tiles // kern_count
    first = kern_pos * per_dev
    region_tiles = tile_count * local_tiles
    region_masters = tile_count * local_masters

    with jax.named_scope("master_spectra"):
        own_re, own_im = spectra(master_mask.astype(jnp.float32), cos_tab, sin_tab)
        own = jnp.stack([own_re, own_im], axis=1)
        if xor_partners(tile_count) and xor_partners(kern_count) and tile_count > 2:
            every = gather_split(own, tile_count, tile_pos, kern_count, kern_pos)
        else:
            every = gather_all(own, "tile", tile_count, tile_pos)

    with jax.named_scope("tile_spectra"):
        mine_mask = lax.dynamic_slice_in_dim(tile_mask, first, per_dev, 0)
        goal = lax.dynamic_slice_in_dim(target, first, per_dev, 0).astype(jnp.float32)
        mine_master = lax.dynamic_slice_in_dim(inst_master, first, per_dev, 0)
        mine_shift = lax.dynamic_slice_in_dim(inst_shift, first, per_dev, 0)
        tile_re, tile_im = spectra(mine_mask.astype(jnp.float32), cos_tab, sin_tab)
        ph_re, ph_im = phase_ramp(mine_shift)
        pick = (mine_master[:, None] == jnp.arange(region_masters, dtype=jnp.int32)[None, :]).astype(
            jnp.float32
        )
        sel = jnp.sum(pick[:, :, None, None, None] * every[None], axis=1)
        sel_re = sel[:, 0]
        sel_im = sel[:, 1]
        spec_re = tile_re + (ph_re * sel_re - ph_im * sel_im)
        spec_im = tile_im + (ph_re * sel_im + ph_im * sel_re)

    dose = corner_dose[0]
    h_re = kernels[0, :, 0]
    h_im = kernels[0, :, 1]
    weights = kernel_weight[0]

    with jax.named_scope("imaging_kernel"):
        x_re = h_re[:, None] * spec_re[None] - h_im[:, None] * spec_im[None]
        x_im = h_re[:, None] * spec_im[None] + h_im[:, None] * spec_re[None]
        count = h_re.shape[0]
        twice = (2.0 * weights)[:, None, None]
        ht_re = jnp.swapaxes(h_re, 1, 2) * twice
        ht_im = jnp.swapaxes(h_im, 1, 2) * twice
        h_cat = jnp.concatenate([ht_re, ht_re, ht_im, -ht_im], axis=-1).reshape(count * B, 128)
        grads_re = []
        grads_im = []
        for j in range(per_dev):
            x_cat = jnp.concatenate(
                [x_re[:, j], x_im[:, j], jnp.zeros((count, B, 128 - 2 * B), jnp.float32)], axis=-1
            ).reshape(count * B, 128)
            acc = imaging(x_cat, goal[j], h_cat, weights, corner_dose)
            grads_re.append((acc[:, :B] + acc[:, 2 * B : 3 * B]).T)
            grads_im.append((acc[:, B : 2 * B] + acc[:, 3 * B :]).T)
        grad_re = jnp.stack(grads_re)
        grad_im = jnp.stack(grads_im)

    with jax.named_scope("gradient_exchange"):
        own_grad = jnp.stack([grad_re, grad_im], axis=1)
        both = gather_all(own_grad, "kern", kern_count, kern_pos)
        corner_count = lax.axis_size("corner")
        mine_tiles = sum_all(both, "corner", corner_count, lax.axis_index("corner"))
        all_re, all_im = phase_ramp(inst_shift)
        back_re = all_re * mine_tiles[:, 0] + all_im * mine_tiles[:, 1]
        back_im = all_re * mine_tiles[:, 1] - all_im * mine_tiles[:, 0]
        own_back = jnp.stack([back_re, back_im], axis=1)
        owner_pick = (
            inst_master[:, None] == jnp.arange(region_masters, dtype=jnp.int32)[None, :]
        ).astype(jnp.float32)
        terms = jnp.sum(owner_pick[:, :, None, None, None] * own_back[:, None], axis=0)
        if xor_partners(tile_count) and xor_partners(kern_count) and tile_count > 2:
            mine_masters = scatter_split(terms, tile_count, tile_pos, kern_count, kern_pos, local_masters)
        else:
            mine_masters = scatter_sum(terms, "tile", tile_count, tile_pos, local_masters)

    with jax.named_scope("pixel_gradients"):
        tile_grad = back_pixels(mine_tiles[:, 0], mine_tiles[:, 1], cos_tab, sin_tab)
        master_grad = back_pixels(mine_masters[:, 0], mine_masters[:, 1], cos_tab, sin_tab)
    return (tile_grad, master_grad)


def solution(mesh):
    return jax.shard_map(
        on_device,
        mesh=mesh,
        in_specs=(
            P(("region", "tile"), None, None),
            P(("region", "tile"), None, None),
            P(("region", "tile"), None, None),
            P(("region", "tile")),
            P(("region", "tile"), None),
            P("corner", None, None, None, None),
            P("corner", None),
            P("corner"),
        ),
        out_specs=(P(("region", "tile"), None, None), P(("region", "tile"), None, None)),
        check_vma=False,
    )
```

```python
import math

import numpy as np
import jax
import jax.numpy as jnp
from jax import lax
from jax.sharding import PartitionSpec as P
from jax.experimental import pallas as pl
from jax.experimental.pallas import tpu as pltpu

P_SIZE = 256
B = 32


precise = lax.Precision.HIGHEST
steepness = 3.0
threshold = 1.0


def band_tables():
    freq = np.arange(B, dtype=np.int64) - B // 2
    pixel = np.arange(P_SIZE, dtype=np.int64)
    angle = (2.0 * math.pi / P_SIZE) * np.mod(freq[:, None] * pixel[None, :], P_SIZE).astype(np.float64)
    return (jnp.asarray(np.cos(angle), jnp.float32), jnp.asarray(-np.sin(angle), jnp.float32))


def phase_ramp(shift):
    freq = jnp.arange(B, dtype=jnp.int32) - B // 2
    total = (
        freq[None, :, None] * shift[:, 0][:, None, None]
        + freq[None, None, :] * shift[:, 1][:, None, None]
    )
    angle = 2.0 * math.pi / P_SIZE * jnp.mod(total, P_SIZE).astype(jnp.float32)
    return (jnp.cos(angle), -jnp.sin(angle))


def spectra(masks, cos_tab, sin_tab):
    rows_re = jnp.einsum("bx,nxy->nby", cos_tab, masks, precision=precise)
    rows_im = jnp.einsum("bx,nxy->nby", sin_tab, masks, precision=precise)
    spec_re = jnp.einsum("nby,cy->nbc", rows_re, cos_tab, precision=precise) - jnp.einsum(
        "nby,cy->nbc", rows_im, sin_tab, precision=precise
    )
    spec_im = jnp.einsum("nby,cy->nbc", rows_re, sin_tab, precision=precise) + jnp.einsum(
        "nby,cy->nbc", rows_im, cos_tab, precision=precise
    )
    return (spec_re, spec_im)


def back_pixels(x_re, x_im, cos_tab, sin_tab):
    half_re = jnp.einsum("bx,nbc->nxc", cos_tab, x_re, precision=precise) + jnp.einsum(
        "bx,nbc->nxc", sin_tab, x_im, precision=precise
    )
    half_im = jnp.einsum("bx,nbc->nxc", cos_tab, x_im, precision=precise) - jnp.einsum(
        "bx,nbc->nxc", sin_tab, x_re, precision=precise
    )
    return jnp.einsum("nxc,cy->nxy", half_re, cos_tab, precision=precise) + jnp.einsum(
        "nxc,cy->nxy", half_im, sin_tab, precision=precise
    )


def dot_full(a, b):
    return jnp.dot(a, b, precision=precise, preferred_element_type=jnp.float32)


def dot_parts(a, b):
    return jnp.dot(a, b, preferred_element_type=jnp.float32)


def split_three(a):
    hi = a.astype(jnp.bfloat16)
    rest = a - hi.astype(jnp.float32)
    mid = rest.astype(jnp.bfloat16)
    lo = (rest - mid.astype(jnp.float32)).astype(jnp.bfloat16)
    return hi, mid, lo


def table_three(table):
    hi = table.astype(jnp.bfloat16)
    rest = table - hi.astype(np.float64)
    mid = rest.astype(jnp.bfloat16)
    lo = (rest - mid.astype(np.float64)).astype(jnp.bfloat16)
    return hi, mid, lo


def imaging_tables():
    freq = np.arange(B, dtype=np.int64) - B // 2
    pixel = np.arange(P_SIZE, dtype=np.int64)
    angle = (2.0 * math.pi / P_SIZE) * np.mod(freq[:, None] * pixel[None, :], P_SIZE).astype(np.float64)
    c_re = np.cos(angle)
    c_im = -np.sin(angle)
    scale = 1.0 / (P_SIZE * P_SIZE)
    right_w = np.zeros((128, 2 * P_SIZE))
    right_w[:B, :P_SIZE] = c_re
    right_w[:B, P_SIZE:] = -c_im
    right_w[B : 2 * B, :P_SIZE] = c_im
    right_w[B : 2 * B, P_SIZE:] = c_re
    left_a = np.zeros((P_SIZE, 128))
    left_a[:, :B] = c_re.T * scale
    left_a[:, B : 2 * B] = -c_im.T * scale
    right_b = np.zeros((2 * P_SIZE, 128))
    right_b[:P_SIZE, :B] = c_re.T * scale
    right_b[:P_SIZE, B : 2 * B] = c_im.T * scale
    right_b[P_SIZE:, :B] = -c_im.T * scale
    right_b[P_SIZE:, B : 2 * B] = c_re.T * scale
    ct_re = c_re.T
    ct_im = c_im.T
    right_c = np.zeros((2 * P_SIZE, 128))
    for col, (top, bottom) in enumerate(
        ((ct_re, -ct_im), (ct_im, ct_re), (ct_im, ct_re), (ct_re, -ct_im))
    ):
        right_c[:P_SIZE, col * B : (col + 1) * B] = top
        right_c[P_SIZE:, col * B : (col + 1) * B] = bottom
    a_hi, a_mid, a_lo = table_three(left_a[:, : 2 * B])
    left_three = np.concatenate([a_hi, a_hi, a_mid, a_hi, a_lo, a_mid], axis=1)
    b_hi, b_mid, b_lo = table_three(right_b)
    right_hm = np.concatenate([b_hi, b_mid], axis=1)
    right_lh = np.concatenate([b_lo, b_hi], axis=0)
    plain = (c_re, c_im, c_re.T, c_im.T, right_w[:B], right_w[B : 2 * B], right_c)
    out = [jnp.asarray(table, jnp.float32) for table in plain]
    return out + [jnp.asarray(table) for table in (left_three, right_hm, right_lh)]


def imaging_body(
    pos_ref, im_ref, sh_ref, w_ref, dose_ref, t_ref, ev_ref, goal_ref, h_ref, hc_ref,
    c_re_ref, c_im_ref, ct_re_ref, ct_im_ref, rw_top, rw_bot, rc_ref, la_ref, rhm_ref, rlh_ref,
    slots_ref, f_buf, i_buf, u_buf,
):
    count = f_buf.shape[0]
    local_tiles = goal_ref.shape[0]
    pos = pos_ref[0]
    master = im_ref[pos]
    pick0 = (lax.broadcasted_iota(jnp.int32, (P_SIZE, 128), 0) == sh_ref[2 * pos]).astype(jnp.float32)
    pick1 = (lax.broadcasted_iota(jnp.int32, (8, P_SIZE), 1) == sh_ref[2 * pos + 1]).astype(jnp.float32)
    e0_re = dot_full(c_re_ref[...], pick0)[:, 0:1]
    e0_im = dot_full(c_im_ref[...], pick0)[:, 0:1]
    e1_re = dot_full(pick1, ct_re_ref[...])[0:1, :]
    e1_im = dot_full(pick1, ct_im_ref[...])[0:1, :]
    ph_re = e0_re * e1_re - e0_im * e1_im
    ph_im = e0_re * e1_im + e0_im * e1_re
    m_re = ev_ref[master, 0]
    m_im = ev_ref[master, 1]
    s_re = t_ref[pos, 0] + (ph_re * m_re - ph_im * m_im)
    s_im = t_ref[pos, 1] + (ph_re * m_im + ph_im * m_re)
    i_buf[...] = jnp.zeros(i_buf.shape, jnp.float32)

    def forward(k, carry):
        h_re = h_ref[k, 0]
        h_im = h_ref[k, 1]
        x_re = h_re * s_re - h_im * s_im
        x_im = h_re * s_im + h_im * s_re
        rows = dot_full(x_re, rw_top[...]) + dot_full(x_im, rw_bot[...])
        swap = jnp.concatenate([-rows[:, P_SIZE:], rows[:, :P_SIZE]], axis=1)
        s_hi, s_mid, s_lo = split_three(jnp.concatenate([rows, swap], axis=0))
        stacked = jnp.concatenate([s_hi, s_mid, s_hi, s_lo, s_hi, s_mid], axis=0)
        field = dot_parts(la_ref[...], stacked)
        f_buf[k] = field
        power = field * field
        i_buf[...] += w_ref[k] * (power[:, :P_SIZE] + power[:, P_SIZE:])
        return carry

    lax.fori_loop(0, count, forward, 0)
    dose = dose_ref[0]
    resist = 1.0 / (1.0 + jnp.exp(-(steepness * (dose * i_buf[...] - threshold))))
    goal = goal_ref[pos].astype(jnp.float32)
    i_buf[...] = 2.0 * (resist - goal) * resist * (1.0 - resist) * steepness * dose

    def backward(k, carry):
        sens = i_buf[...]
        weighted = f_buf[k] * jnp.concatenate([sens, sens], axis=1)
        q_hi, q_mid, q_lo = split_three(weighted)
        first = dot_parts(q_hi, rhm_ref[...]) + dot_parts(q_mid, rhm_ref[...])
        rest = dot_parts(jnp.concatenate([q_hi, q_lo], axis=1), rlh_ref[...])
        half = first[:, :128] + first[:, 128:] + rest
        flip = half.T
        u_buf[pl.ds(pl.multiple_of(k * B, B), B), :] = jnp.concatenate([flip[:B], flip[B : 2 * B]], axis=1)
        return carry

    lax.fori_loop(0, count, backward, 0)
    out = dot_full(u_buf[...], rc_ref[...])
    acc = jnp.sum((hc_ref[...] * out).reshape(count, B, 128), axis=0)
    flip = jnp.concatenate([acc, jnp.zeros((128 - B, 128), jnp.float32)], axis=0).T
    g_re = flip[0:B, 0:B] + flip[2 * B : 3 * B, 0:B]
    g_im = flip[B : 2 * B, 0:B] + flip[3 * B : 4 * B, 0:B]
    slots_ref[...] = jnp.zeros(slots_ref.shape, jnp.float32)
    slots_ref[pos, 0] = g_re
    slots_ref[pos, 1] = g_im
    slots_ref[local_tiles + master, 0] = ph_re * g_re + ph_im * g_im
    slots_ref[local_tiles + master, 1] = ph_re * g_im - ph_im * g_re


def imaging(pos, inst_master, inst_shift, weights, dose, tile_spec, every, target, kerns, h_cat):
    count = weights.shape[0]
    tables = imaging_tables()
    slots = target.shape[0] + every.shape[0]
    vmem = pl.BlockSpec(memory_space=pltpu.VMEM)
    smem = pl.BlockSpec(memory_space=pltpu.SMEM)
    return pl.pallas_call(
        imaging_body,
        out_shape=jax.ShapeDtypeStruct((slots, 2, B, B), jnp.float32),
        in_specs=[smem] * 5 + [vmem] * 5 + [vmem] * len(tables),
        out_specs=vmem,
        scratch_shapes=[
            pltpu.VMEM((count, P_SIZE, 2 * P_SIZE), jnp.float32),
            pltpu.VMEM((P_SIZE, P_SIZE), jnp.float32),
            pltpu.VMEM((count * B, 2 * P_SIZE), jnp.float32),
        ],
    )(pos, inst_master, inst_shift, weights, dose, tile_spec, every, target, kerns, h_cat, *tables)


def xor_partners(count):
    return count & (count - 1) == 0 and count <= 8


def gather_all(x, axis, count, pos):
    if not xor_partners(count):
        return lax.all_gather(x, axis, axis=0, tiled=True)
    size = x.shape[0]
    slot = jnp.arange(count * size, dtype=jnp.int32) // size
    total = jnp.where((slot == pos)[:, None, None, None], jnp.tile(x, (count, 1, 1, 1)), 0.0)
    for step in range(1, count):
        got = lax.ppermute(x, axis, [(i, i ^ step) for i in range(count)])
        hit = (slot == (pos ^ step))[:, None, None, None]
        total = total + jnp.where(hit, jnp.tile(got, (count, 1, 1, 1)), 0.0)
    return total


def sum_all(x, axis, count, pos):
    if not xor_partners(count):
        return lax.psum(x, axis)
    step = 1
    while step < count:
        x = x + lax.ppermute(x, axis, [(i, i ^ step) for i in range(count)])
        step *= 2
    return x


def scatter_sum(x, axis, count, pos, size):
    if not xor_partners(count):
        return lax.psum_scatter(x, axis, scatter_dimension=0, tiled=True)
    total = lax.dynamic_slice_in_dim(x, pos * size, size, 0)
    for step in range(1, count):
        part = lax.dynamic_slice_in_dim(x, (pos ^ step) * size, size, 0)
        total = total + lax.ppermute(part, axis, [(i, i ^ step) for i in range(count)])
    return total


def partner_lists(count, kern_count):
    lists = [[] for _ in range(kern_count)]
    for step in range(1, count):
        lists[step % kern_count].append(step)
    return lists


def chosen_step(lists, round_index, kern_pos):
    pick = jnp.int32(-1)
    for k, steps in enumerate(lists):
        if round_index < len(steps):
            pick = jnp.where(kern_pos == k, jnp.int32(steps[round_index]), pick)
    return pick


def gather_split(x, count, pos, kern_count, kern_pos):
    size = x.shape[0]
    lists = partner_lists(count, kern_count)
    slot = jnp.arange(count * size, dtype=jnp.int32) // size
    spread = lambda part: jnp.tile(part, (count, 1, 1, 1))
    collected = jnp.zeros((count * size,) + x.shape[1:], x.dtype)
    for r in range(max(len(steps) for steps in lists)):
        pairs = []
        for k, steps in enumerate(lists):
            if r < len(steps):
                pairs += [((t ^ steps[r]) * kern_count + k, t * kern_count + k) for t in range(count)]
        got = lax.ppermute(x, ("tile", "kern"), pairs)
        step = chosen_step(lists, r, kern_pos)
        source = jnp.where(step >= 0, pos ^ step, -1)
        collected = collected + jnp.where((slot == source)[:, None, None, None], spread(got), 0.0)
    collected = sum_all(collected, "kern", kern_count, kern_pos)
    return collected + jnp.where((slot == pos)[:, None, None, None], spread(x), 0.0)


def scatter_split(x, count, pos, kern_count, kern_pos, size):
    lists = partner_lists(count, kern_count)
    own = lax.dynamic_slice_in_dim(x, pos * size, size, 0)
    total = jnp.where(kern_pos == 0, own, 0.0)
    for r in range(max(len(steps) for steps in lists)):
        pairs = []
        for k, steps in enumerate(lists):
            if r < len(steps):
                pairs += [(t * kern_count + k, (t ^ steps[r]) * kern_count + k) for t in range(count)]
        step = chosen_step(lists, r, kern_pos)
        target = jnp.where(step >= 0, pos ^ step, 0)
        part = lax.dynamic_slice_in_dim(x, target * size, size, 0)
        total = total + lax.ppermute(part, ("tile", "kern"), pairs)
    return sum_all(total, "kern", kern_count, kern_pos)


def on_device(
    tile_mask, master_mask, target, inst_master, inst_shift, kernels, kernel_weight, corner_dose
):
    cos_tab, sin_tab = band_tables()
    scale = 1.0 / (P_SIZE * P_SIZE)
    local_tiles = tile_mask.shape[0]
    local_masters = master_mask.shape[0]
    tile_count = lax.axis_size("tile")
    tile_pos = lax.axis_index("tile")
    kern_count = lax.axis_size("kern")
    kern_pos = lax.axis_index("kern")
    per_dev = local_tiles // kern_count
    first = kern_pos * per_dev
    region_tiles = tile_count * local_tiles
    region_masters = tile_count * local_masters

    with jax.named_scope("master_spectra"):
        own_re, own_im = spectra(master_mask.astype(jnp.float32), cos_tab, sin_tab)
        own = jnp.stack([own_re, own_im], axis=1)
        if xor_partners(tile_count) and xor_partners(kern_count) and tile_count > 2:
            every = gather_split(own, tile_count, tile_pos, kern_count, kern_pos)
        else:
            every = gather_all(own, "tile", tile_count, tile_pos)

    with jax.named_scope("tile_spectra"):
        tile_re, tile_im = spectra(tile_mask.astype(jnp.float32), cos_tab, sin_tab)
        tile_spec = jnp.stack([tile_re, tile_im], axis=1)

    dose = corner_dose[0]
    kerns = kernels[0]
    h_re = kerns[:, 0]
    h_im = kerns[:, 1]
    weights = kernel_weight[0]

    with jax.named_scope("imaging_kernel"):
        count = h_re.shape[0]
        twice = (2.0 * weights)[:, None, None]
        ht_re = jnp.swapaxes(h_re, 1, 2) * twice
        ht_im = jnp.swapaxes(h_im, 1, 2) * twice
        h_cat = jnp.concatenate([ht_re, ht_re, ht_im, -ht_im], axis=-1).reshape(count * B, 128)
        shifts = inst_shift.reshape(-1)
        slots = None
        for j in range(per_dev):
            pos = jnp.reshape(first + j, (1,)).astype(jnp.int32)
            part = imaging(
                pos, inst_master, shifts, weights, corner_dose, tile_spec, every, target, kerns, h_cat
            )
            slots = part if slots is None else slots + part

    with jax.named_scope("gradient_exchange"):
        corner_count = lax.axis_size("corner")
        slots = sum_all(slots, "kern", kern_count, kern_pos)
        slots = sum_all(slots, "corner", corner_count, lax.axis_index("corner"))
        mine_tiles = slots[:local_tiles]
        terms = slots[local_tiles:]
        if xor_partners(tile_count) and xor_partners(kern_count) and tile_count > 2:
            mine_masters = scatter_split(terms, tile_count, tile_pos, kern_count, kern_pos, local_masters)
        else:
            mine_masters = scatter_sum(terms, "tile", tile_count, tile_pos, local_masters)

    with jax.named_scope("pixel_gradients"):
        tile_grad = back_pixels(mine_tiles[:, 0], mine_tiles[:, 1], cos_tab, sin_tab)
        master_grad = back_pixels(mine_masters[:, 0], mine_masters[:, 1], cos_tab, sin_tab)
    return (tile_grad, master_grad)


def solution(mesh):
    return jax.shard_map(
        on_device,
        mesh=mesh,
        in_specs=(
            P(("region", "tile"), None, None),
            P(("region", "tile"), None, None),
            P(("region", "tile"), None, None),
            P(("region", "tile")),
            P(("region", "tile"), None),
            P("corner", None, None, None, None),
            P("corner", None),
            P("corner"),
        ),
        out_specs=(P(("region", "tile"), None, None), P(("region", "tile"), None, None)),
        check_vma=False,
    )
```

```python
import math

import numpy as np
import jax
import jax.numpy as jnp
from jax import lax
from jax.sharding import PartitionSpec as P
from jax.experimental import pallas as pl
from jax.experimental.pallas import tpu as pltpu

P_SIZE = 256
B = 32


precise = lax.Precision.HIGHEST
steepness = 3.0
threshold = 1.0


def band_tables():
    freq = np.arange(B, dtype=np.int64) - B // 2
    pixel = np.arange(P_SIZE, dtype=np.int64)
    angle = (2.0 * math.pi / P_SIZE) * np.mod(freq[:, None] * pixel[None, :], P_SIZE).astype(np.float64)
    return (jnp.asarray(np.cos(angle), jnp.float32), jnp.asarray(-np.sin(angle), jnp.float32))


def phase_ramp(shift):
    freq = jnp.arange(B, dtype=jnp.int32) - B // 2
    total = (
        freq[None, :, None] * shift[:, 0][:, None, None]
        + freq[None, None, :] * shift[:, 1][:, None, None]
    )
    angle = 2.0 * math.pi / P_SIZE * jnp.mod(total, P_SIZE).astype(jnp.float32)
    return (jnp.cos(angle), -jnp.sin(angle))


def spectra(masks, cos_tab, sin_tab):
    rows_re = jnp.einsum("bx,nxy->nby", cos_tab, masks, precision=precise)
    rows_im = jnp.einsum("bx,nxy->nby", sin_tab, masks, precision=precise)
    spec_re = jnp.einsum("nby,cy->nbc", rows_re, cos_tab, precision=precise) - jnp.einsum(
        "nby,cy->nbc", rows_im, sin_tab, precision=precise
    )
    spec_im = jnp.einsum("nby,cy->nbc", rows_re, sin_tab, precision=precise) + jnp.einsum(
        "nby,cy->nbc", rows_im, cos_tab, precision=precise
    )
    return (spec_re, spec_im)


def back_pixels(x_re, x_im, cos_tab, sin_tab):
    half_re = jnp.einsum("bx,nbc->nxc", cos_tab, x_re, precision=precise) + jnp.einsum(
        "bx,nbc->nxc", sin_tab, x_im, precision=precise
    )
    half_im = jnp.einsum("bx,nbc->nxc", cos_tab, x_im, precision=precise) - jnp.einsum(
        "bx,nbc->nxc", sin_tab, x_re, precision=precise
    )
    return jnp.einsum("nxc,cy->nxy", half_re, cos_tab, precision=precise) + jnp.einsum(
        "nxc,cy->nxy", half_im, sin_tab, precision=precise
    )


def dot_full(a, b):
    return jnp.dot(a, b, precision=precise, preferred_element_type=jnp.float32)


def dot_parts(a, b):
    return jnp.dot(a, b, preferred_element_type=jnp.float32)


def split_three(a):
    hi = a.astype(jnp.bfloat16)
    rest = a - hi.astype(jnp.float32)
    mid = rest.astype(jnp.bfloat16)
    lo = (rest - mid.astype(jnp.float32)).astype(jnp.bfloat16)
    return hi, mid, lo


def table_three(table):
    hi = table.astype(jnp.bfloat16)
    rest = table - hi.astype(np.float64)
    mid = rest.astype(jnp.bfloat16)
    lo = (rest - mid.astype(np.float64)).astype(jnp.bfloat16)
    return hi, mid, lo


def imaging_tables():
    freq = np.arange(B, dtype=np.int64) - B // 2
    pixel = np.arange(P_SIZE, dtype=np.int64)
    angle = (2.0 * math.pi / P_SIZE) * np.mod(freq[:, None] * pixel[None, :], P_SIZE).astype(np.float64)
    c_re = np.cos(angle)
    c_im = -np.sin(angle)
    scale = 1.0 / (P_SIZE * P_SIZE)
    right_w = np.zeros((128, 2 * P_SIZE))
    right_w[:B, :P_SIZE] = c_re
    right_w[:B, P_SIZE:] = -c_im
    right_w[B : 2 * B, :P_SIZE] = c_im
    right_w[B : 2 * B, P_SIZE:] = c_re
    left_a = np.zeros((P_SIZE, 128))
    left_a[:, :B] = c_re.T * scale
    left_a[:, B : 2 * B] = -c_im.T * scale
    right_b = np.zeros((2 * P_SIZE, 128))
    right_b[:P_SIZE, :B] = c_re.T * scale
    right_b[:P_SIZE, B : 2 * B] = c_im.T * scale
    right_b[P_SIZE:, :B] = -c_im.T * scale
    right_b[P_SIZE:, B : 2 * B] = c_re.T * scale
    ct_re = c_re.T
    ct_im = c_im.T
    right_c = np.zeros((2 * P_SIZE, 128))
    for col, (top, bottom) in enumerate(
        ((ct_re, -ct_im), (ct_im, ct_re), (ct_im, ct_re), (ct_re, -ct_im))
    ):
        right_c[:P_SIZE, col * B : (col + 1) * B] = top
        right_c[P_SIZE:, col * B : (col + 1) * B] = bottom
    a_hi, a_mid, a_lo = table_three(left_a[:, : 2 * B])
    left_three = np.concatenate([a_hi, a_hi, a_mid, a_hi, a_lo, a_mid], axis=1)
    b_hi, b_mid, b_lo = table_three(right_b)
    right_hm = np.concatenate([b_hi, b_mid], axis=1)
    right_lh = np.concatenate([b_lo, b_hi], axis=0)
    plain = (c_re, c_im, c_re.T, c_im.T, right_w[:B], right_w[B : 2 * B], right_c)
    out = [jnp.asarray(table, jnp.float32) for table in plain]
    return out + [jnp.asarray(table) for table in (left_three, right_hm, right_lh)]


def imaging_body(
    pos_ref, im_ref, sh_ref, w_ref, dose_ref, t_ref, ev_ref, goal_ref, h_ref, hc_ref,
    c_re_ref, c_im_ref, ct_re_ref, ct_im_ref, rw_top, rw_bot, rc_ref, la_ref, rhm_ref, rlh_ref,
    slots_ref, f_buf, i_buf, u_buf, w_buf, xr_buf, xi_buf,
):
    count = f_buf.shape[0]
    pos = pos_ref[0]
    master = im_ref[pos]
    pick0 = (lax.broadcasted_iota(jnp.int32, (P_SIZE, 128), 0) == sh_ref[2 * pos]).astype(jnp.float32)
    pick1 = (lax.broadcasted_iota(jnp.int32, (8, P_SIZE), 1) == sh_ref[2 * pos + 1]).astype(jnp.float32)
    e0_re = dot_full(c_re_ref[...], pick0)[:, 0:1]
    e0_im = dot_full(c_im_ref[...], pick0)[:, 0:1]
    e1_re = dot_full(pick1, ct_re_ref[...])[0:1, :]
    e1_im = dot_full(pick1, ct_im_ref[...])[0:1, :]
    ph_re = e0_re * e1_re - e0_im * e1_im
    ph_im = e0_re * e1_im + e0_im * e1_re
    m_re = ev_ref[master, 0]
    m_im = ev_ref[master, 1]
    s_re = t_ref[pos, 0] + (ph_re * m_re - ph_im * m_im)
    s_im = t_ref[pos, 1] + (ph_re * m_im + ph_im * m_re)
    i_buf[...] = jnp.zeros(i_buf.shape, jnp.float32)

    def spectrum(k, carry):
        h_re = h_ref[k, 0]
        h_im = h_ref[k, 1]
        rows = pl.ds(pl.multiple_of(k * B, B), B)
        xr_buf[rows, :] = h_re * s_re - h_im * s_im
        xi_buf[rows, :] = h_re * s_im + h_im * s_re
        return carry

    lax.fori_loop(0, count, spectrum, 0)
    w_buf[...] = dot_full(xr_buf[...], rw_top[...]) + dot_full(xi_buf[...], rw_bot[...])

    def forward(k, carry):
        rows = w_buf[pl.ds(pl.multiple_of(k * B, B), B), :]
        swap = jnp.concatenate([-rows[:, P_SIZE:], rows[:, :P_SIZE]], axis=1)
        s_hi, s_mid, s_lo = split_three(jnp.concatenate([rows, swap], axis=0))
        stacked = jnp.concatenate([s_hi, s_mid, s_hi, s_lo, s_hi, s_mid], axis=0)
        field = dot_parts(la_ref[...], stacked)
        f_buf[k] = field
        power = field * field
        i_buf[...] += w_ref[k] * (power[:, :P_SIZE] + power[:, P_SIZE:])
        return carry

    lax.fori_loop(0, count, forward, 0)
    dose = dose_ref[0]
    resist = 1.0 / (1.0 + jnp.exp(-(steepness * (dose * i_buf[...] - threshold))))
    goal = goal_ref[pos].astype(jnp.float32)
    i_buf[...] = 2.0 * (resist - goal) * resist * (1.0 - resist) * steepness * dose

    def backward(k, carry):
        sens = i_buf[...]
        weighted = f_buf[k] * jnp.concatenate([sens, sens], axis=1)
        q_hi, q_mid, q_lo = split_three(weighted)
        first = dot_parts(q_hi, rhm_ref[...]) + dot_parts(q_mid, rhm_ref[...])
        rest = dot_parts(jnp.concatenate([q_hi, q_lo], axis=1), rlh_ref[...])
        half = first[:, :128] + first[:, 128:] + rest
        flip = half.T
        u_buf[pl.ds(pl.multiple_of(k * B, B), B), :] = jnp.concatenate([flip[:B], flip[B : 2 * B]], axis=1)
        return carry

    lax.fori_loop(0, count, backward, 0)
    out = dot_full(u_buf[...], rc_ref[...])
    acc = jnp.sum((hc_ref[...] * out).reshape(count, B, 128), axis=0)
    flip = jnp.concatenate([acc, jnp.zeros((128 - B, 128), jnp.float32)], axis=0).T
    g_re = flip[0:B, 0:B] + flip[2 * B : 3 * B, 0:B]
    g_im = flip[B : 2 * B, 0:B] + flip[3 * B : 4 * B, 0:B]
    slots_ref[0] = g_re
    slots_ref[1] = g_im
    slots_ref[2] = ph_re * g_re + ph_im * g_im
    slots_ref[3] = ph_re * g_im - ph_im * g_re


def imaging(pos, inst_master, inst_shift, weights, dose, tile_spec, every, target, kerns, h_cat):
    count = weights.shape[0]
    tables = imaging_tables()
    vmem = pl.BlockSpec(memory_space=pltpu.VMEM)
    smem = pl.BlockSpec(memory_space=pltpu.SMEM)
    return pl.pallas_call(
        imaging_body,
        out_shape=jax.ShapeDtypeStruct((4, B, B), jnp.float32),
        in_specs=[smem] * 5 + [vmem] * 5 + [vmem] * len(tables),
        out_specs=vmem,
        scratch_shapes=[
            pltpu.VMEM((count, P_SIZE, 2 * P_SIZE), jnp.float32),
            pltpu.VMEM((P_SIZE, P_SIZE), jnp.float32),
            pltpu.VMEM((count * B, 2 * P_SIZE), jnp.float32),
            pltpu.VMEM((count * B, 2 * P_SIZE), jnp.float32),
            pltpu.VMEM((count * B, B), jnp.float32),
            pltpu.VMEM((count * B, B), jnp.float32),
        ],
    )(pos, inst_master, inst_shift, weights, dose, tile_spec, every, target, kerns, h_cat, *tables)


def xor_partners(count):
    return count & (count - 1) == 0 and count <= 8


def gather_all(x, axis, count, pos):
    if not xor_partners(count):
        return lax.all_gather(x, axis, axis=0, tiled=True)
    size = x.shape[0]
    slot = jnp.arange(count * size, dtype=jnp.int32) // size
    total = jnp.where((slot == pos)[:, None, None, None], jnp.tile(x, (count, 1, 1, 1)), 0.0)
    for step in range(1, count):
        got = lax.ppermute(x, axis, [(i, i ^ step) for i in range(count)])
        hit = (slot == (pos ^ step))[:, None, None, None]
        total = total + jnp.where(hit, jnp.tile(got, (count, 1, 1, 1)), 0.0)
    return total


def sum_all(x, axis, count, pos):
    if not xor_partners(count):
        return lax.psum(x, axis)
    step = 1
    while step < count:
        x = x + lax.ppermute(x, axis, [(i, i ^ step) for i in range(count)])
        step *= 2
    return x


def scatter_sum(x, axis, count, pos, size):
    if not xor_partners(count):
        return lax.psum_scatter(x, axis, scatter_dimension=0, tiled=True)
    total = lax.dynamic_slice_in_dim(x, pos * size, size, 0)
    for step in range(1, count):
        part = lax.dynamic_slice_in_dim(x, (pos ^ step) * size, size, 0)
        total = total + lax.ppermute(part, axis, [(i, i ^ step) for i in range(count)])
    return total


def partner_lists(count, kern_count):
    lists = [[] for _ in range(kern_count)]
    for step in range(1, count):
        lists[step % kern_count].append(step)
    return lists


def chosen_step(lists, round_index, kern_pos):
    pick = jnp.int32(-1)
    for k, steps in enumerate(lists):
        if round_index < len(steps):
            pick = jnp.where(kern_pos == k, jnp.int32(steps[round_index]), pick)
    return pick


def gather_split(x, count, pos, kern_count, kern_pos):
    size = x.shape[0]
    lists = partner_lists(count, kern_count)
    slot = jnp.arange(count * size, dtype=jnp.int32) // size
    spread = lambda part: jnp.tile(part, (count, 1, 1, 1))
    collected = jnp.zeros((count * size,) + x.shape[1:], x.dtype)
    for r in range(max(len(steps) for steps in lists)):
        pairs = []
        for k, steps in enumerate(lists):
            if r < len(steps):
                pairs += [((t ^ steps[r]) * kern_count + k, t * kern_count + k) for t in range(count)]
        got = lax.ppermute(x, ("tile", "kern"), pairs)
        step = chosen_step(lists, r, kern_pos)
        source = jnp.where(step >= 0, pos ^ step, -1)
        collected = collected + jnp.where((slot == source)[:, None, None, None], spread(got), 0.0)
    collected = sum_all(collected, "kern", kern_count, kern_pos)
    return collected + jnp.where((slot == pos)[:, None, None, None], spread(x), 0.0)


def scatter_split(x, count, pos, kern_count, kern_pos, size):
    lists = partner_lists(count, kern_count)
    own = lax.dynamic_slice_in_dim(x, pos * size, size, 0)
    total = jnp.where(kern_pos == 0, own, 0.0)
    for r in range(max(len(steps) for steps in lists)):
        pairs = []
        for k, steps in enumerate(lists):
            if r < len(steps):
                pairs += [(t * kern_count + k, (t ^ steps[r]) * kern_count + k) for t in range(count)]
        step = chosen_step(lists, r, kern_pos)
        target = jnp.where(step >= 0, pos ^ step, 0)
        part = lax.dynamic_slice_in_dim(x, target * size, size, 0)
        total = total + lax.ppermute(part, ("tile", "kern"), pairs)
    return sum_all(total, "kern", kern_count, kern_pos)


def on_device(
    tile_mask, master_mask, target, inst_master, inst_shift, kernels, kernel_weight, corner_dose
):
    cos_tab, sin_tab = band_tables()
    scale = 1.0 / (P_SIZE * P_SIZE)
    local_tiles = tile_mask.shape[0]
    local_masters = master_mask.shape[0]
    tile_count = lax.axis_size("tile")
    tile_pos = lax.axis_index("tile")
    kern_count = lax.axis_size("kern")
    kern_pos = lax.axis_index("kern")
    per_dev = local_tiles // kern_count
    first = kern_pos * per_dev
    region_tiles = tile_count * local_tiles
    region_masters = tile_count * local_masters

    with jax.named_scope("master_spectra"):
        own_re, own_im = spectra(master_mask.astype(jnp.float32), cos_tab, sin_tab)
        own = jnp.stack([own_re, own_im], axis=1)
        if xor_partners(tile_count) and xor_partners(kern_count) and tile_count > 2:
            every = gather_split(own, tile_count, tile_pos, kern_count, kern_pos)
        else:
            every = gather_all(own, "tile", tile_count, tile_pos)

    with jax.named_scope("tile_spectra"):
        tile_re, tile_im = spectra(tile_mask.astype(jnp.float32), cos_tab, sin_tab)
        tile_spec = jnp.stack([tile_re, tile_im], axis=1)

    dose = corner_dose[0]
    kerns = kernels[0]
    h_re = kerns[:, 0]
    h_im = kerns[:, 1]
    weights = kernel_weight[0]

    with jax.named_scope("imaging_kernel"):
        count = h_re.shape[0]
        twice = (2.0 * weights)[:, None, None]
        ht_re = jnp.swapaxes(h_re, 1, 2) * twice
        ht_im = jnp.swapaxes(h_im, 1, 2) * twice
        h_cat = jnp.concatenate([ht_re, ht_re, ht_im, -ht_im], axis=-1).reshape(count * B, 128)
        shifts = inst_shift.reshape(-1)
        parts = []
        for j in range(per_dev):
            pos = jnp.reshape(first + j, (1,)).astype(jnp.int32)
            parts.append(
                imaging(pos, inst_master, shifts, weights, corner_dose, tile_spec, every, target, kerns, h_cat)
            )
        comp = jnp.stack(parts)

    with jax.named_scope("gradient_exchange"):
        corner_count = lax.axis_size("corner")
        comp = sum_all(comp, "corner", corner_count, lax.axis_index("corner"))
        both = gather_all(comp, "kern", kern_count, kern_pos)
        mine_tiles = both[:, 0:2]
        owner_pick = (
            inst_master[:, None] == jnp.arange(region_masters, dtype=jnp.int32)[None, :]
        ).astype(jnp.float32)
        terms = jnp.sum(owner_pick[:, :, None, None, None] * both[:, None, 2:4], axis=0)
        if xor_partners(tile_count) and xor_partners(kern_count) and tile_count > 2:
            mine_masters = scatter_split(terms, tile_count, tile_pos, kern_count, kern_pos, local_masters)
        else:
            mine_masters = scatter_sum(terms, "tile", tile_count, tile_pos, local_masters)

    with jax.named_scope("pixel_gradients"):
        tile_grad = back_pixels(mine_tiles[:, 0], mine_tiles[:, 1], cos_tab, sin_tab)
        master_grad = back_pixels(mine_masters[:, 0], mine_masters[:, 1], cos_tab, sin_tab)
    return (tile_grad, master_grad)


def solution(mesh):
    return jax.shard_map(
        on_device,
        mesh=mesh,
        in_specs=(
            P(("region", "tile"), None, None),
            P(("region", "tile"), None, None),
            P(("region", "tile"), None, None),
            P(("region", "tile")),
            P(("region", "tile"), None),
            P("corner", None, None, None, None),
            P("corner", None),
            P("corner"),
        ),
        out_specs=(P(("region", "tile"), None, None), P(("region", "tile"), None, None)),
        check_vma=False,
    )
```

```python
import math

import numpy as np
import jax
import jax.numpy as jnp
from jax import lax
from jax.sharding import PartitionSpec as P
from jax.experimental import pallas as pl
from jax.experimental.pallas import tpu as pltpu

P_SIZE = 256
B = 32


precise = lax.Precision.HIGHEST
steepness = 3.0
threshold = 1.0


def band_tables():
    freq = np.arange(B, dtype=np.int64) - B // 2
    pixel = np.arange(P_SIZE, dtype=np.int64)
    angle = (2.0 * math.pi / P_SIZE) * np.mod(freq[:, None] * pixel[None, :], P_SIZE).astype(np.float64)
    return (jnp.asarray(np.cos(angle), jnp.float32), jnp.asarray(-np.sin(angle), jnp.float32))


def phase_ramp(shift):
    freq = jnp.arange(B, dtype=jnp.int32) - B // 2
    total = (
        freq[None, :, None] * shift[:, 0][:, None, None]
        + freq[None, None, :] * shift[:, 1][:, None, None]
    )
    angle = 2.0 * math.pi / P_SIZE * jnp.mod(total, P_SIZE).astype(jnp.float32)
    return (jnp.cos(angle), -jnp.sin(angle))


def spectra(masks, cos_tab, sin_tab):
    rows_re = jnp.einsum("bx,nxy->nby", cos_tab, masks, precision=precise)
    rows_im = jnp.einsum("bx,nxy->nby", sin_tab, masks, precision=precise)
    spec_re = jnp.einsum("nby,cy->nbc", rows_re, cos_tab, precision=precise) - jnp.einsum(
        "nby,cy->nbc", rows_im, sin_tab, precision=precise
    )
    spec_im = jnp.einsum("nby,cy->nbc", rows_re, sin_tab, precision=precise) + jnp.einsum(
        "nby,cy->nbc", rows_im, cos_tab, precision=precise
    )
    return (spec_re, spec_im)


def back_pixels(x_re, x_im, cos_tab, sin_tab):
    half_re = jnp.einsum("bx,nbc->nxc", cos_tab, x_re, precision=precise) + jnp.einsum(
        "bx,nbc->nxc", sin_tab, x_im, precision=precise
    )
    half_im = jnp.einsum("bx,nbc->nxc", cos_tab, x_im, precision=precise) - jnp.einsum(
        "bx,nbc->nxc", sin_tab, x_re, precision=precise
    )
    return jnp.einsum("nxc,cy->nxy", half_re, cos_tab, precision=precise) + jnp.einsum(
        "nxc,cy->nxy", half_im, sin_tab, precision=precise
    )


def dot_full(a, b):
    return jnp.dot(a, b, precision=precise, preferred_element_type=jnp.float32)


def dot_parts(a, b):
    return jnp.dot(a, b, preferred_element_type=jnp.float32)


def split_three(a):
    hi = a.astype(jnp.bfloat16)
    rest = a - hi.astype(jnp.float32)
    mid = rest.astype(jnp.bfloat16)
    lo = (rest - mid.astype(jnp.float32)).astype(jnp.bfloat16)
    return hi, mid, lo


def table_three(table):
    hi = table.astype(jnp.bfloat16)
    rest = table - hi.astype(np.float64)
    mid = rest.astype(jnp.bfloat16)
    lo = (rest - mid.astype(np.float64)).astype(jnp.bfloat16)
    return hi, mid, lo


def imaging_tables():
    freq = np.arange(B, dtype=np.int64) - B // 2
    pixel = np.arange(P_SIZE, dtype=np.int64)
    angle = (2.0 * math.pi / P_SIZE) * np.mod(freq[:, None] * pixel[None, :], P_SIZE).astype(np.float64)
    c_re = np.cos(angle)
    c_im = -np.sin(angle)
    scale = 1.0 / (P_SIZE * P_SIZE)
    right_w = np.zeros((128, 2 * P_SIZE))
    right_w[:B, :P_SIZE] = c_re
    right_w[:B, P_SIZE:] = -c_im
    right_w[B : 2 * B, :P_SIZE] = c_im
    right_w[B : 2 * B, P_SIZE:] = c_re
    left_a = np.zeros((P_SIZE, 128))
    left_a[:, :B] = c_re.T * scale
    left_a[:, B : 2 * B] = -c_im.T * scale
    right_b = np.zeros((2 * P_SIZE, 128))
    right_b[:P_SIZE, :B] = c_re.T * scale
    right_b[:P_SIZE, B : 2 * B] = c_im.T * scale
    right_b[P_SIZE:, :B] = -c_im.T * scale
    right_b[P_SIZE:, B : 2 * B] = c_re.T * scale
    ct_re = c_re.T
    ct_im = c_im.T
    right_c = np.zeros((2 * P_SIZE, 128))
    for col, (top, bottom) in enumerate(
        ((ct_re, -ct_im), (ct_im, ct_re), (ct_im, ct_re), (ct_re, -ct_im))
    ):
        right_c[:P_SIZE, col * B : (col + 1) * B] = top
        right_c[P_SIZE:, col * B : (col + 1) * B] = bottom
    a_hi, a_mid, a_lo = table_three(left_a[:, : 2 * B])
    left_three = np.concatenate([a_hi, a_hi, a_mid, a_hi, a_lo, a_mid], axis=1)
    b_hi, b_mid, b_lo = table_three(right_b)
    right_hm = np.concatenate([b_hi, b_mid], axis=1)
    right_lh = np.concatenate([b_lo, b_hi], axis=0)
    plain = (c_re, c_im, c_re.T, c_im.T, right_w[:B], right_w[B : 2 * B], right_c)
    out = [jnp.asarray(table, jnp.float32) for table in plain]
    return out + [jnp.asarray(table) for table in (left_three, right_hm, right_lh)]


def imaging_body(
    pos_ref, im_ref, sh_ref, w_ref, dose_ref, t_ref, ev_ref, own_ref, goal_ref, h_ref, hc_ref,
    c_re_ref, c_im_ref, ct_re_ref, ct_im_ref, rw_top, rw_bot, rc_ref, la_ref, rhm_ref, rlh_ref,
    slots_ref, f_buf, i_buf, u_buf, w_buf, xr_buf, xi_buf,
):
    count = f_buf.shape[0]
    pos = pos_ref[0]
    master = im_ref[pos]
    pick0 = (lax.broadcasted_iota(jnp.int32, (P_SIZE, 128), 0) == sh_ref[pos, 0]).astype(jnp.float32)
    pick1 = (lax.broadcasted_iota(jnp.int32, (8, P_SIZE), 1) == sh_ref[pos, 1]).astype(jnp.float32)
    e0_re = dot_full(c_re_ref[...], pick0)[:, 0:1]
    e0_im = dot_full(c_im_ref[...], pick0)[:, 0:1]
    e1_re = dot_full(pick1, ct_re_ref[...])[0:1, :]
    e1_im = dot_full(pick1, ct_im_ref[...])[0:1, :]
    ph_re = e0_re * e1_re - e0_im * e1_im
    ph_im = e0_re * e1_im + e0_im * e1_re
    local_masters = own_ref.shape[0]
    is_own = master // local_masters == pos_ref[1]
    m_re = ev_ref[master, 0] + jnp.where(is_own, own_ref[master % local_masters, 0], 0.0)
    m_im = ev_ref[master, 1] + jnp.where(is_own, own_ref[master % local_masters, 1], 0.0)
    s_re = t_ref[pos, 0] + (ph_re * m_re - ph_im * m_im)
    s_im = t_ref[pos, 1] + (ph_re * m_im + ph_im * m_re)
    i_buf[...] = jnp.zeros(i_buf.shape, jnp.float32)

    def spectrum(k, carry):
        h_re = h_ref[k, 0]
        h_im = h_ref[k, 1]
        rows = pl.ds(pl.multiple_of(k * B, B), B)
        xr_buf[rows, :] = h_re * s_re - h_im * s_im
        xi_buf[rows, :] = h_re * s_im + h_im * s_re
        return carry

    lax.fori_loop(0, count, spectrum, 0)
    w_buf[...] = dot_full(xr_buf[...], rw_top[...]) + dot_full(xi_buf[...], rw_bot[...])

    def forward(k, carry):
        rows = w_buf[pl.ds(pl.multiple_of(k * B, B), B), :]
        swap = jnp.concatenate([-rows[:, P_SIZE:], rows[:, :P_SIZE]], axis=1)
        s_hi, s_mid, s_lo = split_three(jnp.concatenate([rows, swap], axis=0))
        stacked = jnp.concatenate([s_hi, s_mid, s_hi, s_lo, s_hi, s_mid], axis=0)
        field = dot_parts(la_ref[...], stacked)
        f_buf[k] = field
        power = field * field
        i_buf[...] += w_ref[k] * (power[:, :P_SIZE] + power[:, P_SIZE:])
        return carry

    lax.fori_loop(0, count, forward, 0)
    dose = dose_ref[0]
    resist = 1.0 / (1.0 + jnp.exp(-(steepness * (dose * i_buf[...] - threshold))))
    goal = goal_ref[pos].astype(jnp.float32)
    i_buf[...] = 2.0 * (resist - goal) * resist * (1.0 - resist) * steepness * dose

    def backward(k, carry):
        sens = i_buf[...]
        weighted = f_buf[k] * jnp.concatenate([sens, sens], axis=1)
        q_hi, q_mid, q_lo = split_three(weighted)
        first = dot_parts(q_hi, rhm_ref[...]) + dot_parts(q_mid, rhm_ref[...])
        rest = dot_parts(jnp.concatenate([q_hi, q_lo], axis=1), rlh_ref[...])
        half = first[:, :128] + first[:, 128:] + rest
        flip = half.T
        u_buf[pl.ds(pl.multiple_of(k * B, B), B), :] = jnp.concatenate([flip[:B], flip[B : 2 * B]], axis=1)
        return carry

    lax.fori_loop(0, count, backward, 0)
    out = dot_full(u_buf[...], rc_ref[...])
    acc = jnp.sum((hc_ref[...] * out).reshape(count, B, 128), axis=0)
    flip = jnp.concatenate([acc, jnp.zeros((128 - B, 128), jnp.float32)], axis=0).T
    g_re = flip[0:B, 0:B] + flip[2 * B : 3 * B, 0:B]
    g_im = flip[B : 2 * B, 0:B] + flip[3 * B : 4 * B, 0:B]
    slots_ref[0] = g_re
    slots_ref[1] = g_im
    slots_ref[2] = ph_re * g_re + ph_im * g_im
    slots_ref[3] = ph_re * g_im - ph_im * g_re


def imaging(pos, inst_master, inst_shift, weights, dose, tile_spec, every, own, target, kerns, h_cat):
    count = weights.shape[0]
    tables = imaging_tables()
    vmem = pl.BlockSpec(memory_space=pltpu.VMEM)
    smem = pl.BlockSpec(memory_space=pltpu.SMEM)
    return pl.pallas_call(
        imaging_body,
        out_shape=jax.ShapeDtypeStruct((4, B, B), jnp.float32),
        in_specs=[smem] * 5 + [vmem] * 6 + [vmem] * len(tables),
        out_specs=vmem,
        scratch_shapes=[
            pltpu.VMEM((count, P_SIZE, 2 * P_SIZE), jnp.float32),
            pltpu.VMEM((P_SIZE, P_SIZE), jnp.float32),
            pltpu.VMEM((count * B, 2 * P_SIZE), jnp.float32),
            pltpu.VMEM((count * B, 2 * P_SIZE), jnp.float32),
            pltpu.VMEM((count * B, B), jnp.float32),
            pltpu.VMEM((count * B, B), jnp.float32),
        ],
    )(pos, inst_master, inst_shift, weights, dose, tile_spec, every, own, target, kerns, h_cat, *tables)


def pixel_body(x_ref, left_ref, c_re_ref, c_im_ref, out_ref):
    for n in range(out_ref.shape[0]):
        x_re = x_ref[n, 0]
        x_im = x_ref[n, 1]
        half_re = dot_full(left_ref[...], jnp.concatenate([x_re, x_im], axis=0))
        half_im = dot_full(left_ref[...], jnp.concatenate([x_im, -x_re], axis=0))
        out_ref[n] = dot_full(half_re, c_re_ref[...]) + dot_full(half_im, c_im_ref[...])


def pixels(x):
    freq = np.arange(B, dtype=np.int64) - B // 2
    pixel = np.arange(P_SIZE, dtype=np.int64)
    angle = (2.0 * math.pi / P_SIZE) * np.mod(freq[:, None] * pixel[None, :], P_SIZE).astype(np.float64)
    c_re = np.cos(angle)
    c_im = -np.sin(angle)
    left = np.concatenate([c_re.T, c_im.T], axis=1)
    tables = [jnp.asarray(table, jnp.float32) for table in (left, c_re, c_im)]
    vmem = pl.BlockSpec(memory_space=pltpu.VMEM)
    return pl.pallas_call(
        pixel_body,
        out_shape=jax.ShapeDtypeStruct((x.shape[0], P_SIZE, P_SIZE), jnp.float32),
        in_specs=[vmem] * 4,
        out_specs=vmem,
    )(x, *tables)


def xor_partners(count):
    return count & (count - 1) == 0 and count <= 8


def gather_all(x, axis, count, pos):
    if not xor_partners(count):
        return lax.all_gather(x, axis, axis=0, tiled=True)
    size = x.shape[0]
    slot = jnp.arange(count * size, dtype=jnp.int32) // size
    total = jnp.where((slot == pos)[:, None, None, None], jnp.tile(x, (count, 1, 1, 1)), 0.0)
    for step in range(1, count):
        got = lax.ppermute(x, axis, [(i, i ^ step) for i in range(count)])
        hit = (slot == (pos ^ step))[:, None, None, None]
        total = total + jnp.where(hit, jnp.tile(got, (count, 1, 1, 1)), 0.0)
    return total


def sum_all(x, axis, count, pos):
    if not xor_partners(count):
        return lax.psum(x, axis)
    step = 1
    while step < count:
        x = x + lax.ppermute(x, axis, [(i, i ^ step) for i in range(count)])
        step *= 2
    return x


def scatter_sum(x, axis, count, pos, size):
    if not xor_partners(count):
        return lax.psum_scatter(x, axis, scatter_dimension=0, tiled=True)
    total = lax.dynamic_slice_in_dim(x, pos * size, size, 0)
    for step in range(1, count):
        part = lax.dynamic_slice_in_dim(x, (pos ^ step) * size, size, 0)
        total = total + lax.ppermute(part, axis, [(i, i ^ step) for i in range(count)])
    return total


def partner_lists(count, kern_count):
    lists = [[] for _ in range(kern_count)]
    for step in range(1, count):
        lists[step % kern_count].append(step)
    return lists


def chosen_step(lists, round_index, kern_pos):
    pick = jnp.int32(-1)
    for k, steps in enumerate(lists):
        if round_index < len(steps):
            pick = jnp.where(kern_pos == k, jnp.int32(steps[round_index]), pick)
    return pick


def gather_split(x, count, pos, kern_count, kern_pos):
    size = x.shape[0]
    lists = partner_lists(count, kern_count)
    slot = jnp.arange(count * size, dtype=jnp.int32) // size
    spread = lambda part: jnp.tile(part, (count, 1, 1, 1))
    collected = jnp.zeros((count * size,) + x.shape[1:], x.dtype)
    for r in range(max(len(steps) for steps in lists)):
        pairs = []
        for k, steps in enumerate(lists):
            if r < len(steps):
                pairs += [((t ^ steps[r]) * kern_count + k, t * kern_count + k) for t in range(count)]
        got = lax.ppermute(x, ("tile", "kern"), pairs)
        step = chosen_step(lists, r, kern_pos)
        source = jnp.where(step >= 0, pos ^ step, -1)
        collected = collected + jnp.where((slot == source)[:, None, None, None], spread(got), 0.0)
    return sum_all(collected, "kern", kern_count, kern_pos)


def scatter_split(x, count, pos, kern_count, kern_pos, size):
    lists = partner_lists(count, kern_count)
    own = lax.dynamic_slice_in_dim(x, pos * size, size, 0)
    total = jnp.where(kern_pos == 0, own, 0.0)
    for r in range(max(len(steps) for steps in lists)):
        pairs = []
        for k, steps in enumerate(lists):
            if r < len(steps):
                pairs += [(t * kern_count + k, (t ^ steps[r]) * kern_count + k) for t in range(count)]
        step = chosen_step(lists, r, kern_pos)
        target = jnp.where(step >= 0, pos ^ step, 0)
        part = lax.dynamic_slice_in_dim(x, target * size, size, 0)
        total = total + lax.ppermute(part, ("tile", "kern"), pairs)
    return sum_all(total, "kern", kern_count, kern_pos)


def on_device(
    tile_mask, master_mask, target, inst_master, inst_shift, kernels, kernel_weight, corner_dose
):
    cos_tab, sin_tab = band_tables()
    scale = 1.0 / (P_SIZE * P_SIZE)
    local_tiles = tile_mask.shape[0]
    local_masters = master_mask.shape[0]
    tile_count = lax.axis_size("tile")
    tile_pos = lax.axis_index("tile")
    kern_count = lax.axis_size("kern")
    kern_pos = lax.axis_index("kern")
    per_dev = local_tiles // kern_count
    first = kern_pos * per_dev
    region_tiles = tile_count * local_tiles
    region_masters = tile_count * local_masters

    with jax.named_scope("master_spectra"):
        own_re, own_im = spectra(master_mask.astype(jnp.float32), cos_tab, sin_tab)
        own = jnp.stack([own_re, own_im], axis=1)
        if xor_partners(tile_count) and xor_partners(kern_count) and tile_count > 2:
            every = gather_split(own, tile_count, tile_pos, kern_count, kern_pos)
            own_part = own
        else:
            every = gather_all(own, "tile", tile_count, tile_pos)
            own_part = jnp.zeros_like(own)

    with jax.named_scope("tile_spectra"):
        tile_re, tile_im = spectra(tile_mask.astype(jnp.float32), cos_tab, sin_tab)
        tile_spec = jnp.stack([tile_re, tile_im], axis=1)

    dose = corner_dose[0]
    kerns = kernels[0]
    h_re = kerns[:, 0]
    h_im = kerns[:, 1]
    weights = kernel_weight[0]

    with jax.named_scope("imaging_kernel"):
        count = h_re.shape[0]
        twice = (2.0 * weights)[:, None, None]
        ht_re = jnp.swapaxes(h_re, 1, 2) * twice
        ht_im = jnp.swapaxes(h_im, 1, 2) * twice
        h_cat = jnp.concatenate([ht_re, ht_re, ht_im, -ht_im], axis=-1).reshape(count * B, 128)
        parts = []
        for j in range(per_dev):
            pos = jnp.stack([first + j, tile_pos]).astype(jnp.int32)
            parts.append(
                imaging(
                    pos, inst_master, inst_shift, weights, corner_dose, tile_spec, every, own_part, target,
                    kerns, h_cat,
                )
            )
        comp = jnp.stack(parts)

    with jax.named_scope("gradient_exchange"):
        corner_count = lax.axis_size("corner")
        comp = sum_all(comp, "corner", corner_count, lax.axis_index("corner"))
        both = gather_all(comp, "kern", kern_count, kern_pos)
        mine_tiles = both[:, 0:2]
        owner_pick = (
            inst_master[:, None] == jnp.arange(region_masters, dtype=jnp.int32)[None, :]
        ).astype(jnp.float32)
        terms = jnp.sum(owner_pick[:, :, None, None, None] * both[:, None, 2:4], axis=0)
        if xor_partners(tile_count) and xor_partners(kern_count) and tile_count > 2:
            mine_masters = scatter_split(terms, tile_count, tile_pos, kern_count, kern_pos, local_masters)
        else:
            mine_masters = scatter_sum(terms, "tile", tile_count, tile_pos, local_masters)

    with jax.named_scope("pixel_gradients"):
        tile_grad = pixels(mine_tiles)
        master_grad = pixels(mine_masters)
    return (tile_grad, master_grad)


def solution(mesh):
    return jax.shard_map(
        on_device,
        mesh=mesh,
        in_specs=(
            P(("region", "tile"), None, None),
            P(("region", "tile"), None, None),
            P(("region", "tile"), None, None),
            P(("region", "tile")),
            P(("region", "tile"), None),
            P("corner", None, None, None, None),
            P("corner", None),
            P("corner"),
        ),
        out_specs=(P(("region", "tile"), None, None), P(("region", "tile"), None, None)),
        check_vma=False,
    )
```

```python
import math

import numpy as np
import jax
import jax.numpy as jnp
from jax import lax
from jax.sharding import PartitionSpec as P
from jax.experimental import pallas as pl
from jax.experimental.pallas import tpu as pltpu

P_SIZE = 256
B = 32


precise = lax.Precision.HIGHEST
steepness = 3.0
threshold = 1.0


def band_tables():
    freq = np.arange(B, dtype=np.int64) - B // 2
    pixel = np.arange(P_SIZE, dtype=np.int64)
    angle = (2.0 * math.pi / P_SIZE) * np.mod(freq[:, None] * pixel[None, :], P_SIZE).astype(np.float64)
    return (jnp.asarray(np.cos(angle), jnp.float32), jnp.asarray(-np.sin(angle), jnp.float32))


def phase_ramp(shift):
    freq = jnp.arange(B, dtype=jnp.int32) - B // 2
    total = (
        freq[None, :, None] * shift[:, 0][:, None, None]
        + freq[None, None, :] * shift[:, 1][:, None, None]
    )
    angle = 2.0 * math.pi / P_SIZE * jnp.mod(total, P_SIZE).astype(jnp.float32)
    return (jnp.cos(angle), -jnp.sin(angle))


def spectra(masks, cos_tab, sin_tab):
    rows_re = jnp.einsum("bx,nxy->nby", cos_tab, masks, precision=precise)
    rows_im = jnp.einsum("bx,nxy->nby", sin_tab, masks, precision=precise)
    spec_re = jnp.einsum("nby,cy->nbc", rows_re, cos_tab, precision=precise) - jnp.einsum(
        "nby,cy->nbc", rows_im, sin_tab, precision=precise
    )
    spec_im = jnp.einsum("nby,cy->nbc", rows_re, sin_tab, precision=precise) + jnp.einsum(
        "nby,cy->nbc", rows_im, cos_tab, precision=precise
    )
    return (spec_re, spec_im)


def back_pixels(x_re, x_im, cos_tab, sin_tab):
    half_re = jnp.einsum("bx,nbc->nxc", cos_tab, x_re, precision=precise) + jnp.einsum(
        "bx,nbc->nxc", sin_tab, x_im, precision=precise
    )
    half_im = jnp.einsum("bx,nbc->nxc", cos_tab, x_im, precision=precise) - jnp.einsum(
        "bx,nbc->nxc", sin_tab, x_re, precision=precise
    )
    return jnp.einsum("nxc,cy->nxy", half_re, cos_tab, precision=precise) + jnp.einsum(
        "nxc,cy->nxy", half_im, sin_tab, precision=precise
    )


def dot_full(a, b):
    return jnp.dot(a, b, precision=precise, preferred_element_type=jnp.float32)


def dot_parts(a, b):
    return jnp.dot(a, b, preferred_element_type=jnp.float32)


def split_three(a):
    hi = a.astype(jnp.bfloat16)
    rest = a - hi.astype(jnp.float32)
    mid = rest.astype(jnp.bfloat16)
    lo = (rest - mid.astype(jnp.float32)).astype(jnp.bfloat16)
    return hi, mid, lo


def table_three(table):
    hi = table.astype(jnp.bfloat16)
    rest = table - hi.astype(np.float64)
    mid = rest.astype(jnp.bfloat16)
    lo = (rest - mid.astype(np.float64)).astype(jnp.bfloat16)
    return hi, mid, lo


def imaging_tables():
    freq = np.arange(B, dtype=np.int64) - B // 2
    pixel = np.arange(P_SIZE, dtype=np.int64)
    angle = (2.0 * math.pi / P_SIZE) * np.mod(freq[:, None] * pixel[None, :], P_SIZE).astype(np.float64)
    c_re = np.cos(angle)
    c_im = -np.sin(angle)
    scale = 1.0 / (P_SIZE * P_SIZE)
    right_w = np.zeros((128, 2 * P_SIZE))
    right_w[:B, :P_SIZE] = c_re
    right_w[:B, P_SIZE:] = -c_im
    right_w[B : 2 * B, :P_SIZE] = c_im
    right_w[B : 2 * B, P_SIZE:] = c_re
    left_a = np.zeros((P_SIZE, 128))
    left_a[:, :B] = c_re.T * scale
    left_a[:, B : 2 * B] = -c_im.T * scale
    right_b = np.zeros((2 * P_SIZE, 128))
    right_b[:P_SIZE, :B] = c_re.T * scale
    right_b[:P_SIZE, B : 2 * B] = c_im.T * scale
    right_b[P_SIZE:, :B] = -c_im.T * scale
    right_b[P_SIZE:, B : 2 * B] = c_re.T * scale
    ct_re = c_re.T
    ct_im = c_im.T
    right_c = np.zeros((2 * P_SIZE, 128))
    for col, (top, bottom) in enumerate(
        ((ct_re, -ct_im), (ct_im, ct_re), (ct_im, ct_re), (ct_re, -ct_im))
    ):
        right_c[:P_SIZE, col * B : (col + 1) * B] = top
        right_c[P_SIZE:, col * B : (col + 1) * B] = bottom
    a_hi, a_mid, a_lo = table_three(left_a[:, : 2 * B])
    left_three = np.concatenate([a_hi, a_hi, a_mid, a_hi, a_lo, a_mid], axis=1)
    b_hi, b_mid, b_lo = table_three(right_b)
    right_hm = np.concatenate([b_hi, b_mid], axis=1)
    right_lh = np.concatenate([b_lo, b_hi], axis=0)
    plain = (c_re, c_im, c_re.T, c_im.T, right_w[:B], right_w[B : 2 * B], right_c)
    out = [jnp.asarray(table, jnp.float32) for table in plain]
    return out + [jnp.asarray(table) for table in (left_three, right_hm, right_lh)]


def imaging_body(
    pos_ref, im_ref, sh_ref, w_ref, dose_ref, t_ref, ev_ref, ev2_ref, own_ref, goal_ref, h_ref, hc_ref,
    c_re_ref, c_im_ref, ct_re_ref, ct_im_ref, rw_top, rw_bot, rc_ref, la_ref, rhm_ref, rlh_ref,
    slots_ref, f_buf, i_buf, u_buf, w_buf, xr_buf, xi_buf,
):
    count = f_buf.shape[0]
    pos = pos_ref[0]
    master = im_ref[pos]
    pick0 = (lax.broadcasted_iota(jnp.int32, (P_SIZE, 128), 0) == sh_ref[pos, 0]).astype(jnp.float32)
    pick1 = (lax.broadcasted_iota(jnp.int32, (8, P_SIZE), 1) == sh_ref[pos, 1]).astype(jnp.float32)
    e0_re = dot_full(c_re_ref[...], pick0)[:, 0:1]
    e0_im = dot_full(c_im_ref[...], pick0)[:, 0:1]
    e1_re = dot_full(pick1, ct_re_ref[...])[0:1, :]
    e1_im = dot_full(pick1, ct_im_ref[...])[0:1, :]
    ph_re = e0_re * e1_re - e0_im * e1_im
    ph_im = e0_re * e1_im + e0_im * e1_re
    local_masters = own_ref.shape[0]
    is_own = master // local_masters == pos_ref[1]
    m_re = ev_ref[master, 0] + ev2_ref[master, 0] + jnp.where(is_own, own_ref[master % local_masters, 0], 0.0)
    m_im = ev_ref[master, 1] + ev2_ref[master, 1] + jnp.where(is_own, own_ref[master % local_masters, 1], 0.0)
    s_re = t_ref[pos, 0] + (ph_re * m_re - ph_im * m_im)
    s_im = t_ref[pos, 1] + (ph_re * m_im + ph_im * m_re)
    i_buf[...] = jnp.zeros(i_buf.shape, jnp.float32)

    def spectrum(k, carry):
        h_re = h_ref[k, 0]
        h_im = h_ref[k, 1]
        rows = pl.ds(pl.multiple_of(k * B, B), B)
        xr_buf[rows, :] = h_re * s_re - h_im * s_im
        xi_buf[rows, :] = h_re * s_im + h_im * s_re
        return carry

    lax.fori_loop(0, count, spectrum, 0)
    w_buf[...] = dot_full(xr_buf[...], rw_top[...]) + dot_full(xi_buf[...], rw_bot[...])

    def forward(k, carry):
        rows = w_buf[pl.ds(pl.multiple_of(k * B, B), B), :]
        swap = jnp.concatenate([-rows[:, P_SIZE:], rows[:, :P_SIZE]], axis=1)
        s_hi, s_mid, s_lo = split_three(jnp.concatenate([rows, swap], axis=0))
        stacked = jnp.concatenate([s_hi, s_mid, s_hi, s_lo, s_hi, s_mid], axis=0)
        field = dot_parts(la_ref[...], stacked)
        f_buf[k] = field
        power = field * field
        i_buf[...] += w_ref[k] * (power[:, :P_SIZE] + power[:, P_SIZE:])
        return carry

    lax.fori_loop(0, count, forward, 0)
    dose = dose_ref[0]
    resist = 1.0 / (1.0 + jnp.exp(-(steepness * (dose * i_buf[...] - threshold))))
    goal = goal_ref[pos].astype(jnp.float32)
    i_buf[...] = 2.0 * (resist - goal) * resist * (1.0 - resist) * steepness * dose

    def backward(k, carry):
        sens = i_buf[...]
        weighted = f_buf[k] * jnp.concatenate([sens, sens], axis=1)
        q_hi, q_mid, q_lo = split_three(weighted)
        first = dot_parts(q_hi, rhm_ref[...]) + dot_parts(q_mid, rhm_ref[...])
        rest = dot_parts(jnp.concatenate([q_hi, q_lo], axis=1), rlh_ref[...])
        half = first[:, :128] + first[:, 128:] + rest
        flip = half.T
        u_buf[pl.ds(pl.multiple_of(k * B, B), B), :] = jnp.concatenate([flip[:B], flip[B : 2 * B]], axis=1)
        return carry

    lax.fori_loop(0, count, backward, 0)
    out = dot_full(u_buf[...], rc_ref[...])
    acc = jnp.sum((hc_ref[...] * out).reshape(count, B, 128), axis=0)
    flip = jnp.concatenate([acc, jnp.zeros((128 - B, 128), jnp.float32)], axis=0).T
    g_re = flip[0:B, 0:B] + flip[2 * B : 3 * B, 0:B]
    g_im = flip[B : 2 * B, 0:B] + flip[3 * B : 4 * B, 0:B]
    slots_ref[0] = g_re
    slots_ref[1] = g_im
    slots_ref[2] = ph_re * g_re + ph_im * g_im
    slots_ref[3] = ph_re * g_im - ph_im * g_re


def imaging(pos, inst_master, inst_shift, weights, dose, tile_spec, every, own, target, kerns, h_cat):
    if len(every) == 1:
        every = (every[0], jnp.zeros_like(every[0]))
    count = weights.shape[0]
    tables = imaging_tables()
    vmem = pl.BlockSpec(memory_space=pltpu.VMEM)
    smem = pl.BlockSpec(memory_space=pltpu.SMEM)
    return pl.pallas_call(
        imaging_body,
        out_shape=jax.ShapeDtypeStruct((4, B, B), jnp.float32),
        in_specs=[smem] * 5 + [vmem] * 7 + [vmem] * len(tables),
        out_specs=vmem,
        scratch_shapes=[
            pltpu.VMEM((count, P_SIZE, 2 * P_SIZE), jnp.float32),
            pltpu.VMEM((P_SIZE, P_SIZE), jnp.float32),
            pltpu.VMEM((count * B, 2 * P_SIZE), jnp.float32),
            pltpu.VMEM((count * B, 2 * P_SIZE), jnp.float32),
            pltpu.VMEM((count * B, B), jnp.float32),
            pltpu.VMEM((count * B, B), jnp.float32),
        ],
    )(pos, inst_master, inst_shift, weights, dose, tile_spec, *every, own, target, kerns, h_cat, *tables)


def pixel_body(*refs):
    out_ref = refs[-1]
    c_re_ref, c_im_ref, left_ref = refs[-4:-1]
    parts = refs[:-4]
    for n in range(out_ref.shape[0]):
        x_re = sum(part[n, 0] for part in parts)
        x_im = sum(part[n, 1] for part in parts)
        x_both = jnp.concatenate([x_re, x_im], axis=0)
        p_re = dot_full(x_both, c_re_ref[...])
        p_im = dot_full(x_both, c_im_ref[...])
        y_re = p_re[:B] + p_im[B:]
        y_im = p_re[B:] - p_im[:B]
        y_hi, y_mid, y_lo = split_three(jnp.concatenate([y_re, y_im], axis=0))
        stacked = jnp.concatenate([y_hi, y_mid, y_hi, y_lo, y_hi, y_mid], axis=0)
        out_ref[n] = dot_parts(left_ref[...], stacked)


def pixels(*parts):
    freq = np.arange(B, dtype=np.int64) - B // 2
    pixel = np.arange(P_SIZE, dtype=np.int64)
    angle = (2.0 * math.pi / P_SIZE) * np.mod(freq[:, None] * pixel[None, :], P_SIZE).astype(np.float64)
    c_re = np.cos(angle)
    c_im = -np.sin(angle)
    a_hi, a_mid, a_lo = table_three(np.concatenate([c_re.T, c_im.T], axis=1))
    left = np.concatenate([a_hi, a_hi, a_mid, a_hi, a_lo, a_mid], axis=1)
    tables = [jnp.asarray(c_re, jnp.float32), jnp.asarray(c_im, jnp.float32), jnp.asarray(left)]
    vmem = pl.BlockSpec(memory_space=pltpu.VMEM)
    return pl.pallas_call(
        pixel_body,
        out_shape=jax.ShapeDtypeStruct((parts[0].shape[0], P_SIZE, P_SIZE), jnp.float32),
        in_specs=[vmem] * (len(parts) + 3),
        out_specs=vmem,
    )(*parts, *tables)


def xor_partners(count):
    return count & (count - 1) == 0 and count <= 8


def gather_all(x, axis, count, pos):
    if not xor_partners(count):
        return lax.all_gather(x, axis, axis=0, tiled=True)
    size = x.shape[0]
    slot = jnp.arange(count * size, dtype=jnp.int32) // size
    total = jnp.where((slot == pos)[:, None, None, None], jnp.tile(x, (count, 1, 1, 1)), 0.0)
    for step in range(1, count):
        got = lax.ppermute(x, axis, [(i, i ^ step) for i in range(count)])
        hit = (slot == (pos ^ step))[:, None, None, None]
        total = total + jnp.where(hit, jnp.tile(got, (count, 1, 1, 1)), 0.0)
    return total


def sum_all(x, axis, count, pos):
    if not xor_partners(count):
        return lax.psum(x, axis)
    step = 1
    while step < count:
        x = x + lax.ppermute(x, axis, [(i, i ^ step) for i in range(count)])
        step *= 2
    return x


def sum_parts(x, axis, count, pos):
    if count == 2:
        return (x, lax.ppermute(x, axis, [(0, 1), (1, 0)]))
    return (sum_all(x, axis, count, pos),)


def scatter_sum(x, axis, count, pos, size):
    if not xor_partners(count):
        return lax.psum_scatter(x, axis, scatter_dimension=0, tiled=True)
    total = lax.dynamic_slice_in_dim(x, pos * size, size, 0)
    for step in range(1, count):
        part = lax.dynamic_slice_in_dim(x, (pos ^ step) * size, size, 0)
        total = total + lax.ppermute(part, axis, [(i, i ^ step) for i in range(count)])
    return total


def partner_lists(count, kern_count):
    lists = [[] for _ in range(kern_count)]
    for step in range(1, count):
        lists[step % kern_count].append(step)
    return lists


def chosen_step(lists, round_index, kern_pos):
    pick = jnp.int32(-1)
    for k, steps in enumerate(lists):
        if round_index < len(steps):
            pick = jnp.where(kern_pos == k, jnp.int32(steps[round_index]), pick)
    return pick


def gather_split(x, count, pos, kern_count, kern_pos):
    size = x.shape[0]
    lists = partner_lists(count, kern_count)
    slot = jnp.arange(count * size, dtype=jnp.int32) // size
    spread = lambda part: jnp.tile(part, (count, 1, 1, 1))
    collected = jnp.zeros((count * size,) + x.shape[1:], x.dtype)
    for r in range(max(len(steps) for steps in lists)):
        pairs = []
        for k, steps in enumerate(lists):
            if r < len(steps):
                pairs += [((t ^ steps[r]) * kern_count + k, t * kern_count + k) for t in range(count)]
        got = lax.ppermute(x, ("tile", "kern"), pairs)
        step = chosen_step(lists, r, kern_pos)
        source = jnp.where(step >= 0, pos ^ step, -1)
        collected = collected + jnp.where((slot == source)[:, None, None, None], spread(got), 0.0)
    return sum_parts(collected, "kern", kern_count, kern_pos)


def scatter_split(x, count, pos, kern_count, kern_pos, size):
    lists = partner_lists(count, kern_count)
    own = lax.dynamic_slice_in_dim(x, pos * size, size, 0)
    total = jnp.where(kern_pos == 0, own, 0.0)
    for r in range(max(len(steps) for steps in lists)):
        pairs = []
        for k, steps in enumerate(lists):
            if r < len(steps):
                pairs += [(t * kern_count + k, (t ^ steps[r]) * kern_count + k) for t in range(count)]
        step = chosen_step(lists, r, kern_pos)
        target = jnp.where(step >= 0, pos ^ step, 0)
        part = lax.dynamic_slice_in_dim(x, target * size, size, 0)
        total = total + lax.ppermute(part, ("tile", "kern"), pairs)
    return sum_parts(total, "kern", kern_count, kern_pos)


def on_device(
    tile_mask, master_mask, target, inst_master, inst_shift, kernels, kernel_weight, corner_dose
):
    cos_tab, sin_tab = band_tables()
    scale = 1.0 / (P_SIZE * P_SIZE)
    local_tiles = tile_mask.shape[0]
    local_masters = master_mask.shape[0]
    tile_count = lax.axis_size("tile")
    tile_pos = lax.axis_index("tile")
    kern_count = lax.axis_size("kern")
    kern_pos = lax.axis_index("kern")
    per_dev = local_tiles // kern_count
    first = kern_pos * per_dev
    region_tiles = tile_count * local_tiles
    region_masters = tile_count * local_masters

    with jax.named_scope("master_spectra"):
        own_re, own_im = spectra(master_mask.astype(jnp.float32), cos_tab, sin_tab)
        own = jnp.stack([own_re, own_im], axis=1)
        if xor_partners(tile_count) and xor_partners(kern_count) and tile_count > 2:
            every = gather_split(own, tile_count, tile_pos, kern_count, kern_pos)
            own_part = own
        else:
            every = (gather_all(own, "tile", tile_count, tile_pos),)
            own_part = jnp.zeros_like(own)

    with jax.named_scope("tile_spectra"):
        tile_re, tile_im = spectra(tile_mask.astype(jnp.float32), cos_tab, sin_tab)
        tile_spec = jnp.stack([tile_re, tile_im], axis=1)

    dose = corner_dose[0]
    kerns = kernels[0]
    h_re = kerns[:, 0]
    h_im = kerns[:, 1]
    weights = kernel_weight[0]

    with jax.named_scope("imaging_kernel"):
        count = h_re.shape[0]
        twice = (2.0 * weights)[:, None, None]
        ht_re = jnp.swapaxes(h_re, 1, 2) * twice
        ht_im = jnp.swapaxes(h_im, 1, 2) * twice
        h_cat = jnp.concatenate([ht_re, ht_re, ht_im, -ht_im], axis=-1).reshape(count * B, 128)
        parts = []
        for j in range(per_dev):
            pos = jnp.stack([first + j, tile_pos]).astype(jnp.int32)
            parts.append(
                imaging(
                    pos, inst_master, inst_shift, weights, corner_dose, tile_spec, every, own_part, target,
                    kerns, h_cat,
                )
            )
        comp = jnp.stack(parts)

    with jax.named_scope("gradient_exchange"):
        corner_count = lax.axis_size("corner")
        comp = sum_all(comp, "corner", corner_count, lax.axis_index("corner"))
        both = gather_all(comp, "kern", kern_count, kern_pos)
        mine_tiles = both[:, 0:2]
        owner_pick = (
            inst_master[:, None] == jnp.arange(region_masters, dtype=jnp.int32)[None, :]
        ).astype(jnp.float32)
        terms = jnp.sum(owner_pick[:, :, None, None, None] * both[:, None, 2:4], axis=0)
        if xor_partners(tile_count) and xor_partners(kern_count) and tile_count > 2:
            mine_masters = scatter_split(terms, tile_count, tile_pos, kern_count, kern_pos, local_masters)
        else:
            mine_masters = (scatter_sum(terms, "tile", tile_count, tile_pos, local_masters),)

    with jax.named_scope("pixel_gradients"):
        tile_grad = pixels(mine_tiles)
        master_grad = pixels(*mine_masters)
    return (tile_grad, master_grad)


def solution(mesh):
    return jax.shard_map(
        on_device,
        mesh=mesh,
        in_specs=(
            P(("region", "tile"), None, None),
            P(("region", "tile"), None, None),
            P(("region", "tile"), None, None),
            P(("region", "tile")),
            P(("region", "tile"), None),
            P("corner", None, None, None, None),
            P("corner", None),
            P("corner"),
        ),
        out_specs=(P(("region", "tile"), None, None), P(("region", "tile"), None, None)),
        check_vma=False,
    )
```

```python
import math

import numpy as np
import jax
import jax.numpy as jnp
from jax import lax
from jax.sharding import PartitionSpec as P
from jax.experimental import pallas as pl
from jax.experimental.pallas import tpu as pltpu

P_SIZE = 256
B = 32


precise = lax.Precision.HIGHEST
steepness = 3.0
threshold = 1.0


def band_tables():
    freq = np.arange(B, dtype=np.int64) - B // 2
    pixel = np.arange(P_SIZE, dtype=np.int64)
    angle = (2.0 * math.pi / P_SIZE) * np.mod(freq[:, None] * pixel[None, :], P_SIZE).astype(np.float64)
    return (jnp.asarray(np.cos(angle), jnp.float32), jnp.asarray(-np.sin(angle), jnp.float32))


def phase_ramp(shift):
    freq = jnp.arange(B, dtype=jnp.int32) - B // 2
    total = (
        freq[None, :, None] * shift[:, 0][:, None, None]
        + freq[None, None, :] * shift[:, 1][:, None, None]
    )
    angle = 2.0 * math.pi / P_SIZE * jnp.mod(total, P_SIZE).astype(jnp.float32)
    return (jnp.cos(angle), -jnp.sin(angle))


def spectra(masks, cos_tab, sin_tab):
    rows_re = jnp.einsum("bx,nxy->nby", cos_tab, masks, precision=precise)
    rows_im = jnp.einsum("bx,nxy->nby", sin_tab, masks, precision=precise)
    spec_re = jnp.einsum("nby,cy->nbc", rows_re, cos_tab, precision=precise) - jnp.einsum(
        "nby,cy->nbc", rows_im, sin_tab, precision=precise
    )
    spec_im = jnp.einsum("nby,cy->nbc", rows_re, sin_tab, precision=precise) + jnp.einsum(
        "nby,cy->nbc", rows_im, cos_tab, precision=precise
    )
    return (spec_re, spec_im)


def back_pixels(x_re, x_im, cos_tab, sin_tab):
    half_re = jnp.einsum("bx,nbc->nxc", cos_tab, x_re, precision=precise) + jnp.einsum(
        "bx,nbc->nxc", sin_tab, x_im, precision=precise
    )
    half_im = jnp.einsum("bx,nbc->nxc", cos_tab, x_im, precision=precise) - jnp.einsum(
        "bx,nbc->nxc", sin_tab, x_re, precision=precise
    )
    return jnp.einsum("nxc,cy->nxy", half_re, cos_tab, precision=precise) + jnp.einsum(
        "nxc,cy->nxy", half_im, sin_tab, precision=precise
    )


def dot_full(a, b):
    return jnp.dot(a, b, precision=precise, preferred_element_type=jnp.float32)


def dot_parts(a, b):
    return jnp.dot(a, b, preferred_element_type=jnp.float32)


def split_three(a):
    hi = a.astype(jnp.bfloat16)
    rest = a - hi.astype(jnp.float32)
    mid = rest.astype(jnp.bfloat16)
    lo = (rest - mid.astype(jnp.float32)).astype(jnp.bfloat16)
    return hi, mid, lo


def table_three(table):
    hi = table.astype(jnp.bfloat16)
    rest = table - hi.astype(np.float64)
    mid = rest.astype(jnp.bfloat16)
    lo = (rest - mid.astype(np.float64)).astype(jnp.bfloat16)
    return hi, mid, lo


def imaging_tables():
    freq = np.arange(B, dtype=np.int64) - B // 2
    pixel = np.arange(P_SIZE, dtype=np.int64)
    angle = (2.0 * math.pi / P_SIZE) * np.mod(freq[:, None] * pixel[None, :], P_SIZE).astype(np.float64)
    c_re = np.cos(angle)
    c_im = -np.sin(angle)
    scale = 1.0 / (P_SIZE * P_SIZE)
    right_w = np.zeros((128, 2 * P_SIZE))
    right_w[:B, :P_SIZE] = c_re
    right_w[:B, P_SIZE:] = -c_im
    right_w[B : 2 * B, :P_SIZE] = c_im
    right_w[B : 2 * B, P_SIZE:] = c_re
    left_a = np.zeros((P_SIZE, 128))
    left_a[:, :B] = c_re.T * scale
    left_a[:, B : 2 * B] = -c_im.T * scale
    right_b = np.zeros((2 * P_SIZE, 128))
    right_b[:P_SIZE, :B] = c_re.T * scale
    right_b[:P_SIZE, B : 2 * B] = c_im.T * scale
    right_b[P_SIZE:, :B] = -c_im.T * scale
    right_b[P_SIZE:, B : 2 * B] = c_re.T * scale
    ct_re = c_re.T
    ct_im = c_im.T
    right_c = np.zeros((2 * P_SIZE, 128))
    for col, (top, bottom) in enumerate(
        ((ct_re, -ct_im), (ct_im, ct_re), (ct_im, ct_re), (ct_re, -ct_im))
    ):
        right_c[:P_SIZE, col * B : (col + 1) * B] = top
        right_c[P_SIZE:, col * B : (col + 1) * B] = bottom
    a_hi, a_mid, a_lo = table_three(left_a[:, : 2 * B])
    left_three = np.concatenate([a_hi, a_hi, a_mid, a_hi, a_lo, a_mid], axis=1)
    b_hi, b_mid, b_lo = table_three(right_b)
    right_hm = np.concatenate([b_hi, b_mid], axis=1)
    right_lh = np.concatenate([b_lo, b_hi], axis=0)
    plain = (c_re, c_im, c_re.T, c_im.T, right_w[:B], right_w[B : 2 * B], right_c)
    out = [jnp.asarray(table, jnp.float32) for table in plain]
    return out + [jnp.asarray(table) for table in (left_three, right_hm, right_lh)]


def imaging_body(
    pos_ref, im_ref, sh_ref, w_ref, dose_ref, tr_ref, ti_ref, ev_ref, ev2_ref, own_ref, goal_ref, h_ref, hc_ref,
    c_re_ref, c_im_ref, ct_re_ref, ct_im_ref, rw_top, rw_bot, rc_ref, la_ref, rhm_ref, rlh_ref,
    slots_ref, f_buf, i_buf, u_buf, w_buf, xr_buf, xi_buf,
):
    count = f_buf.shape[0]
    pos = pos_ref[0]
    master = im_ref[pos]
    pick0 = (lax.broadcasted_iota(jnp.int32, (P_SIZE, 128), 0) == sh_ref[pos, 0]).astype(jnp.float32)
    pick1 = (lax.broadcasted_iota(jnp.int32, (8, P_SIZE), 1) == sh_ref[pos, 1]).astype(jnp.float32)
    e0_re = dot_full(c_re_ref[...], pick0)[:, 0:1]
    e0_im = dot_full(c_im_ref[...], pick0)[:, 0:1]
    e1_re = dot_full(pick1, ct_re_ref[...])[0:1, :]
    e1_im = dot_full(pick1, ct_im_ref[...])[0:1, :]
    ph_re = e0_re * e1_re - e0_im * e1_im
    ph_im = e0_re * e1_im + e0_im * e1_re
    local_masters = own_ref.shape[0]
    is_own = master // local_masters == pos_ref[1]
    m_re = ev_ref[master, 0] + ev2_ref[master, 0] + jnp.where(is_own, own_ref[master % local_masters, 0], 0.0)
    m_im = ev_ref[master, 1] + ev2_ref[master, 1] + jnp.where(is_own, own_ref[master % local_masters, 1], 0.0)
    s_re = tr_ref[pos] + (ph_re * m_re - ph_im * m_im)
    s_im = ti_ref[pos] + (ph_re * m_im + ph_im * m_re)
    i_buf[...] = jnp.zeros(i_buf.shape, jnp.float32)

    def spectrum(k, carry):
        h_re = h_ref[k, 0]
        h_im = h_ref[k, 1]
        rows = pl.ds(pl.multiple_of(k * B, B), B)
        xr_buf[rows, :] = h_re * s_re - h_im * s_im
        xi_buf[rows, :] = h_re * s_im + h_im * s_re
        return carry

    lax.fori_loop(0, count, spectrum, 0)
    w_buf[...] = dot_full(xr_buf[...], rw_top[...]) + dot_full(xi_buf[...], rw_bot[...])

    def forward(k, carry):
        rows = w_buf[pl.ds(pl.multiple_of(k * B, B), B), :]
        swap = jnp.concatenate([-rows[:, P_SIZE:], rows[:, :P_SIZE]], axis=1)
        s_hi, s_mid, s_lo = split_three(jnp.concatenate([rows, swap], axis=0))
        stacked = jnp.concatenate([s_hi, s_mid, s_hi, s_lo, s_hi, s_mid], axis=0)
        field = dot_parts(la_ref[...], stacked)
        f_buf[k] = field
        power = field * field
        i_buf[...] += w_ref[k] * (power[:, :P_SIZE] + power[:, P_SIZE:])
        return carry

    lax.fori_loop(0, count, forward, 0)
    dose = dose_ref[0]
    resist = 1.0 / (1.0 + jnp.exp(-(steepness * (dose * i_buf[...] - threshold))))
    goal = goal_ref[pos].astype(jnp.float32)
    i_buf[...] = 2.0 * (resist - goal) * resist * (1.0 - resist) * steepness * dose

    def backward(k, carry):
        sens = i_buf[...]
        weighted = f_buf[k] * jnp.concatenate([sens, sens], axis=1)
        q_hi, q_mid, q_lo = split_three(weighted)
        first = dot_parts(q_hi, rhm_ref[...]) + dot_parts(q_mid, rhm_ref[...])
        rest = dot_parts(jnp.concatenate([q_hi, q_lo], axis=1), rlh_ref[...])
        half = first[:, :128] + first[:, 128:] + rest
        flip = half.T
        u_buf[pl.ds(pl.multiple_of(k * B, B), B), :] = jnp.concatenate([flip[:B], flip[B : 2 * B]], axis=1)
        return carry

    lax.fori_loop(0, count, backward, 0)
    out = dot_full(u_buf[...], rc_ref[...])
    acc = jnp.sum((hc_ref[...] * out).reshape(count, B, 128), axis=0)
    flip = jnp.concatenate([acc, jnp.zeros((128 - B, 128), jnp.float32)], axis=0).T
    g_re = flip[0:B, 0:B] + flip[2 * B : 3 * B, 0:B]
    g_im = flip[B : 2 * B, 0:B] + flip[3 * B : 4 * B, 0:B]
    slots_ref[0] = g_re
    slots_ref[1] = g_im
    slots_ref[2] = ph_re * g_re + ph_im * g_im
    slots_ref[3] = ph_re * g_im - ph_im * g_re


def imaging(pos, inst_master, inst_shift, weights, dose, tile_spec, every, own, target, kerns, h_cat):
    if len(every) == 1:
        every = (every[0], jnp.zeros_like(every[0]))
    count = weights.shape[0]
    tables = imaging_tables()
    vmem = pl.BlockSpec(memory_space=pltpu.VMEM)
    smem = pl.BlockSpec(memory_space=pltpu.SMEM)
    return pl.pallas_call(
        imaging_body,
        out_shape=jax.ShapeDtypeStruct((4, B, B), jnp.float32),
        in_specs=[smem] * 5 + [vmem] * 8 + [vmem] * len(tables),
        out_specs=vmem,
        scratch_shapes=[
            pltpu.VMEM((count, P_SIZE, 2 * P_SIZE), jnp.float32),
            pltpu.VMEM((P_SIZE, P_SIZE), jnp.float32),
            pltpu.VMEM((count * B, 2 * P_SIZE), jnp.float32),
            pltpu.VMEM((count * B, 2 * P_SIZE), jnp.float32),
            pltpu.VMEM((count * B, B), jnp.float32),
            pltpu.VMEM((count * B, B), jnp.float32),
        ],
    )(pos, inst_master, inst_shift, weights, dose, *tile_spec, *every, own, target, kerns, h_cat, *tables)


def pixel_body(*refs):
    out_ref = refs[-1]
    c_re_ref, c_im_ref, left_ref = refs[-4:-1]
    parts = refs[:-4]
    for n in range(out_ref.shape[0]):
        x_re = sum(part[n, 0] for part in parts)
        x_im = sum(part[n, 1] for part in parts)
        x_both = jnp.concatenate([x_re, x_im], axis=0)
        p_re = dot_full(x_both, c_re_ref[...])
        p_im = dot_full(x_both, c_im_ref[...])
        y_re = p_re[:B] + p_im[B:]
        y_im = p_re[B:] - p_im[:B]
        y_hi, y_mid, y_lo = split_three(jnp.concatenate([y_re, y_im], axis=0))
        stacked = jnp.concatenate([y_hi, y_mid, y_hi, y_lo, y_hi, y_mid], axis=0)
        out_ref[n] = dot_parts(left_ref[...], stacked)


def pixels(*parts):
    freq = np.arange(B, dtype=np.int64) - B // 2
    pixel = np.arange(P_SIZE, dtype=np.int64)
    angle = (2.0 * math.pi / P_SIZE) * np.mod(freq[:, None] * pixel[None, :], P_SIZE).astype(np.float64)
    c_re = np.cos(angle)
    c_im = -np.sin(angle)
    a_hi, a_mid, a_lo = table_three(np.concatenate([c_re.T, c_im.T], axis=1))
    left = np.concatenate([a_hi, a_hi, a_mid, a_hi, a_lo, a_mid], axis=1)
    tables = [jnp.asarray(c_re, jnp.float32), jnp.asarray(c_im, jnp.float32), jnp.asarray(left)]
    vmem = pl.BlockSpec(memory_space=pltpu.VMEM)
    return pl.pallas_call(
        pixel_body,
        out_shape=jax.ShapeDtypeStruct((parts[0].shape[0], P_SIZE, P_SIZE), jnp.float32),
        in_specs=[vmem] * (len(parts) + 3),
        out_specs=vmem,
    )(*parts, *tables)


def xor_partners(count):
    return count & (count - 1) == 0 and count <= 8


def gather_all(x, axis, count, pos):
    if not xor_partners(count):
        return lax.all_gather(x, axis, axis=0, tiled=True)
    size = x.shape[0]
    slot = jnp.arange(count * size, dtype=jnp.int32) // size
    total = jnp.where((slot == pos)[:, None, None, None], jnp.tile(x, (count, 1, 1, 1)), 0.0)
    for step in range(1, count):
        got = lax.ppermute(x, axis, [(i, i ^ step) for i in range(count)])
        hit = (slot == (pos ^ step))[:, None, None, None]
        total = total + jnp.where(hit, jnp.tile(got, (count, 1, 1, 1)), 0.0)
    return total


def sum_all(x, axis, count, pos):
    if not xor_partners(count):
        return lax.psum(x, axis)
    step = 1
    while step < count:
        x = x + lax.ppermute(x, axis, [(i, i ^ step) for i in range(count)])
        step *= 2
    return x


def sum_parts(x, axis, count, pos):
    if count == 2:
        return (x, lax.ppermute(x, axis, [(0, 1), (1, 0)]))
    return (sum_all(x, axis, count, pos),)


def scatter_sum(x, axis, count, pos, size):
    if not xor_partners(count):
        return lax.psum_scatter(x, axis, scatter_dimension=0, tiled=True)
    total = lax.dynamic_slice_in_dim(x, pos * size, size, 0)
    for step in range(1, count):
        part = lax.dynamic_slice_in_dim(x, (pos ^ step) * size, size, 0)
        total = total + lax.ppermute(part, axis, [(i, i ^ step) for i in range(count)])
    return total


def partner_lists(count, kern_count):
    lists = [[] for _ in range(kern_count)]
    for step in range(1, count):
        lists[step % kern_count].append(step)
    return lists


def chosen_step(lists, round_index, kern_pos):
    pick = jnp.int32(-1)
    for k, steps in enumerate(lists):
        if round_index < len(steps):
            pick = jnp.where(kern_pos == k, jnp.int32(steps[round_index]), pick)
    return pick


def gather_split(x, count, pos, kern_count, kern_pos):
    size = x.shape[0]
    lists = partner_lists(count, kern_count)
    slot = jnp.arange(count * size, dtype=jnp.int32) // size
    spread = lambda part: jnp.tile(part, (count, 1, 1, 1))
    collected = jnp.zeros((count * size,) + x.shape[1:], x.dtype)
    for r in range(max(len(steps) for steps in lists)):
        pairs = []
        for k, steps in enumerate(lists):
            if r < len(steps):
                pairs += [((t ^ steps[r]) * kern_count + k, t * kern_count + k) for t in range(count)]
        got = lax.ppermute(x, ("tile", "kern"), pairs)
        step = chosen_step(lists, r, kern_pos)
        source = jnp.where(step >= 0, pos ^ step, -1)
        collected = collected + jnp.where((slot == source)[:, None, None, None], spread(got), 0.0)
    return sum_parts(collected, "kern", kern_count, kern_pos)


def scatter_split(x, count, pos, kern_count, kern_pos, size, after):
    lists = partner_lists(count, kern_count)
    own = lax.dynamic_slice_in_dim(x, pos * size, size, 0)
    total = jnp.where(kern_pos == 0, own, 0.0)
    for r in range(max(len(steps) for steps in lists)):
        pairs = []
        for k, steps in enumerate(lists):
            if r < len(steps):
                pairs += [(t * kern_count + k, (t ^ steps[r]) * kern_count + k) for t in range(count)]
        step = chosen_step(lists, r, kern_pos)
        target = jnp.where(step >= 0, pos ^ step, 0)
        part = lax.dynamic_slice_in_dim(x, target * size, size, 0)
        total = total + lax.ppermute(part, ("tile", "kern"), pairs)
    total = total + 0.0 * after
    return sum_parts(total, "kern", kern_count, kern_pos)


def on_device(
    tile_mask, master_mask, target, inst_master, inst_shift, kernels, kernel_weight, corner_dose
):
    cos_tab, sin_tab = band_tables()
    scale = 1.0 / (P_SIZE * P_SIZE)
    local_tiles = tile_mask.shape[0]
    local_masters = master_mask.shape[0]
    tile_count = lax.axis_size("tile")
    tile_pos = lax.axis_index("tile")
    kern_count = lax.axis_size("kern")
    kern_pos = lax.axis_index("kern")
    per_dev = local_tiles // kern_count
    first = kern_pos * per_dev
    region_tiles = tile_count * local_tiles
    region_masters = tile_count * local_masters

    with jax.named_scope("master_spectra"):
        own_re, own_im = spectra(master_mask.astype(jnp.float32), cos_tab, sin_tab)
        own = jnp.stack([own_re, own_im], axis=1)
        if xor_partners(tile_count) and xor_partners(kern_count) and tile_count > 2:
            every = gather_split(own, tile_count, tile_pos, kern_count, kern_pos)
            own_part = own
        else:
            every = (gather_all(own, "tile", tile_count, tile_pos),)
            own_part = jnp.zeros_like(own)

    with jax.named_scope("tile_spectra"):
        tile_re, tile_im = spectra(tile_mask.astype(jnp.float32), cos_tab, sin_tab)
        tile_spec = (tile_re, tile_im)

    dose = corner_dose[0]
    kerns = kernels[0]
    h_re = kerns[:, 0]
    h_im = kerns[:, 1]
    weights = kernel_weight[0]

    with jax.named_scope("imaging_kernel"):
        count = h_re.shape[0]
        twice = (2.0 * weights)[:, None, None]
        ht_re = jnp.swapaxes(h_re, 1, 2) * twice
        ht_im = jnp.swapaxes(h_im, 1, 2) * twice
        h_cat = jnp.concatenate([ht_re, ht_re, ht_im, -ht_im], axis=-1).reshape(count * B, 128)
        parts = []
        for j in range(per_dev):
            pos = jnp.stack([first + j, tile_pos]).astype(jnp.int32)
            parts.append(
                imaging(
                    pos, inst_master, inst_shift, weights, corner_dose, tile_spec, every, own_part, target,
                    kerns, h_cat,
                )
            )
        comp = jnp.stack(parts)

    with jax.named_scope("gradient_exchange"):
        corner_count = lax.axis_size("corner")
        comp = sum_all(comp, "corner", corner_count, lax.axis_index("corner"))
        both = gather_all(comp, "kern", kern_count, kern_pos)
        mine_tiles = both[:, 0:2]
        owner_pick = (
            inst_master[:, None] == jnp.arange(region_masters, dtype=jnp.int32)[None, :]
        ).astype(jnp.float32)
        terms = jnp.sum(owner_pick[:, :, None, None, None] * both[:, None, 2:4], axis=0)
        tile_grad = pixels(mine_tiles)
        if xor_partners(tile_count) and xor_partners(kern_count) and tile_count > 2:
            mine_masters = scatter_split(
                terms, tile_count, tile_pos, kern_count, kern_pos, local_masters, tile_grad[0, 0, 0]
            )
        else:
            mine_masters = (scatter_sum(terms, "tile", tile_count, tile_pos, local_masters),)

    with jax.named_scope("pixel_gradients"):
        master_grad = pixels(*mine_masters)
    return (tile_grad, master_grad)


def solution(mesh):
    return jax.shard_map(
        on_device,
        mesh=mesh,
        in_specs=(
            P(("region", "tile"), None, None),
            P(("region", "tile"), None, None),
            P(("region", "tile"), None, None),
            P(("region", "tile")),
            P(("region", "tile"), None),
            P("corner", None, None, None, None),
            P("corner", None),
            P("corner"),
        ),
        out_specs=(P(("region", "tile"), None, None), P(("region", "tile"), None, None)),
        check_vma=False,
    )
```

```python
import functools
import math

import numpy as np
import jax
import jax.numpy as jnp
from jax import lax
from jax.sharding import PartitionSpec as P
from jax.experimental import pallas as pl
from jax.experimental.pallas import tpu as pltpu

P_SIZE = 256
B = 32


precise = lax.Precision.HIGHEST
steepness = 3.0
threshold = 1.0


def band_tables():
    freq = np.arange(B, dtype=np.int64) - B // 2
    pixel = np.arange(P_SIZE, dtype=np.int64)
    angle = (2.0 * math.pi / P_SIZE) * np.mod(freq[:, None] * pixel[None, :], P_SIZE).astype(np.float64)
    return (jnp.asarray(np.cos(angle), jnp.float32), jnp.asarray(-np.sin(angle), jnp.float32))


def phase_ramp(shift):
    freq = jnp.arange(B, dtype=jnp.int32) - B // 2
    total = (
        freq[None, :, None] * shift[:, 0][:, None, None]
        + freq[None, None, :] * shift[:, 1][:, None, None]
    )
    angle = 2.0 * math.pi / P_SIZE * jnp.mod(total, P_SIZE).astype(jnp.float32)
    return (jnp.cos(angle), -jnp.sin(angle))


def spectra(masks, cos_tab, sin_tab):
    rows_re = jnp.einsum("bx,nxy->nby", cos_tab, masks, precision=precise)
    rows_im = jnp.einsum("bx,nxy->nby", sin_tab, masks, precision=precise)
    spec_re = jnp.einsum("nby,cy->nbc", rows_re, cos_tab, precision=precise) - jnp.einsum(
        "nby,cy->nbc", rows_im, sin_tab, precision=precise
    )
    spec_im = jnp.einsum("nby,cy->nbc", rows_re, sin_tab, precision=precise) + jnp.einsum(
        "nby,cy->nbc", rows_im, cos_tab, precision=precise
    )
    return (spec_re, spec_im)


def back_pixels(x_re, x_im, cos_tab, sin_tab):
    half_re = jnp.einsum("bx,nbc->nxc", cos_tab, x_re, precision=precise) + jnp.einsum(
        "bx,nbc->nxc", sin_tab, x_im, precision=precise
    )
    half_im = jnp.einsum("bx,nbc->nxc", cos_tab, x_im, precision=precise) - jnp.einsum(
        "bx,nbc->nxc", sin_tab, x_re, precision=precise
    )
    return jnp.einsum("nxc,cy->nxy", half_re, cos_tab, precision=precise) + jnp.einsum(
        "nxc,cy->nxy", half_im, sin_tab, precision=precise
    )


def dot_full(a, b):
    return jnp.dot(a, b, precision=precise, preferred_element_type=jnp.float32)


def dot_parts(a, b):
    return jnp.dot(a, b, preferred_element_type=jnp.float32)


def split_three(a):
    hi = a.astype(jnp.bfloat16)
    rest = a - hi.astype(jnp.float32)
    mid = rest.astype(jnp.bfloat16)
    lo = (rest - mid.astype(jnp.float32)).astype(jnp.bfloat16)
    return hi, mid, lo


def table_three(table):
    hi = table.astype(jnp.bfloat16)
    rest = table - hi.astype(np.float64)
    mid = rest.astype(jnp.bfloat16)
    lo = (rest - mid.astype(np.float64)).astype(jnp.bfloat16)
    return hi, mid, lo


def imaging_tables():
    freq = np.arange(B, dtype=np.int64) - B // 2
    pixel = np.arange(P_SIZE, dtype=np.int64)
    angle = (2.0 * math.pi / P_SIZE) * np.mod(freq[:, None] * pixel[None, :], P_SIZE).astype(np.float64)
    c_re = np.cos(angle)
    c_im = -np.sin(angle)
    scale = 1.0 / (P_SIZE * P_SIZE)
    right_w = np.zeros((128, 2 * P_SIZE))
    right_w[:B, :P_SIZE] = c_re
    right_w[:B, P_SIZE:] = -c_im
    right_w[B : 2 * B, :P_SIZE] = c_im
    right_w[B : 2 * B, P_SIZE:] = c_re
    left_a = np.zeros((P_SIZE, 128))
    left_a[:, :B] = c_re.T * scale
    left_a[:, B : 2 * B] = -c_im.T * scale
    right_b = np.zeros((2 * P_SIZE, 128))
    right_b[:P_SIZE, :B] = c_re.T * scale
    right_b[:P_SIZE, B : 2 * B] = c_im.T * scale
    right_b[P_SIZE:, :B] = -c_im.T * scale
    right_b[P_SIZE:, B : 2 * B] = c_re.T * scale
    ct_re = c_re.T
    ct_im = c_im.T
    right_c = np.zeros((2 * P_SIZE, 128))
    for col, (top, bottom) in enumerate(
        ((ct_re, -ct_im), (ct_im, ct_re), (ct_im, ct_re), (ct_re, -ct_im))
    ):
        right_c[:P_SIZE, col * B : (col + 1) * B] = top
        right_c[P_SIZE:, col * B : (col + 1) * B] = bottom
    a_hi, a_mid, a_lo = table_three(left_a[:, : 2 * B])
    left_three = np.concatenate([a_hi, a_hi, a_mid, a_hi, a_lo, a_mid], axis=1)
    b_hi, b_mid, b_lo = table_three(right_b)
    right_hm = np.concatenate([b_hi, b_mid], axis=1)
    right_lh = np.concatenate([b_lo, b_hi], axis=0)
    plain = (c_re, c_im, c_re.T, c_im.T, right_w[:B], right_w[B : 2 * B], right_c)
    out = [jnp.asarray(table, jnp.float32) for table in plain]
    return out + [jnp.asarray(table) for table in (left_three, right_hm, right_lh)]


def imaging_body(
    pos_ref, im_ref, sh_ref, w_ref, dose_ref, tr_ref, ti_ref, ev_ref, ev2_ref, own_ref, goal_ref, h_ref, hc_ref,
    c_re_ref, c_im_ref, ct_re_ref, ct_im_ref, rw_top, rw_bot, rc_ref, la_ref, rhm_ref, rlh_ref,
    slots_ref, f_buf, i_buf, u_buf, w_buf, xr_buf, xi_buf,
):
    count = f_buf.shape[0]
    pos = pos_ref[0]
    master = im_ref[pos]
    pick0 = (lax.broadcasted_iota(jnp.int32, (P_SIZE, 128), 0) == sh_ref[pos, 0]).astype(jnp.float32)
    pick1 = (lax.broadcasted_iota(jnp.int32, (8, P_SIZE), 1) == sh_ref[pos, 1]).astype(jnp.float32)
    e0_re = dot_full(c_re_ref[...], pick0)[:, 0:1]
    e0_im = dot_full(c_im_ref[...], pick0)[:, 0:1]
    e1_re = dot_full(pick1, ct_re_ref[...])[0:1, :]
    e1_im = dot_full(pick1, ct_im_ref[...])[0:1, :]
    ph_re = e0_re * e1_re - e0_im * e1_im
    ph_im = e0_re * e1_im + e0_im * e1_re
    local_masters = own_ref.shape[0]
    is_own = master // local_masters == pos_ref[1]
    m_re = ev_ref[master, 0] + ev2_ref[master, 0] + jnp.where(is_own, own_ref[master % local_masters, 0], 0.0)
    m_im = ev_ref[master, 1] + ev2_ref[master, 1] + jnp.where(is_own, own_ref[master % local_masters, 1], 0.0)
    s_re = tr_ref[pos] + (ph_re * m_re - ph_im * m_im)
    s_im = ti_ref[pos] + (ph_re * m_im + ph_im * m_re)
    i_buf[...] = jnp.zeros(i_buf.shape, jnp.float32)

    def spectrum(k, carry):
        h_re = h_ref[k, 0]
        h_im = h_ref[k, 1]
        rows = pl.ds(pl.multiple_of(k * B, B), B)
        xr_buf[rows, :] = h_re * s_re - h_im * s_im
        xi_buf[rows, :] = h_re * s_im + h_im * s_re
        return carry

    lax.fori_loop(0, count, spectrum, 0)
    w_buf[...] = dot_full(xr_buf[...], rw_top[...]) + dot_full(xi_buf[...], rw_bot[...])

    def forward(k, carry):
        rows = w_buf[pl.ds(pl.multiple_of(k * B, B), B), :]
        swap = jnp.concatenate([-rows[:, P_SIZE:], rows[:, :P_SIZE]], axis=1)
        s_hi, s_mid, s_lo = split_three(jnp.concatenate([rows, swap], axis=0))
        stacked = jnp.concatenate([s_hi, s_mid, s_hi, s_lo, s_hi, s_mid], axis=0)
        field = dot_parts(la_ref[...], stacked)
        f_buf[k] = field
        power = field * field
        i_buf[...] += w_ref[k] * (power[:, :P_SIZE] + power[:, P_SIZE:])
        return carry

    lax.fori_loop(0, count, forward, 0)
    dose = dose_ref[0]
    resist = 1.0 / (1.0 + jnp.exp(-(steepness * (dose * i_buf[...] - threshold))))
    goal = goal_ref[pos].astype(jnp.float32)
    i_buf[...] = 2.0 * (resist - goal) * resist * (1.0 - resist) * steepness * dose

    def backward(k, carry):
        sens = i_buf[...]
        weighted = f_buf[k] * jnp.concatenate([sens, sens], axis=1)
        q_hi, q_mid, q_lo = split_three(weighted)
        first = dot_parts(q_hi, rhm_ref[...]) + dot_parts(q_mid, rhm_ref[...])
        rest = dot_parts(jnp.concatenate([q_hi, q_lo], axis=1), rlh_ref[...])
        half = first[:, :128] + first[:, 128:] + rest
        flip = half.T
        u_buf[pl.ds(pl.multiple_of(k * B, B), B), :] = jnp.concatenate([flip[:B], flip[B : 2 * B]], axis=1)
        return carry

    lax.fori_loop(0, count, backward, 0)
    out = dot_full(u_buf[...], rc_ref[...])
    acc = jnp.sum((hc_ref[...] * out).reshape(count, B, 128), axis=0)
    flip = jnp.concatenate([acc, jnp.zeros((128 - B, 128), jnp.float32)], axis=0).T
    g_re = flip[0:B, 0:B] + flip[2 * B : 3 * B, 0:B]
    g_im = flip[B : 2 * B, 0:B] + flip[3 * B : 4 * B, 0:B]
    slots_ref[0] = g_re
    slots_ref[1] = g_im
    slots_ref[2] = ph_re * g_re + ph_im * g_im
    slots_ref[3] = ph_re * g_im - ph_im * g_re


def imaging(pos, inst_master, inst_shift, weights, dose, tile_spec, every, own, target, kerns, h_cat):
    if len(every) == 1:
        every = (every[0], jnp.zeros_like(every[0]))
    count = weights.shape[0]
    tables = imaging_tables()
    vmem = pl.BlockSpec(memory_space=pltpu.VMEM)
    smem = pl.BlockSpec(memory_space=pltpu.SMEM)
    return pl.pallas_call(
        imaging_body,
        out_shape=jax.ShapeDtypeStruct((4, B, B), jnp.float32),
        in_specs=[smem] * 5 + [vmem] * 8 + [vmem] * len(tables),
        out_specs=vmem,
        scratch_shapes=[
            pltpu.VMEM((count, P_SIZE, 2 * P_SIZE), jnp.float32),
            pltpu.VMEM((P_SIZE, P_SIZE), jnp.float32),
            pltpu.VMEM((count * B, 2 * P_SIZE), jnp.float32),
            pltpu.VMEM((count * B, 2 * P_SIZE), jnp.float32),
            pltpu.VMEM((count * B, B), jnp.float32),
            pltpu.VMEM((count * B, B), jnp.float32),
        ],
    )(pos, inst_master, inst_shift, weights, dose, *tile_spec, *every, own, target, kerns, h_cat, *tables)


def pixel_body(*refs, passes):
    if passes:
        out_ref, token_ref = refs[-2:]
        token_ref[...] = jnp.zeros(token_ref.shape, jnp.float32)
        refs = refs[:-2] + (out_ref,)
    out_ref = refs[-1]
    c_re_ref, c_im_ref, left_ref = refs[-4:-1]
    parts = refs[:-4]
    for n in range(out_ref.shape[0]):
        x_re = sum(part[n, 0] for part in parts)
        x_im = sum(part[n, 1] for part in parts)
        x_both = jnp.concatenate([x_re, x_im], axis=0)
        p_re = dot_full(x_both, c_re_ref[...])
        p_im = dot_full(x_both, c_im_ref[...])
        y_re = p_re[:B] + p_im[B:]
        y_im = p_re[B:] - p_im[:B]
        y_hi, y_mid, y_lo = split_three(jnp.concatenate([y_re, y_im], axis=0))
        stacked = jnp.concatenate([y_hi, y_mid, y_hi, y_lo, y_hi, y_mid], axis=0)
        out_ref[n] = dot_parts(left_ref[...], stacked)


def pixels(*parts, token=False):
    freq = np.arange(B, dtype=np.int64) - B // 2
    pixel = np.arange(P_SIZE, dtype=np.int64)
    angle = (2.0 * math.pi / P_SIZE) * np.mod(freq[:, None] * pixel[None, :], P_SIZE).astype(np.float64)
    c_re = np.cos(angle)
    c_im = -np.sin(angle)
    a_hi, a_mid, a_lo = table_three(np.concatenate([c_re.T, c_im.T], axis=1))
    left = np.concatenate([a_hi, a_hi, a_mid, a_hi, a_lo, a_mid], axis=1)
    tables = [jnp.asarray(c_re, jnp.float32), jnp.asarray(c_im, jnp.float32), jnp.asarray(left)]
    vmem = pl.BlockSpec(memory_space=pltpu.VMEM)
    shape = jax.ShapeDtypeStruct((parts[0].shape[0], P_SIZE, P_SIZE), jnp.float32)
    if not token:
        return pl.pallas_call(
            functools.partial(pixel_body, passes=False),
            out_shape=shape,
            in_specs=[vmem] * (len(parts) + 3),
            out_specs=vmem,
        )(*parts, *tables)
    return pl.pallas_call(
        functools.partial(pixel_body, passes=True),
        out_shape=(shape, jax.ShapeDtypeStruct((1, 1, 1, 1), jnp.float32)),
        in_specs=[vmem] * (len(parts) + 3),
        out_specs=(vmem, vmem),
    )(*parts, *tables)


def xor_partners(count):
    return count & (count - 1) == 0 and count <= 8


def gather_all(x, axis, count, pos):
    if not xor_partners(count):
        return lax.all_gather(x, axis, axis=0, tiled=True)
    size = x.shape[0]
    slot = jnp.arange(count * size, dtype=jnp.int32) // size
    total = jnp.where((slot == pos)[:, None, None, None], jnp.tile(x, (count, 1, 1, 1)), 0.0)
    for step in range(1, count):
        got = lax.ppermute(x, axis, [(i, i ^ step) for i in range(count)])
        hit = (slot == (pos ^ step))[:, None, None, None]
        total = total + jnp.where(hit, jnp.tile(got, (count, 1, 1, 1)), 0.0)
    return total


def sum_all(x, axis, count, pos):
    if not xor_partners(count):
        return lax.psum(x, axis)
    step = 1
    while step < count:
        x = x + lax.ppermute(x, axis, [(i, i ^ step) for i in range(count)])
        step *= 2
    return x


def sum_parts(x, axis, count, pos):
    if count == 2:
        return (x, lax.ppermute(x, axis, [(0, 1), (1, 0)]))
    return (sum_all(x, axis, count, pos),)


def scatter_sum(x, axis, count, pos, size):
    if not xor_partners(count):
        return lax.psum_scatter(x, axis, scatter_dimension=0, tiled=True)
    total = lax.dynamic_slice_in_dim(x, pos * size, size, 0)
    for step in range(1, count):
        part = lax.dynamic_slice_in_dim(x, (pos ^ step) * size, size, 0)
        total = total + lax.ppermute(part, axis, [(i, i ^ step) for i in range(count)])
    return total


def partner_lists(count, kern_count):
    lists = [[] for _ in range(kern_count)]
    for step in range(1, count):
        lists[step % kern_count].append(step)
    return lists


def chosen_step(lists, round_index, kern_pos):
    pick = jnp.int32(-1)
    for k, steps in enumerate(lists):
        if round_index < len(steps):
            pick = jnp.where(kern_pos == k, jnp.int32(steps[round_index]), pick)
    return pick


def gather_split(x, count, pos, kern_count, kern_pos):
    size = x.shape[0]
    lists = partner_lists(count, kern_count)
    slot = jnp.arange(count * size, dtype=jnp.int32) // size
    spread = lambda part: jnp.tile(part, (count, 1, 1, 1))
    collected = jnp.zeros((count * size,) + x.shape[1:], x.dtype)
    for r in range(max(len(steps) for steps in lists)):
        pairs = []
        for k, steps in enumerate(lists):
            if r < len(steps):
                pairs += [((t ^ steps[r]) * kern_count + k, t * kern_count + k) for t in range(count)]
        got = lax.ppermute(x, ("tile", "kern"), pairs)
        step = chosen_step(lists, r, kern_pos)
        source = jnp.where(step >= 0, pos ^ step, -1)
        collected = collected + jnp.where((slot == source)[:, None, None, None], spread(got), 0.0)
    return sum_parts(collected, "kern", kern_count, kern_pos)


def scatter_split(x, count, pos, kern_count, kern_pos, size, between):
    lists = partner_lists(count, kern_count)
    own = lax.dynamic_slice_in_dim(x, pos * size, size, 0)
    total = jnp.where(kern_pos == 0, own, 0.0)
    for r in range(max(len(steps) for steps in lists)):
        pairs = []
        for k, steps in enumerate(lists):
            if r < len(steps):
                pairs += [(t * kern_count + k, (t ^ steps[r]) * kern_count + k) for t in range(count)]
        step = chosen_step(lists, r, kern_pos)
        target = jnp.where(step >= 0, pos ^ step, 0)
        part = lax.dynamic_slice_in_dim(x, target * size, size, 0)
        total = total + lax.ppermute(part, ("tile", "kern"), pairs)
    done, token = between()
    total = total + 0.0 * token
    return done, sum_parts(total, "kern", kern_count, kern_pos)


def on_device(
    tile_mask, master_mask, target, inst_master, inst_shift, kernels, kernel_weight, corner_dose
):
    cos_tab, sin_tab = band_tables()
    scale = 1.0 / (P_SIZE * P_SIZE)
    local_tiles = tile_mask.shape[0]
    local_masters = master_mask.shape[0]
    tile_count = lax.axis_size("tile")
    tile_pos = lax.axis_index("tile")
    kern_count = lax.axis_size("kern")
    kern_pos = lax.axis_index("kern")
    per_dev = local_tiles // kern_count
    first = kern_pos * per_dev
    region_tiles = tile_count * local_tiles
    region_masters = tile_count * local_masters

    with jax.named_scope("master_spectra"):
        own_re, own_im = spectra(master_mask.astype(jnp.float32), cos_tab, sin_tab)
        own = jnp.stack([own_re, own_im], axis=1)
        if xor_partners(tile_count) and xor_partners(kern_count) and tile_count > 2:
            every = gather_split(own, tile_count, tile_pos, kern_count, kern_pos)
            own_part = own
        else:
            every = (gather_all(own, "tile", tile_count, tile_pos),)
            own_part = jnp.zeros_like(own)

    with jax.named_scope("tile_spectra"):
        tile_re, tile_im = spectra(tile_mask.astype(jnp.float32), cos_tab, sin_tab)
        tile_spec = (tile_re, tile_im)

    dose = corner_dose[0]
    kerns = kernels[0]
    h_re = kerns[:, 0]
    h_im = kerns[:, 1]
    weights = kernel_weight[0]

    with jax.named_scope("imaging_kernel"):
        count = h_re.shape[0]
        twice = (2.0 * weights)[:, None, None]
        ht_re = jnp.swapaxes(h_re, 1, 2) * twice
        ht_im = jnp.swapaxes(h_im, 1, 2) * twice
        h_cat = jnp.concatenate([ht_re, ht_re, ht_im, -ht_im], axis=-1).reshape(count * B, 128)
        parts = []
        for j in range(per_dev):
            pos = jnp.stack([first + j, tile_pos]).astype(jnp.int32)
            parts.append(
                imaging(
                    pos, inst_master, inst_shift, weights, corner_dose, tile_spec, every, own_part, target,
                    kerns, h_cat,
                )
            )
        comp = jnp.stack(parts)

    with jax.named_scope("gradient_exchange"):
        corner_count = lax.axis_size("corner")
        comp = sum_all(comp, "corner", corner_count, lax.axis_index("corner"))
        both = gather_all(comp, "kern", kern_count, kern_pos)
        mine_tiles = both[:, 0:2]
        owner_pick = (
            inst_master[:, None] == jnp.arange(region_masters, dtype=jnp.int32)[None, :]
        ).astype(jnp.float32)
        terms = jnp.sum(owner_pick[:, :, None, None, None] * both[:, None, 2:4], axis=0)
        if xor_partners(tile_count) and xor_partners(kern_count) and tile_count > 2:
            tile_grad, mine_masters = scatter_split(
                terms, tile_count, tile_pos, kern_count, kern_pos, local_masters,
                lambda: pixels(mine_tiles, token=True),
            )
        else:
            tile_grad = pixels(mine_tiles)
            mine_masters = (scatter_sum(terms, "tile", tile_count, tile_pos, local_masters),)

    with jax.named_scope("pixel_gradients"):
        master_grad = pixels(*mine_masters)
    return (tile_grad, master_grad)


def solution(mesh):
    return jax.shard_map(
        on_device,
        mesh=mesh,
        in_specs=(
            P(("region", "tile"), None, None),
            P(("region", "tile"), None, None),
            P(("region", "tile"), None, None),
            P(("region", "tile")),
            P(("region", "tile"), None),
            P("corner", None, None, None, None),
            P("corner", None),
            P("corner"),
        ),
        out_specs=(P(("region", "tile"), None, None), P(("region", "tile"), None, None)),
        check_vma=False,
    )
```

```python
import functools
import math

import numpy as np
import jax
import jax.numpy as jnp
from jax import lax
from jax.sharding import PartitionSpec as P
from jax.experimental import pallas as pl
from jax.experimental.pallas import tpu as pltpu

P_SIZE = 256
B = 32


precise = lax.Precision.HIGHEST
steepness = 3.0
threshold = 1.0


def band_tables():
    freq = np.arange(B, dtype=np.int64) - B // 2
    pixel = np.arange(P_SIZE, dtype=np.int64)
    angle = (2.0 * math.pi / P_SIZE) * np.mod(freq[:, None] * pixel[None, :], P_SIZE).astype(np.float64)
    return (jnp.asarray(np.cos(angle), jnp.float32), jnp.asarray(-np.sin(angle), jnp.float32))


def phase_ramp(shift):
    freq = jnp.arange(B, dtype=jnp.int32) - B // 2
    total = (
        freq[None, :, None] * shift[:, 0][:, None, None]
        + freq[None, None, :] * shift[:, 1][:, None, None]
    )
    angle = 2.0 * math.pi / P_SIZE * jnp.mod(total, P_SIZE).astype(jnp.float32)
    return (jnp.cos(angle), -jnp.sin(angle))


def spectra(masks, cos_tab, sin_tab):
    rows_re = jnp.einsum("bx,nxy->nby", cos_tab, masks, precision=precise)
    rows_im = jnp.einsum("bx,nxy->nby", sin_tab, masks, precision=precise)
    spec_re = jnp.einsum("nby,cy->nbc", rows_re, cos_tab, precision=precise) - jnp.einsum(
        "nby,cy->nbc", rows_im, sin_tab, precision=precise
    )
    spec_im = jnp.einsum("nby,cy->nbc", rows_re, sin_tab, precision=precise) + jnp.einsum(
        "nby,cy->nbc", rows_im, cos_tab, precision=precise
    )
    return (spec_re, spec_im)


def back_pixels(x_re, x_im, cos_tab, sin_tab):
    half_re = jnp.einsum("bx,nbc->nxc", cos_tab, x_re, precision=precise) + jnp.einsum(
        "bx,nbc->nxc", sin_tab, x_im, precision=precise
    )
    half_im = jnp.einsum("bx,nbc->nxc", cos_tab, x_im, precision=precise) - jnp.einsum(
        "bx,nbc->nxc", sin_tab, x_re, precision=precise
    )
    return jnp.einsum("nxc,cy->nxy", half_re, cos_tab, precision=precise) + jnp.einsum(
        "nxc,cy->nxy", half_im, sin_tab, precision=precise
    )


def dot_full(a, b):
    return jnp.dot(a, b, precision=precise, preferred_element_type=jnp.float32)


def dot_parts(a, b):
    return jnp.dot(a, b, preferred_element_type=jnp.float32)


def split_three(a):
    hi = a.astype(jnp.bfloat16)
    rest = a - hi.astype(jnp.float32)
    mid = rest.astype(jnp.bfloat16)
    lo = (rest - mid.astype(jnp.float32)).astype(jnp.bfloat16)
    return hi, mid, lo


def table_three(table):
    hi = table.astype(jnp.bfloat16)
    rest = table - hi.astype(np.float64)
    mid = rest.astype(jnp.bfloat16)
    lo = (rest - mid.astype(np.float64)).astype(jnp.bfloat16)
    return hi, mid, lo


def imaging_tables():
    freq = np.arange(B, dtype=np.int64) - B // 2
    pixel = np.arange(P_SIZE, dtype=np.int64)
    angle = (2.0 * math.pi / P_SIZE) * np.mod(freq[:, None] * pixel[None, :], P_SIZE).astype(np.float64)
    c_re = np.cos(angle)
    c_im = -np.sin(angle)
    scale = 1.0 / (P_SIZE * P_SIZE)
    right_w = np.zeros((128, 2 * P_SIZE))
    right_w[:B, :P_SIZE] = c_re
    right_w[:B, P_SIZE:] = -c_im
    right_w[B : 2 * B, :P_SIZE] = c_im
    right_w[B : 2 * B, P_SIZE:] = c_re
    left_a = np.zeros((P_SIZE, 128))
    left_a[:, :B] = c_re.T * scale
    left_a[:, B : 2 * B] = -c_im.T * scale
    right_b = np.zeros((2 * P_SIZE, 128))
    right_b[:P_SIZE, :B] = c_re.T * scale
    right_b[:P_SIZE, B : 2 * B] = c_im.T * scale
    right_b[P_SIZE:, :B] = -c_im.T * scale
    right_b[P_SIZE:, B : 2 * B] = c_re.T * scale
    ct_re = c_re.T
    ct_im = c_im.T
    right_c = np.zeros((2 * P_SIZE, 128))
    for col, (top, bottom) in enumerate(
        ((ct_re, -ct_im), (ct_im, ct_re), (ct_im, ct_re), (ct_re, -ct_im))
    ):
        right_c[:P_SIZE, col * B : (col + 1) * B] = top
        right_c[P_SIZE:, col * B : (col + 1) * B] = bottom
    a_hi, a_mid, a_lo = table_three(left_a[:, : 2 * B])
    left_three = np.concatenate([a_hi, a_hi, a_mid, a_hi, a_lo, a_mid], axis=1)
    b_hi, b_mid, b_lo = table_three(right_b)
    right_hm = np.concatenate([b_hi, b_mid], axis=1)
    right_lh = np.concatenate([b_lo, b_hi], axis=0)
    plain = (c_re, c_im, c_re.T, c_im.T, right_w[:B], right_w[B : 2 * B], right_c)
    out = [jnp.asarray(table, jnp.float32) for table in plain]
    return out + [jnp.asarray(table) for table in (left_three, right_hm, right_lh)]


def imaging_body(
    pos_ref, im_ref, sh_ref, w_ref, dose_ref, tr_ref, ti_ref, ev_ref, ev2_ref, own_ref, goal_ref, h_ref, hc_ref,
    c_re_ref, c_im_ref, ct_re_ref, ct_im_ref, rw_top, rw_bot, rc_ref, la_ref, rhm_ref, rlh_ref,
    slots_ref, f_buf, i_buf, u_buf, w_buf, xr_buf, xi_buf,
):
    count = f_buf.shape[0]
    pos = pos_ref[0]
    master = im_ref[pos]
    pick0 = (lax.broadcasted_iota(jnp.int32, (P_SIZE, 128), 0) == sh_ref[pos, 0]).astype(jnp.float32)
    pick1 = (lax.broadcasted_iota(jnp.int32, (8, P_SIZE), 1) == sh_ref[pos, 1]).astype(jnp.float32)
    e0_re = dot_full(c_re_ref[...], pick0)[:, 0:1]
    e0_im = dot_full(c_im_ref[...], pick0)[:, 0:1]
    e1_re = dot_full(pick1, ct_re_ref[...])[0:1, :]
    e1_im = dot_full(pick1, ct_im_ref[...])[0:1, :]
    ph_re = e0_re * e1_re - e0_im * e1_im
    ph_im = e0_re * e1_im + e0_im * e1_re
    local_masters = own_ref.shape[0]
    is_own = master // local_masters == pos_ref[1]
    m_re = ev_ref[master, 0] + ev2_ref[master, 0] + jnp.where(is_own, own_ref[master % local_masters, 0], 0.0)
    m_im = ev_ref[master, 1] + ev2_ref[master, 1] + jnp.where(is_own, own_ref[master % local_masters, 1], 0.0)
    s_re = tr_ref[pos] + (ph_re * m_re - ph_im * m_im)
    s_im = ti_ref[pos] + (ph_re * m_im + ph_im * m_re)
    i_buf[...] = jnp.zeros(i_buf.shape, jnp.float32)

    def spectrum(k, carry):
        h_re = h_ref[k, 0]
        h_im = h_ref[k, 1]
        rows = pl.ds(pl.multiple_of(k * B, B), B)
        xr_buf[rows, :] = h_re * s_re - h_im * s_im
        xi_buf[rows, :] = h_re * s_im + h_im * s_re
        return carry

    lax.fori_loop(0, count, spectrum, 0)
    w_buf[...] = dot_full(xr_buf[...], rw_top[...]) + dot_full(xi_buf[...], rw_bot[...])

    def forward(k, carry):
        rows = w_buf[pl.ds(pl.multiple_of(k * B, B), B), :]
        swap = jnp.concatenate([-rows[:, P_SIZE:], rows[:, :P_SIZE]], axis=1)
        s_hi, s_mid, s_lo = split_three(jnp.concatenate([rows, swap], axis=0))
        stacked = jnp.concatenate([s_hi, s_mid, s_hi, s_lo, s_hi, s_mid], axis=0)
        field = dot_parts(la_ref[...], stacked)
        f_buf[k] = field
        power = field * field
        i_buf[...] += w_ref[k] * (power[:, :P_SIZE] + power[:, P_SIZE:])
        return carry

    lax.fori_loop(0, count, forward, 0)
    dose = dose_ref[0]
    resist = 1.0 / (1.0 + jnp.exp(-(steepness * (dose * i_buf[...] - threshold))))
    goal = goal_ref[pos].astype(jnp.float32)
    i_buf[...] = 2.0 * (resist - goal) * resist * (1.0 - resist) * steepness * dose

    def backward(k, carry):
        sens = i_buf[...]
        weighted = f_buf[k] * jnp.concatenate([sens, sens], axis=1)
        q_hi, q_mid, q_lo = split_three(weighted)
        first = dot_parts(q_hi, rhm_ref[...]) + dot_parts(q_mid, rhm_ref[...])
        rest = dot_parts(jnp.concatenate([q_hi, q_lo], axis=1), rlh_ref[...])
        half = first[:, :128] + first[:, 128:] + rest
        flip = half.T
        u_buf[pl.ds(pl.multiple_of(k * B, B), B), :] = jnp.concatenate([flip[:B], flip[B : 2 * B]], axis=1)
        return carry

    lax.fori_loop(0, count, backward, 0)
    out = dot_full(u_buf[...], rc_ref[...])
    acc = jnp.sum((hc_ref[...] * out).reshape(count, B, 128), axis=0)
    flip = jnp.concatenate([acc, jnp.zeros((128 - B, 128), jnp.float32)], axis=0).T
    g_re = flip[0:B, 0:B] + flip[2 * B : 3 * B, 0:B]
    g_im = flip[B : 2 * B, 0:B] + flip[3 * B : 4 * B, 0:B]
    slots_ref[0] = g_re
    slots_ref[1] = g_im
    slots_ref[2] = ph_re * g_re + ph_im * g_im
    slots_ref[3] = ph_re * g_im - ph_im * g_re


def imaging(pos, inst_master, inst_shift, weights, dose, tile_spec, every, own, target, kerns, h_cat):
    if len(every) == 1:
        every = (every[0], jnp.zeros_like(every[0]))
    count = weights.shape[0]
    tables = imaging_tables()
    vmem = pl.BlockSpec(memory_space=pltpu.VMEM)
    smem = pl.BlockSpec(memory_space=pltpu.SMEM)
    return pl.pallas_call(
        imaging_body,
        out_shape=jax.ShapeDtypeStruct((4, B, B), jnp.float32),
        in_specs=[smem] * 5 + [vmem] * 8 + [vmem] * len(tables),
        out_specs=vmem,
        scratch_shapes=[
            pltpu.VMEM((count, P_SIZE, 2 * P_SIZE), jnp.float32),
            pltpu.VMEM((P_SIZE, P_SIZE), jnp.float32),
            pltpu.VMEM((count * B, 2 * P_SIZE), jnp.float32),
            pltpu.VMEM((count * B, 2 * P_SIZE), jnp.float32),
            pltpu.VMEM((count * B, B), jnp.float32),
            pltpu.VMEM((count * B, B), jnp.float32),
        ],
    )(pos, inst_master, inst_shift, weights, dose, *tile_spec, *every, own, target, kerns, h_cat, *tables)


def pixel_body(*refs, passes):
    if passes:
        out_ref, token_ref = refs[-2:]
        token_ref[...] = jnp.zeros(token_ref.shape, jnp.float32)
        refs = refs[:-2] + (out_ref,)
    out_ref = refs[-1]
    c_re_ref, c_im_ref, left_ref = refs[-4:-1]
    parts = refs[:-4]
    for n in range(out_ref.shape[0]):
        x_re = sum(part[n, 0] for part in parts)
        x_im = sum(part[n, 1] for part in parts)
        x_both = jnp.concatenate([x_re, x_im], axis=0)
        p_re = dot_full(x_both, c_re_ref[...])
        p_im = dot_full(x_both, c_im_ref[...])
        y_re = p_re[:B] + p_im[B:]
        y_im = p_re[B:] - p_im[:B]
        y_hi, y_mid, y_lo = split_three(jnp.concatenate([y_re, y_im], axis=0))
        stacked = jnp.concatenate([y_hi, y_mid, y_hi, y_lo, y_hi, y_mid], axis=0)
        out_ref[n] = dot_parts(left_ref[...], stacked)


def pixels(*parts, token=False):
    freq = np.arange(B, dtype=np.int64) - B // 2
    pixel = np.arange(P_SIZE, dtype=np.int64)
    angle = (2.0 * math.pi / P_SIZE) * np.mod(freq[:, None] * pixel[None, :], P_SIZE).astype(np.float64)
    c_re = np.cos(angle)
    c_im = -np.sin(angle)
    a_hi, a_mid, a_lo = table_three(np.concatenate([c_re.T, c_im.T], axis=1))
    left = np.concatenate([a_hi, a_hi, a_mid, a_hi, a_lo, a_mid], axis=1)
    tables = [jnp.asarray(c_re, jnp.float32), jnp.asarray(c_im, jnp.float32), jnp.asarray(left)]
    vmem = pl.BlockSpec(memory_space=pltpu.VMEM)
    shape = jax.ShapeDtypeStruct((parts[0].shape[0], P_SIZE, P_SIZE), jnp.float32)
    if not token:
        return pl.pallas_call(
            functools.partial(pixel_body, passes=False),
            out_shape=shape,
            in_specs=[vmem] * (len(parts) + 3),
            out_specs=vmem,
        )(*parts, *tables)
    return pl.pallas_call(
        functools.partial(pixel_body, passes=True),
        out_shape=(shape, jax.ShapeDtypeStruct((1, 1, 1, 1), jnp.float32)),
        in_specs=[vmem] * (len(parts) + 3),
        out_specs=(vmem, vmem),
    )(*parts, *tables)


def xor_partners(count):
    return count & (count - 1) == 0 and count <= 8


def gather_all(x, axis, count, pos):
    if not xor_partners(count):
        return lax.all_gather(x, axis, axis=0, tiled=True)
    size = x.shape[0]
    slot = jnp.arange(count * size, dtype=jnp.int32) // size
    total = jnp.where((slot == pos)[:, None, None, None], jnp.tile(x, (count, 1, 1, 1)), 0.0)
    for step in range(1, count):
        got = lax.ppermute(x, axis, [(i, i ^ step) for i in range(count)])
        hit = (slot == (pos ^ step))[:, None, None, None]
        total = total + jnp.where(hit, jnp.tile(got, (count, 1, 1, 1)), 0.0)
    return total


def sum_all(x, axis, count, pos):
    if not xor_partners(count):
        return lax.psum(x, axis)
    step = 1
    while step < count:
        x = x + lax.ppermute(x, axis, [(i, i ^ step) for i in range(count)])
        step *= 2
    return x


def sum_parts(x, axis, count, pos):
    if count == 2:
        return (x, lax.ppermute(x, axis, [(0, 1), (1, 0)]))
    return (sum_all(x, axis, count, pos),)


def scatter_sum(x, axis, count, pos, size):
    if not xor_partners(count):
        return lax.psum_scatter(x, axis, scatter_dimension=0, tiled=True)
    total = lax.dynamic_slice_in_dim(x, pos * size, size, 0)
    for step in range(1, count):
        part = lax.dynamic_slice_in_dim(x, (pos ^ step) * size, size, 0)
        total = total + lax.ppermute(part, axis, [(i, i ^ step) for i in range(count)])
    return total


def partner_lists(count, kern_count):
    lists = [[] for _ in range(kern_count)]
    for step in range(1, count):
        lists[step % kern_count].append(step)
    return lists


def chosen_step(lists, round_index, kern_pos):
    pick = jnp.int32(-1)
    for k, steps in enumerate(lists):
        if round_index < len(steps):
            pick = jnp.where(kern_pos == k, jnp.int32(steps[round_index]), pick)
    return pick


def gather_split(x, count, pos, kern_count, kern_pos):
    size = x.shape[0]
    lists = partner_lists(count, kern_count)
    slot = jnp.arange(count * size, dtype=jnp.int32) // size
    spread = lambda part: jnp.tile(part, (count, 1, 1, 1))
    collected = jnp.zeros((count * size,) + x.shape[1:], x.dtype)
    for r in range(max(len(steps) for steps in lists)):
        pairs = []
        for k, steps in enumerate(lists):
            if r < len(steps):
                pairs += [((t ^ steps[r]) * kern_count + k, t * kern_count + k) for t in range(count)]
        got = lax.ppermute(x, ("tile", "kern"), pairs)
        step = chosen_step(lists, r, kern_pos)
        source = jnp.where(step >= 0, pos ^ step, -1)
        collected = collected + jnp.where((slot == source)[:, None, None, None], spread(got), 0.0)
    return sum_parts(collected, "kern", kern_count, kern_pos)


def scatter_split(x, count, pos, kern_count, kern_pos, size, between):
    lists = partner_lists(count, kern_count)
    own = lax.dynamic_slice_in_dim(x, pos * size, size, 0)
    total = jnp.where(kern_pos == 0, own, 0.0)
    for r in range(max(len(steps) for steps in lists)):
        pairs = []
        for k, steps in enumerate(lists):
            if r < len(steps):
                pairs += [(t * kern_count + k, (t ^ steps[r]) * kern_count + k) for t in range(count)]
        step = chosen_step(lists, r, kern_pos)
        target = jnp.where(step >= 0, pos ^ step, 0)
        part = lax.dynamic_slice_in_dim(x, target * size, size, 0)
        total = total + lax.ppermute(part, ("tile", "kern"), pairs)
    done, token = between()
    total = total + 0.0 * token
    return done, sum_parts(total, "kern", kern_count, kern_pos)


def on_device(
    tile_mask, master_mask, target, inst_master, inst_shift, kernels, kernel_weight, corner_dose
):
    cos_tab, sin_tab = band_tables()
    scale = 1.0 / (P_SIZE * P_SIZE)
    local_tiles = tile_mask.shape[0]
    local_masters = master_mask.shape[0]
    tile_count = lax.axis_size("tile")
    tile_pos = lax.axis_index("tile")
    kern_count = lax.axis_size("kern")
    kern_pos = lax.axis_index("kern")
    per_dev = local_tiles // kern_count
    first = kern_pos * per_dev
    region_tiles = tile_count * local_tiles
    region_masters = tile_count * local_masters

    with jax.named_scope("master_spectra"):
        own_re, own_im = spectra(master_mask.astype(jnp.float32), cos_tab, sin_tab)
        own = jnp.stack([own_re, own_im], axis=1)
        if xor_partners(tile_count) and xor_partners(kern_count) and tile_count > 2:
            every = gather_split(own, tile_count, tile_pos, kern_count, kern_pos)
            own_part = own
        else:
            every = (gather_all(own, "tile", tile_count, tile_pos),)
            own_part = jnp.zeros_like(own)

    with jax.named_scope("tile_spectra"):
        tile_re, tile_im = spectra(tile_mask.astype(jnp.float32), cos_tab, sin_tab)
        tile_spec = (tile_re, tile_im)

    dose = corner_dose[0]
    kerns = kernels[0]
    h_re = kerns[:, 0]
    h_im = kerns[:, 1]
    weights = kernel_weight[0]

    with jax.named_scope("imaging_kernel"):
        count = h_re.shape[0]
        twice = (2.0 * weights)[:, None, None]
        ht_re = jnp.swapaxes(h_re, 1, 2) * twice
        ht_im = jnp.swapaxes(h_im, 1, 2) * twice
        h_cat = jnp.concatenate([ht_re, ht_re, ht_im, -ht_im], axis=-1).reshape(count * B, 128)
        parts = []
        for j in range(per_dev):
            pos = jnp.stack([first + j, tile_pos]).astype(jnp.int32)
            parts.append(
                imaging(
                    pos, inst_master, inst_shift, weights, corner_dose, tile_spec, every, own_part, target,
                    kerns, h_cat,
                )
            )
        comp = jnp.stack(parts)

    with jax.named_scope("gradient_exchange"):
        corner_count = lax.axis_size("corner")
        corner_pos = lax.axis_index("corner")
        if corner_count == 2 and kern_count == 2 and per_dev == 1:
            got = [
                lax.ppermute(comp, ("corner", "kern"), [(i, i ^ step) for i in range(4)])
                for step in (1, 2, 3)
            ]
            mine = comp + got[1]
            other = got[0] + got[2]
            both = jnp.where(kern_pos == 0, jnp.concatenate([mine, other]), jnp.concatenate([other, mine]))
        else:
            comp = sum_all(comp, "corner", corner_count, corner_pos)
            both = gather_all(comp, "kern", kern_count, kern_pos)
        mine_tiles = both[:, 0:2]
        owner_pick = (
            inst_master[:, None] == jnp.arange(region_masters, dtype=jnp.int32)[None, :]
        ).astype(jnp.float32)
        terms = jnp.sum(owner_pick[:, :, None, None, None] * both[:, None, 2:4], axis=0)
        if xor_partners(tile_count) and xor_partners(kern_count) and tile_count > 2:
            tile_grad, mine_masters = scatter_split(
                terms, tile_count, tile_pos, kern_count, kern_pos, local_masters,
                lambda: pixels(mine_tiles, token=True),
            )
        else:
            tile_grad = pixels(mine_tiles)
            mine_masters = (scatter_sum(terms, "tile", tile_count, tile_pos, local_masters),)

    with jax.named_scope("pixel_gradients"):
        master_grad = pixels(*mine_masters)
    return (tile_grad, master_grad)


def solution(mesh):
    return jax.shard_map(
        on_device,
        mesh=mesh,
        in_specs=(
            P(("region", "tile"), None, None),
            P(("region", "tile"), None, None),
            P(("region", "tile"), None, None),
            P(("region", "tile")),
            P(("region", "tile"), None),
            P("corner", None, None, None, None),
            P("corner", None),
            P("corner"),
        ),
        out_specs=(P(("region", "tile"), None, None), P(("region", "tile"), None, None)),
        check_vma=False,
    )
```

```python
import functools
import math

import numpy as np
import jax
import jax.numpy as jnp
from jax import lax
from jax.sharding import PartitionSpec as P
from jax.experimental import pallas as pl
from jax.experimental.pallas import tpu as pltpu

P_SIZE = 256
B = 32


precise = lax.Precision.HIGHEST
steepness = 3.0
threshold = 1.0


def band_tables():
    freq = np.arange(B, dtype=np.int64) - B // 2
    pixel = np.arange(P_SIZE, dtype=np.int64)
    angle = (2.0 * math.pi / P_SIZE) * np.mod(freq[:, None] * pixel[None, :], P_SIZE).astype(np.float64)
    return (jnp.asarray(np.cos(angle), jnp.float32), jnp.asarray(-np.sin(angle), jnp.float32))


def phase_ramp(shift):
    freq = jnp.arange(B, dtype=jnp.int32) - B // 2
    total = (
        freq[None, :, None] * shift[:, 0][:, None, None]
        + freq[None, None, :] * shift[:, 1][:, None, None]
    )
    angle = 2.0 * math.pi / P_SIZE * jnp.mod(total, P_SIZE).astype(jnp.float32)
    return (jnp.cos(angle), -jnp.sin(angle))


def spectra(masks, cos_tab, sin_tab):
    rows_re = jnp.einsum("bx,nxy->nby", cos_tab, masks, precision=precise)
    rows_im = jnp.einsum("bx,nxy->nby", sin_tab, masks, precision=precise)
    spec_re = jnp.einsum("nby,cy->nbc", rows_re, cos_tab, precision=precise) - jnp.einsum(
        "nby,cy->nbc", rows_im, sin_tab, precision=precise
    )
    spec_im = jnp.einsum("nby,cy->nbc", rows_re, sin_tab, precision=precise) + jnp.einsum(
        "nby,cy->nbc", rows_im, cos_tab, precision=precise
    )
    return (spec_re, spec_im)


def back_pixels(x_re, x_im, cos_tab, sin_tab):
    half_re = jnp.einsum("bx,nbc->nxc", cos_tab, x_re, precision=precise) + jnp.einsum(
        "bx,nbc->nxc", sin_tab, x_im, precision=precise
    )
    half_im = jnp.einsum("bx,nbc->nxc", cos_tab, x_im, precision=precise) - jnp.einsum(
        "bx,nbc->nxc", sin_tab, x_re, precision=precise
    )
    return jnp.einsum("nxc,cy->nxy", half_re, cos_tab, precision=precise) + jnp.einsum(
        "nxc,cy->nxy", half_im, sin_tab, precision=precise
    )


def dot_full(a, b):
    return jnp.dot(a, b, precision=precise, preferred_element_type=jnp.float32)


def dot_parts(a, b):
    return jnp.dot(a, b, preferred_element_type=jnp.float32)


def split_three(a):
    hi = a.astype(jnp.bfloat16)
    rest = a - hi.astype(jnp.float32)
    mid = rest.astype(jnp.bfloat16)
    lo = (rest - mid.astype(jnp.float32)).astype(jnp.bfloat16)
    return hi, mid, lo


def table_three(table):
    hi = table.astype(jnp.bfloat16)
    rest = table - hi.astype(np.float64)
    mid = rest.astype(jnp.bfloat16)
    lo = (rest - mid.astype(np.float64)).astype(jnp.bfloat16)
    return hi, mid, lo


def imaging_tables():
    freq = np.arange(B, dtype=np.int64) - B // 2
    pixel = np.arange(P_SIZE, dtype=np.int64)
    angle = (2.0 * math.pi / P_SIZE) * np.mod(freq[:, None] * pixel[None, :], P_SIZE).astype(np.float64)
    c_re = np.cos(angle)
    c_im = -np.sin(angle)
    scale = 1.0 / (P_SIZE * P_SIZE)
    right_w = np.zeros((128, 2 * P_SIZE))
    right_w[:B, :P_SIZE] = c_re
    right_w[:B, P_SIZE:] = -c_im
    right_w[B : 2 * B, :P_SIZE] = c_im
    right_w[B : 2 * B, P_SIZE:] = c_re
    left_a = np.zeros((P_SIZE, 128))
    left_a[:, :B] = c_re.T * scale
    left_a[:, B : 2 * B] = -c_im.T * scale
    right_b = np.zeros((2 * P_SIZE, 128))
    right_b[:P_SIZE, :B] = c_re.T * scale
    right_b[:P_SIZE, B : 2 * B] = c_im.T * scale
    right_b[P_SIZE:, :B] = -c_im.T * scale
    right_b[P_SIZE:, B : 2 * B] = c_re.T * scale
    ct_re = c_re.T
    ct_im = c_im.T
    right_c = np.zeros((2 * P_SIZE, 128))
    for col, (top, bottom) in enumerate(
        ((ct_re, -ct_im), (ct_im, ct_re), (ct_im, ct_re), (ct_re, -ct_im))
    ):
        right_c[:P_SIZE, col * B : (col + 1) * B] = top
        right_c[P_SIZE:, col * B : (col + 1) * B] = bottom
    a_hi, a_mid, a_lo = table_three(left_a[:, : 2 * B])
    left_three = np.concatenate([a_hi, a_hi, a_mid, a_hi, a_lo, a_mid], axis=1)
    b_hi, b_mid, b_lo = table_three(right_b)
    right_hm = np.concatenate([b_hi, b_mid], axis=1)
    right_lh = np.concatenate([b_lo, b_hi], axis=0)
    parts_re = table_three(c_re)
    parts_im = table_three(c_im)
    rows_three = np.concatenate(
        [np.concatenate(parts_re, axis=1), np.concatenate(parts_im, axis=1)], axis=0
    )
    plain = (c_re, c_im, c_re.T, c_im.T, right_w[:B], right_w[B : 2 * B], right_c)
    out = [jnp.asarray(table, jnp.float32) for table in plain]
    return out + [jnp.asarray(table) for table in (left_three, right_hm, right_lh, rows_three)]


def imaging_body(
    pos_ref, im_ref, sh_ref, w_ref, dose_ref, mask_ref, ev_ref, ev2_ref, own_ref, goal_ref, h_ref, hc_ref,
    c_re_ref, c_im_ref, ct_re_ref, ct_im_ref, rw_top, rw_bot, rc_ref, la_ref, rhm_ref, rlh_ref, rows_ref,
    slots_ref, f_buf, i_buf, u_buf, w_buf, xr_buf, xi_buf,
):
    count = f_buf.shape[0]
    pos = pos_ref[0]
    master = im_ref[pos]
    pick0 = (lax.broadcasted_iota(jnp.int32, (P_SIZE, 128), 0) == sh_ref[pos, 0]).astype(jnp.float32)
    pick1 = (lax.broadcasted_iota(jnp.int32, (8, P_SIZE), 1) == sh_ref[pos, 1]).astype(jnp.float32)
    e0_re = dot_full(c_re_ref[...], pick0)[:, 0:1]
    e0_im = dot_full(c_im_ref[...], pick0)[:, 0:1]
    e1_re = dot_full(pick1, ct_re_ref[...])[0:1, :]
    e1_im = dot_full(pick1, ct_im_ref[...])[0:1, :]
    ph_re = e0_re * e1_re - e0_im * e1_im
    ph_im = e0_re * e1_im + e0_im * e1_re
    local_masters = own_ref.shape[0]
    is_own = master // local_masters == pos_ref[1]
    m_re = ev_ref[master, 0] + ev2_ref[master, 0] + jnp.where(is_own, own_ref[master % local_masters, 0], 0.0)
    m_im = ev_ref[master, 1] + ev2_ref[master, 1] + jnp.where(is_own, own_ref[master % local_masters, 1], 0.0)
    mask = mask_ref[pos]
    rows = dot_parts(rows_ref[...], jnp.concatenate([mask, mask, mask], axis=0))
    t_one = dot_full(rows, ct_re_ref[...])
    t_two = dot_full(rows, ct_im_ref[...])
    s_re = t_one[:B] - t_two[B:] + (ph_re * m_re - ph_im * m_im)
    s_im = t_two[:B] + t_one[B:] + (ph_re * m_im + ph_im * m_re)
    i_buf[...] = jnp.zeros(i_buf.shape, jnp.float32)

    def spectrum(k, carry):
        h_re = h_ref[k, 0]
        h_im = h_ref[k, 1]
        rows = pl.ds(pl.multiple_of(k * B, B), B)
        xr_buf[rows, :] = h_re * s_re - h_im * s_im
        xi_buf[rows, :] = h_re * s_im + h_im * s_re
        return carry

    lax.fori_loop(0, count, spectrum, 0)
    w_buf[...] = dot_full(xr_buf[...], rw_top[...]) + dot_full(xi_buf[...], rw_bot[...])

    def forward(k, carry):
        rows = w_buf[pl.ds(pl.multiple_of(k * B, B), B), :]
        swap = jnp.concatenate([-rows[:, P_SIZE:], rows[:, :P_SIZE]], axis=1)
        s_hi, s_mid, s_lo = split_three(jnp.concatenate([rows, swap], axis=0))
        stacked = jnp.concatenate([s_hi, s_mid, s_hi, s_lo, s_hi, s_mid], axis=0)
        field = dot_parts(la_ref[...], stacked)
        f_buf[k] = field
        power = field * field
        i_buf[...] += w_ref[k] * (power[:, :P_SIZE] + power[:, P_SIZE:])
        return carry

    lax.fori_loop(0, count, forward, 0)
    dose = dose_ref[0]
    resist = 1.0 / (1.0 + jnp.exp(-(steepness * (dose * i_buf[...] - threshold))))
    goal = goal_ref[pos].astype(jnp.float32)
    i_buf[...] = 2.0 * (resist - goal) * resist * (1.0 - resist) * steepness * dose

    def backward(k, carry):
        sens = i_buf[...]
        weighted = f_buf[k] * jnp.concatenate([sens, sens], axis=1)
        q_hi, q_mid, q_lo = split_three(weighted)
        first = dot_parts(q_hi, rhm_ref[...]) + dot_parts(q_mid, rhm_ref[...])
        rest = dot_parts(jnp.concatenate([q_hi, q_lo], axis=1), rlh_ref[...])
        half = first[:, :128] + first[:, 128:] + rest
        flip = half.T
        u_buf[pl.ds(pl.multiple_of(k * B, B), B), :] = jnp.concatenate([flip[:B], flip[B : 2 * B]], axis=1)
        return carry

    lax.fori_loop(0, count, backward, 0)
    out = dot_full(u_buf[...], rc_ref[...])
    acc = jnp.sum((hc_ref[...] * out).reshape(count, B, 128), axis=0)
    flip = jnp.concatenate([acc, jnp.zeros((128 - B, 128), jnp.float32)], axis=0).T
    g_re = flip[0:B, 0:B] + flip[2 * B : 3 * B, 0:B]
    g_im = flip[B : 2 * B, 0:B] + flip[3 * B : 4 * B, 0:B]
    slots_ref[0] = g_re
    slots_ref[1] = g_im
    slots_ref[2] = ph_re * g_re + ph_im * g_im
    slots_ref[3] = ph_re * g_im - ph_im * g_re


def imaging(pos, inst_master, inst_shift, weights, dose, tile_mask, every, own, target, kerns, h_cat):
    if len(every) == 1:
        every = (every[0], jnp.zeros_like(every[0]))
    count = weights.shape[0]
    tables = imaging_tables()
    vmem = pl.BlockSpec(memory_space=pltpu.VMEM)
    smem = pl.BlockSpec(memory_space=pltpu.SMEM)
    return pl.pallas_call(
        imaging_body,
        out_shape=jax.ShapeDtypeStruct((4, B, B), jnp.float32),
        in_specs=[smem] * 5 + [vmem] * 7 + [vmem] * len(tables),
        out_specs=vmem,
        scratch_shapes=[
            pltpu.VMEM((count, P_SIZE, 2 * P_SIZE), jnp.float32),
            pltpu.VMEM((P_SIZE, P_SIZE), jnp.float32),
            pltpu.VMEM((count * B, 2 * P_SIZE), jnp.float32),
            pltpu.VMEM((count * B, 2 * P_SIZE), jnp.float32),
            pltpu.VMEM((count * B, B), jnp.float32),
            pltpu.VMEM((count * B, B), jnp.float32),
        ],
    )(pos, inst_master, inst_shift, weights, dose, tile_mask, *every, own, target, kerns, h_cat, *tables)


def pixel_body(*refs, passes):
    if passes:
        out_ref, token_ref = refs[-2:]
        token_ref[...] = jnp.zeros(token_ref.shape, jnp.float32)
        refs = refs[:-2] + (out_ref,)
    out_ref = refs[-1]
    c_re_ref, c_im_ref, left_ref = refs[-4:-1]
    parts = refs[:-4]
    for n in range(out_ref.shape[0]):
        x_re = sum(part[n, 0] for part in parts)
        x_im = sum(part[n, 1] for part in parts)
        x_both = jnp.concatenate([x_re, x_im], axis=0)
        p_re = dot_full(x_both, c_re_ref[...])
        p_im = dot_full(x_both, c_im_ref[...])
        y_re = p_re[:B] + p_im[B:]
        y_im = p_re[B:] - p_im[:B]
        y_hi, y_mid, y_lo = split_three(jnp.concatenate([y_re, y_im], axis=0))
        stacked = jnp.concatenate([y_hi, y_mid, y_hi, y_lo, y_hi, y_mid], axis=0)
        out_ref[n] = dot_parts(left_ref[...], stacked)


def pixels(*parts, token=False):
    freq = np.arange(B, dtype=np.int64) - B // 2
    pixel = np.arange(P_SIZE, dtype=np.int64)
    angle = (2.0 * math.pi / P_SIZE) * np.mod(freq[:, None] * pixel[None, :], P_SIZE).astype(np.float64)
    c_re = np.cos(angle)
    c_im = -np.sin(angle)
    a_hi, a_mid, a_lo = table_three(np.concatenate([c_re.T, c_im.T], axis=1))
    left = np.concatenate([a_hi, a_hi, a_mid, a_hi, a_lo, a_mid], axis=1)
    tables = [jnp.asarray(c_re, jnp.float32), jnp.asarray(c_im, jnp.float32), jnp.asarray(left)]
    vmem = pl.BlockSpec(memory_space=pltpu.VMEM)
    shape = jax.ShapeDtypeStruct((parts[0].shape[0], P_SIZE, P_SIZE), jnp.float32)
    if not token:
        return pl.pallas_call(
            functools.partial(pixel_body, passes=False),
            out_shape=shape,
            in_specs=[vmem] * (len(parts) + 3),
            out_specs=vmem,
        )(*parts, *tables)
    return pl.pallas_call(
        functools.partial(pixel_body, passes=True),
        out_shape=(shape, jax.ShapeDtypeStruct((1, 1, 1, 1), jnp.float32)),
        in_specs=[vmem] * (len(parts) + 3),
        out_specs=(vmem, vmem),
    )(*parts, *tables)


def xor_partners(count):
    return count & (count - 1) == 0 and count <= 8


def gather_all(x, axis, count, pos):
    if not xor_partners(count):
        return lax.all_gather(x, axis, axis=0, tiled=True)
    size = x.shape[0]
    slot = jnp.arange(count * size, dtype=jnp.int32) // size
    total = jnp.where((slot == pos)[:, None, None, None], jnp.tile(x, (count, 1, 1, 1)), 0.0)
    for step in range(1, count):
        got = lax.ppermute(x, axis, [(i, i ^ step) for i in range(count)])
        hit = (slot == (pos ^ step))[:, None, None, None]
        total = total + jnp.where(hit, jnp.tile(got, (count, 1, 1, 1)), 0.0)
    return total


def sum_all(x, axis, count, pos):
    if not xor_partners(count):
        return lax.psum(x, axis)
    step = 1
    while step < count:
        x = x + lax.ppermute(x, axis, [(i, i ^ step) for i in range(count)])
        step *= 2
    return x


def sum_parts(x, axis, count, pos):
    if count == 2:
        return (x, lax.ppermute(x, axis, [(0, 1), (1, 0)]))
    return (sum_all(x, axis, count, pos),)


def scatter_sum(x, axis, count, pos, size):
    if not xor_partners(count):
        return lax.psum_scatter(x, axis, scatter_dimension=0, tiled=True)
    total = lax.dynamic_slice_in_dim(x, pos * size, size, 0)
    for step in range(1, count):
        part = lax.dynamic_slice_in_dim(x, (pos ^ step) * size, size, 0)
        total = total + lax.ppermute(part, axis, [(i, i ^ step) for i in range(count)])
    return total


def partner_lists(count, kern_count):
    lists = [[] for _ in range(kern_count)]
    for step in range(1, count):
        lists[step % kern_count].append(step)
    return lists


def chosen_step(lists, round_index, kern_pos):
    pick = jnp.int32(-1)
    for k, steps in enumerate(lists):
        if round_index < len(steps):
            pick = jnp.where(kern_pos == k, jnp.int32(steps[round_index]), pick)
    return pick


def gather_split(x, count, pos, kern_count, kern_pos):
    size = x.shape[0]
    lists = partner_lists(count, kern_count)
    slot = jnp.arange(count * size, dtype=jnp.int32) // size
    spread = lambda part: jnp.tile(part, (count, 1, 1, 1))
    collected = jnp.zeros((count * size,) + x.shape[1:], x.dtype)
    for r in range(max(len(steps) for steps in lists)):
        pairs = []
        for k, steps in enumerate(lists):
            if r < len(steps):
                pairs += [((t ^ steps[r]) * kern_count + k, t * kern_count + k) for t in range(count)]
        got = lax.ppermute(x, ("tile", "kern"), pairs)
        step = chosen_step(lists, r, kern_pos)
        source = jnp.where(step >= 0, pos ^ step, -1)
        collected = collected + jnp.where((slot == source)[:, None, None, None], spread(got), 0.0)
    return sum_parts(collected, "kern", kern_count, kern_pos)


def scatter_split(x, count, pos, kern_count, kern_pos, size, between):
    lists = partner_lists(count, kern_count)
    own = lax.dynamic_slice_in_dim(x, pos * size, size, 0)
    total = jnp.where(kern_pos == 0, own, 0.0)
    for r in range(max(len(steps) for steps in lists)):
        pairs = []
        for k, steps in enumerate(lists):
            if r < len(steps):
                pairs += [(t * kern_count + k, (t ^ steps[r]) * kern_count + k) for t in range(count)]
        step = chosen_step(lists, r, kern_pos)
        target = jnp.where(step >= 0, pos ^ step, 0)
        part = lax.dynamic_slice_in_dim(x, target * size, size, 0)
        total = total + lax.ppermute(part, ("tile", "kern"), pairs)
    done, token = between()
    total = total + 0.0 * token
    return done, sum_parts(total, "kern", kern_count, kern_pos)


def on_device(
    tile_mask, master_mask, target, inst_master, inst_shift, kernels, kernel_weight, corner_dose
):
    cos_tab, sin_tab = band_tables()
    scale = 1.0 / (P_SIZE * P_SIZE)
    local_tiles = tile_mask.shape[0]
    local_masters = master_mask.shape[0]
    tile_count = lax.axis_size("tile")
    tile_pos = lax.axis_index("tile")
    kern_count = lax.axis_size("kern")
    kern_pos = lax.axis_index("kern")
    per_dev = local_tiles // kern_count
    first = kern_pos * per_dev
    region_tiles = tile_count * local_tiles
    region_masters = tile_count * local_masters

    with jax.named_scope("master_spectra"):
        own_re, own_im = spectra(master_mask.astype(jnp.float32), cos_tab, sin_tab)
        own = jnp.stack([own_re, own_im], axis=1)
        if xor_partners(tile_count) and xor_partners(kern_count) and tile_count > 2:
            every = gather_split(own, tile_count, tile_pos, kern_count, kern_pos)
            own_part = own
        else:
            every = (gather_all(own, "tile", tile_count, tile_pos),)
            own_part = jnp.zeros_like(own)

    dose = corner_dose[0]
    kerns = kernels[0]
    h_re = kerns[:, 0]
    h_im = kerns[:, 1]
    weights = kernel_weight[0]

    with jax.named_scope("imaging_kernel"):
        count = h_re.shape[0]
        twice = (2.0 * weights)[:, None, None]
        ht_re = jnp.swapaxes(h_re, 1, 2) * twice
        ht_im = jnp.swapaxes(h_im, 1, 2) * twice
        h_cat = jnp.concatenate([ht_re, ht_re, ht_im, -ht_im], axis=-1).reshape(count * B, 128)
        parts = []
        for j in range(per_dev):
            pos = jnp.stack([first + j, tile_pos]).astype(jnp.int32)
            parts.append(
                imaging(
                    pos, inst_master, inst_shift, weights, corner_dose, tile_mask, every, own_part, target,
                    kerns, h_cat,
                )
            )
        comp = jnp.stack(parts)

    with jax.named_scope("gradient_exchange"):
        corner_count = lax.axis_size("corner")
        corner_pos = lax.axis_index("corner")
        if corner_count == 2 and kern_count == 2 and per_dev == 1:
            got = [
                lax.ppermute(comp, ("corner", "kern"), [(i, i ^ step) for i in range(4)])
                for step in (1, 2, 3)
            ]
            mine = comp + got[1]
            other = got[0] + got[2]
            both = jnp.where(kern_pos == 0, jnp.concatenate([mine, other]), jnp.concatenate([other, mine]))
        else:
            comp = sum_all(comp, "corner", corner_count, corner_pos)
            both = gather_all(comp, "kern", kern_count, kern_pos)
        mine_tiles = both[:, 0:2]
        owner_pick = (
            inst_master[:, None] == jnp.arange(region_masters, dtype=jnp.int32)[None, :]
        ).astype(jnp.float32)
        terms = jnp.sum(owner_pick[:, :, None, None, None] * both[:, None, 2:4], axis=0)
        if xor_partners(tile_count) and xor_partners(kern_count) and tile_count > 2:
            tile_grad, mine_masters = scatter_split(
                terms, tile_count, tile_pos, kern_count, kern_pos, local_masters,
                lambda: pixels(mine_tiles, token=True),
            )
        else:
            tile_grad = pixels(mine_tiles)
            mine_masters = (scatter_sum(terms, "tile", tile_count, tile_pos, local_masters),)

    with jax.named_scope("pixel_gradients"):
        master_grad = pixels(*mine_masters)
    return (tile_grad, master_grad)


def solution(mesh):
    return jax.shard_map(
        on_device,
        mesh=mesh,
        in_specs=(
            P(("region", "tile"), None, None),
            P(("region", "tile"), None, None),
            P(("region", "tile"), None, None),
            P(("region", "tile")),
            P(("region", "tile"), None),
            P("corner", None, None, None, None),
            P("corner", None),
            P("corner"),
        ),
        out_specs=(P(("region", "tile"), None, None), P(("region", "tile"), None, None)),
        check_vma=False,
    )
```

```python
import functools
import math

import numpy as np
import jax
import jax.numpy as jnp
from jax import lax
from jax.sharding import PartitionSpec as P
from jax.experimental import pallas as pl
from jax.experimental.pallas import tpu as pltpu

P_SIZE = 256
B = 32


precise = lax.Precision.HIGHEST
steepness = 3.0
threshold = 1.0


def band_tables():
    freq = np.arange(B, dtype=np.int64) - B // 2
    pixel = np.arange(P_SIZE, dtype=np.int64)
    angle = (2.0 * math.pi / P_SIZE) * np.mod(freq[:, None] * pixel[None, :], P_SIZE).astype(np.float64)
    return (jnp.asarray(np.cos(angle), jnp.float32), jnp.asarray(-np.sin(angle), jnp.float32))


def phase_ramp(shift):
    freq = jnp.arange(B, dtype=jnp.int32) - B // 2
    total = (
        freq[None, :, None] * shift[:, 0][:, None, None]
        + freq[None, None, :] * shift[:, 1][:, None, None]
    )
    angle = 2.0 * math.pi / P_SIZE * jnp.mod(total, P_SIZE).astype(jnp.float32)
    return (jnp.cos(angle), -jnp.sin(angle))


def spectra(masks, cos_tab, sin_tab):
    rows_re = jnp.einsum("bx,nxy->nby", cos_tab, masks, precision=precise)
    rows_im = jnp.einsum("bx,nxy->nby", sin_tab, masks, precision=precise)
    spec_re = jnp.einsum("nby,cy->nbc", rows_re, cos_tab, precision=precise) - jnp.einsum(
        "nby,cy->nbc", rows_im, sin_tab, precision=precise
    )
    spec_im = jnp.einsum("nby,cy->nbc", rows_re, sin_tab, precision=precise) + jnp.einsum(
        "nby,cy->nbc", rows_im, cos_tab, precision=precise
    )
    return (spec_re, spec_im)


def back_pixels(x_re, x_im, cos_tab, sin_tab):
    half_re = jnp.einsum("bx,nbc->nxc", cos_tab, x_re, precision=precise) + jnp.einsum(
        "bx,nbc->nxc", sin_tab, x_im, precision=precise
    )
    half_im = jnp.einsum("bx,nbc->nxc", cos_tab, x_im, precision=precise) - jnp.einsum(
        "bx,nbc->nxc", sin_tab, x_re, precision=precise
    )
    return jnp.einsum("nxc,cy->nxy", half_re, cos_tab, precision=precise) + jnp.einsum(
        "nxc,cy->nxy", half_im, sin_tab, precision=precise
    )


def dot_full(a, b):
    return jnp.dot(a, b, precision=precise, preferred_element_type=jnp.float32)


def dot_parts(a, b):
    return jnp.dot(a, b, preferred_element_type=jnp.float32)


def split_three(a):
    hi = a.astype(jnp.bfloat16)
    rest = a - hi.astype(jnp.float32)
    mid = rest.astype(jnp.bfloat16)
    lo = (rest - mid.astype(jnp.float32)).astype(jnp.bfloat16)
    return hi, mid, lo


def table_three(table):
    hi = table.astype(jnp.bfloat16)
    rest = table - hi.astype(np.float64)
    mid = rest.astype(jnp.bfloat16)
    lo = (rest - mid.astype(np.float64)).astype(jnp.bfloat16)
    return hi, mid, lo


def imaging_tables():
    freq = np.arange(B, dtype=np.int64) - B // 2
    pixel = np.arange(P_SIZE, dtype=np.int64)
    angle = (2.0 * math.pi / P_SIZE) * np.mod(freq[:, None] * pixel[None, :], P_SIZE).astype(np.float64)
    c_re = np.cos(angle)
    c_im = -np.sin(angle)
    scale = 1.0 / (P_SIZE * P_SIZE)
    right_w = np.zeros((128, 2 * P_SIZE))
    right_w[:B, :P_SIZE] = c_re
    right_w[:B, P_SIZE:] = -c_im
    right_w[B : 2 * B, :P_SIZE] = c_im
    right_w[B : 2 * B, P_SIZE:] = c_re
    left_a = np.zeros((P_SIZE, 128))
    left_a[:, :B] = c_re.T * scale
    left_a[:, B : 2 * B] = -c_im.T * scale
    right_b = np.zeros((2 * P_SIZE, 128))
    right_b[:P_SIZE, :B] = c_re.T * scale
    right_b[:P_SIZE, B : 2 * B] = c_im.T * scale
    right_b[P_SIZE:, :B] = -c_im.T * scale
    right_b[P_SIZE:, B : 2 * B] = c_re.T * scale
    ct_re = c_re.T
    ct_im = c_im.T
    right_c = np.zeros((2 * P_SIZE, 128))
    for col, (top, bottom) in enumerate(
        ((ct_re, -ct_im), (ct_im, ct_re), (ct_im, ct_re), (ct_re, -ct_im))
    ):
        right_c[:P_SIZE, col * B : (col + 1) * B] = top
        right_c[P_SIZE:, col * B : (col + 1) * B] = bottom
    a_hi, a_mid, a_lo = table_three(left_a[:, : 2 * B])
    left_three = np.concatenate([a_hi, a_hi, a_mid, a_hi, a_lo, a_mid], axis=1)
    b_hi, b_mid, b_lo = table_three(right_b)
    right_hm = np.concatenate([b_hi, b_mid], axis=1)
    right_lh = np.concatenate([b_lo, b_hi], axis=0)
    parts_re = table_three(c_re)
    parts_im = table_three(c_im)
    rows_three = np.concatenate(
        [np.concatenate(parts_re, axis=1), np.concatenate(parts_im, axis=1)], axis=0
    )
    plain = (c_re, c_im, c_re.T, c_im.T, right_w[:B], right_w[B : 2 * B], right_c)
    out = [jnp.asarray(table, jnp.float32) for table in plain]
    return out + [jnp.asarray(table) for table in (left_three, right_hm, right_lh, rows_three)]


def imaging_body(
    im_ref, sh_ref, w_ref, dose_ref, mask_ref, ev_ref, ev2_ref, own_ref, goal_ref, h_ref, hc_ref,
    c_re_ref, c_im_ref, ct_re_ref, ct_im_ref, rw_top, rw_bot, rc_ref, la_ref, rhm_ref, rlh_ref, rows_ref,
    slots_ref, f_buf, i_buf, u_buf, w_buf, xr_buf, xi_buf, *, per_dev, offset,
):
    count = f_buf.shape[0]
    pos = lax.axis_index("kern") * per_dev + offset
    master = im_ref[pos]
    pick0 = (lax.broadcasted_iota(jnp.int32, (P_SIZE, 128), 0) == sh_ref[pos, 0]).astype(jnp.float32)
    pick1 = (lax.broadcasted_iota(jnp.int32, (8, P_SIZE), 1) == sh_ref[pos, 1]).astype(jnp.float32)
    e0_re = dot_full(c_re_ref[...], pick0)[:, 0:1]
    e0_im = dot_full(c_im_ref[...], pick0)[:, 0:1]
    e1_re = dot_full(pick1, ct_re_ref[...])[0:1, :]
    e1_im = dot_full(pick1, ct_im_ref[...])[0:1, :]
    ph_re = e0_re * e1_re - e0_im * e1_im
    ph_im = e0_re * e1_im + e0_im * e1_re
    local_masters = own_ref.shape[0]
    is_own = master // local_masters == lax.axis_index("tile")
    m_re = ev_ref[master, 0] + ev2_ref[master, 0] + jnp.where(is_own, own_ref[master % local_masters, 0], 0.0)
    m_im = ev_ref[master, 1] + ev2_ref[master, 1] + jnp.where(is_own, own_ref[master % local_masters, 1], 0.0)
    mask = mask_ref[pos]
    rows = dot_parts(rows_ref[...], jnp.concatenate([mask, mask, mask], axis=0))
    t_one = dot_full(rows, ct_re_ref[...])
    t_two = dot_full(rows, ct_im_ref[...])
    s_re = t_one[:B] - t_two[B:] + (ph_re * m_re - ph_im * m_im)
    s_im = t_two[:B] + t_one[B:] + (ph_re * m_im + ph_im * m_re)
    i_buf[...] = jnp.zeros(i_buf.shape, jnp.float32)

    def spectrum(k, carry):
        h_re = h_ref[k, 0]
        h_im = h_ref[k, 1]
        rows = pl.ds(pl.multiple_of(k * B, B), B)
        xr_buf[rows, :] = h_re * s_re - h_im * s_im
        xi_buf[rows, :] = h_re * s_im + h_im * s_re
        return carry

    lax.fori_loop(0, count, spectrum, 0)
    w_buf[...] = dot_full(xr_buf[...], rw_top[...]) + dot_full(xi_buf[...], rw_bot[...])

    def forward(k, carry):
        rows = w_buf[pl.ds(pl.multiple_of(k * B, B), B), :]
        swap = jnp.concatenate([-rows[:, P_SIZE:], rows[:, :P_SIZE]], axis=1)
        s_hi, s_mid, s_lo = split_three(jnp.concatenate([rows, swap], axis=0))
        stacked = jnp.concatenate([s_hi, s_mid, s_hi, s_lo, s_hi, s_mid], axis=0)
        field = dot_parts(la_ref[...], stacked)
        f_buf[k] = field
        power = field * field
        i_buf[...] += w_ref[k] * (power[:, :P_SIZE] + power[:, P_SIZE:])
        return carry

    lax.fori_loop(0, count, forward, 0)
    dose = dose_ref[0]
    resist = 1.0 / (1.0 + jnp.exp(-(steepness * (dose * i_buf[...] - threshold))))
    goal = goal_ref[pos].astype(jnp.float32)
    i_buf[...] = 2.0 * (resist - goal) * resist * (1.0 - resist) * steepness * dose

    def backward(k, carry):
        sens = i_buf[...]
        weighted = f_buf[k] * jnp.concatenate([sens, sens], axis=1)
        q_hi, q_mid, q_lo = split_three(weighted)
        first = dot_parts(q_hi, rhm_ref[...]) + dot_parts(q_mid, rhm_ref[...])
        rest = dot_parts(jnp.concatenate([q_hi, q_lo], axis=1), rlh_ref[...])
        half = first[:, :128] + first[:, 128:] + rest
        flip = half.T
        u_buf[pl.ds(pl.multiple_of(k * B, B), B), :] = jnp.concatenate([flip[:B], flip[B : 2 * B]], axis=1)
        return carry

    lax.fori_loop(0, count, backward, 0)
    out = dot_full(u_buf[...], rc_ref[...])
    acc = jnp.sum((hc_ref[...] * out).reshape(count, B, 128), axis=0)
    flip = jnp.concatenate([acc, jnp.zeros((128 - B, 128), jnp.float32)], axis=0).T
    g_re = flip[0:B, 0:B] + flip[2 * B : 3 * B, 0:B]
    g_im = flip[B : 2 * B, 0:B] + flip[3 * B : 4 * B, 0:B]
    slots_ref[0] = g_re
    slots_ref[1] = g_im
    slots_ref[2] = ph_re * g_re + ph_im * g_im
    slots_ref[3] = ph_re * g_im - ph_im * g_re


def imaging(per_dev, offset, inst_master, inst_shift, weights, dose, tile_mask, every, own, target, kerns, h_cat):
    if len(every) == 1:
        every = (every[0], jnp.zeros_like(every[0]))
    count = weights.shape[0]
    tables = imaging_tables()
    vmem = pl.BlockSpec(memory_space=pltpu.VMEM)
    smem = pl.BlockSpec(memory_space=pltpu.SMEM)
    return pl.pallas_call(
        functools.partial(imaging_body, per_dev=per_dev, offset=offset),
        out_shape=jax.ShapeDtypeStruct((4, B, B), jnp.float32),
        in_specs=[smem] * 4 + [vmem] * 7 + [vmem] * len(tables),
        out_specs=vmem,
        scratch_shapes=[
            pltpu.VMEM((count, P_SIZE, 2 * P_SIZE), jnp.float32),
            pltpu.VMEM((P_SIZE, P_SIZE), jnp.float32),
            pltpu.VMEM((count * B, 2 * P_SIZE), jnp.float32),
            pltpu.VMEM((count * B, 2 * P_SIZE), jnp.float32),
            pltpu.VMEM((count * B, B), jnp.float32),
            pltpu.VMEM((count * B, B), jnp.float32),
        ],
    )(inst_master, inst_shift, weights, dose, tile_mask, *every, own, target, kerns, h_cat, *tables)


def pixel_body(*refs, passes):
    if passes:
        out_ref, token_ref = refs[-2:]
        token_ref[...] = jnp.zeros(token_ref.shape, jnp.float32)
        refs = refs[:-2] + (out_ref,)
    out_ref = refs[-1]
    c_re_ref, c_im_ref, left_ref = refs[-4:-1]
    parts = refs[:-4]
    for n in range(out_ref.shape[0]):
        x_re = sum(part[n, 0] for part in parts)
        x_im = sum(part[n, 1] for part in parts)
        x_both = jnp.concatenate([x_re, x_im], axis=0)
        p_re = dot_full(x_both, c_re_ref[...])
        p_im = dot_full(x_both, c_im_ref[...])
        y_re = p_re[:B] + p_im[B:]
        y_im = p_re[B:] - p_im[:B]
        y_hi, y_mid, y_lo = split_three(jnp.concatenate([y_re, y_im], axis=0))
        stacked = jnp.concatenate([y_hi, y_mid, y_hi, y_lo, y_hi, y_mid], axis=0)
        out_ref[n] = dot_parts(left_ref[...], stacked)


def pixels(*parts, token=False):
    freq = np.arange(B, dtype=np.int64) - B // 2
    pixel = np.arange(P_SIZE, dtype=np.int64)
    angle = (2.0 * math.pi / P_SIZE) * np.mod(freq[:, None] * pixel[None, :], P_SIZE).astype(np.float64)
    c_re = np.cos(angle)
    c_im = -np.sin(angle)
    a_hi, a_mid, a_lo = table_three(np.concatenate([c_re.T, c_im.T], axis=1))
    left = np.concatenate([a_hi, a_hi, a_mid, a_hi, a_lo, a_mid], axis=1)
    tables = [jnp.asarray(c_re, jnp.float32), jnp.asarray(c_im, jnp.float32), jnp.asarray(left)]
    vmem = pl.BlockSpec(memory_space=pltpu.VMEM)
    shape = jax.ShapeDtypeStruct((parts[0].shape[0], P_SIZE, P_SIZE), jnp.float32)
    if not token:
        return pl.pallas_call(
            functools.partial(pixel_body, passes=False),
            out_shape=shape,
            in_specs=[vmem] * (len(parts) + 3),
            out_specs=vmem,
        )(*parts, *tables)
    return pl.pallas_call(
        functools.partial(pixel_body, passes=True),
        out_shape=(shape, jax.ShapeDtypeStruct((1, 1, 1, 1), jnp.float32)),
        in_specs=[vmem] * (len(parts) + 3),
        out_specs=(vmem, vmem),
    )(*parts, *tables)


def xor_partners(count):
    return count & (count - 1) == 0 and count <= 8


def gather_all(x, axis, count, pos):
    if not xor_partners(count):
        return lax.all_gather(x, axis, axis=0, tiled=True)
    size = x.shape[0]
    slot = jnp.arange(count * size, dtype=jnp.int32) // size
    total = jnp.where((slot == pos)[:, None, None, None], jnp.tile(x, (count, 1, 1, 1)), 0.0)
    for step in range(1, count):
        got = lax.ppermute(x, axis, [(i, i ^ step) for i in range(count)])
        hit = (slot == (pos ^ step))[:, None, None, None]
        total = total + jnp.where(hit, jnp.tile(got, (count, 1, 1, 1)), 0.0)
    return total


def sum_all(x, axis, count, pos):
    if not xor_partners(count):
        return lax.psum(x, axis)
    step = 1
    while step < count:
        x = x + lax.ppermute(x, axis, [(i, i ^ step) for i in range(count)])
        step *= 2
    return x


def sum_parts(x, axis, count, pos):
    if count == 2:
        return (x, lax.ppermute(x, axis, [(0, 1), (1, 0)]))
    return (sum_all(x, axis, count, pos),)


def scatter_sum(x, axis, count, pos, size):
    if not xor_partners(count):
        return lax.psum_scatter(x, axis, scatter_dimension=0, tiled=True)
    total = lax.dynamic_slice_in_dim(x, pos * size, size, 0)
    for step in range(1, count):
        part = lax.dynamic_slice_in_dim(x, (pos ^ step) * size, size, 0)
        total = total + lax.ppermute(part, axis, [(i, i ^ step) for i in range(count)])
    return total


def partner_lists(count, kern_count):
    lists = [[] for _ in range(kern_count)]
    for step in range(1, count):
        lists[step % kern_count].append(step)
    return lists


def chosen_step(lists, round_index, kern_pos):
    pick = jnp.int32(-1)
    for k, steps in enumerate(lists):
        if round_index < len(steps):
            pick = jnp.where(kern_pos == k, jnp.int32(steps[round_index]), pick)
    return pick


def gather_split(x, count, pos, kern_count, kern_pos):
    size = x.shape[0]
    lists = partner_lists(count, kern_count)
    slot = jnp.arange(count * size, dtype=jnp.int32) // size
    spread = lambda part: jnp.tile(part, (count, 1, 1, 1))
    collected = jnp.zeros((count * size,) + x.shape[1:], x.dtype)
    for r in range(max(len(steps) for steps in lists)):
        pairs = []
        for k, steps in enumerate(lists):
            if r < len(steps):
                pairs += [((t ^ steps[r]) * kern_count + k, t * kern_count + k) for t in range(count)]
        got = lax.ppermute(x, ("tile", "kern"), pairs)
        step = chosen_step(lists, r, kern_pos)
        source = jnp.where(step >= 0, pos ^ step, -1)
        collected = collected + jnp.where((slot == source)[:, None, None, None], spread(got), 0.0)
    return sum_parts(collected, "kern", kern_count, kern_pos)


def scatter_split(x, count, pos, kern_count, kern_pos, size, between):
    lists = partner_lists(count, kern_count)
    own = lax.dynamic_slice_in_dim(x, pos * size, size, 0)
    total = jnp.where(kern_pos == 0, own, 0.0)
    for r in range(max(len(steps) for steps in lists)):
        pairs = []
        for k, steps in enumerate(lists):
            if r < len(steps):
                pairs += [(t * kern_count + k, (t ^ steps[r]) * kern_count + k) for t in range(count)]
        step = chosen_step(lists, r, kern_pos)
        target = jnp.where(step >= 0, pos ^ step, 0)
        part = lax.dynamic_slice_in_dim(x, target * size, size, 0)
        total = total + lax.ppermute(part, ("tile", "kern"), pairs)
    done, token = between()
    total = total + 0.0 * token
    return done, sum_parts(total, "kern", kern_count, kern_pos)


def on_device(
    tile_mask, master_mask, target, inst_master, inst_shift, kernels, kernel_weight, corner_dose
):
    cos_tab, sin_tab = band_tables()
    scale = 1.0 / (P_SIZE * P_SIZE)
    local_tiles = tile_mask.shape[0]
    local_masters = master_mask.shape[0]
    tile_count = lax.axis_size("tile")
    tile_pos = lax.axis_index("tile")
    kern_count = lax.axis_size("kern")
    kern_pos = lax.axis_index("kern")
    per_dev = local_tiles // kern_count
    first = kern_pos * per_dev
    region_tiles = tile_count * local_tiles
    region_masters = tile_count * local_masters

    with jax.named_scope("master_spectra"):
        own_re, own_im = spectra(master_mask.astype(jnp.float32), cos_tab, sin_tab)
        own = jnp.stack([own_re, own_im], axis=1)
        if xor_partners(tile_count) and xor_partners(kern_count) and tile_count > 2:
            every = gather_split(own, tile_count, tile_pos, kern_count, kern_pos)
            own_part = own
        else:
            every = (gather_all(own, "tile", tile_count, tile_pos),)
            own_part = jnp.zeros_like(own)

    dose = corner_dose[0]
    kerns = kernels[0]
    h_re = kerns[:, 0]
    h_im = kerns[:, 1]
    weights = kernel_weight[0]

    with jax.named_scope("imaging_kernel"):
        count = h_re.shape[0]
        twice = (2.0 * weights)[:, None, None]
        ht_re = jnp.swapaxes(h_re, 1, 2) * twice
        ht_im = jnp.swapaxes(h_im, 1, 2) * twice
        h_cat = jnp.concatenate([ht_re, ht_re, ht_im, -ht_im], axis=-1).reshape(count * B, 128)
        parts = []
        for j in range(per_dev):
            parts.append(
                imaging(
                    per_dev, j, inst_master, inst_shift, weights, corner_dose, tile_mask, every, own_part, target,
                    kerns, h_cat,
                )
            )
        comp = jnp.stack(parts)

    with jax.named_scope("gradient_exchange"):
        corner_count = lax.axis_size("corner")
        corner_pos = lax.axis_index("corner")
        if corner_count == 2 and kern_count == 2 and per_dev == 1:
            got = [
                lax.ppermute(comp, ("corner", "kern"), [(i, i ^ step) for i in range(4)])
                for step in (1, 2, 3)
            ]
            mine = comp + got[1]
            other = got[0] + got[2]
            both = jnp.where(kern_pos == 0, jnp.concatenate([mine, other]), jnp.concatenate([other, mine]))
        else:
            comp = sum_all(comp, "corner", corner_count, corner_pos)
            both = gather_all(comp, "kern", kern_count, kern_pos)
        mine_tiles = both[:, 0:2]
        owner_pick = (
            inst_master[:, None] == jnp.arange(region_masters, dtype=jnp.int32)[None, :]
        ).astype(jnp.float32)
        terms = jnp.sum(owner_pick[:, :, None, None, None] * both[:, None, 2:4], axis=0)
        if xor_partners(tile_count) and xor_partners(kern_count) and tile_count > 2:
            tile_grad, mine_masters = scatter_split(
                terms, tile_count, tile_pos, kern_count, kern_pos, local_masters,
                lambda: pixels(mine_tiles, token=True),
            )
        else:
            tile_grad = pixels(mine_tiles)
            mine_masters = (scatter_sum(terms, "tile", tile_count, tile_pos, local_masters),)

    with jax.named_scope("pixel_gradients"):
        master_grad = pixels(*mine_masters)
    return (tile_grad, master_grad)


def solution(mesh):
    return jax.shard_map(
        on_device,
        mesh=mesh,
        in_specs=(
            P(("region", "tile"), None, None),
            P(("region", "tile"), None, None),
            P(("region", "tile"), None, None),
            P(("region", "tile")),
            P(("region", "tile"), None),
            P("corner", None, None, None, None),
            P("corner", None),
            P("corner"),
        ),
        out_specs=(P(("region", "tile"), None, None), P(("region", "tile"), None, None)),
        check_vma=False,
    )
```

```python
import functools
import math

import numpy as np
import jax
import jax.numpy as jnp
from jax import lax
from jax.sharding import PartitionSpec as P
from jax.experimental import pallas as pl
from jax.experimental.pallas import tpu as pltpu

P_SIZE = 256
B = 32


precise = lax.Precision.HIGHEST
steepness = 3.0
threshold = 1.0


def band_tables():
    freq = np.arange(B, dtype=np.int64) - B // 2
    pixel = np.arange(P_SIZE, dtype=np.int64)
    angle = (2.0 * math.pi / P_SIZE) * np.mod(freq[:, None] * pixel[None, :], P_SIZE).astype(np.float64)
    return (jnp.asarray(np.cos(angle), jnp.float32), jnp.asarray(-np.sin(angle), jnp.float32))


def phase_ramp(shift):
    freq = jnp.arange(B, dtype=jnp.int32) - B // 2
    total = (
        freq[None, :, None] * shift[:, 0][:, None, None]
        + freq[None, None, :] * shift[:, 1][:, None, None]
    )
    angle = 2.0 * math.pi / P_SIZE * jnp.mod(total, P_SIZE).astype(jnp.float32)
    return (jnp.cos(angle), -jnp.sin(angle))


def spectra(masks, cos_tab, sin_tab):
    rows_re = jnp.einsum("bx,nxy->nby", cos_tab, masks, precision=precise)
    rows_im = jnp.einsum("bx,nxy->nby", sin_tab, masks, precision=precise)
    spec_re = jnp.einsum("nby,cy->nbc", rows_re, cos_tab, precision=precise) - jnp.einsum(
        "nby,cy->nbc", rows_im, sin_tab, precision=precise
    )
    spec_im = jnp.einsum("nby,cy->nbc", rows_re, sin_tab, precision=precise) + jnp.einsum(
        "nby,cy->nbc", rows_im, cos_tab, precision=precise
    )
    return (spec_re, spec_im)


def back_pixels(x_re, x_im, cos_tab, sin_tab):
    half_re = jnp.einsum("bx,nbc->nxc", cos_tab, x_re, precision=precise) + jnp.einsum(
        "bx,nbc->nxc", sin_tab, x_im, precision=precise
    )
    half_im = jnp.einsum("bx,nbc->nxc", cos_tab, x_im, precision=precise) - jnp.einsum(
        "bx,nbc->nxc", sin_tab, x_re, precision=precise
    )
    return jnp.einsum("nxc,cy->nxy", half_re, cos_tab, precision=precise) + jnp.einsum(
        "nxc,cy->nxy", half_im, sin_tab, precision=precise
    )


def dot_full(a, b):
    return jnp.dot(a, b, precision=precise, preferred_element_type=jnp.float32)


def dot_parts(a, b):
    return jnp.dot(a, b, preferred_element_type=jnp.float32)


def split_three(a):
    hi = a.astype(jnp.bfloat16)
    rest = a - hi.astype(jnp.float32)
    mid = rest.astype(jnp.bfloat16)
    lo = (rest - mid.astype(jnp.float32)).astype(jnp.bfloat16)
    return hi, mid, lo


def table_three(table):
    hi = table.astype(jnp.bfloat16)
    rest = table - hi.astype(np.float64)
    mid = rest.astype(jnp.bfloat16)
    lo = (rest - mid.astype(np.float64)).astype(jnp.bfloat16)
    return hi, mid, lo


def imaging_tables():
    freq = np.arange(B, dtype=np.int64) - B // 2
    pixel = np.arange(P_SIZE, dtype=np.int64)
    angle = (2.0 * math.pi / P_SIZE) * np.mod(freq[:, None] * pixel[None, :], P_SIZE).astype(np.float64)
    c_re = np.cos(angle)
    c_im = -np.sin(angle)
    scale = 1.0 / (P_SIZE * P_SIZE)
    right_w = np.zeros((128, 2 * P_SIZE))
    right_w[:B, :P_SIZE] = c_re
    right_w[:B, P_SIZE:] = -c_im
    right_w[B : 2 * B, :P_SIZE] = c_im
    right_w[B : 2 * B, P_SIZE:] = c_re
    left_a = np.zeros((P_SIZE, 128))
    left_a[:, :B] = c_re.T * scale
    left_a[:, B : 2 * B] = -c_im.T * scale
    right_b = np.zeros((2 * P_SIZE, 128))
    right_b[:P_SIZE, :B] = c_re.T * scale
    right_b[:P_SIZE, B : 2 * B] = c_im.T * scale
    right_b[P_SIZE:, :B] = -c_im.T * scale
    right_b[P_SIZE:, B : 2 * B] = c_re.T * scale
    ct_re = c_re.T
    ct_im = c_im.T
    right_c = np.zeros((2 * P_SIZE, 128))
    for col, (top, bottom) in enumerate(
        ((ct_re, -ct_im), (ct_im, ct_re), (ct_im, ct_re), (ct_re, -ct_im))
    ):
        right_c[:P_SIZE, col * B : (col + 1) * B] = top
        right_c[P_SIZE:, col * B : (col + 1) * B] = bottom
    a_hi, a_mid, a_lo = table_three(left_a[:, : 2 * B])
    left_three = np.concatenate([a_hi, a_hi, a_mid, a_hi, a_lo, a_mid], axis=1)
    b_hi, b_mid, b_lo = table_three(right_b)
    right_hm = np.concatenate([b_hi, b_mid], axis=1)
    right_lh = np.concatenate([b_lo, b_hi], axis=0)
    parts_re = table_three(c_re)
    parts_im = table_three(c_im)
    rows_three = np.concatenate(
        [np.concatenate(parts_re, axis=1), np.concatenate(parts_im, axis=1)], axis=0
    )
    plain = (c_re, c_im, c_re.T, c_im.T, right_w[:B], right_w[B : 2 * B], right_c)
    out = [jnp.asarray(table, jnp.float32) for table in plain]
    return out + [jnp.asarray(table) for table in (left_three, right_hm, right_lh, rows_three)]


def imaging_body(
    pos_ref, im_ref, sh_ref, w_ref, dose_ref, mask_ref, ev_ref, ev2_ref, own_ref, goal_ref, h_ref, hc_ref,
    c_re_ref, c_im_ref, ct_re_ref, ct_im_ref, rw_top, rw_bot, rc_ref, la_ref, rhm_ref, rlh_ref, rows_ref,
    slots_ref, f_buf, i_buf, u_buf, w_buf, xr_buf, xi_buf,
):
    count = f_buf.shape[0]
    pos = pos_ref[0]
    master = im_ref[pos]
    pick0 = (lax.broadcasted_iota(jnp.int32, (P_SIZE, 128), 0) == sh_ref[pos, 0]).astype(jnp.float32)
    pick1 = (lax.broadcasted_iota(jnp.int32, (8, P_SIZE), 1) == sh_ref[pos, 1]).astype(jnp.float32)
    e0_re = dot_full(c_re_ref[...], pick0)[:, 0:1]
    e0_im = dot_full(c_im_ref[...], pick0)[:, 0:1]
    e1_re = dot_full(pick1, ct_re_ref[...])[0:1, :]
    e1_im = dot_full(pick1, ct_im_ref[...])[0:1, :]
    ph_re = e0_re * e1_re - e0_im * e1_im
    ph_im = e0_re * e1_im + e0_im * e1_re
    local_masters = own_ref.shape[0]
    is_own = master // local_masters == pos_ref[1]
    m_re = ev_ref[master, 0] + ev2_ref[master, 0] + jnp.where(is_own, own_ref[master % local_masters, 0], 0.0)
    m_im = ev_ref[master, 1] + ev2_ref[master, 1] + jnp.where(is_own, own_ref[master % local_masters, 1], 0.0)
    mask = mask_ref[pos]
    rows = dot_parts(rows_ref[...], jnp.concatenate([mask, mask, mask], axis=0))
    t_one = dot_full(rows, ct_re_ref[...])
    t_two = dot_full(rows, ct_im_ref[...])
    s_re = t_one[:B] - t_two[B:] + (ph_re * m_re - ph_im * m_im)
    s_im = t_two[:B] + t_one[B:] + (ph_re * m_im + ph_im * m_re)
    i_buf[...] = jnp.zeros(i_buf.shape, jnp.float32)

    def spectrum(k, carry):
        h_re = h_ref[k, 0]
        h_im = h_ref[k, 1]
        rows = pl.ds(pl.multiple_of(k * B, B), B)
        xr_buf[rows, :] = h_re * s_re - h_im * s_im
        xi_buf[rows, :] = h_re * s_im + h_im * s_re
        return carry

    lax.fori_loop(0, count, spectrum, 0)
    w_buf[...] = dot_full(xr_buf[...], rw_top[...]) + dot_full(xi_buf[...], rw_bot[...])

    def forward(k, carry):
        rows = w_buf[pl.ds(pl.multiple_of(k * B, B), B), :]
        swap = jnp.concatenate([-rows[:, P_SIZE:], rows[:, :P_SIZE]], axis=1)
        s_hi, s_mid, s_lo = split_three(jnp.concatenate([rows, swap], axis=0))
        stacked = jnp.concatenate([s_hi, s_mid, s_hi, s_lo, s_hi, s_mid], axis=0)
        field = dot_parts(la_ref[...], stacked)
        f_buf[k] = field
        power = field * field
        i_buf[...] += w_ref[k] * (power[:, :P_SIZE] + power[:, P_SIZE:])
        return carry

    lax.fori_loop(0, count, forward, 0)
    dose = dose_ref[0]
    resist = 1.0 / (1.0 + jnp.exp(-(steepness * (dose * i_buf[...] - threshold))))
    goal = goal_ref[pos].astype(jnp.float32)
    i_buf[...] = 2.0 * (resist - goal) * resist * (1.0 - resist) * steepness * dose

    def backward(k, carry):
        sens = i_buf[...]
        weighted = f_buf[k] * jnp.concatenate([sens, sens], axis=1)
        q_hi, q_mid, q_lo = split_three(weighted)
        first = dot_parts(q_hi, rhm_ref[...]) + dot_parts(q_mid, rhm_ref[...])
        rest = dot_parts(jnp.concatenate([q_hi, q_lo], axis=1), rlh_ref[...])
        half = first[:, :128] + first[:, 128:] + rest
        flip = half.T
        u_buf[pl.ds(pl.multiple_of(k * B, B), B), :] = jnp.concatenate([flip[:B], flip[B : 2 * B]], axis=1)
        return carry

    lax.fori_loop(0, count, backward, 0)
    out = dot_full(u_buf[...], rc_ref[...])
    acc = jnp.sum((hc_ref[...] * out).reshape(count, B, 128), axis=0)
    flip = jnp.concatenate([acc, jnp.zeros((128 - B, 128), jnp.float32)], axis=0).T
    g_re = flip[0:B, 0:B] + flip[2 * B : 3 * B, 0:B]
    g_im = flip[B : 2 * B, 0:B] + flip[3 * B : 4 * B, 0:B]
    slots_ref[0] = g_re
    slots_ref[1] = g_im
    slots_ref[2] = ph_re * g_re + ph_im * g_im
    slots_ref[3] = ph_re * g_im - ph_im * g_re


def imaging(pos, inst_master, inst_shift, weights, dose, tile_mask, every, own, target, kerns, h_cat):
    if len(every) == 1:
        every = (every[0], jnp.zeros_like(every[0]))
    count = weights.shape[0]
    tables = imaging_tables()
    vmem = pl.BlockSpec(memory_space=pltpu.VMEM)
    smem = pl.BlockSpec(memory_space=pltpu.SMEM)
    return pl.pallas_call(
        imaging_body,
        out_shape=jax.ShapeDtypeStruct((4, B, B), jnp.float32),
        in_specs=[smem] * 5 + [vmem] * 7 + [vmem] * len(tables),
        out_specs=vmem,
        scratch_shapes=[
            pltpu.VMEM((count, P_SIZE, 2 * P_SIZE), jnp.float32),
            pltpu.VMEM((P_SIZE, P_SIZE), jnp.float32),
            pltpu.VMEM((count * B, 2 * P_SIZE), jnp.float32),
            pltpu.VMEM((count * B, 2 * P_SIZE), jnp.float32),
            pltpu.VMEM((count * B, B), jnp.float32),
            pltpu.VMEM((count * B, B), jnp.float32),
        ],
    )(pos, inst_master, inst_shift, weights, dose, tile_mask, *every, own, target, kerns, h_cat, *tables)


def pixel_body(*refs, passes):
    if passes:
        out_ref, token_ref = refs[-2:]
        token_ref[...] = jnp.zeros(token_ref.shape, jnp.float32)
        refs = refs[:-2] + (out_ref,)
    out_ref = refs[-1]
    c_re_ref, c_im_ref, left_ref = refs[-4:-1]
    parts = refs[:-4]
    for n in range(out_ref.shape[0]):
        x_re = sum(part[n, 0] for part in parts)
        x_im = sum(part[n, 1] for part in parts)
        x_both = jnp.concatenate([x_re, x_im], axis=0)
        p_re = dot_full(x_both, c_re_ref[...])
        p_im = dot_full(x_both, c_im_ref[...])
        y_re = p_re[:B] + p_im[B:]
        y_im = p_re[B:] - p_im[:B]
        y_hi, y_mid, y_lo = split_three(jnp.concatenate([y_re, y_im], axis=0))
        stacked = jnp.concatenate([y_hi, y_mid, y_hi, y_lo, y_hi, y_mid], axis=0)
        out_ref[n] = dot_parts(left_ref[...], stacked)


def group_pixel_body(comp_ref, g0_ref, g1_ref, g2_ref, c_re_ref, c_im_ref, left_ref, out_ref, token_ref):
    token_ref[...] = jnp.zeros(token_ref.shape, jnp.float32)
    own = lax.axis_index("kern")
    for n in range(out_ref.shape[0]):
        mine = n == own
        planes = []
        for c in range(2):
            planes.append(
                jnp.where(mine, comp_ref[0, c] + g1_ref[0, c], g0_ref[0, c] + g2_ref[0, c])
            )
        x_both = jnp.concatenate(planes, axis=0)
        p_re = dot_full(x_both, c_re_ref[...])
        p_im = dot_full(x_both, c_im_ref[...])
        y_re = p_re[:B] + p_im[B:]
        y_im = p_re[B:] - p_im[:B]
        y_hi, y_mid, y_lo = split_three(jnp.concatenate([y_re, y_im], axis=0))
        stacked = jnp.concatenate([y_hi, y_mid, y_hi, y_lo, y_hi, y_mid], axis=0)
        out_ref[n] = dot_parts(left_ref[...], stacked)


def group_pixels(comp, got):
    freq = np.arange(B, dtype=np.int64) - B // 2
    pixel = np.arange(P_SIZE, dtype=np.int64)
    angle = (2.0 * math.pi / P_SIZE) * np.mod(freq[:, None] * pixel[None, :], P_SIZE).astype(np.float64)
    c_re = np.cos(angle)
    c_im = -np.sin(angle)
    a_hi, a_mid, a_lo = table_three(np.concatenate([c_re.T, c_im.T], axis=1))
    left = np.concatenate([a_hi, a_hi, a_mid, a_hi, a_lo, a_mid], axis=1)
    tables = [jnp.asarray(c_re, jnp.float32), jnp.asarray(c_im, jnp.float32), jnp.asarray(left)]
    vmem = pl.BlockSpec(memory_space=pltpu.VMEM)
    shape = jax.ShapeDtypeStruct((2, P_SIZE, P_SIZE), jnp.float32)
    return pl.pallas_call(
        group_pixel_body,
        out_shape=(shape, jax.ShapeDtypeStruct((1, 1, 1, 1), jnp.float32)),
        in_specs=[vmem] * 7,
        out_specs=(vmem, vmem),
    )(comp, *got, *tables)


def pixels(*parts, token=False):
    freq = np.arange(B, dtype=np.int64) - B // 2
    pixel = np.arange(P_SIZE, dtype=np.int64)
    angle = (2.0 * math.pi / P_SIZE) * np.mod(freq[:, None] * pixel[None, :], P_SIZE).astype(np.float64)
    c_re = np.cos(angle)
    c_im = -np.sin(angle)
    a_hi, a_mid, a_lo = table_three(np.concatenate([c_re.T, c_im.T], axis=1))
    left = np.concatenate([a_hi, a_hi, a_mid, a_hi, a_lo, a_mid], axis=1)
    tables = [jnp.asarray(c_re, jnp.float32), jnp.asarray(c_im, jnp.float32), jnp.asarray(left)]
    vmem = pl.BlockSpec(memory_space=pltpu.VMEM)
    shape = jax.ShapeDtypeStruct((parts[0].shape[0], P_SIZE, P_SIZE), jnp.float32)
    if not token:
        return pl.pallas_call(
            functools.partial(pixel_body, passes=False),
            out_shape=shape,
            in_specs=[vmem] * (len(parts) + 3),
            out_specs=vmem,
        )(*parts, *tables)
    return pl.pallas_call(
        functools.partial(pixel_body, passes=True),
        out_shape=(shape, jax.ShapeDtypeStruct((1, 1, 1, 1), jnp.float32)),
        in_specs=[vmem] * (len(parts) + 3),
        out_specs=(vmem, vmem),
    )(*parts, *tables)


def xor_partners(count):
    return count & (count - 1) == 0 and count <= 8


def gather_all(x, axis, count, pos):
    if not xor_partners(count):
        return lax.all_gather(x, axis, axis=0, tiled=True)
    size = x.shape[0]
    slot = jnp.arange(count * size, dtype=jnp.int32) // size
    total = jnp.where((slot == pos)[:, None, None, None], jnp.tile(x, (count, 1, 1, 1)), 0.0)
    for step in range(1, count):
        got = lax.ppermute(x, axis, [(i, i ^ step) for i in range(count)])
        hit = (slot == (pos ^ step))[:, None, None, None]
        total = total + jnp.where(hit, jnp.tile(got, (count, 1, 1, 1)), 0.0)
    return total


def sum_all(x, axis, count, pos):
    if not xor_partners(count):
        return lax.psum(x, axis)
    step = 1
    while step < count:
        x = x + lax.ppermute(x, axis, [(i, i ^ step) for i in range(count)])
        step *= 2
    return x


def sum_parts(x, axis, count, pos):
    if count == 2:
        return (x, lax.ppermute(x, axis, [(0, 1), (1, 0)]))
    return (sum_all(x, axis, count, pos),)


def scatter_sum(x, axis, count, pos, size):
    if not xor_partners(count):
        return lax.psum_scatter(x, axis, scatter_dimension=0, tiled=True)
    total = lax.dynamic_slice_in_dim(x, pos * size, size, 0)
    for step in range(1, count):
        part = lax.dynamic_slice_in_dim(x, (pos ^ step) * size, size, 0)
        total = total + lax.ppermute(part, axis, [(i, i ^ step) for i in range(count)])
    return total


def partner_lists(count, kern_count):
    lists = [[] for _ in range(kern_count)]
    for step in range(1, count):
        lists[step % kern_count].append(step)
    return lists


def chosen_step(lists, round_index, kern_pos):
    pick = jnp.int32(-1)
    for k, steps in enumerate(lists):
        if round_index < len(steps):
            pick = jnp.where(kern_pos == k, jnp.int32(steps[round_index]), pick)
    return pick


def gather_split(x, count, pos, kern_count, kern_pos):
    size = x.shape[0]
    lists = partner_lists(count, kern_count)
    slot = jnp.arange(count * size, dtype=jnp.int32) // size
    spread = lambda part: jnp.tile(part, (count, 1, 1, 1))
    collected = jnp.zeros((count * size,) + x.shape[1:], x.dtype)
    for r in range(max(len(steps) for steps in lists)):
        pairs = []
        for k, steps in enumerate(lists):
            if r < len(steps):
                pairs += [((t ^ steps[r]) * kern_count + k, t * kern_count + k) for t in range(count)]
        got = lax.ppermute(x, ("tile", "kern"), pairs)
        step = chosen_step(lists, r, kern_pos)
        source = jnp.where(step >= 0, pos ^ step, -1)
        collected = collected + jnp.where((slot == source)[:, None, None, None], spread(got), 0.0)
    return sum_parts(collected, "kern", kern_count, kern_pos)


def scatter_split(x, count, pos, kern_count, kern_pos, size, between):
    lists = partner_lists(count, kern_count)
    own = lax.dynamic_slice_in_dim(x, pos * size, size, 0)
    total = jnp.where(kern_pos == 0, own, 0.0)
    for r in range(max(len(steps) for steps in lists)):
        pairs = []
        for k, steps in enumerate(lists):
            if r < len(steps):
                pairs += [(t * kern_count + k, (t ^ steps[r]) * kern_count + k) for t in range(count)]
        step = chosen_step(lists, r, kern_pos)
        target = jnp.where(step >= 0, pos ^ step, 0)
        part = lax.dynamic_slice_in_dim(x, target * size, size, 0)
        total = total + lax.ppermute(part, ("tile", "kern"), pairs)
    done, token = between()
    total = total + 0.0 * token
    return done, sum_parts(total, "kern", kern_count, kern_pos)


def on_device(
    tile_mask, master_mask, target, inst_master, inst_shift, kernels, kernel_weight, corner_dose
):
    cos_tab, sin_tab = band_tables()
    scale = 1.0 / (P_SIZE * P_SIZE)
    local_tiles = tile_mask.shape[0]
    local_masters = master_mask.shape[0]
    tile_count = lax.axis_size("tile")
    tile_pos = lax.axis_index("tile")
    kern_count = lax.axis_size("kern")
    kern_pos = lax.axis_index("kern")
    per_dev = local_tiles // kern_count
    first = kern_pos * per_dev
    region_tiles = tile_count * local_tiles
    region_masters = tile_count * local_masters

    with jax.named_scope("master_spectra"):
        own_re, own_im = spectra(master_mask.astype(jnp.float32), cos_tab, sin_tab)
        own = jnp.stack([own_re, own_im], axis=1)
        if xor_partners(tile_count) and xor_partners(kern_count) and tile_count > 2:
            every = gather_split(own, tile_count, tile_pos, kern_count, kern_pos)
            own_part = own
        else:
            every = (gather_all(own, "tile", tile_count, tile_pos),)
            own_part = jnp.zeros_like(own)

    dose = corner_dose[0]
    kerns = kernels[0]
    h_re = kerns[:, 0]
    h_im = kerns[:, 1]
    weights = kernel_weight[0]

    with jax.named_scope("imaging_kernel"):
        count = h_re.shape[0]
        twice = (2.0 * weights)[:, None, None]
        ht_re = jnp.swapaxes(h_re, 1, 2) * twice
        ht_im = jnp.swapaxes(h_im, 1, 2) * twice
        h_cat = jnp.concatenate([ht_re, ht_re, ht_im, -ht_im], axis=-1).reshape(count * B, 128)
        parts = []
        for j in range(per_dev):
            pos = jnp.stack([first + j, tile_pos]).astype(jnp.int32)
            parts.append(
                imaging(
                    pos, inst_master, inst_shift, weights, corner_dose, tile_mask, every, own_part, target,
                    kerns, h_cat,
                )
            )
        comp = jnp.stack(parts)

    with jax.named_scope("gradient_exchange"):
        corner_count = lax.axis_size("corner")
        corner_pos = lax.axis_index("corner")
        if corner_count == 2 and kern_count == 2 and per_dev == 1:
            got = [
                lax.ppermute(comp, ("corner", "kern"), [(i, i ^ step) for i in range(4)])
                for step in (1, 2, 3)
            ]
            mine = comp + got[1]
            other = got[0] + got[2]
            both = jnp.where(kern_pos == 0, jnp.concatenate([mine, other]), jnp.concatenate([other, mine]))
            tile_pixels = lambda: group_pixels(comp, got)
        else:
            comp = sum_all(comp, "corner", corner_count, corner_pos)
            both = gather_all(comp, "kern", kern_count, kern_pos)
            tile_pixels = lambda: pixels(both[:, 0:2], token=True)
        mine_tiles = both[:, 0:2]
        owner_pick = (
            inst_master[:, None] == jnp.arange(region_masters, dtype=jnp.int32)[None, :]
        ).astype(jnp.float32)
        if corner_count == 2 and kern_count == 2 and per_dev == 1:
            pick_mine = jnp.where(kern_pos == 0, owner_pick[0], owner_pick[1])
            pick_other = jnp.where(kern_pos == 0, owner_pick[1], owner_pick[0])
            terms = (
                pick_mine[:, None, None, None] * (comp[0, 2:4] + got[1][0, 2:4])[None]
                + pick_other[:, None, None, None] * (got[0][0, 2:4] + got[2][0, 2:4])[None]
            )
        else:
            terms = jnp.sum(owner_pick[:, :, None, None, None] * both[:, None, 2:4], axis=0)
        if xor_partners(tile_count) and xor_partners(kern_count) and tile_count > 2:
            tile_grad, mine_masters = scatter_split(
                terms, tile_count, tile_pos, kern_count, kern_pos, local_masters,
                tile_pixels,
            )
        else:
            tile_grad = pixels(mine_tiles)
            mine_masters = (scatter_sum(terms, "tile", tile_count, tile_pos, local_masters),)

    with jax.named_scope("pixel_gradients"):
        master_grad = pixels(*mine_masters)
    return (tile_grad, master_grad)


def solution(mesh):
    return jax.shard_map(
        on_device,
        mesh=mesh,
        in_specs=(
            P(("region", "tile"), None, None),
            P(("region", "tile"), None, None),
            P(("region", "tile"), None, None),
            P(("region", "tile")),
            P(("region", "tile"), None),
            P("corner", None, None, None, None),
            P("corner", None),
            P("corner"),
        ),
        out_specs=(P(("region", "tile"), None, None), P(("region", "tile"), None, None)),
        check_vma=False,
    )
```

```python
import functools
import math

import numpy as np
import jax
import jax.numpy as jnp
from jax import lax
from jax.sharding import PartitionSpec as P
from jax.experimental import pallas as pl
from jax.experimental.pallas import tpu as pltpu

P_SIZE = 256
B = 32


precise = lax.Precision.HIGHEST
steepness = 3.0
threshold = 1.0


def band_tables():
    freq = np.arange(B, dtype=np.int64) - B // 2
    pixel = np.arange(P_SIZE, dtype=np.int64)
    angle = (2.0 * math.pi / P_SIZE) * np.mod(freq[:, None] * pixel[None, :], P_SIZE).astype(np.float64)
    return (jnp.asarray(np.cos(angle), jnp.float32), jnp.asarray(-np.sin(angle), jnp.float32))


def phase_ramp(shift):
    freq = jnp.arange(B, dtype=jnp.int32) - B // 2
    total = (
        freq[None, :, None] * shift[:, 0][:, None, None]
        + freq[None, None, :] * shift[:, 1][:, None, None]
    )
    angle = 2.0 * math.pi / P_SIZE * jnp.mod(total, P_SIZE).astype(jnp.float32)
    return (jnp.cos(angle), -jnp.sin(angle))


def spectra(masks, cos_tab, sin_tab):
    rows_re = jnp.einsum("bx,nxy->nby", cos_tab, masks, precision=precise)
    rows_im = jnp.einsum("bx,nxy->nby", sin_tab, masks, precision=precise)
    spec_re = jnp.einsum("nby,cy->nbc", rows_re, cos_tab, precision=precise) - jnp.einsum(
        "nby,cy->nbc", rows_im, sin_tab, precision=precise
    )
    spec_im = jnp.einsum("nby,cy->nbc", rows_re, sin_tab, precision=precise) + jnp.einsum(
        "nby,cy->nbc", rows_im, cos_tab, precision=precise
    )
    return (spec_re, spec_im)


def back_pixels(x_re, x_im, cos_tab, sin_tab):
    half_re = jnp.einsum("bx,nbc->nxc", cos_tab, x_re, precision=precise) + jnp.einsum(
        "bx,nbc->nxc", sin_tab, x_im, precision=precise
    )
    half_im = jnp.einsum("bx,nbc->nxc", cos_tab, x_im, precision=precise) - jnp.einsum(
        "bx,nbc->nxc", sin_tab, x_re, precision=precise
    )
    return jnp.einsum("nxc,cy->nxy", half_re, cos_tab, precision=precise) + jnp.einsum(
        "nxc,cy->nxy", half_im, sin_tab, precision=precise
    )


def dot_full(a, b):
    return jnp.dot(a, b, precision=precise, preferred_element_type=jnp.float32)


def dot_parts(a, b):
    return jnp.dot(a, b, preferred_element_type=jnp.float32)


def split_three(a):
    hi = a.astype(jnp.bfloat16)
    rest = a - hi.astype(jnp.float32)
    mid = rest.astype(jnp.bfloat16)
    lo = (rest - mid.astype(jnp.float32)).astype(jnp.bfloat16)
    return hi, mid, lo


def table_three(table):
    hi = table.astype(jnp.bfloat16)
    rest = table - hi.astype(np.float64)
    mid = rest.astype(jnp.bfloat16)
    lo = (rest - mid.astype(np.float64)).astype(jnp.bfloat16)
    return hi, mid, lo


def imaging_tables():
    freq = np.arange(B, dtype=np.int64) - B // 2
    pixel = np.arange(P_SIZE, dtype=np.int64)
    angle = (2.0 * math.pi / P_SIZE) * np.mod(freq[:, None] * pixel[None, :], P_SIZE).astype(np.float64)
    c_re = np.cos(angle)
    c_im = -np.sin(angle)
    scale = 1.0 / (P_SIZE * P_SIZE)
    right_w = np.zeros((128, 2 * P_SIZE))
    right_w[:B, :P_SIZE] = c_re
    right_w[:B, P_SIZE:] = -c_im
    right_w[B : 2 * B, :P_SIZE] = c_im
    right_w[B : 2 * B, P_SIZE:] = c_re
    left_a = np.zeros((P_SIZE, 128))
    left_a[:, :B] = c_re.T * scale
    left_a[:, B : 2 * B] = -c_im.T * scale
    right_b = np.zeros((2 * P_SIZE, 128))
    right_b[:P_SIZE, :B] = c_re.T * scale
    right_b[:P_SIZE, B : 2 * B] = c_im.T * scale
    right_b[P_SIZE:, :B] = -c_im.T * scale
    right_b[P_SIZE:, B : 2 * B] = c_re.T * scale
    ct_re = c_re.T
    ct_im = c_im.T
    right_c = np.zeros((2 * P_SIZE, 128))
    for col, (top, bottom) in enumerate(
        ((ct_re, -ct_im), (ct_im, ct_re), (ct_im, ct_re), (ct_re, -ct_im))
    ):
        right_c[:P_SIZE, col * B : (col + 1) * B] = top
        right_c[P_SIZE:, col * B : (col + 1) * B] = bottom
    a_hi, a_mid, a_lo = table_three(left_a[:, : 2 * B])
    left_three = np.concatenate([a_hi, a_hi, a_mid, a_hi, a_lo, a_mid], axis=1)
    b_hi, b_mid, b_lo = table_three(right_b)
    right_hm = np.concatenate([b_hi, b_mid], axis=1)
    right_lh = np.concatenate([b_lo, b_hi], axis=0)
    parts_re = table_three(c_re)
    parts_im = table_three(c_im)
    rows_three = np.concatenate(
        [np.concatenate(parts_re, axis=1), np.concatenate(parts_im, axis=1)], axis=0
    )
    plain = (c_re, c_im, c_re.T, c_im.T, right_w[:B], right_w[B : 2 * B], right_c)
    out = [jnp.asarray(table, jnp.float32) for table in plain]
    return out + [jnp.asarray(table) for table in (left_three, right_hm, right_lh, rows_three)]


def imaging_body(*refs, group):
    if group:
        pos_ref, im_ref, sh_ref, w_ref, dose_ref, mask_ref = refs[:6]
        fetched_ref, r1_ref, r2_ref, r3_ref = refs[6:10]
        rest = refs[10:]
    else:
        pos_ref, im_ref, sh_ref, w_ref, dose_ref, mask_ref, ev_ref, ev2_ref = refs[:8]
        rest = refs[8:]
    (
        own_ref, goal_ref, h_ref, hc_ref,
        c_re_ref, c_im_ref, ct_re_ref, ct_im_ref, rw_top, rw_bot, rc_ref, la_ref, rhm_ref, rlh_ref, rows_ref,
        slots_ref, f_buf, i_buf, u_buf, w_buf, xr_buf, xi_buf,
    ) = rest
    count = f_buf.shape[0]
    pos = pos_ref[0]
    master = im_ref[pos]
    pick0 = (lax.broadcasted_iota(jnp.int32, (P_SIZE, 128), 0) == sh_ref[pos, 0]).astype(jnp.float32)
    pick1 = (lax.broadcasted_iota(jnp.int32, (8, P_SIZE), 1) == sh_ref[pos, 1]).astype(jnp.float32)
    e0_re = dot_full(c_re_ref[...], pick0)[:, 0:1]
    e0_im = dot_full(c_im_ref[...], pick0)[:, 0:1]
    e1_re = dot_full(pick1, ct_re_ref[...])[0:1, :]
    e1_im = dot_full(pick1, ct_im_ref[...])[0:1, :]
    ph_re = e0_re * e1_re - e0_im * e1_im
    ph_im = e0_re * e1_im + e0_im * e1_re
    local_masters = own_ref.shape[0]
    is_own = master // local_masters == pos_ref[1]
    if group:
        far = jnp.bitwise_xor(master, pos_ref[1])
        step = jnp.bitwise_xor(lax.axis_index("corner") * 2 + lax.axis_index("kern"), far)

        def choose(c):
            picked = jnp.where(step == 1, r1_ref[0, c], jnp.where(step == 2, r2_ref[0, c], r3_ref[0, c]))
            picked = jnp.where(step == 0, fetched_ref[0, c], picked)
            return jnp.where(far == 0, own_ref[0, c], picked)

        m_re = choose(0)
        m_im = choose(1)
    else:
        m_re = ev_ref[master, 0] + ev2_ref[master, 0] + jnp.where(is_own, own_ref[master % local_masters, 0], 0.0)
        m_im = ev_ref[master, 1] + ev2_ref[master, 1] + jnp.where(is_own, own_ref[master % local_masters, 1], 0.0)
    mask = mask_ref[pos]
    rows = dot_parts(rows_ref[...], jnp.concatenate([mask, mask, mask], axis=0))
    t_one = dot_full(rows, ct_re_ref[...])
    t_two = dot_full(rows, ct_im_ref[...])
    s_re = t_one[:B] - t_two[B:] + (ph_re * m_re - ph_im * m_im)
    s_im = t_two[:B] + t_one[B:] + (ph_re * m_im + ph_im * m_re)
    i_buf[...] = jnp.zeros(i_buf.shape, jnp.float32)

    def spectrum(k, carry):
        h_re = h_ref[k, 0]
        h_im = h_ref[k, 1]
        rows = pl.ds(pl.multiple_of(k * B, B), B)
        xr_buf[rows, :] = h_re * s_re - h_im * s_im
        xi_buf[rows, :] = h_re * s_im + h_im * s_re
        return carry

    lax.fori_loop(0, count, spectrum, 0)
    w_buf[...] = dot_full(xr_buf[...], rw_top[...]) + dot_full(xi_buf[...], rw_bot[...])

    def forward(k, carry):
        rows = w_buf[pl.ds(pl.multiple_of(k * B, B), B), :]
        swap = jnp.concatenate([-rows[:, P_SIZE:], rows[:, :P_SIZE]], axis=1)
        s_hi, s_mid, s_lo = split_three(jnp.concatenate([rows, swap], axis=0))
        stacked = jnp.concatenate([s_hi, s_mid, s_hi, s_lo, s_hi, s_mid], axis=0)
        field = dot_parts(la_ref[...], stacked)
        f_buf[k] = field
        power = field * field
        i_buf[...] += w_ref[k] * (power[:, :P_SIZE] + power[:, P_SIZE:])
        return carry

    lax.fori_loop(0, count, forward, 0)
    dose = dose_ref[0]
    resist = 1.0 / (1.0 + jnp.exp(-(steepness * (dose * i_buf[...] - threshold))))
    goal = goal_ref[pos].astype(jnp.float32)
    i_buf[...] = 2.0 * (resist - goal) * resist * (1.0 - resist) * steepness * dose

    def backward(k, carry):
        sens = i_buf[...]
        weighted = f_buf[k] * jnp.concatenate([sens, sens], axis=1)
        q_hi, q_mid, q_lo = split_three(weighted)
        first = dot_parts(q_hi, rhm_ref[...]) + dot_parts(q_mid, rhm_ref[...])
        rest = dot_parts(jnp.concatenate([q_hi, q_lo], axis=1), rlh_ref[...])
        half = first[:, :128] + first[:, 128:] + rest
        flip = half.T
        u_buf[pl.ds(pl.multiple_of(k * B, B), B), :] = jnp.concatenate([flip[:B], flip[B : 2 * B]], axis=1)
        return carry

    lax.fori_loop(0, count, backward, 0)
    out = dot_full(u_buf[...], rc_ref[...])
    acc = jnp.sum((hc_ref[...] * out).reshape(count, B, 128), axis=0)
    flip = jnp.concatenate([acc, jnp.zeros((128 - B, 128), jnp.float32)], axis=0).T
    g_re = flip[0:B, 0:B] + flip[2 * B : 3 * B, 0:B]
    g_im = flip[B : 2 * B, 0:B] + flip[3 * B : 4 * B, 0:B]
    slots_ref[0] = g_re
    slots_ref[1] = g_im
    slots_ref[2] = ph_re * g_re + ph_im * g_im
    slots_ref[3] = ph_re * g_im - ph_im * g_re


def imaging(pos, inst_master, inst_shift, weights, dose, tile_mask, every, own, target, kerns, h_cat):
    group = len(every) == 4
    if len(every) == 1:
        every = (every[0], jnp.zeros_like(every[0]))
    count = weights.shape[0]
    tables = imaging_tables()
    vmem = pl.BlockSpec(memory_space=pltpu.VMEM)
    smem = pl.BlockSpec(memory_space=pltpu.SMEM)
    return pl.pallas_call(
        functools.partial(imaging_body, group=group),
        out_shape=jax.ShapeDtypeStruct((4, B, B), jnp.float32),
        in_specs=[smem] * 5 + [vmem] * (5 + len(every)) + [vmem] * len(tables),
        out_specs=vmem,
        scratch_shapes=[
            pltpu.VMEM((count, P_SIZE, 2 * P_SIZE), jnp.float32),
            pltpu.VMEM((P_SIZE, P_SIZE), jnp.float32),
            pltpu.VMEM((count * B, 2 * P_SIZE), jnp.float32),
            pltpu.VMEM((count * B, 2 * P_SIZE), jnp.float32),
            pltpu.VMEM((count * B, B), jnp.float32),
            pltpu.VMEM((count * B, B), jnp.float32),
        ],
    )(pos, inst_master, inst_shift, weights, dose, tile_mask, *every, own, target, kerns, h_cat, *tables)


def pixel_body(*refs, passes):
    if passes:
        out_ref, token_ref = refs[-2:]
        token_ref[...] = jnp.zeros(token_ref.shape, jnp.float32)
        refs = refs[:-2] + (out_ref,)
    out_ref = refs[-1]
    c_re_ref, c_im_ref, left_ref = refs[-4:-1]
    parts = refs[:-4]
    for n in range(out_ref.shape[0]):
        x_re = sum(part[n, 0] for part in parts)
        x_im = sum(part[n, 1] for part in parts)
        x_both = jnp.concatenate([x_re, x_im], axis=0)
        p_re = dot_full(x_both, c_re_ref[...])
        p_im = dot_full(x_both, c_im_ref[...])
        y_re = p_re[:B] + p_im[B:]
        y_im = p_re[B:] - p_im[:B]
        y_hi, y_mid, y_lo = split_three(jnp.concatenate([y_re, y_im], axis=0))
        stacked = jnp.concatenate([y_hi, y_mid, y_hi, y_lo, y_hi, y_mid], axis=0)
        out_ref[n] = dot_parts(left_ref[...], stacked)


def group_pixel_body(comp_ref, g0_ref, g1_ref, g2_ref, c_re_ref, c_im_ref, left_ref, out_ref, token_ref):
    token_ref[...] = jnp.zeros(token_ref.shape, jnp.float32)
    own = lax.axis_index("kern")
    for n in range(out_ref.shape[0]):
        mine = n == own
        planes = []
        for c in range(2):
            planes.append(
                jnp.where(mine, comp_ref[0, c] + g1_ref[0, c], g0_ref[0, c] + g2_ref[0, c])
            )
        x_both = jnp.concatenate(planes, axis=0)
        p_re = dot_full(x_both, c_re_ref[...])
        p_im = dot_full(x_both, c_im_ref[...])
        y_re = p_re[:B] + p_im[B:]
        y_im = p_re[B:] - p_im[:B]
        y_hi, y_mid, y_lo = split_three(jnp.concatenate([y_re, y_im], axis=0))
        stacked = jnp.concatenate([y_hi, y_mid, y_hi, y_lo, y_hi, y_mid], axis=0)
        out_ref[n] = dot_parts(left_ref[...], stacked)


def group_pixels(comp, got):
    freq = np.arange(B, dtype=np.int64) - B // 2
    pixel = np.arange(P_SIZE, dtype=np.int64)
    angle = (2.0 * math.pi / P_SIZE) * np.mod(freq[:, None] * pixel[None, :], P_SIZE).astype(np.float64)
    c_re = np.cos(angle)
    c_im = -np.sin(angle)
    a_hi, a_mid, a_lo = table_three(np.concatenate([c_re.T, c_im.T], axis=1))
    left = np.concatenate([a_hi, a_hi, a_mid, a_hi, a_lo, a_mid], axis=1)
    tables = [jnp.asarray(c_re, jnp.float32), jnp.asarray(c_im, jnp.float32), jnp.asarray(left)]
    vmem = pl.BlockSpec(memory_space=pltpu.VMEM)
    shape = jax.ShapeDtypeStruct((2, P_SIZE, P_SIZE), jnp.float32)
    return pl.pallas_call(
        group_pixel_body,
        out_shape=(shape, jax.ShapeDtypeStruct((1, 1, 1, 1), jnp.float32)),
        in_specs=[vmem] * 7,
        out_specs=(vmem, vmem),
    )(comp, *got, *tables)


def pixels(*parts, token=False):
    freq = np.arange(B, dtype=np.int64) - B // 2
    pixel = np.arange(P_SIZE, dtype=np.int64)
    angle = (2.0 * math.pi / P_SIZE) * np.mod(freq[:, None] * pixel[None, :], P_SIZE).astype(np.float64)
    c_re = np.cos(angle)
    c_im = -np.sin(angle)
    a_hi, a_mid, a_lo = table_three(np.concatenate([c_re.T, c_im.T], axis=1))
    left = np.concatenate([a_hi, a_hi, a_mid, a_hi, a_lo, a_mid], axis=1)
    tables = [jnp.asarray(c_re, jnp.float32), jnp.asarray(c_im, jnp.float32), jnp.asarray(left)]
    vmem = pl.BlockSpec(memory_space=pltpu.VMEM)
    shape = jax.ShapeDtypeStruct((parts[0].shape[0], P_SIZE, P_SIZE), jnp.float32)
    if not token:
        return pl.pallas_call(
            functools.partial(pixel_body, passes=False),
            out_shape=shape,
            in_specs=[vmem] * (len(parts) + 3),
            out_specs=vmem,
        )(*parts, *tables)
    return pl.pallas_call(
        functools.partial(pixel_body, passes=True),
        out_shape=(shape, jax.ShapeDtypeStruct((1, 1, 1, 1), jnp.float32)),
        in_specs=[vmem] * (len(parts) + 3),
        out_specs=(vmem, vmem),
    )(*parts, *tables)


def xor_partners(count):
    return count & (count - 1) == 0 and count <= 8


def gather_all(x, axis, count, pos):
    if not xor_partners(count):
        return lax.all_gather(x, axis, axis=0, tiled=True)
    size = x.shape[0]
    slot = jnp.arange(count * size, dtype=jnp.int32) // size
    total = jnp.where((slot == pos)[:, None, None, None], jnp.tile(x, (count, 1, 1, 1)), 0.0)
    for step in range(1, count):
        got = lax.ppermute(x, axis, [(i, i ^ step) for i in range(count)])
        hit = (slot == (pos ^ step))[:, None, None, None]
        total = total + jnp.where(hit, jnp.tile(got, (count, 1, 1, 1)), 0.0)
    return total


def sum_all(x, axis, count, pos):
    if not xor_partners(count):
        return lax.psum(x, axis)
    step = 1
    while step < count:
        x = x + lax.ppermute(x, axis, [(i, i ^ step) for i in range(count)])
        step *= 2
    return x


def sum_parts(x, axis, count, pos):
    if count == 2:
        return (x, lax.ppermute(x, axis, [(0, 1), (1, 0)]))
    return (sum_all(x, axis, count, pos),)


def scatter_sum(x, axis, count, pos, size):
    if not xor_partners(count):
        return lax.psum_scatter(x, axis, scatter_dimension=0, tiled=True)
    total = lax.dynamic_slice_in_dim(x, pos * size, size, 0)
    for step in range(1, count):
        part = lax.dynamic_slice_in_dim(x, (pos ^ step) * size, size, 0)
        total = total + lax.ppermute(part, axis, [(i, i ^ step) for i in range(count)])
    return total


def partner_lists(count, kern_count):
    lists = [[] for _ in range(kern_count)]
    for step in range(1, count):
        lists[step % kern_count].append(step)
    return lists


def chosen_step(lists, round_index, kern_pos):
    pick = jnp.int32(-1)
    for k, steps in enumerate(lists):
        if round_index < len(steps):
            pick = jnp.where(kern_pos == k, jnp.int32(steps[round_index]), pick)
    return pick


def gather_split(x, count, pos, kern_count, kern_pos):
    size = x.shape[0]
    lists = partner_lists(count, kern_count)
    slot = jnp.arange(count * size, dtype=jnp.int32) // size
    spread = lambda part: jnp.tile(part, (count, 1, 1, 1))
    collected = jnp.zeros((count * size,) + x.shape[1:], x.dtype)
    for r in range(max(len(steps) for steps in lists)):
        pairs = []
        for k, steps in enumerate(lists):
            if r < len(steps):
                pairs += [((t ^ steps[r]) * kern_count + k, t * kern_count + k) for t in range(count)]
        got = lax.ppermute(x, ("tile", "kern"), pairs)
        step = chosen_step(lists, r, kern_pos)
        source = jnp.where(step >= 0, pos ^ step, -1)
        collected = collected + jnp.where((slot == source)[:, None, None, None], spread(got), 0.0)
    return sum_parts(collected, "kern", kern_count, kern_pos)


def scatter_split(x, count, pos, kern_count, kern_pos, size, between):
    lists = partner_lists(count, kern_count)
    own = lax.dynamic_slice_in_dim(x, pos * size, size, 0)
    total = jnp.where(kern_pos == 0, own, 0.0)
    for r in range(max(len(steps) for steps in lists)):
        pairs = []
        for k, steps in enumerate(lists):
            if r < len(steps):
                pairs += [(t * kern_count + k, (t ^ steps[r]) * kern_count + k) for t in range(count)]
        step = chosen_step(lists, r, kern_pos)
        target = jnp.where(step >= 0, pos ^ step, 0)
        part = lax.dynamic_slice_in_dim(x, target * size, size, 0)
        total = total + lax.ppermute(part, ("tile", "kern"), pairs)
    done, token = between()
    total = total + 0.0 * token
    return done, sum_parts(total, "kern", kern_count, kern_pos)


def on_device(
    tile_mask, master_mask, target, inst_master, inst_shift, kernels, kernel_weight, corner_dose
):
    cos_tab, sin_tab = band_tables()
    scale = 1.0 / (P_SIZE * P_SIZE)
    local_tiles = tile_mask.shape[0]
    local_masters = master_mask.shape[0]
    tile_count = lax.axis_size("tile")
    tile_pos = lax.axis_index("tile")
    kern_count = lax.axis_size("kern")
    kern_pos = lax.axis_index("kern")
    per_dev = local_tiles // kern_count
    first = kern_pos * per_dev
    region_tiles = tile_count * local_tiles
    region_masters = tile_count * local_masters

    with jax.named_scope("master_spectra"):
        own_re, own_im = spectra(master_mask.astype(jnp.float32), cos_tab, sin_tab)
        own = jnp.stack([own_re, own_im], axis=1)
        corner_count = lax.axis_size("corner")
        if tile_count == 4 and corner_count == 2 and kern_count == 2 and local_masters == 1:
            pairs = [((t ^ g) * 4 + g, t * 4 + g) for t in range(4) for g in range(1, 4)]
            fetched = lax.ppermute(own, ("tile", "corner", "kern"), pairs)
            every = (fetched,) + tuple(
                lax.ppermute(fetched, ("corner", "kern"), [(i, i ^ step) for i in range(4)])
                for step in (1, 2, 3)
            )
            own_part = own
        elif xor_partners(tile_count) and xor_partners(kern_count) and tile_count > 2:
            every = gather_split(own, tile_count, tile_pos, kern_count, kern_pos)
            own_part = own
        else:
            every = (gather_all(own, "tile", tile_count, tile_pos),)
            own_part = jnp.zeros_like(own)

    dose = corner_dose[0]
    kerns = kernels[0]
    h_re = kerns[:, 0]
    h_im = kerns[:, 1]
    weights = kernel_weight[0]

    with jax.named_scope("imaging_kernel"):
        count = h_re.shape[0]
        twice = (2.0 * weights)[:, None, None]
        ht_re = jnp.swapaxes(h_re, 1, 2) * twice
        ht_im = jnp.swapaxes(h_im, 1, 2) * twice
        h_cat = jnp.concatenate([ht_re, ht_re, ht_im, -ht_im], axis=-1).reshape(count * B, 128)
        parts = []
        for j in range(per_dev):
            pos = jnp.stack([first + j, tile_pos]).astype(jnp.int32)
            parts.append(
                imaging(
                    pos, inst_master, inst_shift, weights, corner_dose, tile_mask, every, own_part, target,
                    kerns, h_cat,
                )
            )
        comp = jnp.stack(parts)

    with jax.named_scope("gradient_exchange"):
        corner_count = lax.axis_size("corner")
        corner_pos = lax.axis_index("corner")
        if corner_count == 2 and kern_count == 2 and per_dev == 1:
            got = [
                lax.ppermute(comp, ("corner", "kern"), [(i, i ^ step) for i in range(4)])
                for step in (1, 2, 3)
            ]
            mine = comp + got[1]
            other = got[0] + got[2]
            both = jnp.where(kern_pos == 0, jnp.concatenate([mine, other]), jnp.concatenate([other, mine]))
            tile_pixels = lambda: group_pixels(comp, got)
        else:
            comp = sum_all(comp, "corner", corner_count, corner_pos)
            both = gather_all(comp, "kern", kern_count, kern_pos)
            tile_pixels = lambda: pixels(both[:, 0:2], token=True)
        mine_tiles = both[:, 0:2]
        owner_pick = (
            inst_master[:, None] == jnp.arange(region_masters, dtype=jnp.int32)[None, :]
        ).astype(jnp.float32)
        if corner_count == 2 and kern_count == 2 and per_dev == 1:
            pick_mine = jnp.where(kern_pos == 0, owner_pick[0], owner_pick[1])
            pick_other = jnp.where(kern_pos == 0, owner_pick[1], owner_pick[0])
            terms = (
                pick_mine[:, None, None, None] * (comp[0, 2:4] + got[1][0, 2:4])[None]
                + pick_other[:, None, None, None] * (got[0][0, 2:4] + got[2][0, 2:4])[None]
            )
        else:
            terms = jnp.sum(owner_pick[:, :, None, None, None] * both[:, None, 2:4], axis=0)
        if xor_partners(tile_count) and xor_partners(kern_count) and tile_count > 2:
            tile_grad, mine_masters = scatter_split(
                terms, tile_count, tile_pos, kern_count, kern_pos, local_masters,
                tile_pixels,
            )
        else:
            tile_grad = pixels(mine_tiles)
            mine_masters = (scatter_sum(terms, "tile", tile_count, tile_pos, local_masters),)

    with jax.named_scope("pixel_gradients"):
        master_grad = pixels(*mine_masters)
    return (tile_grad, master_grad)


def solution(mesh):
    return jax.shard_map(
        on_device,
        mesh=mesh,
        in_specs=(
            P(("region", "tile"), None, None),
            P(("region", "tile"), None, None),
            P(("region", "tile"), None, None),
            P(("region", "tile")),
            P(("region", "tile"), None),
            P("corner", None, None, None, None),
            P("corner", None),
            P("corner"),
        ),
        out_specs=(P(("region", "tile"), None, None), P(("region", "tile"), None, None)),
        check_vma=False,
    )
```

```python
import functools
import math

import numpy as np
import jax
import jax.numpy as jnp
from jax import lax
from jax.sharding import PartitionSpec as P
from jax.experimental import pallas as pl
from jax.experimental.pallas import tpu as pltpu

P_SIZE = 256
B = 32


precise = lax.Precision.HIGHEST
steepness = 3.0
threshold = 1.0


def band_tables():
    freq = np.arange(B, dtype=np.int64) - B // 2
    pixel = np.arange(P_SIZE, dtype=np.int64)
    angle = (2.0 * math.pi / P_SIZE) * np.mod(freq[:, None] * pixel[None, :], P_SIZE).astype(np.float64)
    return (jnp.asarray(np.cos(angle), jnp.float32), jnp.asarray(-np.sin(angle), jnp.float32))


def phase_ramp(shift):
    freq = jnp.arange(B, dtype=jnp.int32) - B // 2
    total = (
        freq[None, :, None] * shift[:, 0][:, None, None]
        + freq[None, None, :] * shift[:, 1][:, None, None]
    )
    angle = 2.0 * math.pi / P_SIZE * jnp.mod(total, P_SIZE).astype(jnp.float32)
    return (jnp.cos(angle), -jnp.sin(angle))


def spectra(masks, cos_tab, sin_tab):
    rows_re = jnp.einsum("bx,nxy->nby", cos_tab, masks, precision=precise)
    rows_im = jnp.einsum("bx,nxy->nby", sin_tab, masks, precision=precise)
    spec_re = jnp.einsum("nby,cy->nbc", rows_re, cos_tab, precision=precise) - jnp.einsum(
        "nby,cy->nbc", rows_im, sin_tab, precision=precise
    )
    spec_im = jnp.einsum("nby,cy->nbc", rows_re, sin_tab, precision=precise) + jnp.einsum(
        "nby,cy->nbc", rows_im, cos_tab, precision=precise
    )
    return (spec_re, spec_im)


def back_pixels(x_re, x_im, cos_tab, sin_tab):
    half_re = jnp.einsum("bx,nbc->nxc", cos_tab, x_re, precision=precise) + jnp.einsum(
        "bx,nbc->nxc", sin_tab, x_im, precision=precise
    )
    half_im = jnp.einsum("bx,nbc->nxc", cos_tab, x_im, precision=precise) - jnp.einsum(
        "bx,nbc->nxc", sin_tab, x_re, precision=precise
    )
    return jnp.einsum("nxc,cy->nxy", half_re, cos_tab, precision=precise) + jnp.einsum(
        "nxc,cy->nxy", half_im, sin_tab, precision=precise
    )


def dot_full(a, b):
    return jnp.dot(a, b, precision=precise, preferred_element_type=jnp.float32)


def dot_parts(a, b):
    return jnp.dot(a, b, preferred_element_type=jnp.float32)


def split_three(a):
    hi = a.astype(jnp.bfloat16)
    rest = a - hi.astype(jnp.float32)
    mid = rest.astype(jnp.bfloat16)
    lo = (rest - mid.astype(jnp.float32)).astype(jnp.bfloat16)
    return hi, mid, lo


def table_three(table):
    hi = table.astype(jnp.bfloat16)
    rest = table - hi.astype(np.float64)
    mid = rest.astype(jnp.bfloat16)
    lo = (rest - mid.astype(np.float64)).astype(jnp.bfloat16)
    return hi, mid, lo


def imaging_tables():
    freq = np.arange(B, dtype=np.int64) - B // 2
    pixel = np.arange(P_SIZE, dtype=np.int64)
    angle = (2.0 * math.pi / P_SIZE) * np.mod(freq[:, None] * pixel[None, :], P_SIZE).astype(np.float64)
    c_re = np.cos(angle)
    c_im = -np.sin(angle)
    scale = 1.0 / (P_SIZE * P_SIZE)
    right_w = np.zeros((128, 2 * P_SIZE))
    right_w[:B, :P_SIZE] = c_re
    right_w[:B, P_SIZE:] = -c_im
    right_w[B : 2 * B, :P_SIZE] = c_im
    right_w[B : 2 * B, P_SIZE:] = c_re
    left_a = np.zeros((P_SIZE, 128))
    left_a[:, :B] = c_re.T * scale
    left_a[:, B : 2 * B] = -c_im.T * scale
    right_b = np.zeros((2 * P_SIZE, 128))
    right_b[:P_SIZE, :B] = c_re.T * scale
    right_b[:P_SIZE, B : 2 * B] = c_im.T * scale
    right_b[P_SIZE:, :B] = -c_im.T * scale
    right_b[P_SIZE:, B : 2 * B] = c_re.T * scale
    ct_re = c_re.T
    ct_im = c_im.T
    right_c = np.zeros((2 * P_SIZE, 128))
    for col, (top, bottom) in enumerate(
        ((ct_re, -ct_im), (ct_im, ct_re), (ct_im, ct_re), (ct_re, -ct_im))
    ):
        right_c[:P_SIZE, col * B : (col + 1) * B] = top
        right_c[P_SIZE:, col * B : (col + 1) * B] = bottom
    a_hi, a_mid, a_lo = table_three(left_a[:, : 2 * B])
    left_three = np.concatenate([a_hi, a_hi, a_mid, a_hi, a_lo, a_mid], axis=1)
    b_hi, b_mid, b_lo = table_three(right_b)
    right_hm = np.concatenate([b_hi, b_mid], axis=1)
    right_lh = np.concatenate([b_lo, b_hi], axis=0)
    parts_re = table_three(c_re)
    parts_im = table_three(c_im)
    rows_three = np.concatenate(
        [np.concatenate(parts_re, axis=1), np.concatenate(parts_im, axis=1)], axis=0
    )
    cols_re = np.concatenate(table_three(c_re.T), axis=0)
    cols_im = np.concatenate(table_three(c_im.T), axis=0)
    plain = (c_re, c_im, c_re.T, c_im.T, right_w[:B], right_w[B : 2 * B], right_c)
    out = [jnp.asarray(table, jnp.float32) for table in plain]
    bf = (left_three, right_hm, right_lh, rows_three, cols_re, cols_im)
    return out + [jnp.asarray(table) for table in bf]


def imaging_body(
    pos_ref, im_ref, sh_ref, w_ref, dose_ref, mask_ref, ev_ref, ev2_ref, own_ref, goal_ref, h_ref, hc_ref,
    c_re_ref, c_im_ref, ct_re_ref, ct_im_ref, rw_top, rw_bot, rc_ref, la_ref, rhm_ref, rlh_ref, rows_ref, cre_ref, cim_ref,
    slots_ref, f_buf, i_buf, u_buf, w_buf, xr_buf, xi_buf,
):
    count = f_buf.shape[0]
    pos = pos_ref[0]
    master = im_ref[pos]
    pick0 = (lax.broadcasted_iota(jnp.int32, (P_SIZE, 128), 0) == sh_ref[pos, 0]).astype(jnp.bfloat16)
    pick1 = (lax.broadcasted_iota(jnp.int32, (8, P_SIZE), 1) == sh_ref[pos, 1]).astype(jnp.bfloat16)
    e0 = dot_parts(rows_ref[...], jnp.concatenate([pick0, pick0, pick0], axis=0))
    e0_re = e0[:B, 0:1]
    e0_im = e0[B:, 0:1]
    pick1 = jnp.concatenate([pick1, pick1, pick1], axis=1)
    e1_re = dot_parts(pick1, cre_ref[...])[0:1, :]
    e1_im = dot_parts(pick1, cim_ref[...])[0:1, :]
    ph_re = e0_re * e1_re - e0_im * e1_im
    ph_im = e0_re * e1_im + e0_im * e1_re
    local_masters = own_ref.shape[0]
    is_own = master // local_masters == pos_ref[1]
    m_re = ev_ref[master, 0] + ev2_ref[master, 0] + jnp.where(is_own, own_ref[master % local_masters, 0], 0.0)
    m_im = ev_ref[master, 1] + ev2_ref[master, 1] + jnp.where(is_own, own_ref[master % local_masters, 1], 0.0)
    mask = mask_ref[pos]
    rows = dot_parts(rows_ref[...], jnp.concatenate([mask, mask, mask], axis=0))
    t_one = dot_full(rows, ct_re_ref[...])
    t_two = dot_full(rows, ct_im_ref[...])
    s_re = t_one[:B] - t_two[B:] + (ph_re * m_re - ph_im * m_im)
    s_im = t_two[:B] + t_one[B:] + (ph_re * m_im + ph_im * m_re)
    i_buf[...] = jnp.zeros(i_buf.shape, jnp.float32)

    def spectrum(k, carry):
        h_re = h_ref[k, 0]
        h_im = h_ref[k, 1]
        rows = pl.ds(pl.multiple_of(k * B, B), B)
        xr_buf[rows, :] = h_re * s_re - h_im * s_im
        xi_buf[rows, :] = h_re * s_im + h_im * s_re
        return carry

    lax.fori_loop(0, count, spectrum, 0)
    w_buf[...] = dot_full(xr_buf[...], rw_top[...]) + dot_full(xi_buf[...], rw_bot[...])

    def forward(k, carry):
        rows = w_buf[pl.ds(pl.multiple_of(k * B, B), B), :]
        swap = jnp.concatenate([-rows[:, P_SIZE:], rows[:, :P_SIZE]], axis=1)
        s_hi, s_mid, s_lo = split_three(jnp.concatenate([rows, swap], axis=0))
        stacked = jnp.concatenate([s_hi, s_mid, s_hi, s_lo, s_hi, s_mid], axis=0)
        field = dot_parts(la_ref[...], stacked)
        f_buf[k] = field
        power = field * field
        i_buf[...] += w_ref[k] * (power[:, :P_SIZE] + power[:, P_SIZE:])
        return carry

    lax.fori_loop(0, count, forward, 0)
    dose = dose_ref[0]
    resist = 1.0 / (1.0 + jnp.exp(-(steepness * (dose * i_buf[...] - threshold))))
    goal = goal_ref[pos].astype(jnp.float32)
    i_buf[...] = 2.0 * (resist - goal) * resist * (1.0 - resist) * steepness * dose

    def backward(k, carry):
        sens = i_buf[...]
        weighted = f_buf[k] * jnp.concatenate([sens, sens], axis=1)
        q_hi, q_mid, q_lo = split_three(weighted)
        first = dot_parts(q_hi, rhm_ref[...]) + dot_parts(q_mid, rhm_ref[...])
        rest = dot_parts(jnp.concatenate([q_hi, q_lo], axis=1), rlh_ref[...])
        half = first[:, :128] + first[:, 128:] + rest
        flip = half.T
        u_buf[pl.ds(pl.multiple_of(k * B, B), B), :] = jnp.concatenate([flip[:B], flip[B : 2 * B]], axis=1)
        return carry

    lax.fori_loop(0, count, backward, 0)
    out = dot_full(u_buf[...], rc_ref[...])
    acc = jnp.sum((hc_ref[...] * out).reshape(count, B, 128), axis=0)
    flip = jnp.concatenate([acc, jnp.zeros((128 - B, 128), jnp.float32)], axis=0).T
    g_re = flip[0:B, 0:B] + flip[2 * B : 3 * B, 0:B]
    g_im = flip[B : 2 * B, 0:B] + flip[3 * B : 4 * B, 0:B]
    slots_ref[0] = g_re
    slots_ref[1] = g_im
    slots_ref[2] = ph_re * g_re + ph_im * g_im
    slots_ref[3] = ph_re * g_im - ph_im * g_re


def imaging(pos, inst_master, inst_shift, weights, dose, tile_mask, every, own, target, kerns, h_cat):
    if len(every) == 1:
        every = (every[0], jnp.zeros_like(every[0]))
    count = weights.shape[0]
    tables = imaging_tables()
    vmem = pl.BlockSpec(memory_space=pltpu.VMEM)
    smem = pl.BlockSpec(memory_space=pltpu.SMEM)
    return pl.pallas_call(
        imaging_body,
        out_shape=jax.ShapeDtypeStruct((4, B, B), jnp.float32),
        in_specs=[smem] * 5 + [vmem] * 7 + [vmem] * len(tables),
        out_specs=vmem,
        scratch_shapes=[
            pltpu.VMEM((count, P_SIZE, 2 * P_SIZE), jnp.float32),
            pltpu.VMEM((P_SIZE, P_SIZE), jnp.float32),
            pltpu.VMEM((count * B, 2 * P_SIZE), jnp.float32),
            pltpu.VMEM((count * B, 2 * P_SIZE), jnp.float32),
            pltpu.VMEM((count * B, B), jnp.float32),
            pltpu.VMEM((count * B, B), jnp.float32),
        ],
    )(pos, inst_master, inst_shift, weights, dose, tile_mask, *every, own, target, kerns, h_cat, *tables)


def pixel_body(*refs, passes):
    if passes:
        out_ref, token_ref = refs[-2:]
        token_ref[...] = jnp.zeros(token_ref.shape, jnp.float32)
        refs = refs[:-2] + (out_ref,)
    out_ref = refs[-1]
    c_re_ref, c_im_ref, left_ref = refs[-4:-1]
    parts = refs[:-4]
    for n in range(out_ref.shape[0]):
        x_re = sum(part[n, 0] for part in parts)
        x_im = sum(part[n, 1] for part in parts)
        x_both = jnp.concatenate([x_re, x_im], axis=0)
        p_re = dot_full(x_both, c_re_ref[...])
        p_im = dot_full(x_both, c_im_ref[...])
        y_re = p_re[:B] + p_im[B:]
        y_im = p_re[B:] - p_im[:B]
        y_hi, y_mid, y_lo = split_three(jnp.concatenate([y_re, y_im], axis=0))
        stacked = jnp.concatenate([y_hi, y_mid, y_hi, y_lo, y_hi, y_mid], axis=0)
        out_ref[n] = dot_parts(left_ref[...], stacked)


def group_pixel_body(comp_ref, g0_ref, g1_ref, g2_ref, c_re_ref, c_im_ref, left_ref, out_ref, token_ref):
    token_ref[...] = jnp.zeros(token_ref.shape, jnp.float32)
    own = lax.axis_index("kern")
    for n in range(out_ref.shape[0]):
        mine = n == own
        planes = []
        for c in range(2):
            planes.append(
                jnp.where(mine, comp_ref[0, c] + g1_ref[0, c], g0_ref[0, c] + g2_ref[0, c])
            )
        x_both = jnp.concatenate(planes, axis=0)
        p_re = dot_full(x_both, c_re_ref[...])
        p_im = dot_full(x_both, c_im_ref[...])
        y_re = p_re[:B] + p_im[B:]
        y_im = p_re[B:] - p_im[:B]
        y_hi, y_mid, y_lo = split_three(jnp.concatenate([y_re, y_im], axis=0))
        stacked = jnp.concatenate([y_hi, y_mid, y_hi, y_lo, y_hi, y_mid], axis=0)
        out_ref[n] = dot_parts(left_ref[...], stacked)


def group_pixels(comp, got):
    freq = np.arange(B, dtype=np.int64) - B // 2
    pixel = np.arange(P_SIZE, dtype=np.int64)
    angle = (2.0 * math.pi / P_SIZE) * np.mod(freq[:, None] * pixel[None, :], P_SIZE).astype(np.float64)
    c_re = np.cos(angle)
    c_im = -np.sin(angle)
    a_hi, a_mid, a_lo = table_three(np.concatenate([c_re.T, c_im.T], axis=1))
    left = np.concatenate([a_hi, a_hi, a_mid, a_hi, a_lo, a_mid], axis=1)
    tables = [jnp.asarray(c_re, jnp.float32), jnp.asarray(c_im, jnp.float32), jnp.asarray(left)]
    vmem = pl.BlockSpec(memory_space=pltpu.VMEM)
    shape = jax.ShapeDtypeStruct((2, P_SIZE, P_SIZE), jnp.float32)
    return pl.pallas_call(
        group_pixel_body,
        out_shape=(shape, jax.ShapeDtypeStruct((1, 1, 1, 1), jnp.float32)),
        in_specs=[vmem] * 7,
        out_specs=(vmem, vmem),
    )(comp, *got, *tables)


def pixels(*parts, token=False):
    freq = np.arange(B, dtype=np.int64) - B // 2
    pixel = np.arange(P_SIZE, dtype=np.int64)
    angle = (2.0 * math.pi / P_SIZE) * np.mod(freq[:, None] * pixel[None, :], P_SIZE).astype(np.float64)
    c_re = np.cos(angle)
    c_im = -np.sin(angle)
    a_hi, a_mid, a_lo = table_three(np.concatenate([c_re.T, c_im.T], axis=1))
    left = np.concatenate([a_hi, a_hi, a_mid, a_hi, a_lo, a_mid], axis=1)
    tables = [jnp.asarray(c_re, jnp.float32), jnp.asarray(c_im, jnp.float32), jnp.asarray(left)]
    vmem = pl.BlockSpec(memory_space=pltpu.VMEM)
    shape = jax.ShapeDtypeStruct((parts[0].shape[0], P_SIZE, P_SIZE), jnp.float32)
    if not token:
        return pl.pallas_call(
            functools.partial(pixel_body, passes=False),
            out_shape=shape,
            in_specs=[vmem] * (len(parts) + 3),
            out_specs=vmem,
        )(*parts, *tables)
    return pl.pallas_call(
        functools.partial(pixel_body, passes=True),
        out_shape=(shape, jax.ShapeDtypeStruct((1, 1, 1, 1), jnp.float32)),
        in_specs=[vmem] * (len(parts) + 3),
        out_specs=(vmem, vmem),
    )(*parts, *tables)


def xor_partners(count):
    return count & (count - 1) == 0 and count <= 8


def gather_all(x, axis, count, pos):
    if not xor_partners(count):
        return lax.all_gather(x, axis, axis=0, tiled=True)
    size = x.shape[0]
    slot = jnp.arange(count * size, dtype=jnp.int32) // size
    total = jnp.where((slot == pos)[:, None, None, None], jnp.tile(x, (count, 1, 1, 1)), 0.0)
    for step in range(1, count):
        got = lax.ppermute(x, axis, [(i, i ^ step) for i in range(count)])
        hit = (slot == (pos ^ step))[:, None, None, None]
        total = total + jnp.where(hit, jnp.tile(got, (count, 1, 1, 1)), 0.0)
    return total


def sum_all(x, axis, count, pos):
    if not xor_partners(count):
        return lax.psum(x, axis)
    step = 1
    while step < count:
        x = x + lax.ppermute(x, axis, [(i, i ^ step) for i in range(count)])
        step *= 2
    return x


def sum_parts(x, axis, count, pos):
    if count == 2:
        return (x, lax.ppermute(x, axis, [(0, 1), (1, 0)]))
    return (sum_all(x, axis, count, pos),)


def scatter_sum(x, axis, count, pos, size):
    if not xor_partners(count):
        return lax.psum_scatter(x, axis, scatter_dimension=0, tiled=True)
    total = lax.dynamic_slice_in_dim(x, pos * size, size, 0)
    for step in range(1, count):
        part = lax.dynamic_slice_in_dim(x, (pos ^ step) * size, size, 0)
        total = total + lax.ppermute(part, axis, [(i, i ^ step) for i in range(count)])
    return total


def partner_lists(count, kern_count):
    lists = [[] for _ in range(kern_count)]
    for step in range(1, count):
        lists[step % kern_count].append(step)
    return lists


def chosen_step(lists, round_index, kern_pos):
    pick = jnp.int32(-1)
    for k, steps in enumerate(lists):
        if round_index < len(steps):
            pick = jnp.where(kern_pos == k, jnp.int32(steps[round_index]), pick)
    return pick


def gather_split(x, count, pos, kern_count, kern_pos):
    size = x.shape[0]
    lists = partner_lists(count, kern_count)
    slot = jnp.arange(count * size, dtype=jnp.int32) // size
    spread = lambda part: jnp.tile(part, (count, 1, 1, 1))
    collected = jnp.zeros((count * size,) + x.shape[1:], x.dtype)
    for r in range(max(len(steps) for steps in lists)):
        pairs = []
        for k, steps in enumerate(lists):
            if r < len(steps):
                pairs += [((t ^ steps[r]) * kern_count + k, t * kern_count + k) for t in range(count)]
        got = lax.ppermute(x, ("tile", "kern"), pairs)
        step = chosen_step(lists, r, kern_pos)
        source = jnp.where(step >= 0, pos ^ step, -1)
        collected = collected + jnp.where((slot == source)[:, None, None, None], spread(got), 0.0)
    return sum_parts(collected, "kern", kern_count, kern_pos)


def scatter_split(x, count, pos, kern_count, kern_pos, size, between):
    lists = partner_lists(count, kern_count)
    own = lax.dynamic_slice_in_dim(x, pos * size, size, 0)
    total = jnp.where(kern_pos == 0, own, 0.0)
    for r in range(max(len(steps) for steps in lists)):
        pairs = []
        for k, steps in enumerate(lists):
            if r < len(steps):
                pairs += [(t * kern_count + k, (t ^ steps[r]) * kern_count + k) for t in range(count)]
        step = chosen_step(lists, r, kern_pos)
        target = jnp.where(step >= 0, pos ^ step, 0)
        part = lax.dynamic_slice_in_dim(x, target * size, size, 0)
        total = total + lax.ppermute(part, ("tile", "kern"), pairs)
    done, token = between()
    total = total + 0.0 * token
    return done, sum_parts(total, "kern", kern_count, kern_pos)


def on_device(
    tile_mask, master_mask, target, inst_master, inst_shift, kernels, kernel_weight, corner_dose
):
    cos_tab, sin_tab = band_tables()
    scale = 1.0 / (P_SIZE * P_SIZE)
    local_tiles = tile_mask.shape[0]
    local_masters = master_mask.shape[0]
    tile_count = lax.axis_size("tile")
    tile_pos = lax.axis_index("tile")
    kern_count = lax.axis_size("kern")
    kern_pos = lax.axis_index("kern")
    per_dev = local_tiles // kern_count
    first = kern_pos * per_dev
    region_tiles = tile_count * local_tiles
    region_masters = tile_count * local_masters

    with jax.named_scope("master_spectra"):
        own_re, own_im = spectra(master_mask.astype(jnp.float32), cos_tab, sin_tab)
        own = jnp.stack([own_re, own_im], axis=1)
        if xor_partners(tile_count) and xor_partners(kern_count) and tile_count > 2:
            every = gather_split(own, tile_count, tile_pos, kern_count, kern_pos)
            own_part = own
        else:
            every = (gather_all(own, "tile", tile_count, tile_pos),)
            own_part = jnp.zeros_like(own)

    dose = corner_dose[0]
    kerns = kernels[0]
    h_re = kerns[:, 0]
    h_im = kerns[:, 1]
    weights = kernel_weight[0]

    with jax.named_scope("imaging_kernel"):
        count = h_re.shape[0]
        twice = (2.0 * weights)[:, None, None]
        ht_re = jnp.swapaxes(h_re, 1, 2) * twice
        ht_im = jnp.swapaxes(h_im, 1, 2) * twice
        h_cat = jnp.concatenate([ht_re, ht_re, ht_im, -ht_im], axis=-1).reshape(count * B, 128)
        parts = []
        for j in range(per_dev):
            pos = jnp.stack([first + j, tile_pos]).astype(jnp.int32)
            parts.append(
                imaging(
                    pos, inst_master, inst_shift, weights, corner_dose, tile_mask, every, own_part, target,
                    kerns, h_cat,
                )
            )
        comp = jnp.stack(parts)

    with jax.named_scope("gradient_exchange"):
        corner_count = lax.axis_size("corner")
        corner_pos = lax.axis_index("corner")
        if corner_count == 2 and kern_count == 2 and per_dev == 1:
            got = [
                lax.ppermute(comp, ("corner", "kern"), [(i, i ^ step) for i in range(4)])
                for step in (1, 2, 3)
            ]
            mine = comp + got[1]
            other = got[0] + got[2]
            both = jnp.where(kern_pos == 0, jnp.concatenate([mine, other]), jnp.concatenate([other, mine]))
            tile_pixels = lambda: group_pixels(comp, got)
        else:
            comp = sum_all(comp, "corner", corner_count, corner_pos)
            both = gather_all(comp, "kern", kern_count, kern_pos)
            tile_pixels = lambda: pixels(both[:, 0:2], token=True)
        mine_tiles = both[:, 0:2]
        owner_pick = (
            inst_master[:, None] == jnp.arange(region_masters, dtype=jnp.int32)[None, :]
        ).astype(jnp.float32)
        if corner_count == 2 and kern_count == 2 and per_dev == 1:
            pick_mine = jnp.where(kern_pos == 0, owner_pick[0], owner_pick[1])
            pick_other = jnp.where(kern_pos == 0, owner_pick[1], owner_pick[0])
            terms = (
                pick_mine[:, None, None, None] * (comp[0, 2:4] + got[1][0, 2:4])[None]
                + pick_other[:, None, None, None] * (got[0][0, 2:4] + got[2][0, 2:4])[None]
            )
        else:
            terms = jnp.sum(owner_pick[:, :, None, None, None] * both[:, None, 2:4], axis=0)
        if xor_partners(tile_count) and xor_partners(kern_count) and tile_count > 2:
            tile_grad, mine_masters = scatter_split(
                terms, tile_count, tile_pos, kern_count, kern_pos, local_masters,
                tile_pixels,
            )
        else:
            tile_grad = pixels(mine_tiles)
            mine_masters = (scatter_sum(terms, "tile", tile_count, tile_pos, local_masters),)

    with jax.named_scope("pixel_gradients"):
        master_grad = pixels(*mine_masters)
    return (tile_grad, master_grad)


def solution(mesh):
    return jax.shard_map(
        on_device,
        mesh=mesh,
        in_specs=(
            P(("region", "tile"), None, None),
            P(("region", "tile"), None, None),
            P(("region", "tile"), None, None),
            P(("region", "tile")),
            P(("region", "tile"), None),
            P("corner", None, None, None, None),
            P("corner", None),
            P("corner"),
        ),
        out_specs=(P(("region", "tile"), None, None), P(("region", "tile"), None, None)),
        check_vma=False,
    )
```

```python
import functools
import math

import numpy as np
import jax
import jax.numpy as jnp
from jax import lax
from jax.sharding import PartitionSpec as P
from jax.experimental import pallas as pl
from jax.experimental.pallas import tpu as pltpu

P_SIZE = 256
B = 32


precise = lax.Precision.HIGHEST
steepness = 3.0
threshold = 1.0


def band_tables():
    freq = np.arange(B, dtype=np.int64) - B // 2
    pixel = np.arange(P_SIZE, dtype=np.int64)
    angle = (2.0 * math.pi / P_SIZE) * np.mod(freq[:, None] * pixel[None, :], P_SIZE).astype(np.float64)
    return (jnp.asarray(np.cos(angle), jnp.float32), jnp.asarray(-np.sin(angle), jnp.float32))


def phase_ramp(shift):
    freq = jnp.arange(B, dtype=jnp.int32) - B // 2
    total = (
        freq[None, :, None] * shift[:, 0][:, None, None]
        + freq[None, None, :] * shift[:, 1][:, None, None]
    )
    angle = 2.0 * math.pi / P_SIZE * jnp.mod(total, P_SIZE).astype(jnp.float32)
    return (jnp.cos(angle), -jnp.sin(angle))


def spectra(masks, cos_tab, sin_tab):
    rows_re = jnp.einsum("bx,nxy->nby", cos_tab, masks, precision=precise)
    rows_im = jnp.einsum("bx,nxy->nby", sin_tab, masks, precision=precise)
    spec_re = jnp.einsum("nby,cy->nbc", rows_re, cos_tab, precision=precise) - jnp.einsum(
        "nby,cy->nbc", rows_im, sin_tab, precision=precise
    )
    spec_im = jnp.einsum("nby,cy->nbc", rows_re, sin_tab, precision=precise) + jnp.einsum(
        "nby,cy->nbc", rows_im, cos_tab, precision=precise
    )
    return (spec_re, spec_im)


def back_pixels(x_re, x_im, cos_tab, sin_tab):
    half_re = jnp.einsum("bx,nbc->nxc", cos_tab, x_re, precision=precise) + jnp.einsum(
        "bx,nbc->nxc", sin_tab, x_im, precision=precise
    )
    half_im = jnp.einsum("bx,nbc->nxc", cos_tab, x_im, precision=precise) - jnp.einsum(
        "bx,nbc->nxc", sin_tab, x_re, precision=precise
    )
    return jnp.einsum("nxc,cy->nxy", half_re, cos_tab, precision=precise) + jnp.einsum(
        "nxc,cy->nxy", half_im, sin_tab, precision=precise
    )


def dot_full(a, b):
    return jnp.dot(a, b, precision=precise, preferred_element_type=jnp.float32)


def dot_parts(a, b):
    return jnp.dot(a, b, preferred_element_type=jnp.float32)


def split_three(a):
    hi = a.astype(jnp.bfloat16)
    rest = a - hi.astype(jnp.float32)
    mid = rest.astype(jnp.bfloat16)
    lo = (rest - mid.astype(jnp.float32)).astype(jnp.bfloat16)
    return hi, mid, lo


def table_three(table):
    hi = table.astype(jnp.bfloat16)
    rest = table - hi.astype(np.float64)
    mid = rest.astype(jnp.bfloat16)
    lo = (rest - mid.astype(np.float64)).astype(jnp.bfloat16)
    return hi, mid, lo


def imaging_tables():
    freq = np.arange(B, dtype=np.int64) - B // 2
    pixel = np.arange(P_SIZE, dtype=np.int64)
    angle = (2.0 * math.pi / P_SIZE) * np.mod(freq[:, None] * pixel[None, :], P_SIZE).astype(np.float64)
    c_re = np.cos(angle)
    c_im = -np.sin(angle)
    scale = 1.0 / (P_SIZE * P_SIZE)
    right_w = np.zeros((128, 2 * P_SIZE))
    right_w[:B, :P_SIZE] = c_re
    right_w[:B, P_SIZE:] = -c_im
    right_w[B : 2 * B, :P_SIZE] = c_im
    right_w[B : 2 * B, P_SIZE:] = c_re
    left_a = np.zeros((P_SIZE, 128))
    left_a[:, :B] = c_re.T * scale
    left_a[:, B : 2 * B] = -c_im.T * scale
    right_b = np.zeros((2 * P_SIZE, 128))
    right_b[:P_SIZE, :B] = c_re.T * scale
    right_b[:P_SIZE, B : 2 * B] = c_im.T * scale
    right_b[P_SIZE:, :B] = -c_im.T * scale
    right_b[P_SIZE:, B : 2 * B] = c_re.T * scale
    ct_re = c_re.T
    ct_im = c_im.T
    right_c = np.zeros((2 * P_SIZE, 128))
    for col, (top, bottom) in enumerate(
        ((ct_re, -ct_im), (ct_im, ct_re), (ct_im, ct_re), (ct_re, -ct_im))
    ):
        right_c[:P_SIZE, col * B : (col + 1) * B] = top
        right_c[P_SIZE:, col * B : (col + 1) * B] = bottom
    a_hi, a_mid, a_lo = table_three(left_a[:, : 2 * B])
    left_three = np.concatenate([a_hi, a_hi, a_mid, a_hi, a_lo, a_mid], axis=1)
    b_hi, b_mid, b_lo = table_three(right_b)
    right_hm = np.concatenate([b_hi, b_mid], axis=1)
    right_lh = np.concatenate([b_lo, b_hi], axis=0)
    parts_re = table_three(c_re)
    parts_im = table_three(c_im)
    rows_three = np.concatenate(
        [np.concatenate(parts_re, axis=1), np.concatenate(parts_im, axis=1)], axis=0
    )
    cols_re = np.concatenate(table_three(c_re.T), axis=0)
    cols_im = np.concatenate(table_three(c_im.T), axis=0)
    plain = (c_re, c_im, c_re.T, c_im.T, right_w[:B], right_w[B : 2 * B], right_c)
    out = [jnp.asarray(table, jnp.float32) for table in plain]
    six = []
    for table in (c_re.T, c_im.T):
        t_hi, t_mid, t_lo = table_three(table)
        six.append(np.concatenate([t_hi, t_mid, t_hi, t_lo, t_hi, t_mid], axis=0))
    c_hi, c_mid, c_lo = table_three(right_c)
    c_hm = np.concatenate([c_hi, c_mid], axis=1)
    c_lh = np.concatenate([c_lo, c_hi], axis=0)
    bf = (left_three, right_hm, right_lh, rows_three, cols_re, cols_im, six[0], six[1], c_hm, c_lh)
    return out + [jnp.asarray(table) for table in bf]


def imaging_body(
    pos_ref, im_ref, sh_ref, w_ref, dose_ref, mask_ref, ev_ref, ev2_ref, own_ref, goal_ref, h_ref, hc_ref,
    c_re_ref, c_im_ref, ct_re_ref, ct_im_ref, rw_top, rw_bot, rc_ref, la_ref, rhm_ref, rlh_ref, rows_ref, cre_ref, cim_ref,
        six_re, six_im, chm_ref, clh_ref,
    slots_ref, f_buf, i_buf, u_buf, w_buf, xr_buf, xi_buf,
):
    count = f_buf.shape[0]
    pos = pos_ref[0]
    master = im_ref[pos]
    pick0 = (lax.broadcasted_iota(jnp.int32, (P_SIZE, 128), 0) == sh_ref[pos, 0]).astype(jnp.bfloat16)
    pick1 = (lax.broadcasted_iota(jnp.int32, (8, P_SIZE), 1) == sh_ref[pos, 1]).astype(jnp.bfloat16)
    e0 = dot_parts(rows_ref[...], jnp.concatenate([pick0, pick0, pick0], axis=0))
    e0_re = e0[:B, 0:1]
    e0_im = e0[B:, 0:1]
    pick1 = jnp.concatenate([pick1, pick1, pick1], axis=1)
    e1_re = dot_parts(pick1, cre_ref[...])[0:1, :]
    e1_im = dot_parts(pick1, cim_ref[...])[0:1, :]
    ph_re = e0_re * e1_re - e0_im * e1_im
    ph_im = e0_re * e1_im + e0_im * e1_re
    local_masters = own_ref.shape[0]
    is_own = master // local_masters == pos_ref[1]
    m_re = ev_ref[master, 0] + ev2_ref[master, 0] + jnp.where(is_own, own_ref[master % local_masters, 0], 0.0)
    m_im = ev_ref[master, 1] + ev2_ref[master, 1] + jnp.where(is_own, own_ref[master % local_masters, 1], 0.0)
    mask = mask_ref[pos]
    rows = dot_parts(rows_ref[...], jnp.concatenate([mask, mask, mask], axis=0))
    r_hi, r_mid, r_lo = split_three(rows)
    packed = jnp.concatenate([r_hi, r_hi, r_mid, r_hi, r_lo, r_mid], axis=1)
    t_one = dot_parts(packed, six_re[...])
    t_two = dot_parts(packed, six_im[...])
    s_re = t_one[:B] - t_two[B:] + (ph_re * m_re - ph_im * m_im)
    s_im = t_two[:B] + t_one[B:] + (ph_re * m_im + ph_im * m_re)
    i_buf[...] = jnp.zeros(i_buf.shape, jnp.float32)

    def spectrum(k, carry):
        h_re = h_ref[k, 0]
        h_im = h_ref[k, 1]
        rows = pl.ds(pl.multiple_of(k * B, B), B)
        xr_buf[rows, :] = h_re * s_re - h_im * s_im
        xi_buf[rows, :] = h_re * s_im + h_im * s_re
        return carry

    lax.fori_loop(0, count, spectrum, 0)
    w_buf[...] = dot_full(xr_buf[...], rw_top[...]) + dot_full(xi_buf[...], rw_bot[...])

    def forward(k, carry):
        rows = w_buf[pl.ds(pl.multiple_of(k * B, B), B), :]
        swap = jnp.concatenate([-rows[:, P_SIZE:], rows[:, :P_SIZE]], axis=1)
        s_hi, s_mid, s_lo = split_three(jnp.concatenate([rows, swap], axis=0))
        stacked = jnp.concatenate([s_hi, s_mid, s_hi, s_lo, s_hi, s_mid], axis=0)
        field = dot_parts(la_ref[...], stacked)
        f_buf[k] = field
        power = field * field
        i_buf[...] += w_ref[k] * (power[:, :P_SIZE] + power[:, P_SIZE:])
        return carry

    lax.fori_loop(0, count, forward, 0)
    dose = dose_ref[0]
    resist = 1.0 / (1.0 + jnp.exp(-(steepness * (dose * i_buf[...] - threshold))))
    goal = goal_ref[pos].astype(jnp.float32)
    i_buf[...] = 2.0 * (resist - goal) * resist * (1.0 - resist) * steepness * dose

    def backward(k, carry):
        sens = i_buf[...]
        weighted = f_buf[k] * jnp.concatenate([sens, sens], axis=1)
        q_hi, q_mid, q_lo = split_three(weighted)
        first = dot_parts(q_hi, rhm_ref[...]) + dot_parts(q_mid, rhm_ref[...])
        rest = dot_parts(jnp.concatenate([q_hi, q_lo], axis=1), rlh_ref[...])
        half = first[:, :128] + first[:, 128:] + rest
        flip = half.T
        u_buf[pl.ds(pl.multiple_of(k * B, B), B), :] = jnp.concatenate([flip[:B], flip[B : 2 * B]], axis=1)
        return carry

    lax.fori_loop(0, count, backward, 0)
    u_hi, u_mid, u_lo = split_three(u_buf[...])
    first = dot_parts(u_hi, chm_ref[...]) + dot_parts(u_mid, chm_ref[...])
    out = first[:, :128] + first[:, 128:] + dot_parts(jnp.concatenate([u_hi, u_lo], axis=1), clh_ref[...])
    acc = jnp.sum((hc_ref[...] * out).reshape(count, B, 128), axis=0)
    flip = jnp.concatenate([acc, jnp.zeros((128 - B, 128), jnp.float32)], axis=0).T
    g_re = flip[0:B, 0:B] + flip[2 * B : 3 * B, 0:B]
    g_im = flip[B : 2 * B, 0:B] + flip[3 * B : 4 * B, 0:B]
    slots_ref[0] = g_re
    slots_ref[1] = g_im
    slots_ref[2] = ph_re * g_re + ph_im * g_im
    slots_ref[3] = ph_re * g_im - ph_im * g_re


def imaging(pos, inst_master, inst_shift, weights, dose, tile_mask, every, own, target, kerns, h_cat):
    if len(every) == 1:
        every = (every[0], jnp.zeros_like(every[0]))
    count = weights.shape[0]
    tables = imaging_tables()
    vmem = pl.BlockSpec(memory_space=pltpu.VMEM)
    smem = pl.BlockSpec(memory_space=pltpu.SMEM)
    return pl.pallas_call(
        imaging_body,
        out_shape=jax.ShapeDtypeStruct((4, B, B), jnp.float32),
        in_specs=[smem] * 5 + [vmem] * 7 + [vmem] * len(tables),
        out_specs=vmem,
        scratch_shapes=[
            pltpu.VMEM((count, P_SIZE, 2 * P_SIZE), jnp.float32),
            pltpu.VMEM((P_SIZE, P_SIZE), jnp.float32),
            pltpu.VMEM((count * B, 2 * P_SIZE), jnp.float32),
            pltpu.VMEM((count * B, 2 * P_SIZE), jnp.float32),
            pltpu.VMEM((count * B, B), jnp.float32),
            pltpu.VMEM((count * B, B), jnp.float32),
        ],
    )(pos, inst_master, inst_shift, weights, dose, tile_mask, *every, own, target, kerns, h_cat, *tables)


def pixel_body(*refs, passes):
    if passes:
        out_ref, token_ref = refs[-2:]
        token_ref[...] = jnp.zeros(token_ref.shape, jnp.float32)
        refs = refs[:-2] + (out_ref,)
    out_ref = refs[-1]
    c_re_ref, c_im_ref, left_ref = refs[-4:-1]
    parts = refs[:-4]
    for n in range(out_ref.shape[0]):
        x_re = sum(part[n, 0] for part in parts)
        x_im = sum(part[n, 1] for part in parts)
        x_both = jnp.concatenate([x_re, x_im], axis=0)
        p_re = dot_full(x_both, c_re_ref[...])
        p_im = dot_full(x_both, c_im_ref[...])
        y_re = p_re[:B] + p_im[B:]
        y_im = p_re[B:] - p_im[:B]
        y_hi, y_mid, y_lo = split_three(jnp.concatenate([y_re, y_im], axis=0))
        stacked = jnp.concatenate([y_hi, y_mid, y_hi, y_lo, y_hi, y_mid], axis=0)
        out_ref[n] = dot_parts(left_ref[...], stacked)


def group_pixel_body(comp_ref, g0_ref, g1_ref, g2_ref, c_re_ref, c_im_ref, left_ref, out_ref, token_ref):
    token_ref[...] = jnp.zeros(token_ref.shape, jnp.float32)
    own = lax.axis_index("kern")
    for n in range(out_ref.shape[0]):
        mine = n == own
        planes = []
        for c in range(2):
            planes.append(
                jnp.where(mine, comp_ref[0, c] + g1_ref[0, c], g0_ref[0, c] + g2_ref[0, c])
            )
        x_both = jnp.concatenate(planes, axis=0)
        p_re = dot_full(x_both, c_re_ref[...])
        p_im = dot_full(x_both, c_im_ref[...])
        y_re = p_re[:B] + p_im[B:]
        y_im = p_re[B:] - p_im[:B]
        y_hi, y_mid, y_lo = split_three(jnp.concatenate([y_re, y_im], axis=0))
        stacked = jnp.concatenate([y_hi, y_mid, y_hi, y_lo, y_hi, y_mid], axis=0)
        out_ref[n] = dot_parts(left_ref[...], stacked)


def group_pixels(comp, got):
    freq = np.arange(B, dtype=np.int64) - B // 2
    pixel = np.arange(P_SIZE, dtype=np.int64)
    angle = (2.0 * math.pi / P_SIZE) * np.mod(freq[:, None] * pixel[None, :], P_SIZE).astype(np.float64)
    c_re = np.cos(angle)
    c_im = -np.sin(angle)
    a_hi, a_mid, a_lo = table_three(np.concatenate([c_re.T, c_im.T], axis=1))
    left = np.concatenate([a_hi, a_hi, a_mid, a_hi, a_lo, a_mid], axis=1)
    tables = [jnp.asarray(c_re, jnp.float32), jnp.asarray(c_im, jnp.float32), jnp.asarray(left)]
    vmem = pl.BlockSpec(memory_space=pltpu.VMEM)
    shape = jax.ShapeDtypeStruct((2, P_SIZE, P_SIZE), jnp.float32)
    return pl.pallas_call(
        group_pixel_body,
        out_shape=(shape, jax.ShapeDtypeStruct((1, 1, 1, 1), jnp.float32)),
        in_specs=[vmem] * 7,
        out_specs=(vmem, vmem),
    )(comp, *got, *tables)


def pixels(*parts, token=False):
    freq = np.arange(B, dtype=np.int64) - B // 2
    pixel = np.arange(P_SIZE, dtype=np.int64)
    angle = (2.0 * math.pi / P_SIZE) * np.mod(freq[:, None] * pixel[None, :], P_SIZE).astype(np.float64)
    c_re = np.cos(angle)
    c_im = -np.sin(angle)
    a_hi, a_mid, a_lo = table_three(np.concatenate([c_re.T, c_im.T], axis=1))
    left = np.concatenate([a_hi, a_hi, a_mid, a_hi, a_lo, a_mid], axis=1)
    tables = [jnp.asarray(c_re, jnp.float32), jnp.asarray(c_im, jnp.float32), jnp.asarray(left)]
    vmem = pl.BlockSpec(memory_space=pltpu.VMEM)
    shape = jax.ShapeDtypeStruct((parts[0].shape[0], P_SIZE, P_SIZE), jnp.float32)
    if not token:
        return pl.pallas_call(
            functools.partial(pixel_body, passes=False),
            out_shape=shape,
            in_specs=[vmem] * (len(parts) + 3),
            out_specs=vmem,
        )(*parts, *tables)
    return pl.pallas_call(
        functools.partial(pixel_body, passes=True),
        out_shape=(shape, jax.ShapeDtypeStruct((1, 1, 1, 1), jnp.float32)),
        in_specs=[vmem] * (len(parts) + 3),
        out_specs=(vmem, vmem),
    )(*parts, *tables)


def xor_partners(count):
    return count & (count - 1) == 0 and count <= 8


def gather_all(x, axis, count, pos):
    if not xor_partners(count):
        return lax.all_gather(x, axis, axis=0, tiled=True)
    size = x.shape[0]
    slot = jnp.arange(count * size, dtype=jnp.int32) // size
    total = jnp.where((slot == pos)[:, None, None, None], jnp.tile(x, (count, 1, 1, 1)), 0.0)
    for step in range(1, count):
        got = lax.ppermute(x, axis, [(i, i ^ step) for i in range(count)])
        hit = (slot == (pos ^ step))[:, None, None, None]
        total = total + jnp.where(hit, jnp.tile(got, (count, 1, 1, 1)), 0.0)
    return total


def sum_all(x, axis, count, pos):
    if not xor_partners(count):
        return lax.psum(x, axis)
    step = 1
    while step < count:
        x = x + lax.ppermute(x, axis, [(i, i ^ step) for i in range(count)])
        step *= 2
    return x


def sum_parts(x, axis, count, pos):
    if count == 2:
        return (x, lax.ppermute(x, axis, [(0, 1), (1, 0)]))
    return (sum_all(x, axis, count, pos),)


def scatter_sum(x, axis, count, pos, size):
    if not xor_partners(count):
        return lax.psum_scatter(x, axis, scatter_dimension=0, tiled=True)
    total = lax.dynamic_slice_in_dim(x, pos * size, size, 0)
    for step in range(1, count):
        part = lax.dynamic_slice_in_dim(x, (pos ^ step) * size, size, 0)
        total = total + lax.ppermute(part, axis, [(i, i ^ step) for i in range(count)])
    return total


def partner_lists(count, kern_count):
    lists = [[] for _ in range(kern_count)]
    for step in range(1, count):
        lists[step % kern_count].append(step)
    return lists


def chosen_step(lists, round_index, kern_pos):
    pick = jnp.int32(-1)
    for k, steps in enumerate(lists):
        if round_index < len(steps):
            pick = jnp.where(kern_pos == k, jnp.int32(steps[round_index]), pick)
    return pick


def gather_split(x, count, pos, kern_count, kern_pos):
    size = x.shape[0]
    lists = partner_lists(count, kern_count)
    slot = jnp.arange(count * size, dtype=jnp.int32) // size
    spread = lambda part: jnp.tile(part, (count, 1, 1, 1))
    collected = jnp.zeros((count * size,) + x.shape[1:], x.dtype)
    for r in range(max(len(steps) for steps in lists)):
        pairs = []
        for k, steps in enumerate(lists):
            if r < len(steps):
                pairs += [((t ^ steps[r]) * kern_count + k, t * kern_count + k) for t in range(count)]
        got = lax.ppermute(x, ("tile", "kern"), pairs)
        step = chosen_step(lists, r, kern_pos)
        source = jnp.where(step >= 0, pos ^ step, -1)
        collected = collected + jnp.where((slot == source)[:, None, None, None], spread(got), 0.0)
    return sum_parts(collected, "kern", kern_count, kern_pos)


def scatter_split(x, count, pos, kern_count, kern_pos, size, between):
    lists = partner_lists(count, kern_count)
    own = lax.dynamic_slice_in_dim(x, pos * size, size, 0)
    total = jnp.where(kern_pos == 0, own, 0.0)
    for r in range(max(len(steps) for steps in lists)):
        pairs = []
        for k, steps in enumerate(lists):
            if r < len(steps):
                pairs += [(t * kern_count + k, (t ^ steps[r]) * kern_count + k) for t in range(count)]
        step = chosen_step(lists, r, kern_pos)
        target = jnp.where(step >= 0, pos ^ step, 0)
        part = lax.dynamic_slice_in_dim(x, target * size, size, 0)
        total = total + lax.ppermute(part, ("tile", "kern"), pairs)
    done, token = between()
    total = total + 0.0 * token
    return done, sum_parts(total, "kern", kern_count, kern_pos)


def on_device(
    tile_mask, master_mask, target, inst_master, inst_shift, kernels, kernel_weight, corner_dose
):
    cos_tab, sin_tab = band_tables()
    scale = 1.0 / (P_SIZE * P_SIZE)
    local_tiles = tile_mask.shape[0]
    local_masters = master_mask.shape[0]
    tile_count = lax.axis_size("tile")
    tile_pos = lax.axis_index("tile")
    kern_count = lax.axis_size("kern")
    kern_pos = lax.axis_index("kern")
    per_dev = local_tiles // kern_count
    first = kern_pos * per_dev
    region_tiles = tile_count * local_tiles
    region_masters = tile_count * local_masters

    with jax.named_scope("master_spectra"):
        own_re, own_im = spectra(master_mask.astype(jnp.float32), cos_tab, sin_tab)
        own = jnp.stack([own_re, own_im], axis=1)
        if xor_partners(tile_count) and xor_partners(kern_count) and tile_count > 2:
            every = gather_split(own, tile_count, tile_pos, kern_count, kern_pos)
            own_part = own
        else:
            every = (gather_all(own, "tile", tile_count, tile_pos),)
            own_part = jnp.zeros_like(own)

    dose = corner_dose[0]
    kerns = kernels[0]
    h_re = kerns[:, 0]
    h_im = kerns[:, 1]
    weights = kernel_weight[0]

    with jax.named_scope("imaging_kernel"):
        count = h_re.shape[0]
        twice = (2.0 * weights)[:, None, None]
        ht_re = jnp.swapaxes(h_re, 1, 2) * twice
        ht_im = jnp.swapaxes(h_im, 1, 2) * twice
        h_cat = jnp.concatenate([ht_re, ht_re, ht_im, -ht_im], axis=-1).reshape(count * B, 128)
        parts = []
        for j in range(per_dev):
            pos = jnp.stack([first + j, tile_pos]).astype(jnp.int32)
            parts.append(
                imaging(
                    pos, inst_master, inst_shift, weights, corner_dose, tile_mask, every, own_part, target,
                    kerns, h_cat,
                )
            )
        comp = jnp.stack(parts)

    with jax.named_scope("gradient_exchange"):
        corner_count = lax.axis_size("corner")
        corner_pos = lax.axis_index("corner")
        if corner_count == 2 and kern_count == 2 and per_dev == 1:
            got = [
                lax.ppermute(comp, ("corner", "kern"), [(i, i ^ step) for i in range(4)])
                for step in (1, 2, 3)
            ]
            mine = comp + got[1]
            other = got[0] + got[2]
            both = jnp.where(kern_pos == 0, jnp.concatenate([mine, other]), jnp.concatenate([other, mine]))
            tile_pixels = lambda: group_pixels(comp, got)
        else:
            comp = sum_all(comp, "corner", corner_count, corner_pos)
            both = gather_all(comp, "kern", kern_count, kern_pos)
            tile_pixels = lambda: pixels(both[:, 0:2], token=True)
        mine_tiles = both[:, 0:2]
        owner_pick = (
            inst_master[:, None] == jnp.arange(region_masters, dtype=jnp.int32)[None, :]
        ).astype(jnp.float32)
        if corner_count == 2 and kern_count == 2 and per_dev == 1:
            pick_mine = jnp.where(kern_pos == 0, owner_pick[0], owner_pick[1])
            pick_other = jnp.where(kern_pos == 0, owner_pick[1], owner_pick[0])
            terms = (
                pick_mine[:, None, None, None] * (comp[0, 2:4] + got[1][0, 2:4])[None]
                + pick_other[:, None, None, None] * (got[0][0, 2:4] + got[2][0, 2:4])[None]
            )
        else:
            terms = jnp.sum(owner_pick[:, :, None, None, None] * both[:, None, 2:4], axis=0)
        if xor_partners(tile_count) and xor_partners(kern_count) and tile_count > 2:
            tile_grad, mine_masters = scatter_split(
                terms, tile_count, tile_pos, kern_count, kern_pos, local_masters,
                tile_pixels,
            )
        else:
            tile_grad = pixels(mine_tiles)
            mine_masters = (scatter_sum(terms, "tile", tile_count, tile_pos, local_masters),)

    with jax.named_scope("pixel_gradients"):
        master_grad = pixels(*mine_masters)
    return (tile_grad, master_grad)


def solution(mesh):
    return jax.shard_map(
        on_device,
        mesh=mesh,
        in_specs=(
            P(("region", "tile"), None, None),
            P(("region", "tile"), None, None),
            P(("region", "tile"), None, None),
            P(("region", "tile")),
            P(("region", "tile"), None),
            P("corner", None, None, None, None),
            P("corner", None),
            P("corner"),
        ),
        out_specs=(P(("region", "tile"), None, None), P(("region", "tile"), None, None)),
        check_vma=False,
    )
```

```python
import functools
import math

import numpy as np
import jax
import jax.numpy as jnp
from jax import lax
from jax.sharding import PartitionSpec as P
from jax.experimental import pallas as pl
from jax.experimental.pallas import tpu as pltpu

P_SIZE = 256
B = 32


precise = lax.Precision.HIGHEST
steepness = 3.0
threshold = 1.0


def band_tables():
    freq = np.arange(B, dtype=np.int64) - B // 2
    pixel = np.arange(P_SIZE, dtype=np.int64)
    angle = (2.0 * math.pi / P_SIZE) * np.mod(freq[:, None] * pixel[None, :], P_SIZE).astype(np.float64)
    return (jnp.asarray(np.cos(angle), jnp.float32), jnp.asarray(-np.sin(angle), jnp.float32))


def phase_ramp(shift):
    freq = jnp.arange(B, dtype=jnp.int32) - B // 2
    total = (
        freq[None, :, None] * shift[:, 0][:, None, None]
        + freq[None, None, :] * shift[:, 1][:, None, None]
    )
    angle = 2.0 * math.pi / P_SIZE * jnp.mod(total, P_SIZE).astype(jnp.float32)
    return (jnp.cos(angle), -jnp.sin(angle))


def spectra(masks, cos_tab, sin_tab):
    rows_re = jnp.einsum("bx,nxy->nby", cos_tab, masks, precision=precise)
    rows_im = jnp.einsum("bx,nxy->nby", sin_tab, masks, precision=precise)
    spec_re = jnp.einsum("nby,cy->nbc", rows_re, cos_tab, precision=precise) - jnp.einsum(
        "nby,cy->nbc", rows_im, sin_tab, precision=precise
    )
    spec_im = jnp.einsum("nby,cy->nbc", rows_re, sin_tab, precision=precise) + jnp.einsum(
        "nby,cy->nbc", rows_im, cos_tab, precision=precise
    )
    return (spec_re, spec_im)


def back_pixels(x_re, x_im, cos_tab, sin_tab):
    half_re = jnp.einsum("bx,nbc->nxc", cos_tab, x_re, precision=precise) + jnp.einsum(
        "bx,nbc->nxc", sin_tab, x_im, precision=precise
    )
    half_im = jnp.einsum("bx,nbc->nxc", cos_tab, x_im, precision=precise) - jnp.einsum(
        "bx,nbc->nxc", sin_tab, x_re, precision=precise
    )
    return jnp.einsum("nxc,cy->nxy", half_re, cos_tab, precision=precise) + jnp.einsum(
        "nxc,cy->nxy", half_im, sin_tab, precision=precise
    )


def dot_full(a, b):
    return jnp.dot(a, b, precision=precise, preferred_element_type=jnp.float32)


def dot_parts(a, b):
    return jnp.dot(a, b, preferred_element_type=jnp.float32)


def split_three(a):
    hi = a.astype(jnp.bfloat16)
    rest = a - hi.astype(jnp.float32)
    mid = rest.astype(jnp.bfloat16)
    lo = (rest - mid.astype(jnp.float32)).astype(jnp.bfloat16)
    return hi, mid, lo


def table_three(table):
    hi = table.astype(jnp.bfloat16)
    rest = table - hi.astype(np.float64)
    mid = rest.astype(jnp.bfloat16)
    lo = (rest - mid.astype(np.float64)).astype(jnp.bfloat16)
    return hi, mid, lo


def imaging_tables():
    freq = np.arange(B, dtype=np.int64) - B // 2
    pixel = np.arange(P_SIZE, dtype=np.int64)
    angle = (2.0 * math.pi / P_SIZE) * np.mod(freq[:, None] * pixel[None, :], P_SIZE).astype(np.float64)
    c_re = np.cos(angle)
    c_im = -np.sin(angle)
    scale = 1.0 / (P_SIZE * P_SIZE)
    right_w = np.zeros((128, 2 * P_SIZE))
    right_w[:B, :P_SIZE] = c_re
    right_w[:B, P_SIZE:] = -c_im
    right_w[B : 2 * B, :P_SIZE] = c_im
    right_w[B : 2 * B, P_SIZE:] = c_re
    left_a = np.zeros((P_SIZE, 128))
    left_a[:, :B] = c_re.T * scale
    left_a[:, B : 2 * B] = -c_im.T * scale
    right_b = np.zeros((2 * P_SIZE, 128))
    right_b[:P_SIZE, :B] = c_re.T * scale
    right_b[:P_SIZE, B : 2 * B] = c_im.T * scale
    right_b[P_SIZE:, :B] = -c_im.T * scale
    right_b[P_SIZE:, B : 2 * B] = c_re.T * scale
    ct_re = c_re.T
    ct_im = c_im.T
    right_c = np.zeros((2 * P_SIZE, 128))
    for col, (top, bottom) in enumerate(
        ((ct_re, -ct_im), (ct_im, ct_re), (ct_im, ct_re), (ct_re, -ct_im))
    ):
        right_c[:P_SIZE, col * B : (col + 1) * B] = top
        right_c[P_SIZE:, col * B : (col + 1) * B] = bottom
    a_hi, a_mid, a_lo = table_three(left_a[:, : 2 * B])
    left_three = np.concatenate([a_hi, a_hi, a_mid, a_hi, a_lo, a_mid], axis=1)
    b_hi, b_mid, b_lo = table_three(right_b)
    right_hm = np.concatenate([b_hi, b_mid], axis=1)
    right_lh = np.concatenate([b_lo, b_hi], axis=0)
    parts_re = table_three(c_re)
    parts_im = table_three(c_im)
    rows_three = np.concatenate(
        [np.concatenate(parts_re, axis=1), np.concatenate(parts_im, axis=1)], axis=0
    )
    plain = (c_re, c_im, c_re.T, c_im.T, right_w[:B], right_w[B : 2 * B], right_c)
    out = [jnp.asarray(table, jnp.float32) for table in plain]
    bf = (left_three, right_hm, right_lh, rows_three)
    return out + [jnp.asarray(table) for table in bf]


def imaging_body(
    pos_ref, im_ref, sh_ref, w_ref, dose_ref, mask_ref, ev_ref, ev2_ref, own_ref, goal_ref, h_ref, hc_ref,
    c_re_ref, c_im_ref, ct_re_ref, ct_im_ref, rw_top, rw_bot, rc_ref, la_ref, rhm_ref, rlh_ref, rows_ref,
    slots_ref, f_buf, i_buf, u_buf, w_buf, xr_buf, xi_buf,
):
    count = f_buf.shape[0]
    pos = pos_ref[0]
    master = im_ref[pos]
    pick0 = (lax.broadcasted_iota(jnp.int32, (P_SIZE, 128), 0) == sh_ref[pos, 0]).astype(jnp.bfloat16)
    pick1 = (lax.broadcasted_iota(jnp.int32, (P_SIZE, 128), 0) == sh_ref[pos, 1]).astype(jnp.bfloat16)
    e0 = dot_parts(rows_ref[...], jnp.concatenate([pick0, pick0, pick0], axis=0))
    e0_re = e0[:B, 0:1]
    e0_im = e0[B:, 0:1]
    e1 = dot_parts(rows_ref[...], jnp.concatenate([pick1, pick1, pick1], axis=0))
    fill = jnp.zeros((128 - B, 128), jnp.float32)
    e1_re = jnp.concatenate([e1[:B], fill], axis=0).T[0:1, 0:B]
    e1_im = jnp.concatenate([e1[B:], fill], axis=0).T[0:1, 0:B]
    ph_re = e0_re * e1_re - e0_im * e1_im
    ph_im = e0_re * e1_im + e0_im * e1_re
    local_masters = own_ref.shape[0]
    is_own = master // local_masters == pos_ref[1]
    m_re = ev_ref[master, 0] + ev2_ref[master, 0] + jnp.where(is_own, own_ref[master % local_masters, 0], 0.0)
    m_im = ev_ref[master, 1] + ev2_ref[master, 1] + jnp.where(is_own, own_ref[master % local_masters, 1], 0.0)
    mask = mask_ref[pos]
    rows = dot_parts(rows_ref[...], jnp.concatenate([mask, mask, mask], axis=0))
    t_one = dot_full(rows, ct_re_ref[...])
    t_two = dot_full(rows, ct_im_ref[...])
    s_re = t_one[:B] - t_two[B:] + (ph_re * m_re - ph_im * m_im)
    s_im = t_two[:B] + t_one[B:] + (ph_re * m_im + ph_im * m_re)
    i_buf[...] = jnp.zeros(i_buf.shape, jnp.float32)

    def spectrum(k, carry):
        h_re = h_ref[k, 0]
        h_im = h_ref[k, 1]
        rows = pl.ds(pl.multiple_of(k * B, B), B)
        xr_buf[rows, :] = h_re * s_re - h_im * s_im
        xi_buf[rows, :] = h_re * s_im + h_im * s_re
        return carry

    lax.fori_loop(0, count, spectrum, 0)
    w_buf[...] = dot_full(xr_buf[...], rw_top[...]) + dot_full(xi_buf[...], rw_bot[...])

    def forward(k, carry):
        rows = w_buf[pl.ds(pl.multiple_of(k * B, B), B), :]
        swap = jnp.concatenate([-rows[:, P_SIZE:], rows[:, :P_SIZE]], axis=1)
        s_hi, s_mid, s_lo = split_three(jnp.concatenate([rows, swap], axis=0))
        stacked = jnp.concatenate([s_hi, s_mid, s_hi, s_lo, s_hi, s_mid], axis=0)
        field = dot_parts(la_ref[...], stacked)
        f_buf[k] = field
        power = field * field
        i_buf[...] += w_ref[k] * (power[:, :P_SIZE] + power[:, P_SIZE:])
        return carry

    lax.fori_loop(0, count, forward, 0)
    dose = dose_ref[0]
    resist = 1.0 / (1.0 + jnp.exp(-(steepness * (dose * i_buf[...] - threshold))))
    goal = goal_ref[pos].astype(jnp.float32)
    i_buf[...] = 2.0 * (resist - goal) * resist * (1.0 - resist) * steepness * dose

    def backward(k, carry):
        sens = i_buf[...]
        weighted = f_buf[k] * jnp.concatenate([sens, sens], axis=1)
        q_hi, q_mid, q_lo = split_three(weighted)
        first = dot_parts(q_hi, rhm_ref[...]) + dot_parts(q_mid, rhm_ref[...])
        rest = dot_parts(jnp.concatenate([q_hi, q_lo], axis=1), rlh_ref[...])
        half = first[:, :128] + first[:, 128:] + rest
        flip = half.T
        u_buf[pl.ds(pl.multiple_of(k * B, B), B), :] = jnp.concatenate([flip[:B], flip[B : 2 * B]], axis=1)
        return carry

    lax.fori_loop(0, count, backward, 0)
    out = dot_full(u_buf[...], rc_ref[...])
    acc = jnp.sum((hc_ref[...] * out).reshape(count, B, 128), axis=0)
    flip = jnp.concatenate([acc, jnp.zeros((128 - B, 128), jnp.float32)], axis=0).T
    g_re = flip[0:B, 0:B] + flip[2 * B : 3 * B, 0:B]
    g_im = flip[B : 2 * B, 0:B] + flip[3 * B : 4 * B, 0:B]
    slots_ref[0] = g_re
    slots_ref[1] = g_im
    slots_ref[2] = ph_re * g_re + ph_im * g_im
    slots_ref[3] = ph_re * g_im - ph_im * g_re


def imaging(pos, inst_master, inst_shift, weights, dose, tile_mask, every, own, target, kerns, h_cat):
    if len(every) == 1:
        every = (every[0], jnp.zeros_like(every[0]))
    count = weights.shape[0]
    tables = imaging_tables()
    vmem = pl.BlockSpec(memory_space=pltpu.VMEM)
    smem = pl.BlockSpec(memory_space=pltpu.SMEM)
    return pl.pallas_call(
        imaging_body,
        out_shape=jax.ShapeDtypeStruct((4, B, B), jnp.float32),
        in_specs=[smem] * 5 + [vmem] * 7 + [vmem] * len(tables),
        out_specs=vmem,
        scratch_shapes=[
            pltpu.VMEM((count, P_SIZE, 2 * P_SIZE), jnp.float32),
            pltpu.VMEM((P_SIZE, P_SIZE), jnp.float32),
            pltpu.VMEM((count * B, 2 * P_SIZE), jnp.float32),
            pltpu.VMEM((count * B, 2 * P_SIZE), jnp.float32),
            pltpu.VMEM((count * B, B), jnp.float32),
            pltpu.VMEM((count * B, B), jnp.float32),
        ],
    )(pos, inst_master, inst_shift, weights, dose, tile_mask, *every, own, target, kerns, h_cat, *tables)


def pixel_body(*refs, passes):
    if passes:
        out_ref, token_ref = refs[-2:]
        token_ref[...] = jnp.zeros(token_ref.shape, jnp.float32)
        refs = refs[:-2] + (out_ref,)
    out_ref = refs[-1]
    c_re_ref, c_im_ref, left_ref = refs[-4:-1]
    parts = refs[:-4]
    for n in range(out_ref.shape[0]):
        x_re = sum(part[n, 0] for part in parts)
        x_im = sum(part[n, 1] for part in parts)
        x_both = jnp.concatenate([x_re, x_im], axis=0)
        p_re = dot_full(x_both, c_re_ref[...])
        p_im = dot_full(x_both, c_im_ref[...])
        y_re = p_re[:B] + p_im[B:]
        y_im = p_re[B:] - p_im[:B]
        y_hi, y_mid, y_lo = split_three(jnp.concatenate([y_re, y_im], axis=0))
        stacked = jnp.concatenate([y_hi, y_mid, y_hi, y_lo, y_hi, y_mid], axis=0)
        out_ref[n] = dot_parts(left_ref[...], stacked)


def group_pixel_body(comp_ref, g0_ref, g1_ref, g2_ref, c_re_ref, c_im_ref, left_ref, out_ref, token_ref):
    token_ref[...] = jnp.zeros(token_ref.shape, jnp.float32)
    own = lax.axis_index("kern")
    for n in range(out_ref.shape[0]):
        mine = n == own
        planes = []
        for c in range(2):
            planes.append(
                jnp.where(mine, comp_ref[0, c] + g1_ref[0, c], g0_ref[0, c] + g2_ref[0, c])
            )
        x_both = jnp.concatenate(planes, axis=0)
        p_re = dot_full(x_both, c_re_ref[...])
        p_im = dot_full(x_both, c_im_ref[...])
        y_re = p_re[:B] + p_im[B:]
        y_im = p_re[B:] - p_im[:B]
        y_hi, y_mid, y_lo = split_three(jnp.concatenate([y_re, y_im], axis=0))
        stacked = jnp.concatenate([y_hi, y_mid, y_hi, y_lo, y_hi, y_mid], axis=0)
        out_ref[n] = dot_parts(left_ref[...], stacked)


def group_pixels(comp, got):
    freq = np.arange(B, dtype=np.int64) - B // 2
    pixel = np.arange(P_SIZE, dtype=np.int64)
    angle = (2.0 * math.pi / P_SIZE) * np.mod(freq[:, None] * pixel[None, :], P_SIZE).astype(np.float64)
    c_re = np.cos(angle)
    c_im = -np.sin(angle)
    a_hi, a_mid, a_lo = table_three(np.concatenate([c_re.T, c_im.T], axis=1))
    left = np.concatenate([a_hi, a_hi, a_mid, a_hi, a_lo, a_mid], axis=1)
    tables = [jnp.asarray(c_re, jnp.float32), jnp.asarray(c_im, jnp.float32), jnp.asarray(left)]
    vmem = pl.BlockSpec(memory_space=pltpu.VMEM)
    shape = jax.ShapeDtypeStruct((2, P_SIZE, P_SIZE), jnp.float32)
    return pl.pallas_call(
        group_pixel_body,
        out_shape=(shape, jax.ShapeDtypeStruct((1, 1, 1, 1), jnp.float32)),
        in_specs=[vmem] * 7,
        out_specs=(vmem, vmem),
    )(comp, *got, *tables)


def pixels(*parts, token=False):
    freq = np.arange(B, dtype=np.int64) - B // 2
    pixel = np.arange(P_SIZE, dtype=np.int64)
    angle = (2.0 * math.pi / P_SIZE) * np.mod(freq[:, None] * pixel[None, :], P_SIZE).astype(np.float64)
    c_re = np.cos(angle)
    c_im = -np.sin(angle)
    a_hi, a_mid, a_lo = table_three(np.concatenate([c_re.T, c_im.T], axis=1))
    left = np.concatenate([a_hi, a_hi, a_mid, a_hi, a_lo, a_mid], axis=1)
    tables = [jnp.asarray(c_re, jnp.float32), jnp.asarray(c_im, jnp.float32), jnp.asarray(left)]
    vmem = pl.BlockSpec(memory_space=pltpu.VMEM)
    shape = jax.ShapeDtypeStruct((parts[0].shape[0], P_SIZE, P_SIZE), jnp.float32)
    if not token:
        return pl.pallas_call(
            functools.partial(pixel_body, passes=False),
            out_shape=shape,
            in_specs=[vmem] * (len(parts) + 3),
            out_specs=vmem,
        )(*parts, *tables)
    return pl.pallas_call(
        functools.partial(pixel_body, passes=True),
        out_shape=(shape, jax.ShapeDtypeStruct((1, 1, 1, 1), jnp.float32)),
        in_specs=[vmem] * (len(parts) + 3),
        out_specs=(vmem, vmem),
    )(*parts, *tables)


def xor_partners(count):
    return count & (count - 1) == 0 and count <= 8


def gather_all(x, axis, count, pos):
    if not xor_partners(count):
        return lax.all_gather(x, axis, axis=0, tiled=True)
    size = x.shape[0]
    slot = jnp.arange(count * size, dtype=jnp.int32) // size
    total = jnp.where((slot == pos)[:, None, None, None], jnp.tile(x, (count, 1, 1, 1)), 0.0)
    for step in range(1, count):
        got = lax.ppermute(x, axis, [(i, i ^ step) for i in range(count)])
        hit = (slot == (pos ^ step))[:, None, None, None]
        total = total + jnp.where(hit, jnp.tile(got, (count, 1, 1, 1)), 0.0)
    return total


def sum_all(x, axis, count, pos):
    if not xor_partners(count):
        return lax.psum(x, axis)
    step = 1
    while step < count:
        x = x + lax.ppermute(x, axis, [(i, i ^ step) for i in range(count)])
        step *= 2
    return x


def sum_parts(x, axis, count, pos):
    if count == 2:
        return (x, lax.ppermute(x, axis, [(0, 1), (1, 0)]))
    return (sum_all(x, axis, count, pos),)


def scatter_sum(x, axis, count, pos, size):
    if not xor_partners(count):
        return lax.psum_scatter(x, axis, scatter_dimension=0, tiled=True)
    total = lax.dynamic_slice_in_dim(x, pos * size, size, 0)
    for step in range(1, count):
        part = lax.dynamic_slice_in_dim(x, (pos ^ step) * size, size, 0)
        total = total + lax.ppermute(part, axis, [(i, i ^ step) for i in range(count)])
    return total


def partner_lists(count, kern_count):
    lists = [[] for _ in range(kern_count)]
    for step in range(1, count):
        lists[step % kern_count].append(step)
    return lists


def chosen_step(lists, round_index, kern_pos):
    pick = jnp.int32(-1)
    for k, steps in enumerate(lists):
        if round_index < len(steps):
            pick = jnp.where(kern_pos == k, jnp.int32(steps[round_index]), pick)
    return pick


def gather_split(x, count, pos, kern_count, kern_pos):
    size = x.shape[0]
    lists = partner_lists(count, kern_count)
    slot = jnp.arange(count * size, dtype=jnp.int32) // size
    spread = lambda part: jnp.tile(part, (count, 1, 1, 1))
    collected = jnp.zeros((count * size,) + x.shape[1:], x.dtype)
    for r in range(max(len(steps) for steps in lists)):
        pairs = []
        for k, steps in enumerate(lists):
            if r < len(steps):
                pairs += [((t ^ steps[r]) * kern_count + k, t * kern_count + k) for t in range(count)]
        got = lax.ppermute(x, ("tile", "kern"), pairs)
        step = chosen_step(lists, r, kern_pos)
        source = jnp.where(step >= 0, pos ^ step, -1)
        collected = collected + jnp.where((slot == source)[:, None, None, None], spread(got), 0.0)
    return sum_parts(collected, "kern", kern_count, kern_pos)


def scatter_split(x, count, pos, kern_count, kern_pos, size, between):
    lists = partner_lists(count, kern_count)
    own = lax.dynamic_slice_in_dim(x, pos * size, size, 0)
    total = jnp.where(kern_pos == 0, own, 0.0)
    for r in range(max(len(steps) for steps in lists)):
        pairs = []
        for k, steps in enumerate(lists):
            if r < len(steps):
                pairs += [(t * kern_count + k, (t ^ steps[r]) * kern_count + k) for t in range(count)]
        step = chosen_step(lists, r, kern_pos)
        target = jnp.where(step >= 0, pos ^ step, 0)
        part = lax.dynamic_slice_in_dim(x, target * size, size, 0)
        total = total + lax.ppermute(part, ("tile", "kern"), pairs)
    done, token = between()
    total = total + 0.0 * token
    return done, sum_parts(total, "kern", kern_count, kern_pos)


def on_device(
    tile_mask, master_mask, target, inst_master, inst_shift, kernels, kernel_weight, corner_dose
):
    cos_tab, sin_tab = band_tables()
    scale = 1.0 / (P_SIZE * P_SIZE)
    local_tiles = tile_mask.shape[0]
    local_masters = master_mask.shape[0]
    tile_count = lax.axis_size("tile")
    tile_pos = lax.axis_index("tile")
    kern_count = lax.axis_size("kern")
    kern_pos = lax.axis_index("kern")
    per_dev = local_tiles // kern_count
    first = kern_pos * per_dev
    region_tiles = tile_count * local_tiles
    region_masters = tile_count * local_masters

    with jax.named_scope("master_spectra"):
        own_re, own_im = spectra(master_mask.astype(jnp.float32), cos_tab, sin_tab)
        own = jnp.stack([own_re, own_im], axis=1)
        if xor_partners(tile_count) and xor_partners(kern_count) and tile_count > 2:
            every = gather_split(own, tile_count, tile_pos, kern_count, kern_pos)
            own_part = own
        else:
            every = (gather_all(own, "tile", tile_count, tile_pos),)
            own_part = jnp.zeros_like(own)

    dose = corner_dose[0]
    kerns = kernels[0]
    h_re = kerns[:, 0]
    h_im = kerns[:, 1]
    weights = kernel_weight[0]

    with jax.named_scope("imaging_kernel"):
        count = h_re.shape[0]
        twice = (2.0 * weights)[:, None, None]
        ht_re = jnp.swapaxes(h_re, 1, 2) * twice
        ht_im = jnp.swapaxes(h_im, 1, 2) * twice
        h_cat = jnp.concatenate([ht_re, ht_re, ht_im, -ht_im], axis=-1).reshape(count * B, 128)
        parts = []
        for j in range(per_dev):
            pos = jnp.stack([first + j, tile_pos]).astype(jnp.int32)
            parts.append(
                imaging(
                    pos, inst_master, inst_shift, weights, corner_dose, tile_mask, every, own_part, target,
                    kerns, h_cat,
                )
            )
        comp = jnp.stack(parts)

    with jax.named_scope("gradient_exchange"):
        corner_count = lax.axis_size("corner")
        corner_pos = lax.axis_index("corner")
        if corner_count == 2 and kern_count == 2 and per_dev == 1:
            got = [
                lax.ppermute(comp, ("corner", "kern"), [(i, i ^ step) for i in range(4)])
                for step in (1, 2, 3)
            ]
            mine = comp + got[1]
            other = got[0] + got[2]
            both = jnp.where(kern_pos == 0, jnp.concatenate([mine, other]), jnp.concatenate([other, mine]))
            tile_pixels = lambda: group_pixels(comp, got)
        else:
            comp = sum_all(comp, "corner", corner_count, corner_pos)
            both = gather_all(comp, "kern", kern_count, kern_pos)
            tile_pixels = lambda: pixels(both[:, 0:2], token=True)
        mine_tiles = both[:, 0:2]
        owner_pick = (
            inst_master[:, None] == jnp.arange(region_masters, dtype=jnp.int32)[None, :]
        ).astype(jnp.float32)
        if corner_count == 2 and kern_count == 2 and per_dev == 1:
            pick_mine = jnp.where(kern_pos == 0, owner_pick[0], owner_pick[1])
            pick_other = jnp.where(kern_pos == 0, owner_pick[1], owner_pick[0])
            terms = (
                pick_mine[:, None, None, None] * (comp[0, 2:4] + got[1][0, 2:4])[None]
                + pick_other[:, None, None, None] * (got[0][0, 2:4] + got[2][0, 2:4])[None]
            )
        else:
            terms = jnp.sum(owner_pick[:, :, None, None, None] * both[:, None, 2:4], axis=0)
        if xor_partners(tile_count) and xor_partners(kern_count) and tile_count > 2:
            tile_grad, mine_masters = scatter_split(
                terms, tile_count, tile_pos, kern_count, kern_pos, local_masters,
                tile_pixels,
            )
        else:
            tile_grad = pixels(mine_tiles)
            mine_masters = (scatter_sum(terms, "tile", tile_count, tile_pos, local_masters),)

    with jax.named_scope("pixel_gradients"):
        master_grad = pixels(*mine_masters)
    return (tile_grad, master_grad)


def solution(mesh):
    return jax.shard_map(
        on_device,
        mesh=mesh,
        in_specs=(
            P(("region", "tile"), None, None),
            P(("region", "tile"), None, None),
            P(("region", "tile"), None, None),
            P(("region", "tile")),
            P(("region", "tile"), None),
            P("corner", None, None, None, None),
            P("corner", None),
            P("corner"),
        ),
        out_specs=(P(("region", "tile"), None, None), P(("region", "tile"), None, None)),
        check_vma=False,
    )
```

```python
import functools
import math

import numpy as np
import jax
import jax.numpy as jnp
from jax import lax
from jax.sharding import PartitionSpec as P
from jax.experimental import pallas as pl
from jax.experimental.pallas import tpu as pltpu

P_SIZE = 256
B = 32


precise = lax.Precision.HIGHEST
steepness = 3.0
threshold = 1.0


def band_tables():
    freq = np.arange(B, dtype=np.int64) - B // 2
    pixel = np.arange(P_SIZE, dtype=np.int64)
    angle = (2.0 * math.pi / P_SIZE) * np.mod(freq[:, None] * pixel[None, :], P_SIZE).astype(np.float64)
    return (jnp.asarray(np.cos(angle), jnp.float32), jnp.asarray(-np.sin(angle), jnp.float32))


def phase_ramp(shift):
    freq = jnp.arange(B, dtype=jnp.int32) - B // 2
    total = (
        freq[None, :, None] * shift[:, 0][:, None, None]
        + freq[None, None, :] * shift[:, 1][:, None, None]
    )
    angle = 2.0 * math.pi / P_SIZE * jnp.mod(total, P_SIZE).astype(jnp.float32)
    return (jnp.cos(angle), -jnp.sin(angle))


def spectra(masks, cos_tab, sin_tab):
    rows_re = jnp.einsum("bx,nxy->nby", cos_tab, masks, precision=precise)
    rows_im = jnp.einsum("bx,nxy->nby", sin_tab, masks, precision=precise)
    spec_re = jnp.einsum("nby,cy->nbc", rows_re, cos_tab, precision=precise) - jnp.einsum(
        "nby,cy->nbc", rows_im, sin_tab, precision=precise
    )
    spec_im = jnp.einsum("nby,cy->nbc", rows_re, sin_tab, precision=precise) + jnp.einsum(
        "nby,cy->nbc", rows_im, cos_tab, precision=precise
    )
    return (spec_re, spec_im)


def back_pixels(x_re, x_im, cos_tab, sin_tab):
    half_re = jnp.einsum("bx,nbc->nxc", cos_tab, x_re, precision=precise) + jnp.einsum(
        "bx,nbc->nxc", sin_tab, x_im, precision=precise
    )
    half_im = jnp.einsum("bx,nbc->nxc", cos_tab, x_im, precision=precise) - jnp.einsum(
        "bx,nbc->nxc", sin_tab, x_re, precision=precise
    )
    return jnp.einsum("nxc,cy->nxy", half_re, cos_tab, precision=precise) + jnp.einsum(
        "nxc,cy->nxy", half_im, sin_tab, precision=precise
    )


def dot_full(a, b):
    return jnp.dot(a, b, precision=precise, preferred_element_type=jnp.float32)


def dot_parts(a, b):
    return jnp.dot(a, b, preferred_element_type=jnp.float32)


def split_three(a):
    hi = a.astype(jnp.bfloat16)
    rest = a - hi.astype(jnp.float32)
    mid = rest.astype(jnp.bfloat16)
    lo = (rest - mid.astype(jnp.float32)).astype(jnp.bfloat16)
    return hi, mid, lo


def table_three(table):
    hi = table.astype(jnp.bfloat16)
    rest = table - hi.astype(np.float64)
    mid = rest.astype(jnp.bfloat16)
    lo = (rest - mid.astype(np.float64)).astype(jnp.bfloat16)
    return hi, mid, lo


def imaging_tables():
    freq = np.arange(B, dtype=np.int64) - B // 2
    pixel = np.arange(P_SIZE, dtype=np.int64)
    angle = (2.0 * math.pi / P_SIZE) * np.mod(freq[:, None] * pixel[None, :], P_SIZE).astype(np.float64)
    c_re = np.cos(angle)
    c_im = -np.sin(angle)
    scale = 1.0 / (P_SIZE * P_SIZE)
    right_w = np.zeros((128, 2 * P_SIZE))
    right_w[:B, :P_SIZE] = c_re
    right_w[:B, P_SIZE:] = -c_im
    right_w[B : 2 * B, :P_SIZE] = c_im
    right_w[B : 2 * B, P_SIZE:] = c_re
    left_a = np.zeros((P_SIZE, 128))
    left_a[:, :B] = c_re.T * scale
    left_a[:, B : 2 * B] = -c_im.T * scale
    right_b = np.zeros((2 * P_SIZE, 128))
    right_b[:P_SIZE, :B] = c_re.T * scale
    right_b[:P_SIZE, B : 2 * B] = c_im.T * scale
    right_b[P_SIZE:, :B] = -c_im.T * scale
    right_b[P_SIZE:, B : 2 * B] = c_re.T * scale
    ct_re = c_re.T
    ct_im = c_im.T
    right_c = np.zeros((2 * P_SIZE, 128))
    for col, (top, bottom) in enumerate(
        ((ct_re, -ct_im), (ct_im, ct_re), (ct_im, ct_re), (ct_re, -ct_im))
    ):
        right_c[:P_SIZE, col * B : (col + 1) * B] = top
        right_c[P_SIZE:, col * B : (col + 1) * B] = bottom
    a_hi, a_mid, a_lo = table_three(left_a[:, : 2 * B])
    left_three = np.concatenate([a_hi, a_hi, a_mid, a_hi, a_lo, a_mid], axis=1)
    b_hi, b_mid, b_lo = table_three(right_b)
    right_hm = np.concatenate([b_hi, b_mid], axis=1)
    right_lh = np.concatenate([b_lo, b_hi], axis=0)
    parts_re = table_three(c_re)
    parts_im = table_three(c_im)
    rows_three = np.concatenate(
        [np.concatenate(parts_re, axis=1), np.concatenate(parts_im, axis=1)], axis=0
    )
    cols_re = np.concatenate(table_three(c_re.T), axis=0)
    cols_im = np.concatenate(table_three(c_im.T), axis=0)
    plain = (c_re, c_im, c_re.T, c_im.T, right_w[:B], right_w[B : 2 * B], right_c)
    out = [jnp.asarray(table, jnp.float32) for table in plain]
    c_hi, c_mid, c_lo = table_three(right_c)
    c_hm = np.concatenate([c_hi, c_mid], axis=1)
    c_lh = np.concatenate([c_lo, c_hi], axis=0)
    bf = (left_three, right_hm, right_lh, rows_three, cols_re, cols_im, c_hm, c_lh)
    return out + [jnp.asarray(table) for table in bf]


def imaging_body(
    pos_ref, im_ref, sh_ref, w_ref, dose_ref, mask_ref, ev_ref, ev2_ref, own_ref, goal_ref, h_ref, hc_ref,
    c_re_ref, c_im_ref, ct_re_ref, ct_im_ref, rw_top, rw_bot, rc_ref, la_ref, rhm_ref, rlh_ref, rows_ref, cre_ref, cim_ref,
    chm_ref, clh_ref,
    slots_ref, f_buf, i_buf, u_buf, w_buf, xr_buf, xi_buf,
):
    count = f_buf.shape[0]
    pos = pos_ref[0]
    master = im_ref[pos]
    pick0 = (lax.broadcasted_iota(jnp.int32, (P_SIZE, 128), 0) == sh_ref[pos, 0]).astype(jnp.bfloat16)
    pick1 = (lax.broadcasted_iota(jnp.int32, (8, P_SIZE), 1) == sh_ref[pos, 1]).astype(jnp.bfloat16)
    e0 = dot_parts(rows_ref[...], jnp.concatenate([pick0, pick0, pick0], axis=0))
    e0_re = e0[:B, 0:1]
    e0_im = e0[B:, 0:1]
    pick1 = jnp.concatenate([pick1, pick1, pick1], axis=1)
    e1_re = dot_parts(pick1, cre_ref[...])[0:1, :]
    e1_im = dot_parts(pick1, cim_ref[...])[0:1, :]
    ph_re = e0_re * e1_re - e0_im * e1_im
    ph_im = e0_re * e1_im + e0_im * e1_re
    local_masters = own_ref.shape[0]
    is_own = master // local_masters == pos_ref[1]
    m_re = ev_ref[master, 0] + ev2_ref[master, 0] + jnp.where(is_own, own_ref[master % local_masters, 0], 0.0)
    m_im = ev_ref[master, 1] + ev2_ref[master, 1] + jnp.where(is_own, own_ref[master % local_masters, 1], 0.0)
    mask = mask_ref[pos]
    rows = dot_parts(rows_ref[...], jnp.concatenate([mask, mask, mask], axis=0))
    t_one = dot_full(rows, ct_re_ref[...])
    t_two = dot_full(rows, ct_im_ref[...])
    s_re = t_one[:B] - t_two[B:] + (ph_re * m_re - ph_im * m_im)
    s_im = t_two[:B] + t_one[B:] + (ph_re * m_im + ph_im * m_re)
    i_buf[...] = jnp.zeros(i_buf.shape, jnp.float32)

    def spectrum(k, carry):
        h_re = h_ref[k, 0]
        h_im = h_ref[k, 1]
        rows = pl.ds(pl.multiple_of(k * B, B), B)
        xr_buf[rows, :] = h_re * s_re - h_im * s_im
        xi_buf[rows, :] = h_re * s_im + h_im * s_re
        return carry

    lax.fori_loop(0, count, spectrum, 0)
    w_buf[...] = dot_full(xr_buf[...], rw_top[...]) + dot_full(xi_buf[...], rw_bot[...])

    def forward(k, carry):
        rows = w_buf[pl.ds(pl.multiple_of(k * B, B), B), :]
        swap = jnp.concatenate([-rows[:, P_SIZE:], rows[:, :P_SIZE]], axis=1)
        s_hi, s_mid, s_lo = split_three(jnp.concatenate([rows, swap], axis=0))
        stacked = jnp.concatenate([s_hi, s_mid, s_hi, s_lo, s_hi, s_mid], axis=0)
        field = dot_parts(la_ref[...], stacked)
        f_buf[k] = field
        power = field * field
        i_buf[...] += w_ref[k] * (power[:, :P_SIZE] + power[:, P_SIZE:])
        return carry

    lax.fori_loop(0, count, forward, 0)
    dose = dose_ref[0]
    resist = 1.0 / (1.0 + jnp.exp(-(steepness * (dose * i_buf[...] - threshold))))
    goal = goal_ref[pos].astype(jnp.float32)
    i_buf[...] = 2.0 * (resist - goal) * resist * (1.0 - resist) * steepness * dose

    def backward(k, carry):
        sens = i_buf[...]
        weighted = f_buf[k] * jnp.concatenate([sens, sens], axis=1)
        q_hi, q_mid, q_lo = split_three(weighted)
        first = dot_parts(q_hi, rhm_ref[...]) + dot_parts(q_mid, rhm_ref[...])
        rest = dot_parts(jnp.concatenate([q_hi, q_lo], axis=1), rlh_ref[...])
        half = first[:, :128] + first[:, 128:] + rest
        flip = half.T
        u_buf[pl.ds(pl.multiple_of(k * B, B), B), :] = jnp.concatenate([flip[:B], flip[B : 2 * B]], axis=1)
        return carry

    lax.fori_loop(0, count, backward, 0)
    u_hi, u_mid, u_lo = split_three(u_buf[...])
    first = dot_parts(u_hi, chm_ref[...]) + dot_parts(u_mid, chm_ref[...])
    out = first[:, :128] + first[:, 128:] + dot_parts(jnp.concatenate([u_hi, u_lo], axis=1), clh_ref[...])
    acc = jnp.sum((hc_ref[...] * out).reshape(count, B, 128), axis=0)
    flip = jnp.concatenate([acc, jnp.zeros((128 - B, 128), jnp.float32)], axis=0).T
    g_re = flip[0:B, 0:B] + flip[2 * B : 3 * B, 0:B]
    g_im = flip[B : 2 * B, 0:B] + flip[3 * B : 4 * B, 0:B]
    slots_ref[0] = g_re
    slots_ref[1] = g_im
    slots_ref[2] = ph_re * g_re + ph_im * g_im
    slots_ref[3] = ph_re * g_im - ph_im * g_re


def imaging(pos, inst_master, inst_shift, weights, dose, tile_mask, every, own, target, kerns, h_cat):
    if len(every) == 1:
        every = (every[0], jnp.zeros_like(every[0]))
    count = weights.shape[0]
    tables = imaging_tables()
    vmem = pl.BlockSpec(memory_space=pltpu.VMEM)
    smem = pl.BlockSpec(memory_space=pltpu.SMEM)
    return pl.pallas_call(
        imaging_body,
        out_shape=jax.ShapeDtypeStruct((4, B, B), jnp.float32),
        in_specs=[smem] * 5 + [vmem] * 7 + [vmem] * len(tables),
        out_specs=vmem,
        scratch_shapes=[
            pltpu.VMEM((count, P_SIZE, 2 * P_SIZE), jnp.float32),
            pltpu.VMEM((P_SIZE, P_SIZE), jnp.float32),
            pltpu.VMEM((count * B, 2 * P_SIZE), jnp.float32),
            pltpu.VMEM((count * B, 2 * P_SIZE), jnp.float32),
            pltpu.VMEM((count * B, B), jnp.float32),
            pltpu.VMEM((count * B, B), jnp.float32),
        ],
    )(pos, inst_master, inst_shift, weights, dose, tile_mask, *every, own, target, kerns, h_cat, *tables)


def pixel_body(*refs, passes):
    if passes:
        out_ref, token_ref = refs[-2:]
        token_ref[...] = jnp.zeros(token_ref.shape, jnp.float32)
        refs = refs[:-2] + (out_ref,)
    out_ref = refs[-1]
    c_re_ref, c_im_ref, left_ref = refs[-4:-1]
    parts = refs[:-4]
    for n in range(out_ref.shape[0]):
        x_re = sum(part[n, 0] for part in parts)
        x_im = sum(part[n, 1] for part in parts)
        x_both = jnp.concatenate([x_re, x_im], axis=0)
        p_re = dot_full(x_both, c_re_ref[...])
        p_im = dot_full(x_both, c_im_ref[...])
        y_re = p_re[:B] + p_im[B:]
        y_im = p_re[B:] - p_im[:B]
        y_hi, y_mid, y_lo = split_three(jnp.concatenate([y_re, y_im], axis=0))
        stacked = jnp.concatenate([y_hi, y_mid, y_hi, y_lo, y_hi, y_mid], axis=0)
        out_ref[n] = dot_parts(left_ref[...], stacked)


def group_pixel_body(comp_ref, g0_ref, g1_ref, g2_ref, c_re_ref, c_im_ref, left_ref, out_ref, token_ref):
    token_ref[...] = jnp.zeros(token_ref.shape, jnp.float32)
    own = lax.axis_index("kern")
    for n in range(out_ref.shape[0]):
        mine = n == own
        planes = []
        for c in range(2):
            planes.append(
                jnp.where(mine, comp_ref[0, c] + g1_ref[0, c], g0_ref[0, c] + g2_ref[0, c])
            )
        x_both = jnp.concatenate(planes, axis=0)
        p_re = dot_full(x_both, c_re_ref[...])
        p_im = dot_full(x_both, c_im_ref[...])
        y_re = p_re[:B] + p_im[B:]
        y_im = p_re[B:] - p_im[:B]
        y_hi, y_mid, y_lo = split_three(jnp.concatenate([y_re, y_im], axis=0))
        stacked = jnp.concatenate([y_hi, y_mid, y_hi, y_lo, y_hi, y_mid], axis=0)
        out_ref[n] = dot_parts(left_ref[...], stacked)


def group_pixels(comp, got):
    freq = np.arange(B, dtype=np.int64) - B // 2
    pixel = np.arange(P_SIZE, dtype=np.int64)
    angle = (2.0 * math.pi / P_SIZE) * np.mod(freq[:, None] * pixel[None, :], P_SIZE).astype(np.float64)
    c_re = np.cos(angle)
    c_im = -np.sin(angle)
    a_hi, a_mid, a_lo = table_three(np.concatenate([c_re.T, c_im.T], axis=1))
    left = np.concatenate([a_hi, a_hi, a_mid, a_hi, a_lo, a_mid], axis=1)
    tables = [jnp.asarray(c_re, jnp.float32), jnp.asarray(c_im, jnp.float32), jnp.asarray(left)]
    vmem = pl.BlockSpec(memory_space=pltpu.VMEM)
    shape = jax.ShapeDtypeStruct((2, P_SIZE, P_SIZE), jnp.float32)
    return pl.pallas_call(
        group_pixel_body,
        out_shape=(shape, jax.ShapeDtypeStruct((1, 1, 1, 1), jnp.float32)),
        in_specs=[vmem] * 7,
        out_specs=(vmem, vmem),
    )(comp, *got, *tables)


def pixels(*parts, token=False):
    freq = np.arange(B, dtype=np.int64) - B // 2
    pixel = np.arange(P_SIZE, dtype=np.int64)
    angle = (2.0 * math.pi / P_SIZE) * np.mod(freq[:, None] * pixel[None, :], P_SIZE).astype(np.float64)
    c_re = np.cos(angle)
    c_im = -np.sin(angle)
    a_hi, a_mid, a_lo = table_three(np.concatenate([c_re.T, c_im.T], axis=1))
    left = np.concatenate([a_hi, a_hi, a_mid, a_hi, a_lo, a_mid], axis=1)
    tables = [jnp.asarray(c_re, jnp.float32), jnp.asarray(c_im, jnp.float32), jnp.asarray(left)]
    vmem = pl.BlockSpec(memory_space=pltpu.VMEM)
    shape = jax.ShapeDtypeStruct((parts[0].shape[0], P_SIZE, P_SIZE), jnp.float32)
    if not token:
        return pl.pallas_call(
            functools.partial(pixel_body, passes=False),
            out_shape=shape,
            in_specs=[vmem] * (len(parts) + 3),
            out_specs=vmem,
        )(*parts, *tables)
    return pl.pallas_call(
        functools.partial(pixel_body, passes=True),
        out_shape=(shape, jax.ShapeDtypeStruct((1, 1, 1, 1), jnp.float32)),
        in_specs=[vmem] * (len(parts) + 3),
        out_specs=(vmem, vmem),
    )(*parts, *tables)


def xor_partners(count):
    return count & (count - 1) == 0 and count <= 8


def gather_all(x, axis, count, pos):
    if not xor_partners(count):
        return lax.all_gather(x, axis, axis=0, tiled=True)
    size = x.shape[0]
    slot = jnp.arange(count * size, dtype=jnp.int32) // size
    total = jnp.where((slot == pos)[:, None, None, None], jnp.tile(x, (count, 1, 1, 1)), 0.0)
    for step in range(1, count):
        got = lax.ppermute(x, axis, [(i, i ^ step) for i in range(count)])
        hit = (slot == (pos ^ step))[:, None, None, None]
        total = total + jnp.where(hit, jnp.tile(got, (count, 1, 1, 1)), 0.0)
    return total


def sum_all(x, axis, count, pos):
    if not xor_partners(count):
        return lax.psum(x, axis)
    step = 1
    while step < count:
        x = x + lax.ppermute(x, axis, [(i, i ^ step) for i in range(count)])
        step *= 2
    return x


def sum_parts(x, axis, count, pos):
    if count == 2:
        return (x, lax.ppermute(x, axis, [(0, 1), (1, 0)]))
    return (sum_all(x, axis, count, pos),)


def scatter_sum(x, axis, count, pos, size):
    if not xor_partners(count):
        return lax.psum_scatter(x, axis, scatter_dimension=0, tiled=True)
    total = lax.dynamic_slice_in_dim(x, pos * size, size, 0)
    for step in range(1, count):
        part = lax.dynamic_slice_in_dim(x, (pos ^ step) * size, size, 0)
        total = total + lax.ppermute(part, axis, [(i, i ^ step) for i in range(count)])
    return total


def partner_lists(count, kern_count):
    lists = [[] for _ in range(kern_count)]
    for step in range(1, count):
        lists[step % kern_count].append(step)
    return lists


def chosen_step(lists, round_index, kern_pos):
    pick = jnp.int32(-1)
    for k, steps in enumerate(lists):
        if round_index < len(steps):
            pick = jnp.where(kern_pos == k, jnp.int32(steps[round_index]), pick)
    return pick


def gather_split(x, count, pos, kern_count, kern_pos):
    size = x.shape[0]
    lists = partner_lists(count, kern_count)
    slot = jnp.arange(count * size, dtype=jnp.int32) // size
    spread = lambda part: jnp.tile(part, (count, 1, 1, 1))
    collected = jnp.zeros((count * size,) + x.shape[1:], x.dtype)
    for r in range(max(len(steps) for steps in lists)):
        pairs = []
        for k, steps in enumerate(lists):
            if r < len(steps):
                pairs += [((t ^ steps[r]) * kern_count + k, t * kern_count + k) for t in range(count)]
        got = lax.ppermute(x, ("tile", "kern"), pairs)
        step = chosen_step(lists, r, kern_pos)
        source = jnp.where(step >= 0, pos ^ step, -1)
        collected = collected + jnp.where((slot == source)[:, None, None, None], spread(got), 0.0)
    return sum_parts(collected, "kern", kern_count, kern_pos)


def scatter_split(x, count, pos, kern_count, kern_pos, size, between):
    lists = partner_lists(count, kern_count)
    own = lax.dynamic_slice_in_dim(x, pos * size, size, 0)
    total = jnp.where(kern_pos == 0, own, 0.0)
    for r in range(max(len(steps) for steps in lists)):
        pairs = []
        for k, steps in enumerate(lists):
            if r < len(steps):
                pairs += [(t * kern_count + k, (t ^ steps[r]) * kern_count + k) for t in range(count)]
        step = chosen_step(lists, r, kern_pos)
        target = jnp.where(step >= 0, pos ^ step, 0)
        part = lax.dynamic_slice_in_dim(x, target * size, size, 0)
        total = total + lax.ppermute(part, ("tile", "kern"), pairs)
    done, token = between()
    total = total + 0.0 * token
    return done, sum_parts(total, "kern", kern_count, kern_pos)


def on_device(
    tile_mask, master_mask, target, inst_master, inst_shift, kernels, kernel_weight, corner_dose
):
    cos_tab, sin_tab = band_tables()
    scale = 1.0 / (P_SIZE * P_SIZE)
    local_tiles = tile_mask.shape[0]
    local_masters = master_mask.shape[0]
    tile_count = lax.axis_size("tile")
    tile_pos = lax.axis_index("tile")
    kern_count = lax.axis_size("kern")
    kern_pos = lax.axis_index("kern")
    per_dev = local_tiles // kern_count
    first = kern_pos * per_dev
    region_tiles = tile_count * local_tiles
    region_masters = tile_count * local_masters

    with jax.named_scope("master_spectra"):
        own_re, own_im = spectra(master_mask.astype(jnp.float32), cos_tab, sin_tab)
        own = jnp.stack([own_re, own_im], axis=1)
        if xor_partners(tile_count) and xor_partners(kern_count) and tile_count > 2:
            every = gather_split(own, tile_count, tile_pos, kern_count, kern_pos)
            own_part = own
        else:
            every = (gather_all(own, "tile", tile_count, tile_pos),)
            own_part = jnp.zeros_like(own)

    dose = corner_dose[0]
    kerns = kernels[0]
    h_re = kerns[:, 0]
    h_im = kerns[:, 1]
    weights = kernel_weight[0]

    with jax.named_scope("imaging_kernel"):
        count = h_re.shape[0]
        twice = (2.0 * weights)[:, None, None]
        ht_re = jnp.swapaxes(h_re, 1, 2) * twice
        ht_im = jnp.swapaxes(h_im, 1, 2) * twice
        h_cat = jnp.concatenate([ht_re, ht_re, ht_im, -ht_im], axis=-1).reshape(count * B, 128)
        parts = []
        for j in range(per_dev):
            pos = jnp.stack([first + j, tile_pos]).astype(jnp.int32)
            parts.append(
                imaging(
                    pos, inst_master, inst_shift, weights, corner_dose, tile_mask, every, own_part, target,
                    kerns, h_cat,
                )
            )
        comp = jnp.stack(parts)

    with jax.named_scope("gradient_exchange"):
        corner_count = lax.axis_size("corner")
        corner_pos = lax.axis_index("corner")
        if corner_count == 2 and kern_count == 2 and per_dev == 1:
            got = [
                lax.ppermute(comp, ("corner", "kern"), [(i, i ^ step) for i in range(4)])
                for step in (1, 2, 3)
            ]
            mine = comp + got[1]
            other = got[0] + got[2]
            both = jnp.where(kern_pos == 0, jnp.concatenate([mine, other]), jnp.concatenate([other, mine]))
            tile_pixels = lambda: group_pixels(comp, got)
        else:
            comp = sum_all(comp, "corner", corner_count, corner_pos)
            both = gather_all(comp, "kern", kern_count, kern_pos)
            tile_pixels = lambda: pixels(both[:, 0:2], token=True)
        mine_tiles = both[:, 0:2]
        owner_pick = (
            inst_master[:, None] == jnp.arange(region_masters, dtype=jnp.int32)[None, :]
        ).astype(jnp.float32)
        if corner_count == 2 and kern_count == 2 and per_dev == 1:
            pick_mine = jnp.where(kern_pos == 0, owner_pick[0], owner_pick[1])
            pick_other = jnp.where(kern_pos == 0, owner_pick[1], owner_pick[0])
            terms = (
                pick_mine[:, None, None, None] * (comp[0, 2:4] + got[1][0, 2:4])[None]
                + pick_other[:, None, None, None] * (got[0][0, 2:4] + got[2][0, 2:4])[None]
            )
        else:
            terms = jnp.sum(owner_pick[:, :, None, None, None] * both[:, None, 2:4], axis=0)
        if xor_partners(tile_count) and xor_partners(kern_count) and tile_count > 2:
            tile_grad, mine_masters = scatter_split(
                terms, tile_count, tile_pos, kern_count, kern_pos, local_masters,
                tile_pixels,
            )
        else:
            tile_grad = pixels(mine_tiles)
            mine_masters = (scatter_sum(terms, "tile", tile_count, tile_pos, local_masters),)

    with jax.named_scope("pixel_gradients"):
        master_grad = pixels(*mine_masters)
    return (tile_grad, master_grad)


def solution(mesh):
    return jax.shard_map(
        on_device,
        mesh=mesh,
        in_specs=(
            P(("region", "tile"), None, None),
            P(("region", "tile"), None, None),
            P(("region", "tile"), None, None),
            P(("region", "tile")),
            P(("region", "tile"), None),
            P("corner", None, None, None, None),
            P("corner", None),
            P("corner"),
        ),
        out_specs=(P(("region", "tile"), None, None), P(("region", "tile"), None, None)),
        check_vma=False,
    )
```

```python
import functools
import math

import numpy as np
import jax
import jax.numpy as jnp
from jax import lax
from jax.sharding import PartitionSpec as P
from jax.experimental import pallas as pl
from jax.experimental.pallas import tpu as pltpu

P_SIZE = 256
B = 32


precise = lax.Precision.HIGHEST
steepness = 3.0
threshold = 1.0


def band_tables():
    freq = np.arange(B, dtype=np.int64) - B // 2
    pixel = np.arange(P_SIZE, dtype=np.int64)
    angle = (2.0 * math.pi / P_SIZE) * np.mod(freq[:, None] * pixel[None, :], P_SIZE).astype(np.float64)
    return (jnp.asarray(np.cos(angle), jnp.float32), jnp.asarray(-np.sin(angle), jnp.float32))


def phase_ramp(shift):
    freq = jnp.arange(B, dtype=jnp.int32) - B // 2
    total = (
        freq[None, :, None] * shift[:, 0][:, None, None]
        + freq[None, None, :] * shift[:, 1][:, None, None]
    )
    angle = 2.0 * math.pi / P_SIZE * jnp.mod(total, P_SIZE).astype(jnp.float32)
    return (jnp.cos(angle), -jnp.sin(angle))


def spectra(masks, cos_tab, sin_tab):
    rows_re = jnp.einsum("bx,nxy->nby", cos_tab, masks, precision=precise)
    rows_im = jnp.einsum("bx,nxy->nby", sin_tab, masks, precision=precise)
    spec_re = jnp.einsum("nby,cy->nbc", rows_re, cos_tab, precision=precise) - jnp.einsum(
        "nby,cy->nbc", rows_im, sin_tab, precision=precise
    )
    spec_im = jnp.einsum("nby,cy->nbc", rows_re, sin_tab, precision=precise) + jnp.einsum(
        "nby,cy->nbc", rows_im, cos_tab, precision=precise
    )
    return (spec_re, spec_im)


def back_pixels(x_re, x_im, cos_tab, sin_tab):
    half_re = jnp.einsum("bx,nbc->nxc", cos_tab, x_re, precision=precise) + jnp.einsum(
        "bx,nbc->nxc", sin_tab, x_im, precision=precise
    )
    half_im = jnp.einsum("bx,nbc->nxc", cos_tab, x_im, precision=precise) - jnp.einsum(
        "bx,nbc->nxc", sin_tab, x_re, precision=precise
    )
    return jnp.einsum("nxc,cy->nxy", half_re, cos_tab, precision=precise) + jnp.einsum(
        "nxc,cy->nxy", half_im, sin_tab, precision=precise
    )


def dot_full(a, b):
    return jnp.dot(a, b, precision=precise, preferred_element_type=jnp.float32)


def dot_parts(a, b):
    return jnp.dot(a, b, preferred_element_type=jnp.float32)


def split_three(a):
    hi = a.astype(jnp.bfloat16)
    rest = a - hi.astype(jnp.float32)
    mid = rest.astype(jnp.bfloat16)
    lo = (rest - mid.astype(jnp.float32)).astype(jnp.bfloat16)
    return hi, mid, lo


def table_three(table):
    hi = table.astype(jnp.bfloat16)
    rest = table - hi.astype(np.float64)
    mid = rest.astype(jnp.bfloat16)
    lo = (rest - mid.astype(np.float64)).astype(jnp.bfloat16)
    return hi, mid, lo


def imaging_tables():
    freq = np.arange(B, dtype=np.int64) - B // 2
    pixel = np.arange(P_SIZE, dtype=np.int64)
    angle = (2.0 * math.pi / P_SIZE) * np.mod(freq[:, None] * pixel[None, :], P_SIZE).astype(np.float64)
    c_re = np.cos(angle)
    c_im = -np.sin(angle)
    scale = 1.0 / (P_SIZE * P_SIZE)
    right_w = np.zeros((128, 2 * P_SIZE))
    right_w[:B, :P_SIZE] = c_re
    right_w[:B, P_SIZE:] = -c_im
    right_w[B : 2 * B, :P_SIZE] = c_im
    right_w[B : 2 * B, P_SIZE:] = c_re
    left_a = np.zeros((P_SIZE, 128))
    left_a[:, :B] = c_re.T * scale
    left_a[:, B : 2 * B] = -c_im.T * scale
    right_b = np.zeros((2 * P_SIZE, 128))
    right_b[:P_SIZE, :B] = c_re.T * scale
    right_b[:P_SIZE, B : 2 * B] = c_im.T * scale
    right_b[P_SIZE:, :B] = -c_im.T * scale
    right_b[P_SIZE:, B : 2 * B] = c_re.T * scale
    ct_re = c_re.T
    ct_im = c_im.T
    right_c = np.zeros((2 * P_SIZE, 128))
    for col, (top, bottom) in enumerate(
        ((ct_re, -ct_im), (ct_im, ct_re), (ct_im, ct_re), (ct_re, -ct_im))
    ):
        right_c[:P_SIZE, col * B : (col + 1) * B] = top
        right_c[P_SIZE:, col * B : (col + 1) * B] = bottom
    a_hi, a_mid, a_lo = table_three(left_a[:, : 2 * B])
    left_three = np.concatenate([a_hi, a_hi, a_mid, a_hi, a_lo, a_mid], axis=1)
    b_hi, b_mid, b_lo = table_three(right_b)
    right_hm = np.concatenate([b_hi, b_mid], axis=1)
    right_lh = np.concatenate([b_lo, b_hi], axis=0)
    parts_re = table_three(c_re)
    parts_im = table_three(c_im)
    rows_three = np.concatenate(
        [np.concatenate(parts_re, axis=1), np.concatenate(parts_im, axis=1)], axis=0
    )
    cols_re = np.concatenate(table_three(c_re.T), axis=0)
    cols_im = np.concatenate(table_three(c_im.T), axis=0)
    plain = (c_re, c_im, c_re.T, c_im.T, right_w[:B], right_w[B : 2 * B], right_c)
    out = [jnp.asarray(table, jnp.float32) for table in plain]
    bf = (left_three, right_hm, right_lh, rows_three, cols_re, cols_im)
    return out + [jnp.asarray(table) for table in bf]


def imaging_body(
    pos_ref, im_ref, sh_ref, w_ref, dose_ref, mask_ref, ev_ref, ev2_ref, own_ref, goal_ref, h_ref, hc_ref,
    c_re_ref, c_im_ref, ct_re_ref, ct_im_ref, rw_top, rw_bot, rc_ref, la_ref, rhm_ref, rlh_ref, rows_ref, cre_ref, cim_ref,
    slots_ref, f_buf, i_buf, u_buf, w_buf, xr_buf, xi_buf,
):
    count = f_buf.shape[0]
    pos = pos_ref[0]
    master = im_ref[pos]
    pick0 = (lax.broadcasted_iota(jnp.int32, (P_SIZE, 128), 0) == sh_ref[pos, 0]).astype(jnp.bfloat16)
    pick1 = (lax.broadcasted_iota(jnp.int32, (8, P_SIZE), 1) == sh_ref[pos, 1]).astype(jnp.bfloat16)
    e0 = dot_parts(rows_ref[...], jnp.concatenate([pick0, pick0, pick0], axis=0))
    e0_re = e0[:B, 0:1]
    e0_im = e0[B:, 0:1]
    pick1 = jnp.concatenate([pick1, pick1, pick1], axis=1)
    e1_re = dot_parts(pick1, cre_ref[...])[0:1, :]
    e1_im = dot_parts(pick1, cim_ref[...])[0:1, :]
    ph_re = e0_re * e1_re - e0_im * e1_im
    ph_im = e0_re * e1_im + e0_im * e1_re
    local_masters = own_ref.shape[0]
    is_own = master // local_masters == pos_ref[1]
    m_re = ev_ref[master, 0] + ev2_ref[master, 0] + jnp.where(is_own, own_ref[master % local_masters, 0], 0.0)
    m_im = ev_ref[master, 1] + ev2_ref[master, 1] + jnp.where(is_own, own_ref[master % local_masters, 1], 0.0)
    mask = mask_ref[pos]
    rows = dot_parts(rows_ref[...], jnp.concatenate([mask, mask, mask], axis=0))
    t_one = dot_full(rows, ct_re_ref[...])
    t_two = dot_full(rows, ct_im_ref[...])
    s_re = t_one[:B] - t_two[B:] + (ph_re * m_re - ph_im * m_im)
    s_im = t_two[:B] + t_one[B:] + (ph_re * m_im + ph_im * m_re)
    i_buf[...] = jnp.zeros(i_buf.shape, jnp.float32)

    def spectrum(k, carry):
        h_re = h_ref[k, 0]
        h_im = h_ref[k, 1]
        rows = pl.ds(pl.multiple_of(k * B, B), B)
        xr_buf[rows, :] = h_re * s_re - h_im * s_im
        xi_buf[rows, :] = h_re * s_im + h_im * s_re
        return carry

    lax.fori_loop(0, count, spectrum, 0, unroll=True)
    w_buf[...] = dot_full(xr_buf[...], rw_top[...]) + dot_full(xi_buf[...], rw_bot[...])

    def forward(k, carry):
        rows = w_buf[pl.ds(pl.multiple_of(k * B, B), B), :]
        swap = jnp.concatenate([-rows[:, P_SIZE:], rows[:, :P_SIZE]], axis=1)
        s_hi, s_mid, s_lo = split_three(jnp.concatenate([rows, swap], axis=0))
        stacked = jnp.concatenate([s_hi, s_mid, s_hi, s_lo, s_hi, s_mid], axis=0)
        field = dot_parts(la_ref[...], stacked)
        f_buf[k] = field
        power = field * field
        i_buf[...] += w_ref[k] * (power[:, :P_SIZE] + power[:, P_SIZE:])
        return carry

    lax.fori_loop(0, count, forward, 0, unroll=2)
    dose = dose_ref[0]
    resist = 1.0 / (1.0 + jnp.exp(-(steepness * (dose * i_buf[...] - threshold))))
    goal = goal_ref[pos].astype(jnp.float32)
    i_buf[...] = 2.0 * (resist - goal) * resist * (1.0 - resist) * steepness * dose

    def backward(k, carry):
        sens = i_buf[...]
        weighted = f_buf[k] * jnp.concatenate([sens, sens], axis=1)
        q_hi, q_mid, q_lo = split_three(weighted)
        first = dot_parts(q_hi, rhm_ref[...]) + dot_parts(q_mid, rhm_ref[...])
        rest = dot_parts(jnp.concatenate([q_hi, q_lo], axis=1), rlh_ref[...])
        half = first[:, :128] + first[:, 128:] + rest
        flip = half.T
        u_buf[pl.ds(pl.multiple_of(k * B, B), B), :] = jnp.concatenate([flip[:B], flip[B : 2 * B]], axis=1)
        return carry

    lax.fori_loop(0, count, backward, 0, unroll=2)
    out = dot_full(u_buf[...], rc_ref[...])
    acc = jnp.sum((hc_ref[...] * out).reshape(count, B, 128), axis=0)
    flip = jnp.concatenate([acc, jnp.zeros((128 - B, 128), jnp.float32)], axis=0).T
    g_re = flip[0:B, 0:B] + flip[2 * B : 3 * B, 0:B]
    g_im = flip[B : 2 * B, 0:B] + flip[3 * B : 4 * B, 0:B]
    slots_ref[0] = g_re
    slots_ref[1] = g_im
    slots_ref[2] = ph_re * g_re + ph_im * g_im
    slots_ref[3] = ph_re * g_im - ph_im * g_re


def imaging(pos, inst_master, inst_shift, weights, dose, tile_mask, every, own, target, kerns, h_cat):
    if len(every) == 1:
        every = (every[0], jnp.zeros_like(every[0]))
    count = weights.shape[0]
    tables = imaging_tables()
    vmem = pl.BlockSpec(memory_space=pltpu.VMEM)
    smem = pl.BlockSpec(memory_space=pltpu.SMEM)
    return pl.pallas_call(
        imaging_body,
        out_shape=jax.ShapeDtypeStruct((4, B, B), jnp.float32),
        in_specs=[smem] * 5 + [vmem] * 7 + [vmem] * len(tables),
        out_specs=vmem,
        scratch_shapes=[
            pltpu.VMEM((count, P_SIZE, 2 * P_SIZE), jnp.float32),
            pltpu.VMEM((P_SIZE, P_SIZE), jnp.float32),
            pltpu.VMEM((count * B, 2 * P_SIZE), jnp.float32),
            pltpu.VMEM((count * B, 2 * P_SIZE), jnp.float32),
            pltpu.VMEM((count * B, B), jnp.float32),
            pltpu.VMEM((count * B, B), jnp.float32),
        ],
    )(pos, inst_master, inst_shift, weights, dose, tile_mask, *every, own, target, kerns, h_cat, *tables)


def pixel_body(*refs, passes):
    if passes:
        out_ref, token_ref = refs[-2:]
        token_ref[...] = jnp.zeros(token_ref.shape, jnp.float32)
        refs = refs[:-2] + (out_ref,)
    out_ref = refs[-1]
    c_re_ref, c_im_ref, left_ref = refs[-4:-1]
    parts = refs[:-4]
    for n in range(out_ref.shape[0]):
        x_re = sum(part[n, 0] for part in parts)
        x_im = sum(part[n, 1] for part in parts)
        x_both = jnp.concatenate([x_re, x_im], axis=0)
        p_re = dot_full(x_both, c_re_ref[...])
        p_im = dot_full(x_both, c_im_ref[...])
        y_re = p_re[:B] + p_im[B:]
        y_im = p_re[B:] - p_im[:B]
        y_hi, y_mid, y_lo = split_three(jnp.concatenate([y_re, y_im], axis=0))
        stacked = jnp.concatenate([y_hi, y_mid, y_hi, y_lo, y_hi, y_mid], axis=0)
        out_ref[n] = dot_parts(left_ref[...], stacked)


def group_pixel_body(comp_ref, g0_ref, g1_ref, g2_ref, c_re_ref, c_im_ref, left_ref, out_ref, token_ref):
    token_ref[...] = jnp.zeros(token_ref.shape, jnp.float32)
    own = lax.axis_index("kern")
    for n in range(out_ref.shape[0]):
        mine = n == own
        planes = []
        for c in range(2):
            planes.append(
                jnp.where(mine, comp_ref[0, c] + g1_ref[0, c], g0_ref[0, c] + g2_ref[0, c])
            )
        x_both = jnp.concatenate(planes, axis=0)
        p_re = dot_full(x_both, c_re_ref[...])
        p_im = dot_full(x_both, c_im_ref[...])
        y_re = p_re[:B] + p_im[B:]
        y_im = p_re[B:] - p_im[:B]
        y_hi, y_mid, y_lo = split_three(jnp.concatenate([y_re, y_im], axis=0))
        stacked = jnp.concatenate([y_hi, y_mid, y_hi, y_lo, y_hi, y_mid], axis=0)
        out_ref[n] = dot_parts(left_ref[...], stacked)


def group_pixels(comp, got):
    freq = np.arange(B, dtype=np.int64) - B // 2
    pixel = np.arange(P_SIZE, dtype=np.int64)
    angle = (2.0 * math.pi / P_SIZE) * np.mod(freq[:, None] * pixel[None, :], P_SIZE).astype(np.float64)
    c_re = np.cos(angle)
    c_im = -np.sin(angle)
    a_hi, a_mid, a_lo = table_three(np.concatenate([c_re.T, c_im.T], axis=1))
    left = np.concatenate([a_hi, a_hi, a_mid, a_hi, a_lo, a_mid], axis=1)
    tables = [jnp.asarray(c_re, jnp.float32), jnp.asarray(c_im, jnp.float32), jnp.asarray(left)]
    vmem = pl.BlockSpec(memory_space=pltpu.VMEM)
    shape = jax.ShapeDtypeStruct((2, P_SIZE, P_SIZE), jnp.float32)
    return pl.pallas_call(
        group_pixel_body,
        out_shape=(shape, jax.ShapeDtypeStruct((1, 1, 1, 1), jnp.float32)),
        in_specs=[vmem] * 7,
        out_specs=(vmem, vmem),
    )(comp, *got, *tables)


def pixels(*parts, token=False):
    freq = np.arange(B, dtype=np.int64) - B // 2
    pixel = np.arange(P_SIZE, dtype=np.int64)
    angle = (2.0 * math.pi / P_SIZE) * np.mod(freq[:, None] * pixel[None, :], P_SIZE).astype(np.float64)
    c_re = np.cos(angle)
    c_im = -np.sin(angle)
    a_hi, a_mid, a_lo = table_three(np.concatenate([c_re.T, c_im.T], axis=1))
    left = np.concatenate([a_hi, a_hi, a_mid, a_hi, a_lo, a_mid], axis=1)
    tables = [jnp.asarray(c_re, jnp.float32), jnp.asarray(c_im, jnp.float32), jnp.asarray(left)]
    vmem = pl.BlockSpec(memory_space=pltpu.VMEM)
    shape = jax.ShapeDtypeStruct((parts[0].shape[0], P_SIZE, P_SIZE), jnp.float32)
    if not token:
        return pl.pallas_call(
            functools.partial(pixel_body, passes=False),
            out_shape=shape,
            in_specs=[vmem] * (len(parts) + 3),
            out_specs=vmem,
        )(*parts, *tables)
    return pl.pallas_call(
        functools.partial(pixel_body, passes=True),
        out_shape=(shape, jax.ShapeDtypeStruct((1, 1, 1, 1), jnp.float32)),
        in_specs=[vmem] * (len(parts) + 3),
        out_specs=(vmem, vmem),
    )(*parts, *tables)


def xor_partners(count):
    return count & (count - 1) == 0 and count <= 8


def gather_all(x, axis, count, pos):
    if not xor_partners(count):
        return lax.all_gather(x, axis, axis=0, tiled=True)
    size = x.shape[0]
    slot = jnp.arange(count * size, dtype=jnp.int32) // size
    total = jnp.where((slot == pos)[:, None, None, None], jnp.tile(x, (count, 1, 1, 1)), 0.0)
    for step in range(1, count):
        got = lax.ppermute(x, axis, [(i, i ^ step) for i in range(count)])
        hit = (slot == (pos ^ step))[:, None, None, None]
        total = total + jnp.where(hit, jnp.tile(got, (count, 1, 1, 1)), 0.0)
    return total


def sum_all(x, axis, count, pos):
    if not xor_partners(count):
        return lax.psum(x, axis)
    step = 1
    while step < count:
        x = x + lax.ppermute(x, axis, [(i, i ^ step) for i in range(count)])
        step *= 2
    return x


def sum_parts(x, axis, count, pos):
    if count == 2:
        return (x, lax.ppermute(x, axis, [(0, 1), (1, 0)]))
    return (sum_all(x, axis, count, pos),)


def scatter_sum(x, axis, count, pos, size):
    if not xor_partners(count):
        return lax.psum_scatter(x, axis, scatter_dimension=0, tiled=True)
    total = lax.dynamic_slice_in_dim(x, pos * size, size, 0)
    for step in range(1, count):
        part = lax.dynamic_slice_in_dim(x, (pos ^ step) * size, size, 0)
        total = total + lax.ppermute(part, axis, [(i, i ^ step) for i in range(count)])
    return total


def partner_lists(count, kern_count):
    lists = [[] for _ in range(kern_count)]
    for step in range(1, count):
        lists[step % kern_count].append(step)
    return lists


def chosen_step(lists, round_index, kern_pos):
    pick = jnp.int32(-1)
    for k, steps in enumerate(lists):
        if round_index < len(steps):
            pick = jnp.where(kern_pos == k, jnp.int32(steps[round_index]), pick)
    return pick


def gather_split(x, count, pos, kern_count, kern_pos):
    size = x.shape[0]
    lists = partner_lists(count, kern_count)
    slot = jnp.arange(count * size, dtype=jnp.int32) // size
    spread = lambda part: jnp.tile(part, (count, 1, 1, 1))
    collected = jnp.zeros((count * size,) + x.shape[1:], x.dtype)
    for r in range(max(len(steps) for steps in lists)):
        pairs = []
        for k, steps in enumerate(lists):
            if r < len(steps):
                pairs += [((t ^ steps[r]) * kern_count + k, t * kern_count + k) for t in range(count)]
        got = lax.ppermute(x, ("tile", "kern"), pairs)
        step = chosen_step(lists, r, kern_pos)
        source = jnp.where(step >= 0, pos ^ step, -1)
        collected = collected + jnp.where((slot == source)[:, None, None, None], spread(got), 0.0)
    return sum_parts(collected, "kern", kern_count, kern_pos)


def scatter_split(x, count, pos, kern_count, kern_pos, size, between):
    lists = partner_lists(count, kern_count)
    own = lax.dynamic_slice_in_dim(x, pos * size, size, 0)
    total = jnp.where(kern_pos == 0, own, 0.0)
    for r in range(max(len(steps) for steps in lists)):
        pairs = []
        for k, steps in enumerate(lists):
            if r < len(steps):
                pairs += [(t * kern_count + k, (t ^ steps[r]) * kern_count + k) for t in range(count)]
        step = chosen_step(lists, r, kern_pos)
        target = jnp.where(step >= 0, pos ^ step, 0)
        part = lax.dynamic_slice_in_dim(x, target * size, size, 0)
        total = total + lax.ppermute(part, ("tile", "kern"), pairs)
    done, token = between()
    total = total + 0.0 * token
    return done, sum_parts(total, "kern", kern_count, kern_pos)


def on_device(
    tile_mask, master_mask, target, inst_master, inst_shift, kernels, kernel_weight, corner_dose
):
    cos_tab, sin_tab = band_tables()
    scale = 1.0 / (P_SIZE * P_SIZE)
    local_tiles = tile_mask.shape[0]
    local_masters = master_mask.shape[0]
    tile_count = lax.axis_size("tile")
    tile_pos = lax.axis_index("tile")
    kern_count = lax.axis_size("kern")
    kern_pos = lax.axis_index("kern")
    per_dev = local_tiles // kern_count
    first = kern_pos * per_dev
    region_tiles = tile_count * local_tiles
    region_masters = tile_count * local_masters

    with jax.named_scope("master_spectra"):
        own_re, own_im = spectra(master_mask.astype(jnp.float32), cos_tab, sin_tab)
        own = jnp.stack([own_re, own_im], axis=1)
        if xor_partners(tile_count) and xor_partners(kern_count) and tile_count > 2:
            every = gather_split(own, tile_count, tile_pos, kern_count, kern_pos)
            own_part = own
        else:
            every = (gather_all(own, "tile", tile_count, tile_pos),)
            own_part = jnp.zeros_like(own)

    dose = corner_dose[0]
    kerns = kernels[0]
    h_re = kerns[:, 0]
    h_im = kerns[:, 1]
    weights = kernel_weight[0]

    with jax.named_scope("imaging_kernel"):
        count = h_re.shape[0]
        twice = (2.0 * weights)[:, None, None]
        ht_re = jnp.swapaxes(h_re, 1, 2) * twice
        ht_im = jnp.swapaxes(h_im, 1, 2) * twice
        h_cat = jnp.concatenate([ht_re, ht_re, ht_im, -ht_im], axis=-1).reshape(count * B, 128)
        parts = []
        for j in range(per_dev):
            pos = jnp.stack([first + j, tile_pos]).astype(jnp.int32)
            parts.append(
                imaging(
                    pos, inst_master, inst_shift, weights, corner_dose, tile_mask, every, own_part, target,
                    kerns, h_cat,
                )
            )
        comp = jnp.stack(parts)

    with jax.named_scope("gradient_exchange"):
        corner_count = lax.axis_size("corner")
        corner_pos = lax.axis_index("corner")
        if corner_count == 2 and kern_count == 2 and per_dev == 1:
            got = [
                lax.ppermute(comp, ("corner", "kern"), [(i, i ^ step) for i in range(4)])
                for step in (1, 2, 3)
            ]
            mine = comp + got[1]
            other = got[0] + got[2]
            both = jnp.where(kern_pos == 0, jnp.concatenate([mine, other]), jnp.concatenate([other, mine]))
            tile_pixels = lambda: group_pixels(comp, got)
        else:
            comp = sum_all(comp, "corner", corner_count, corner_pos)
            both = gather_all(comp, "kern", kern_count, kern_pos)
            tile_pixels = lambda: pixels(both[:, 0:2], token=True)
        mine_tiles = both[:, 0:2]
        owner_pick = (
            inst_master[:, None] == jnp.arange(region_masters, dtype=jnp.int32)[None, :]
        ).astype(jnp.float32)
        if corner_count == 2 and kern_count == 2 and per_dev == 1:
            pick_mine = jnp.where(kern_pos == 0, owner_pick[0], owner_pick[1])
            pick_other = jnp.where(kern_pos == 0, owner_pick[1], owner_pick[0])
            terms = (
                pick_mine[:, None, None, None] * (comp[0, 2:4] + got[1][0, 2:4])[None]
                + pick_other[:, None, None, None] * (got[0][0, 2:4] + got[2][0, 2:4])[None]
            )
        else:
            terms = jnp.sum(owner_pick[:, :, None, None, None] * both[:, None, 2:4], axis=0)
        if xor_partners(tile_count) and xor_partners(kern_count) and tile_count > 2:
            tile_grad, mine_masters = scatter_split(
                terms, tile_count, tile_pos, kern_count, kern_pos, local_masters,
                tile_pixels,
            )
        else:
            tile_grad = pixels(mine_tiles)
            mine_masters = (scatter_sum(terms, "tile", tile_count, tile_pos, local_masters),)

    with jax.named_scope("pixel_gradients"):
        master_grad = pixels(*mine_masters)
    return (tile_grad, master_grad)


def solution(mesh):
    return jax.shard_map(
        on_device,
        mesh=mesh,
        in_specs=(
            P(("region", "tile"), None, None),
            P(("region", "tile"), None, None),
            P(("region", "tile"), None, None),
            P(("region", "tile")),
            P(("region", "tile"), None),
            P("corner", None, None, None, None),
            P("corner", None),
            P("corner"),
        ),
        out_specs=(P(("region", "tile"), None, None), P(("region", "tile"), None, None)),
        check_vma=False,
    )
```

```python
import functools
import math

import numpy as np
import jax
import jax.numpy as jnp
from jax import lax
from jax.sharding import PartitionSpec as P
from jax.experimental import pallas as pl
from jax.experimental.pallas import tpu as pltpu

P_SIZE = 256
B = 32


precise = lax.Precision.HIGHEST
steepness = 3.0
threshold = 1.0


def band_tables():
    freq = np.arange(B, dtype=np.int64) - B // 2
    pixel = np.arange(P_SIZE, dtype=np.int64)
    angle = (2.0 * math.pi / P_SIZE) * np.mod(freq[:, None] * pixel[None, :], P_SIZE).astype(np.float64)
    return (jnp.asarray(np.cos(angle), jnp.float32), jnp.asarray(-np.sin(angle), jnp.float32))


def phase_ramp(shift):
    freq = jnp.arange(B, dtype=jnp.int32) - B // 2
    total = (
        freq[None, :, None] * shift[:, 0][:, None, None]
        + freq[None, None, :] * shift[:, 1][:, None, None]
    )
    angle = 2.0 * math.pi / P_SIZE * jnp.mod(total, P_SIZE).astype(jnp.float32)
    return (jnp.cos(angle), -jnp.sin(angle))


def spectra(masks, cos_tab, sin_tab):
    rows_re = jnp.einsum("bx,nxy->nby", cos_tab, masks, precision=precise)
    rows_im = jnp.einsum("bx,nxy->nby", sin_tab, masks, precision=precise)
    spec_re = jnp.einsum("nby,cy->nbc", rows_re, cos_tab, precision=precise) - jnp.einsum(
        "nby,cy->nbc", rows_im, sin_tab, precision=precise
    )
    spec_im = jnp.einsum("nby,cy->nbc", rows_re, sin_tab, precision=precise) + jnp.einsum(
        "nby,cy->nbc", rows_im, cos_tab, precision=precise
    )
    return (spec_re, spec_im)


def back_pixels(x_re, x_im, cos_tab, sin_tab):
    half_re = jnp.einsum("bx,nbc->nxc", cos_tab, x_re, precision=precise) + jnp.einsum(
        "bx,nbc->nxc", sin_tab, x_im, precision=precise
    )
    half_im = jnp.einsum("bx,nbc->nxc", cos_tab, x_im, precision=precise) - jnp.einsum(
        "bx,nbc->nxc", sin_tab, x_re, precision=precise
    )
    return jnp.einsum("nxc,cy->nxy", half_re, cos_tab, precision=precise) + jnp.einsum(
        "nxc,cy->nxy", half_im, sin_tab, precision=precise
    )


def dot_full(a, b):
    return jnp.dot(a, b, precision=precise, preferred_element_type=jnp.float32)


def dot_parts(a, b):
    return jnp.dot(a, b, preferred_element_type=jnp.float32)


def split_three(a):
    hi = a.astype(jnp.bfloat16)
    rest = a - hi.astype(jnp.float32)
    mid = rest.astype(jnp.bfloat16)
    lo = (rest - mid.astype(jnp.float32)).astype(jnp.bfloat16)
    return hi, mid, lo


def table_three(table):
    hi = table.astype(jnp.bfloat16)
    rest = table - hi.astype(np.float64)
    mid = rest.astype(jnp.bfloat16)
    lo = (rest - mid.astype(np.float64)).astype(jnp.bfloat16)
    return hi, mid, lo


def imaging_tables():
    freq = np.arange(B, dtype=np.int64) - B // 2
    pixel = np.arange(P_SIZE, dtype=np.int64)
    angle = (2.0 * math.pi / P_SIZE) * np.mod(freq[:, None] * pixel[None, :], P_SIZE).astype(np.float64)
    c_re = np.cos(angle)
    c_im = -np.sin(angle)
    scale = 1.0 / (P_SIZE * P_SIZE)
    right_w = np.zeros((128, 2 * P_SIZE))
    right_w[:B, :P_SIZE] = c_re
    right_w[:B, P_SIZE:] = -c_im
    right_w[B : 2 * B, :P_SIZE] = c_im
    right_w[B : 2 * B, P_SIZE:] = c_re
    left_a = np.zeros((P_SIZE, 128))
    left_a[:, :B] = c_re.T * scale
    left_a[:, B : 2 * B] = -c_im.T * scale
    right_b = np.zeros((2 * P_SIZE, 128))
    right_b[:P_SIZE, :B] = c_re.T * scale
    right_b[:P_SIZE, B : 2 * B] = c_im.T * scale
    right_b[P_SIZE:, :B] = -c_im.T * scale
    right_b[P_SIZE:, B : 2 * B] = c_re.T * scale
    ct_re = c_re.T
    ct_im = c_im.T
    right_c = np.zeros((2 * P_SIZE, 128))
    for col, (top, bottom) in enumerate(
        ((ct_re, -ct_im), (ct_im, ct_re), (ct_im, ct_re), (ct_re, -ct_im))
    ):
        right_c[:P_SIZE, col * B : (col + 1) * B] = top
        right_c[P_SIZE:, col * B : (col + 1) * B] = bottom
    a_hi, a_mid, a_lo = table_three(left_a[:, : 2 * B])
    left_three = np.concatenate([a_hi, a_hi, a_mid, a_hi, a_lo, a_mid], axis=1)
    b_hi, b_mid, b_lo = table_three(right_b)
    right_hm = np.concatenate([b_hi, b_mid], axis=1)
    right_lh = np.concatenate([b_lo, b_hi], axis=0)
    parts_re = table_three(c_re)
    parts_im = table_three(c_im)
    rows_three = np.concatenate(
        [np.concatenate(parts_re, axis=1), np.concatenate(parts_im, axis=1)], axis=0
    )
    cols_re = np.concatenate(table_three(c_re.T), axis=0)
    cols_im = np.concatenate(table_three(c_im.T), axis=0)
    plain = (c_re, c_im, c_re.T, c_im.T, right_w[:B], right_w[B : 2 * B], right_c)
    out = [jnp.asarray(table, jnp.float32) for table in plain]
    bf = (left_three, right_hm, right_lh, rows_three, cols_re, cols_im)
    return out + [jnp.asarray(table) for table in bf]


def imaging_body(
    pos_ref, im_ref, sh_ref, w_ref, dose_ref, mask_ref, ev_ref, ev2_ref, own_ref, goal_ref, h_ref, hc_ref,
    c_re_ref, c_im_ref, ct_re_ref, ct_im_ref, rw_top, rw_bot, rc_ref, la_ref, rhm_ref, rlh_ref, rows_ref, cre_ref, cim_ref,
    slots_ref, f_buf, i_buf, u_buf, w_buf, xr_buf, xi_buf,
):
    count = f_buf.shape[0]
    pos = pos_ref[0]
    master = im_ref[pos]
    pick0 = (lax.broadcasted_iota(jnp.int32, (P_SIZE, 128), 0) == sh_ref[pos, 0]).astype(jnp.bfloat16)
    pick1 = (lax.broadcasted_iota(jnp.int32, (8, P_SIZE), 1) == sh_ref[pos, 1]).astype(jnp.bfloat16)
    e0 = dot_parts(rows_ref[...], jnp.concatenate([pick0, pick0, pick0], axis=0))
    e0_re = e0[:B, 0:1]
    e0_im = e0[B:, 0:1]
    pick1 = jnp.concatenate([pick1, pick1, pick1], axis=1)
    e1_re = dot_parts(pick1, cre_ref[...])[0:1, :]
    e1_im = dot_parts(pick1, cim_ref[...])[0:1, :]
    ph_re = e0_re * e1_re - e0_im * e1_im
    ph_im = e0_re * e1_im + e0_im * e1_re
    local_masters = own_ref.shape[0]
    is_own = master // local_masters == pos_ref[1]
    m_re = ev_ref[master, 0] + ev2_ref[master, 0] + jnp.where(is_own, own_ref[master % local_masters, 0], 0.0)
    m_im = ev_ref[master, 1] + ev2_ref[master, 1] + jnp.where(is_own, own_ref[master % local_masters, 1], 0.0)
    mask = mask_ref[pos]
    rows = dot_parts(rows_ref[...], jnp.concatenate([mask, mask, mask], axis=0))
    t_one = dot_full(rows, ct_re_ref[...])
    t_two = dot_full(rows, ct_im_ref[...])
    s_re = t_one[:B] - t_two[B:] + (ph_re * m_re - ph_im * m_im)
    s_im = t_two[:B] + t_one[B:] + (ph_re * m_im + ph_im * m_re)
    i_buf[...] = jnp.zeros(i_buf.shape, jnp.float32)

    def spectrum(k, carry):
        h_re = h_ref[k, 0]
        h_im = h_ref[k, 1]
        rows = pl.ds(pl.multiple_of(k * B, B), B)
        xr_buf[rows, :] = h_re * s_re - h_im * s_im
        xi_buf[rows, :] = h_re * s_im + h_im * s_re
        return carry

    lax.fori_loop(0, count, spectrum, 0, unroll=True)
    w_buf[...] = dot_full(xr_buf[...], rw_top[...]) + dot_full(xi_buf[...], rw_bot[...])

    def forward(k, carry):
        rows = w_buf[pl.ds(pl.multiple_of(k * B, B), B), :]
        swap = jnp.concatenate([-rows[:, P_SIZE:], rows[:, :P_SIZE]], axis=1)
        s_hi, s_mid, s_lo = split_three(jnp.concatenate([rows, swap], axis=0))
        stacked = jnp.concatenate([s_hi, s_mid, s_hi, s_lo, s_hi, s_mid], axis=0)
        field = dot_parts(la_ref[...], stacked)
        f_buf[k] = field
        power = field * field
        i_buf[...] += w_ref[k] * (power[:, :P_SIZE] + power[:, P_SIZE:])
        return carry

    lax.fori_loop(0, count, forward, 0, unroll=4)
    dose = dose_ref[0]
    resist = 1.0 / (1.0 + jnp.exp(-(steepness * (dose * i_buf[...] - threshold))))
    goal = goal_ref[pos].astype(jnp.float32)
    i_buf[...] = 2.0 * (resist - goal) * resist * (1.0 - resist) * steepness * dose

    def backward(k, carry):
        sens = i_buf[...]
        weighted = f_buf[k] * jnp.concatenate([sens, sens], axis=1)
        q_hi, q_mid, q_lo = split_three(weighted)
        first = dot_parts(q_hi, rhm_ref[...]) + dot_parts(q_mid, rhm_ref[...])
        rest = dot_parts(jnp.concatenate([q_hi, q_lo], axis=1), rlh_ref[...])
        half = first[:, :128] + first[:, 128:] + rest
        flip = half.T
        u_buf[pl.ds(pl.multiple_of(k * B, B), B), :] = jnp.concatenate([flip[:B], flip[B : 2 * B]], axis=1)
        return carry

    lax.fori_loop(0, count, backward, 0, unroll=4)
    out = dot_full(u_buf[...], rc_ref[...])
    acc = jnp.sum((hc_ref[...] * out).reshape(count, B, 128), axis=0)
    flip = jnp.concatenate([acc, jnp.zeros((128 - B, 128), jnp.float32)], axis=0).T
    g_re = flip[0:B, 0:B] + flip[2 * B : 3 * B, 0:B]
    g_im = flip[B : 2 * B, 0:B] + flip[3 * B : 4 * B, 0:B]
    slots_ref[0] = g_re
    slots_ref[1] = g_im
    slots_ref[2] = ph_re * g_re + ph_im * g_im
    slots_ref[3] = ph_re * g_im - ph_im * g_re


def imaging(pos, inst_master, inst_shift, weights, dose, tile_mask, every, own, target, kerns, h_cat):
    if len(every) == 1:
        every = (every[0], jnp.zeros_like(every[0]))
    count = weights.shape[0]
    tables = imaging_tables()
    vmem = pl.BlockSpec(memory_space=pltpu.VMEM)
    smem = pl.BlockSpec(memory_space=pltpu.SMEM)
    return pl.pallas_call(
        imaging_body,
        out_shape=jax.ShapeDtypeStruct((4, B, B), jnp.float32),
        in_specs=[smem] * 5 + [vmem] * 7 + [vmem] * len(tables),
        out_specs=vmem,
        scratch_shapes=[
            pltpu.VMEM((count, P_SIZE, 2 * P_SIZE), jnp.float32),
            pltpu.VMEM((P_SIZE, P_SIZE), jnp.float32),
            pltpu.VMEM((count * B, 2 * P_SIZE), jnp.float32),
            pltpu.VMEM((count * B, 2 * P_SIZE), jnp.float32),
            pltpu.VMEM((count * B, B), jnp.float32),
            pltpu.VMEM((count * B, B), jnp.float32),
        ],
    )(pos, inst_master, inst_shift, weights, dose, tile_mask, *every, own, target, kerns, h_cat, *tables)


def pixel_body(*refs, passes):
    if passes:
        out_ref, token_ref = refs[-2:]
        token_ref[...] = jnp.zeros(token_ref.shape, jnp.float32)
        refs = refs[:-2] + (out_ref,)
    out_ref = refs[-1]
    c_re_ref, c_im_ref, left_ref = refs[-4:-1]
    parts = refs[:-4]
    for n in range(out_ref.shape[0]):
        x_re = sum(part[n, 0] for part in parts)
        x_im = sum(part[n, 1] for part in parts)
        x_both = jnp.concatenate([x_re, x_im], axis=0)
        p_re = dot_full(x_both, c_re_ref[...])
        p_im = dot_full(x_both, c_im_ref[...])
        y_re = p_re[:B] + p_im[B:]
        y_im = p_re[B:] - p_im[:B]
        y_hi, y_mid, y_lo = split_three(jnp.concatenate([y_re, y_im], axis=0))
        stacked = jnp.concatenate([y_hi, y_mid, y_hi, y_lo, y_hi, y_mid], axis=0)
        out_ref[n] = dot_parts(left_ref[...], stacked)


def group_pixel_body(comp_ref, g0_ref, g1_ref, g2_ref, c_re_ref, c_im_ref, left_ref, out_ref, token_ref):
    token_ref[...] = jnp.zeros(token_ref.shape, jnp.float32)
    own = lax.axis_index("kern")
    for n in range(out_ref.shape[0]):
        mine = n == own
        planes = []
        for c in range(2):
            planes.append(
                jnp.where(mine, comp_ref[0, c] + g1_ref[0, c], g0_ref[0, c] + g2_ref[0, c])
            )
        x_both = jnp.concatenate(planes, axis=0)
        p_re = dot_full(x_both, c_re_ref[...])
        p_im = dot_full(x_both, c_im_ref[...])
        y_re = p_re[:B] + p_im[B:]
        y_im = p_re[B:] - p_im[:B]
        y_hi, y_mid, y_lo = split_three(jnp.concatenate([y_re, y_im], axis=0))
        stacked = jnp.concatenate([y_hi, y_mid, y_hi, y_lo, y_hi, y_mid], axis=0)
        out_ref[n] = dot_parts(left_ref[...], stacked)


def group_pixels(comp, got):
    freq = np.arange(B, dtype=np.int64) - B // 2
    pixel = np.arange(P_SIZE, dtype=np.int64)
    angle = (2.0 * math.pi / P_SIZE) * np.mod(freq[:, None] * pixel[None, :], P_SIZE).astype(np.float64)
    c_re = np.cos(angle)
    c_im = -np.sin(angle)
    a_hi, a_mid, a_lo = table_three(np.concatenate([c_re.T, c_im.T], axis=1))
    left = np.concatenate([a_hi, a_hi, a_mid, a_hi, a_lo, a_mid], axis=1)
    tables = [jnp.asarray(c_re, jnp.float32), jnp.asarray(c_im, jnp.float32), jnp.asarray(left)]
    vmem = pl.BlockSpec(memory_space=pltpu.VMEM)
    shape = jax.ShapeDtypeStruct((2, P_SIZE, P_SIZE), jnp.float32)
    return pl.pallas_call(
        group_pixel_body,
        out_shape=(shape, jax.ShapeDtypeStruct((1, 1, 1, 1), jnp.float32)),
        in_specs=[vmem] * 7,
        out_specs=(vmem, vmem),
    )(comp, *got, *tables)


def pixels(*parts, token=False):
    freq = np.arange(B, dtype=np.int64) - B // 2
    pixel = np.arange(P_SIZE, dtype=np.int64)
    angle = (2.0 * math.pi / P_SIZE) * np.mod(freq[:, None] * pixel[None, :], P_SIZE).astype(np.float64)
    c_re = np.cos(angle)
    c_im = -np.sin(angle)
    a_hi, a_mid, a_lo = table_three(np.concatenate([c_re.T, c_im.T], axis=1))
    left = np.concatenate([a_hi, a_hi, a_mid, a_hi, a_lo, a_mid], axis=1)
    tables = [jnp.asarray(c_re, jnp.float32), jnp.asarray(c_im, jnp.float32), jnp.asarray(left)]
    vmem = pl.BlockSpec(memory_space=pltpu.VMEM)
    shape = jax.ShapeDtypeStruct((parts[0].shape[0], P_SIZE, P_SIZE), jnp.float32)
    if not token:
        return pl.pallas_call(
            functools.partial(pixel_body, passes=False),
            out_shape=shape,
            in_specs=[vmem] * (len(parts) + 3),
            out_specs=vmem,
        )(*parts, *tables)
    return pl.pallas_call(
        functools.partial(pixel_body, passes=True),
        out_shape=(shape, jax.ShapeDtypeStruct((1, 1, 1, 1), jnp.float32)),
        in_specs=[vmem] * (len(parts) + 3),
        out_specs=(vmem, vmem),
    )(*parts, *tables)


def xor_partners(count):
    return count & (count - 1) == 0 and count <= 8


def gather_all(x, axis, count, pos):
    if not xor_partners(count):
        return lax.all_gather(x, axis, axis=0, tiled=True)
    size = x.shape[0]
    slot = jnp.arange(count * size, dtype=jnp.int32) // size
    total = jnp.where((slot == pos)[:, None, None, None], jnp.tile(x, (count, 1, 1, 1)), 0.0)
    for step in range(1, count):
        got = lax.ppermute(x, axis, [(i, i ^ step) for i in range(count)])
        hit = (slot == (pos ^ step))[:, None, None, None]
        total = total + jnp.where(hit, jnp.tile(got, (count, 1, 1, 1)), 0.0)
    return total


def sum_all(x, axis, count, pos):
    if not xor_partners(count):
        return lax.psum(x, axis)
    step = 1
    while step < count:
        x = x + lax.ppermute(x, axis, [(i, i ^ step) for i in range(count)])
        step *= 2
    return x


def sum_parts(x, axis, count, pos):
    if count == 2:
        return (x, lax.ppermute(x, axis, [(0, 1), (1, 0)]))
    return (sum_all(x, axis, count, pos),)


def scatter_sum(x, axis, count, pos, size):
    if not xor_partners(count):
        return lax.psum_scatter(x, axis, scatter_dimension=0, tiled=True)
    total = lax.dynamic_slice_in_dim(x, pos * size, size, 0)
    for step in range(1, count):
        part = lax.dynamic_slice_in_dim(x, (pos ^ step) * size, size, 0)
        total = total + lax.ppermute(part, axis, [(i, i ^ step) for i in range(count)])
    return total


def partner_lists(count, kern_count):
    lists = [[] for _ in range(kern_count)]
    for step in range(1, count):
        lists[step % kern_count].append(step)
    return lists


def chosen_step(lists, round_index, kern_pos):
    pick = jnp.int32(-1)
    for k, steps in enumerate(lists):
        if round_index < len(steps):
            pick = jnp.where(kern_pos == k, jnp.int32(steps[round_index]), pick)
    return pick


def gather_split(x, count, pos, kern_count, kern_pos):
    size = x.shape[0]
    lists = partner_lists(count, kern_count)
    slot = jnp.arange(count * size, dtype=jnp.int32) // size
    spread = lambda part: jnp.tile(part, (count, 1, 1, 1))
    collected = jnp.zeros((count * size,) + x.shape[1:], x.dtype)
    for r in range(max(len(steps) for steps in lists)):
        pairs = []
        for k, steps in enumerate(lists):
            if r < len(steps):
                pairs += [((t ^ steps[r]) * kern_count + k, t * kern_count + k) for t in range(count)]
        got = lax.ppermute(x, ("tile", "kern"), pairs)
        step = chosen_step(lists, r, kern_pos)
        source = jnp.where(step >= 0, pos ^ step, -1)
        collected = collected + jnp.where((slot == source)[:, None, None, None], spread(got), 0.0)
    return sum_parts(collected, "kern", kern_count, kern_pos)


def scatter_split(x, count, pos, kern_count, kern_pos, size, between):
    lists = partner_lists(count, kern_count)
    own = lax.dynamic_slice_in_dim(x, pos * size, size, 0)
    total = jnp.where(kern_pos == 0, own, 0.0)
    for r in range(max(len(steps) for steps in lists)):
        pairs = []
        for k, steps in enumerate(lists):
            if r < len(steps):
                pairs += [(t * kern_count + k, (t ^ steps[r]) * kern_count + k) for t in range(count)]
        step = chosen_step(lists, r, kern_pos)
        target = jnp.where(step >= 0, pos ^ step, 0)
        part = lax.dynamic_slice_in_dim(x, target * size, size, 0)
        total = total + lax.ppermute(part, ("tile", "kern"), pairs)
    done, token = between()
    total = total + 0.0 * token
    return done, sum_parts(total, "kern", kern_count, kern_pos)


def on_device(
    tile_mask, master_mask, target, inst_master, inst_shift, kernels, kernel_weight, corner_dose
):
    cos_tab, sin_tab = band_tables()
    scale = 1.0 / (P_SIZE * P_SIZE)
    local_tiles = tile_mask.shape[0]
    local_masters = master_mask.shape[0]
    tile_count = lax.axis_size("tile")
    tile_pos = lax.axis_index("tile")
    kern_count = lax.axis_size("kern")
    kern_pos = lax.axis_index("kern")
    per_dev = local_tiles // kern_count
    first = kern_pos * per_dev
    region_tiles = tile_count * local_tiles
    region_masters = tile_count * local_masters

    with jax.named_scope("master_spectra"):
        own_re, own_im = spectra(master_mask.astype(jnp.float32), cos_tab, sin_tab)
        own = jnp.stack([own_re, own_im], axis=1)
        if xor_partners(tile_count) and xor_partners(kern_count) and tile_count > 2:
            every = gather_split(own, tile_count, tile_pos, kern_count, kern_pos)
            own_part = own
        else:
            every = (gather_all(own, "tile", tile_count, tile_pos),)
            own_part = jnp.zeros_like(own)

    dose = corner_dose[0]
    kerns = kernels[0]
    h_re = kerns[:, 0]
    h_im = kerns[:, 1]
    weights = kernel_weight[0]

    with jax.named_scope("imaging_kernel"):
        count = h_re.shape[0]
        twice = (2.0 * weights)[:, None, None]
        ht_re = jnp.swapaxes(h_re, 1, 2) * twice
        ht_im = jnp.swapaxes(h_im, 1, 2) * twice
        h_cat = jnp.concatenate([ht_re, ht_re, ht_im, -ht_im], axis=-1).reshape(count * B, 128)
        parts = []
        for j in range(per_dev):
            pos = jnp.stack([first + j, tile_pos]).astype(jnp.int32)
            parts.append(
                imaging(
                    pos, inst_master, inst_shift, weights, corner_dose, tile_mask, every, own_part, target,
                    kerns, h_cat,
                )
            )
        comp = jnp.stack(parts)

    with jax.named_scope("gradient_exchange"):
        corner_count = lax.axis_size("corner")
        corner_pos = lax.axis_index("corner")
        if corner_count == 2 and kern_count == 2 and per_dev == 1:
            got = [
                lax.ppermute(comp, ("corner", "kern"), [(i, i ^ step) for i in range(4)])
                for step in (1, 2, 3)
            ]
            mine = comp + got[1]
            other = got[0] + got[2]
            both = jnp.where(kern_pos == 0, jnp.concatenate([mine, other]), jnp.concatenate([other, mine]))
            tile_pixels = lambda: group_pixels(comp, got)
        else:
            comp = sum_all(comp, "corner", corner_count, corner_pos)
            both = gather_all(comp, "kern", kern_count, kern_pos)
            tile_pixels = lambda: pixels(both[:, 0:2], token=True)
        mine_tiles = both[:, 0:2]
        owner_pick = (
            inst_master[:, None] == jnp.arange(region_masters, dtype=jnp.int32)[None, :]
        ).astype(jnp.float32)
        if corner_count == 2 and kern_count == 2 and per_dev == 1:
            pick_mine = jnp.where(kern_pos == 0, owner_pick[0], owner_pick[1])
            pick_other = jnp.where(kern_pos == 0, owner_pick[1], owner_pick[0])
            terms = (
                pick_mine[:, None, None, None] * (comp[0, 2:4] + got[1][0, 2:4])[None]
                + pick_other[:, None, None, None] * (got[0][0, 2:4] + got[2][0, 2:4])[None]
            )
        else:
            terms = jnp.sum(owner_pick[:, :, None, None, None] * both[:, None, 2:4], axis=0)
        if xor_partners(tile_count) and xor_partners(kern_count) and tile_count > 2:
            tile_grad, mine_masters = scatter_split(
                terms, tile_count, tile_pos, kern_count, kern_pos, local_masters,
                tile_pixels,
            )
        else:
            tile_grad = pixels(mine_tiles)
            mine_masters = (scatter_sum(terms, "tile", tile_count, tile_pos, local_masters),)

    with jax.named_scope("pixel_gradients"):
        master_grad = pixels(*mine_masters)
    return (tile_grad, master_grad)


def solution(mesh):
    return jax.shard_map(
        on_device,
        mesh=mesh,
        in_specs=(
            P(("region", "tile"), None, None),
            P(("region", "tile"), None, None),
            P(("region", "tile"), None, None),
            P(("region", "tile")),
            P(("region", "tile"), None),
            P("corner", None, None, None, None),
            P("corner", None),
            P("corner"),
        ),
        out_specs=(P(("region", "tile"), None, None), P(("region", "tile"), None, None)),
        check_vma=False,
    )
```

```python
import functools
import math

import numpy as np
import jax
import jax.numpy as jnp
from jax import lax
from jax.sharding import PartitionSpec as P
from jax.experimental import pallas as pl
from jax.experimental.pallas import tpu as pltpu

P_SIZE = 256
B = 32


precise = lax.Precision.HIGHEST
steepness = 3.0
threshold = 1.0


def band_tables():
    freq = np.arange(B, dtype=np.int64) - B // 2
    pixel = np.arange(P_SIZE, dtype=np.int64)
    angle = (2.0 * math.pi / P_SIZE) * np.mod(freq[:, None] * pixel[None, :], P_SIZE).astype(np.float64)
    return (jnp.asarray(np.cos(angle), jnp.float32), jnp.asarray(-np.sin(angle), jnp.float32))


def phase_ramp(shift):
    freq = jnp.arange(B, dtype=jnp.int32) - B // 2
    total = (
        freq[None, :, None] * shift[:, 0][:, None, None]
        + freq[None, None, :] * shift[:, 1][:, None, None]
    )
    angle = 2.0 * math.pi / P_SIZE * jnp.mod(total, P_SIZE).astype(jnp.float32)
    return (jnp.cos(angle), -jnp.sin(angle))


def spectra(masks, cos_tab, sin_tab):
    rows_re = jnp.einsum("bx,nxy->nby", cos_tab, masks, precision=precise)
    rows_im = jnp.einsum("bx,nxy->nby", sin_tab, masks, precision=precise)
    spec_re = jnp.einsum("nby,cy->nbc", rows_re, cos_tab, precision=precise) - jnp.einsum(
        "nby,cy->nbc", rows_im, sin_tab, precision=precise
    )
    spec_im = jnp.einsum("nby,cy->nbc", rows_re, sin_tab, precision=precise) + jnp.einsum(
        "nby,cy->nbc", rows_im, cos_tab, precision=precise
    )
    return (spec_re, spec_im)


def back_pixels(x_re, x_im, cos_tab, sin_tab):
    half_re = jnp.einsum("bx,nbc->nxc", cos_tab, x_re, precision=precise) + jnp.einsum(
        "bx,nbc->nxc", sin_tab, x_im, precision=precise
    )
    half_im = jnp.einsum("bx,nbc->nxc", cos_tab, x_im, precision=precise) - jnp.einsum(
        "bx,nbc->nxc", sin_tab, x_re, precision=precise
    )
    return jnp.einsum("nxc,cy->nxy", half_re, cos_tab, precision=precise) + jnp.einsum(
        "nxc,cy->nxy", half_im, sin_tab, precision=precise
    )


def dot_full(a, b):
    return jnp.dot(a, b, precision=precise, preferred_element_type=jnp.float32)


def dot_parts(a, b):
    return jnp.dot(a, b, preferred_element_type=jnp.float32)


def split_three(a):
    hi = a.astype(jnp.bfloat16)
    rest = a - hi.astype(jnp.float32)
    mid = rest.astype(jnp.bfloat16)
    lo = (rest - mid.astype(jnp.float32)).astype(jnp.bfloat16)
    return hi, mid, lo


def table_three(table):
    hi = table.astype(jnp.bfloat16)
    rest = table - hi.astype(np.float64)
    mid = rest.astype(jnp.bfloat16)
    lo = (rest - mid.astype(np.float64)).astype(jnp.bfloat16)
    return hi, mid, lo


def imaging_tables():
    freq = np.arange(B, dtype=np.int64) - B // 2
    pixel = np.arange(P_SIZE, dtype=np.int64)
    angle = (2.0 * math.pi / P_SIZE) * np.mod(freq[:, None] * pixel[None, :], P_SIZE).astype(np.float64)
    c_re = np.cos(angle)
    c_im = -np.sin(angle)
    scale = 1.0 / (P_SIZE * P_SIZE)
    right_w = np.zeros((128, 2 * P_SIZE))
    right_w[:B, :P_SIZE] = c_re
    right_w[:B, P_SIZE:] = -c_im
    right_w[B : 2 * B, :P_SIZE] = c_im
    right_w[B : 2 * B, P_SIZE:] = c_re
    left_a = np.zeros((P_SIZE, 128))
    left_a[:, :B] = c_re.T * scale
    left_a[:, B : 2 * B] = -c_im.T * scale
    right_b = np.zeros((2 * P_SIZE, 128))
    right_b[:P_SIZE, :B] = c_re.T * scale
    right_b[:P_SIZE, B : 2 * B] = c_im.T * scale
    right_b[P_SIZE:, :B] = -c_im.T * scale
    right_b[P_SIZE:, B : 2 * B] = c_re.T * scale
    ct_re = c_re.T
    ct_im = c_im.T
    right_c = np.zeros((2 * P_SIZE, 128))
    for col, (top, bottom) in enumerate(
        ((ct_re, -ct_im), (ct_im, ct_re), (ct_im, ct_re), (ct_re, -ct_im))
    ):
        right_c[:P_SIZE, col * B : (col + 1) * B] = top
        right_c[P_SIZE:, col * B : (col + 1) * B] = bottom
    a_hi, a_mid, a_lo = table_three(left_a[:, : 2 * B])
    left_three = np.concatenate([a_hi, a_hi, a_mid, a_hi, a_lo, a_mid], axis=1)
    b_hi, b_mid, b_lo = table_three(right_b)
    right_hm = np.concatenate([b_hi, b_mid], axis=1)
    right_lh = np.concatenate([b_lo, b_hi], axis=0)
    parts_re = table_three(c_re)
    parts_im = table_three(c_im)
    rows_three = np.concatenate(
        [np.concatenate(parts_re, axis=1), np.concatenate(parts_im, axis=1)], axis=0
    )
    cols_re = np.concatenate(table_three(c_re.T), axis=0)
    cols_im = np.concatenate(table_three(c_im.T), axis=0)
    plain = (c_re, c_im, c_re.T, c_im.T, right_w[:B], right_w[B : 2 * B], right_c)
    out = [jnp.asarray(table, jnp.float32) for table in plain]
    bf = (left_three, right_hm, right_lh, rows_three, cols_re, cols_im)
    return out + [jnp.asarray(table) for table in bf]


def imaging_body(
    pos_ref, im_ref, sh_ref, w_ref, dose_ref, mask_ref, ev_ref, ev2_ref, own_ref, goal_ref, h_ref, hc_ref,
    c_re_ref, c_im_ref, ct_re_ref, ct_im_ref, rw_top, rw_bot, rc_ref, la_ref, rhm_ref, rlh_ref, rows_ref, cre_ref, cim_ref,
    slots_ref, f_buf, i_buf, u_buf, w_buf, xr_buf, xi_buf,
):
    count = f_buf.shape[0]
    pos = pos_ref[0]
    master = im_ref[pos]
    pick0 = (lax.broadcasted_iota(jnp.int32, (P_SIZE, 128), 0) == sh_ref[pos, 0]).astype(jnp.bfloat16)
    pick1 = (lax.broadcasted_iota(jnp.int32, (8, P_SIZE), 1) == sh_ref[pos, 1]).astype(jnp.bfloat16)
    e0 = dot_parts(rows_ref[...], jnp.concatenate([pick0, pick0, pick0], axis=0))
    e0_re = e0[:B, 0:1]
    e0_im = e0[B:, 0:1]
    pick1 = jnp.concatenate([pick1, pick1, pick1], axis=1)
    e1_re = dot_parts(pick1, cre_ref[...])[0:1, :]
    e1_im = dot_parts(pick1, cim_ref[...])[0:1, :]
    ph_re = e0_re * e1_re - e0_im * e1_im
    ph_im = e0_re * e1_im + e0_im * e1_re
    local_masters = own_ref.shape[0]
    is_own = master // local_masters == pos_ref[1]
    m_re = ev_ref[master, 0] + ev2_ref[master, 0] + jnp.where(is_own, own_ref[master % local_masters, 0], 0.0)
    m_im = ev_ref[master, 1] + ev2_ref[master, 1] + jnp.where(is_own, own_ref[master % local_masters, 1], 0.0)
    mask = mask_ref[pos]
    rows = dot_parts(rows_ref[...], jnp.concatenate([mask, mask, mask], axis=0))
    t_one = dot_full(rows, ct_re_ref[...])
    t_two = dot_full(rows, ct_im_ref[...])
    s_re = t_one[:B] - t_two[B:] + (ph_re * m_re - ph_im * m_im)
    s_im = t_two[:B] + t_one[B:] + (ph_re * m_im + ph_im * m_re)
    i_buf[...] = jnp.zeros(i_buf.shape, jnp.float32)

    def spectrum(k, carry):
        h_re = h_ref[k, 0]
        h_im = h_ref[k, 1]
        rows = pl.ds(pl.multiple_of(k * B, B), B)
        xr_buf[rows, :] = h_re * s_re - h_im * s_im
        xi_buf[rows, :] = h_re * s_im + h_im * s_re
        return carry

    lax.fori_loop(0, count, spectrum, 0, unroll=True)
    w_buf[...] = dot_full(xr_buf[...], rw_top[...]) + dot_full(xi_buf[...], rw_bot[...])

    def forward(k, carry):
        rows = w_buf[pl.ds(pl.multiple_of(k * B, B), B), :]
        swap = jnp.concatenate([-rows[:, P_SIZE:], rows[:, :P_SIZE]], axis=1)
        s_hi, s_mid, s_lo = split_three(jnp.concatenate([rows, swap], axis=0))
        stacked = jnp.concatenate([s_hi, s_mid, s_hi, s_lo, s_hi, s_mid], axis=0)
        field = dot_parts(la_ref[...], stacked)
        f_buf[k] = field
        power = field * field
        i_buf[...] += w_ref[k] * (power[:, :P_SIZE] + power[:, P_SIZE:])
        return carry

    lax.fori_loop(0, count, forward, 0, unroll=True)
    dose = dose_ref[0]
    resist = 1.0 / (1.0 + jnp.exp(-(steepness * (dose * i_buf[...] - threshold))))
    goal = goal_ref[pos].astype(jnp.float32)
    i_buf[...] = 2.0 * (resist - goal) * resist * (1.0 - resist) * steepness * dose

    def backward(k, carry):
        sens = i_buf[...]
        weighted = f_buf[k] * jnp.concatenate([sens, sens], axis=1)
        q_hi, q_mid, q_lo = split_three(weighted)
        first = dot_parts(q_hi, rhm_ref[...]) + dot_parts(q_mid, rhm_ref[...])
        rest = dot_parts(jnp.concatenate([q_hi, q_lo], axis=1), rlh_ref[...])
        half = first[:, :128] + first[:, 128:] + rest
        flip = half.T
        u_buf[pl.ds(pl.multiple_of(k * B, B), B), :] = jnp.concatenate([flip[:B], flip[B : 2 * B]], axis=1)
        return carry

    lax.fori_loop(0, count, backward, 0, unroll=True)
    out = dot_full(u_buf[...], rc_ref[...])
    acc = jnp.sum((hc_ref[...] * out).reshape(count, B, 128), axis=0)
    flip = jnp.concatenate([acc, jnp.zeros((128 - B, 128), jnp.float32)], axis=0).T
    g_re = flip[0:B, 0:B] + flip[2 * B : 3 * B, 0:B]
    g_im = flip[B : 2 * B, 0:B] + flip[3 * B : 4 * B, 0:B]
    slots_ref[0] = g_re
    slots_ref[1] = g_im
    slots_ref[2] = ph_re * g_re + ph_im * g_im
    slots_ref[3] = ph_re * g_im - ph_im * g_re


def imaging(pos, inst_master, inst_shift, weights, dose, tile_mask, every, own, target, kerns, h_cat):
    if len(every) == 1:
        every = (every[0], jnp.zeros_like(every[0]))
    count = weights.shape[0]
    tables = imaging_tables()
    vmem = pl.BlockSpec(memory_space=pltpu.VMEM)
    smem = pl.BlockSpec(memory_space=pltpu.SMEM)
    return pl.pallas_call(
        imaging_body,
        out_shape=jax.ShapeDtypeStruct((4, B, B), jnp.float32),
        in_specs=[smem] * 5 + [vmem] * 7 + [vmem] * len(tables),
        out_specs=vmem,
        scratch_shapes=[
            pltpu.VMEM((count, P_SIZE, 2 * P_SIZE), jnp.float32),
            pltpu.VMEM((P_SIZE, P_SIZE), jnp.float32),
            pltpu.VMEM((count * B, 2 * P_SIZE), jnp.float32),
            pltpu.VMEM((count * B, 2 * P_SIZE), jnp.float32),
            pltpu.VMEM((count * B, B), jnp.float32),
            pltpu.VMEM((count * B, B), jnp.float32),
        ],
    )(pos, inst_master, inst_shift, weights, dose, tile_mask, *every, own, target, kerns, h_cat, *tables)


def pixel_body(*refs, passes):
    if passes:
        out_ref, token_ref = refs[-2:]
        token_ref[...] = jnp.zeros(token_ref.shape, jnp.float32)
        refs = refs[:-2] + (out_ref,)
    out_ref = refs[-1]
    c_re_ref, c_im_ref, left_ref = refs[-4:-1]
    parts = refs[:-4]
    for n in range(out_ref.shape[0]):
        x_re = sum(part[n, 0] for part in parts)
        x_im = sum(part[n, 1] for part in parts)
        x_both = jnp.concatenate([x_re, x_im], axis=0)
        p_re = dot_full(x_both, c_re_ref[...])
        p_im = dot_full(x_both, c_im_ref[...])
        y_re = p_re[:B] + p_im[B:]
        y_im = p_re[B:] - p_im[:B]
        y_hi, y_mid, y_lo = split_three(jnp.concatenate([y_re, y_im], axis=0))
        stacked = jnp.concatenate([y_hi, y_mid, y_hi, y_lo, y_hi, y_mid], axis=0)
        out_ref[n] = dot_parts(left_ref[...], stacked)


def group_pixel_body(comp_ref, g0_ref, g1_ref, g2_ref, c_re_ref, c_im_ref, left_ref, out_ref, token_ref):
    token_ref[...] = jnp.zeros(token_ref.shape, jnp.float32)
    own = lax.axis_index("kern")
    for n in range(out_ref.shape[0]):
        mine = n == own
        planes = []
        for c in range(2):
            planes.append(
                jnp.where(mine, comp_ref[0, c] + g1_ref[0, c], g0_ref[0, c] + g2_ref[0, c])
            )
        x_both = jnp.concatenate(planes, axis=0)
        p_re = dot_full(x_both, c_re_ref[...])
        p_im = dot_full(x_both, c_im_ref[...])
        y_re = p_re[:B] + p_im[B:]
        y_im = p_re[B:] - p_im[:B]
        y_hi, y_mid, y_lo = split_three(jnp.concatenate([y_re, y_im], axis=0))
        stacked = jnp.concatenate([y_hi, y_mid, y_hi, y_lo, y_hi, y_mid], axis=0)
        out_ref[n] = dot_parts(left_ref[...], stacked)


def group_pixels(comp, got):
    freq = np.arange(B, dtype=np.int64) - B // 2
    pixel = np.arange(P_SIZE, dtype=np.int64)
    angle = (2.0 * math.pi / P_SIZE) * np.mod(freq[:, None] * pixel[None, :], P_SIZE).astype(np.float64)
    c_re = np.cos(angle)
    c_im = -np.sin(angle)
    a_hi, a_mid, a_lo = table_three(np.concatenate([c_re.T, c_im.T], axis=1))
    left = np.concatenate([a_hi, a_hi, a_mid, a_hi, a_lo, a_mid], axis=1)
    tables = [jnp.asarray(c_re, jnp.float32), jnp.asarray(c_im, jnp.float32), jnp.asarray(left)]
    vmem = pl.BlockSpec(memory_space=pltpu.VMEM)
    shape = jax.ShapeDtypeStruct((2, P_SIZE, P_SIZE), jnp.float32)
    return pl.pallas_call(
        group_pixel_body,
        out_shape=(shape, jax.ShapeDtypeStruct((1, 1, 1, 1), jnp.float32)),
        in_specs=[vmem] * 7,
        out_specs=(vmem, vmem),
    )(comp, *got, *tables)


def pixels(*parts, token=False):
    freq = np.arange(B, dtype=np.int64) - B // 2
    pixel = np.arange(P_SIZE, dtype=np.int64)
    angle = (2.0 * math.pi / P_SIZE) * np.mod(freq[:, None] * pixel[None, :], P_SIZE).astype(np.float64)
    c_re = np.cos(angle)
    c_im = -np.sin(angle)
    a_hi, a_mid, a_lo = table_three(np.concatenate([c_re.T, c_im.T], axis=1))
    left = np.concatenate([a_hi, a_hi, a_mid, a_hi, a_lo, a_mid], axis=1)
    tables = [jnp.asarray(c_re, jnp.float32), jnp.asarray(c_im, jnp.float32), jnp.asarray(left)]
    vmem = pl.BlockSpec(memory_space=pltpu.VMEM)
    shape = jax.ShapeDtypeStruct((parts[0].shape[0], P_SIZE, P_SIZE), jnp.float32)
    if not token:
        return pl.pallas_call(
            functools.partial(pixel_body, passes=False),
            out_shape=shape,
            in_specs=[vmem] * (len(parts) + 3),
            out_specs=vmem,
        )(*parts, *tables)
    return pl.pallas_call(
        functools.partial(pixel_body, passes=True),
        out_shape=(shape, jax.ShapeDtypeStruct((1, 1, 1, 1), jnp.float32)),
        in_specs=[vmem] * (len(parts) + 3),
        out_specs=(vmem, vmem),
    )(*parts, *tables)


def xor_partners(count):
    return count & (count - 1) == 0 and count <= 8


def gather_all(x, axis, count, pos):
    if not xor_partners(count):
        return lax.all_gather(x, axis, axis=0, tiled=True)
    size = x.shape[0]
    slot = jnp.arange(count * size, dtype=jnp.int32) // size
    total = jnp.where((slot == pos)[:, None, None, None], jnp.tile(x, (count, 1, 1, 1)), 0.0)
    for step in range(1, count):
        got = lax.ppermute(x, axis, [(i, i ^ step) for i in range(count)])
        hit = (slot == (pos ^ step))[:, None, None, None]
        total = total + jnp.where(hit, jnp.tile(got, (count, 1, 1, 1)), 0.0)
    return total


def sum_all(x, axis, count, pos):
    if not xor_partners(count):
        return lax.psum(x, axis)
    step = 1
    while step < count:
        x = x + lax.ppermute(x, axis, [(i, i ^ step) for i in range(count)])
        step *= 2
    return x


def sum_parts(x, axis, count, pos):
    if count == 2:
        return (x, lax.ppermute(x, axis, [(0, 1), (1, 0)]))
    return (sum_all(x, axis, count, pos),)


def scatter_sum(x, axis, count, pos, size):
    if not xor_partners(count):
        return lax.psum_scatter(x, axis, scatter_dimension=0, tiled=True)
    total = lax.dynamic_slice_in_dim(x, pos * size, size, 0)
    for step in range(1, count):
        part = lax.dynamic_slice_in_dim(x, (pos ^ step) * size, size, 0)
        total = total + lax.ppermute(part, axis, [(i, i ^ step) for i in range(count)])
    return total


def partner_lists(count, kern_count):
    lists = [[] for _ in range(kern_count)]
    for step in range(1, count):
        lists[step % kern_count].append(step)
    return lists


def chosen_step(lists, round_index, kern_pos):
    pick = jnp.int32(-1)
    for k, steps in enumerate(lists):
        if round_index < len(steps):
            pick = jnp.where(kern_pos == k, jnp.int32(steps[round_index]), pick)
    return pick


def gather_split(x, count, pos, kern_count, kern_pos):
    size = x.shape[0]
    lists = partner_lists(count, kern_count)
    slot = jnp.arange(count * size, dtype=jnp.int32) // size
    spread = lambda part: jnp.tile(part, (count, 1, 1, 1))
    collected = jnp.zeros((count * size,) + x.shape[1:], x.dtype)
    for r in range(max(len(steps) for steps in lists)):
        pairs = []
        for k, steps in enumerate(lists):
            if r < len(steps):
                pairs += [((t ^ steps[r]) * kern_count + k, t * kern_count + k) for t in range(count)]
        got = lax.ppermute(x, ("tile", "kern"), pairs)
        step = chosen_step(lists, r, kern_pos)
        source = jnp.where(step >= 0, pos ^ step, -1)
        collected = collected + jnp.where((slot == source)[:, None, None, None], spread(got), 0.0)
    return sum_parts(collected, "kern", kern_count, kern_pos)


def scatter_split(x, count, pos, kern_count, kern_pos, size, between):
    lists = partner_lists(count, kern_count)
    own = lax.dynamic_slice_in_dim(x, pos * size, size, 0)
    total = jnp.where(kern_pos == 0, own, 0.0)
    for r in range(max(len(steps) for steps in lists)):
        pairs = []
        for k, steps in enumerate(lists):
            if r < len(steps):
                pairs += [(t * kern_count + k, (t ^ steps[r]) * kern_count + k) for t in range(count)]
        step = chosen_step(lists, r, kern_pos)
        target = jnp.where(step >= 0, pos ^ step, 0)
        part = lax.dynamic_slice_in_dim(x, target * size, size, 0)
        total = total + lax.ppermute(part, ("tile", "kern"), pairs)
    done, token = between()
    total = total + 0.0 * token
    return done, sum_parts(total, "kern", kern_count, kern_pos)


def on_device(
    tile_mask, master_mask, target, inst_master, inst_shift, kernels, kernel_weight, corner_dose
):
    cos_tab, sin_tab = band_tables()
    scale = 1.0 / (P_SIZE * P_SIZE)
    local_tiles = tile_mask.shape[0]
    local_masters = master_mask.shape[0]
    tile_count = lax.axis_size("tile")
    tile_pos = lax.axis_index("tile")
    kern_count = lax.axis_size("kern")
    kern_pos = lax.axis_index("kern")
    per_dev = local_tiles // kern_count
    first = kern_pos * per_dev
    region_tiles = tile_count * local_tiles
    region_masters = tile_count * local_masters

    with jax.named_scope("master_spectra"):
        own_re, own_im = spectra(master_mask.astype(jnp.float32), cos_tab, sin_tab)
        own = jnp.stack([own_re, own_im], axis=1)
        if xor_partners(tile_count) and xor_partners(kern_count) and tile_count > 2:
            every = gather_split(own, tile_count, tile_pos, kern_count, kern_pos)
            own_part = own
        else:
            every = (gather_all(own, "tile", tile_count, tile_pos),)
            own_part = jnp.zeros_like(own)

    dose = corner_dose[0]
    kerns = kernels[0]
    h_re = kerns[:, 0]
    h_im = kerns[:, 1]
    weights = kernel_weight[0]

    with jax.named_scope("imaging_kernel"):
        count = h_re.shape[0]
        twice = (2.0 * weights)[:, None, None]
        ht_re = jnp.swapaxes(h_re, 1, 2) * twice
        ht_im = jnp.swapaxes(h_im, 1, 2) * twice
        h_cat = jnp.concatenate([ht_re, ht_re, ht_im, -ht_im], axis=-1).reshape(count * B, 128)
        parts = []
        for j in range(per_dev):
            pos = jnp.stack([first + j, tile_pos]).astype(jnp.int32)
            parts.append(
                imaging(
                    pos, inst_master, inst_shift, weights, corner_dose, tile_mask, every, own_part, target,
                    kerns, h_cat,
                )
            )
        comp = jnp.stack(parts)

    with jax.named_scope("gradient_exchange"):
        corner_count = lax.axis_size("corner")
        corner_pos = lax.axis_index("corner")
        if corner_count == 2 and kern_count == 2 and per_dev == 1:
            got = [
                lax.ppermute(comp, ("corner", "kern"), [(i, i ^ step) for i in range(4)])
                for step in (1, 2, 3)
            ]
            mine = comp + got[1]
            other = got[0] + got[2]
            both = jnp.where(kern_pos == 0, jnp.concatenate([mine, other]), jnp.concatenate([other, mine]))
            tile_pixels = lambda: group_pixels(comp, got)
        else:
            comp = sum_all(comp, "corner", corner_count, corner_pos)
            both = gather_all(comp, "kern", kern_count, kern_pos)
            tile_pixels = lambda: pixels(both[:, 0:2], token=True)
        mine_tiles = both[:, 0:2]
        owner_pick = (
            inst_master[:, None] == jnp.arange(region_masters, dtype=jnp.int32)[None, :]
        ).astype(jnp.float32)
        if corner_count == 2 and kern_count == 2 and per_dev == 1:
            pick_mine = jnp.where(kern_pos == 0, owner_pick[0], owner_pick[1])
            pick_other = jnp.where(kern_pos == 0, owner_pick[1], owner_pick[0])
            terms = (
                pick_mine[:, None, None, None] * (comp[0, 2:4] + got[1][0, 2:4])[None]
                + pick_other[:, None, None, None] * (got[0][0, 2:4] + got[2][0, 2:4])[None]
            )
        else:
            terms = jnp.sum(owner_pick[:, :, None, None, None] * both[:, None, 2:4], axis=0)
        if xor_partners(tile_count) and xor_partners(kern_count) and tile_count > 2:
            tile_grad, mine_masters = scatter_split(
                terms, tile_count, tile_pos, kern_count, kern_pos, local_masters,
                tile_pixels,
            )
        else:
            tile_grad = pixels(mine_tiles)
            mine_masters = (scatter_sum(terms, "tile", tile_count, tile_pos, local_masters),)

    with jax.named_scope("pixel_gradients"):
        master_grad = pixels(*mine_masters)
    return (tile_grad, master_grad)


def solution(mesh):
    return jax.shard_map(
        on_device,
        mesh=mesh,
        in_specs=(
            P(("region", "tile"), None, None),
            P(("region", "tile"), None, None),
            P(("region", "tile"), None, None),
            P(("region", "tile")),
            P(("region", "tile"), None),
            P("corner", None, None, None, None),
            P("corner", None),
            P("corner"),
        ),
        out_specs=(P(("region", "tile"), None, None), P(("region", "tile"), None, None)),
        check_vma=False,
    )
```
